256 devices in a mesh: gx: 16 (over y, x), gy: 16 (over z, core).
Axes of the slice: x: 4, y: 4, z: 8, core: 2. Of those that a mesh axis runs over, the one named last changes fastest.
Arguments:
- state: float32 [6, 256, 49152], P(None, 'gx', 'gy'), as said below
- shock_height: float32 [256, 32], P('gx'), may hold values from 0.9 to 1.1
- wall_segment: int32 [256], P('gx'), may hold values from 0 to 15, never falling along the last dimension, each value on 1 to 32 neighbouring positions
- segment_level: int32 [16], replicated, may hold values from 0 to 15
- blow_table: float32 [16, 32], replicated, may hold values from 0.1 to 1.5
Outputs:
- state_new: float32 [6, 256, 49152], P(None, 'gx', 'gy')
- shock_new: float32 [256, 32], P('gx')
The draws below stay inside these ranges and needn't reach their ends.
Inputs may be any that keep to these rules, and one draw needn't show every extreme that they name: `state`: each cell has density in [0.5, 2], p / density in [0.6, 2.5], q5 / density in [0.05, 0.6], u in [0, 2], v and w in [-1, 1]. `wall_segment`: segment numbers never fall along the stream; each segment covers 1 to 32 cells.
All inputs are finite; a program needn't handle non-finite values.
Results may differ from the reference program's by a relative error of at most 0.00002.
Values sent between devices are 32-bit elements; how exact they have to be, the bound alone decides.
No kernel may reach another device: no remote copies, remote signals or barrier semaphores. Data moves between devices by JAX's collectives and lax.ppermute only.
A program may use at most 64 MiB of HBM per device.

```python
import math
import jax
import jax.numpy as jnp
import numpy as np
from jax import lax

CX = 16
NZ = 32
NLEV = 16
SEG_MOST = 32
NX = 256
NY = 1536
NSEG = 16
N_GX = 16


def draw_state(key, part):
    noise_child_seeds = jax.random.split(key, 6)
    processor_arrangement = (NX, NY * NZ)
    specific_volume_inverse = 0.5 * jnp.exp(jax.random.uniform(noise_child_seeds[0], processor_arrangement, jnp.float32, 0.0, math.log(4.0)))
    streamwise_flow_speed = 1.0 + jnp.clip(0.4 * jax.random.normal(noise_child_seeds[1], processor_arrangement, jnp.float32), -1.0, 1.0)
    normal_flow_speed = jnp.clip(0.4 * jax.random.normal(noise_child_seeds[2], processor_arrangement, jnp.float32), -1.0, 1.0)
    crosswise_flow_speed = jnp.clip(0.4 * jax.random.normal(noise_child_seeds[3], processor_arrangement, jnp.float32), -1.0, 1.0)
    heavy_particle_kelvin = 0.6 * jnp.exp(jax.random.uniform(noise_child_seeds[4], processor_arrangement, jnp.float32, 0.0, math.log(2.5 / 0.6)))
    oscillator_share = 0.05 * jnp.exp(jax.random.uniform(noise_child_seeds[5], processor_arrangement, jnp.float32, 0.0, math.log(12.0)))
    stagnation_enthalpy_sum = specific_volume_inverse * heavy_particle_kelvin / 0.4 + 0.5 * specific_volume_inverse * (streamwise_flow_speed * streamwise_flow_speed + normal_flow_speed * normal_flow_speed + crosswise_flow_speed * crosswise_flow_speed) + specific_volume_inverse * oscillator_share
    return jnp.stack([specific_volume_inverse, specific_volume_inverse * streamwise_flow_speed, specific_volume_inverse * normal_flow_speed, specific_volume_inverse * crosswise_flow_speed, stagnation_enthalpy_sum, specific_volume_inverse * oscillator_share]).astype(jnp.float32)


def with_ends(values, own_key, smallest, top_value):
    longest = values.shape.index(max(values.shape))
    spots = []
    for shift in (0, 1):
        where = [jax.random.randint(jax.random.fold_in(own_key, axis), (), 0, length) for axis, length in enumerate(values.shape)]
        where[longest] = (where[longest] + shift) % values.shape[longest]
        spots.append(tuple(where))
    return values.at[spots[0]].set(smallest).at[spots[1]].set(top_value)


def block_scale(own_key, dims, cuts, least, high):
    gain = 1.0
    for dim, blocks in cuts:
        heights = jax.random.uniform(jax.random.fold_in(jax.random.fold_in(own_key, 6), dim), (blocks,), jnp.float32, least / len(cuts), high / len(cuts))
        gain = gain * jnp.repeat(jnp.exp(heights), dims[dim] // blocks).reshape((-1,) + (1,) * (len(dims) - 1 - dim))
    return gain


def split_up(count, total, most, lean):
    portions = [(1 << 20) // math.isqrt(rank ** lean) + 1 for rank in range(2, count + 1)]
    rest, holding = total - most - (count - 1), [1] * (count - 1)
    while rest > 0:
        candidates = [i for i in range(count - 1) if holding[i] < most]
        pool, budget = sum([portions[i] for i in candidates]), rest
        for i in candidates:
            extra = min(most - holding[i], max(1, budget * portions[i] // pool), rest)
            holding[i] = holding[i] + extra
            rest = rest - extra
    return np.array([most] + holding)


def uneven(rng, count, total, reach, lean):
    if count == 2:
        one = jax.random.randint(rng, (), max(1, total - reach), min(reach, total - 1) + 1)
        return jnp.stack([one, total - one])
    tallies = jnp.asarray(split_up(count, total, reach, lean), jnp.int32)
    twos = (count - 1) // 2
    giver, sink = tallies[1:1 + 2 * twos:2], tallies[2:2 + 2 * twos:2]
    room = jnp.minimum(giver - 1, reach - sink)
    moved = jax.random.randint(jax.random.fold_in(rng, 1), (twos,), 0, 1 << 20) % (room + 1)
    tallies = tallies.at[1:1 + 2 * twos:2].set(giver - moved).at[2:2 + 2 * twos:2].set(sink + moved)
    return tallies[jax.random.permutation(jax.random.fold_in(rng, 2), count)]


def setup_inputs(seed: int = 0) -> dict:
    seeds = jax.random.split(jax.random.key(seed), 6)
    state = draw_state(jax.random.fold_in(seeds[5], 71), 0)
    shock_height = jnp.clip(0.9 + 0.20000005 * jax.random.uniform(seeds[1], (NX, NZ), jnp.float32) ** block_scale(seeds[1], (NX, NZ), ((0, 16),), -0.2, 0.2), 0.9, 1.1)
    wall_segment = jnp.searchsorted(jnp.cumsum(uneven(seeds[2], NSEG, NX, SEG_MOST, 0)), jnp.arange(NX), side="right").astype(jnp.int32)
    segment_level = with_ends(jax.random.randint(seeds[3], (NSEG,), 0, NLEV), jax.random.fold_in(seeds[3], 1), 0, NLEV - 1).astype(jnp.int32)
    blow_table = jnp.clip(jax.random.uniform(seeds[4], (NLEV, NZ), jnp.float32, 0.1, 1.5), 0.1, 1.5)
    return dict(state=state, shock_height=shock_height, wall_segment=wall_segment, segment_level=segment_level, blow_table=blow_table)


HEAT_RATIO = 1.4
STREAM_STEP = 0.05
SPAN_STEP = 0.05
STRETCH_RATE = 2.0
CHARACTER_KELVIN = 3.0
WHITE_LAW_FACTOR = 1.0
LANDAU_TELLER = 0.002
FREE_PRESSURE = 0.1
FREE_MACH = 6.0
COURANT = 0.05

def zshift(values, offset, planes):
    length = values.shape[-1]
    plane_at = jnp.arange(length, dtype=jnp.int32) % planes
    if offset > 0:
        return jnp.where(plane_at >= offset, jnp.roll(values, offset, axis=-1), jnp.roll(values, offset - planes, axis=-1))
    return jnp.where(plane_at < planes + offset, jnp.roll(values, offset, axis=-1), jnp.roll(values, offset + planes, axis=-1))

def primitives(conserved):
    specific_volume_inverse = conserved[0]
    vel_x = conserved[1] / specific_volume_inverse
    vel_y = conserved[2] / specific_volume_inverse
    vel_z = conserved[3] / specific_volume_inverse
    thermodynamic_stress = (HEAT_RATIO - 1.0) * (conserved[4] - 0.5 * (conserved[1] * vel_x + conserved[2] * vel_y + conserved[3] * vel_z) - conserved[5])
    sound_speed = jnp.sqrt(HEAT_RATIO * thermodynamic_stress / specific_volume_inverse)
    return (specific_volume_inverse, vel_x, vel_y, vel_z, thermodynamic_stress, sound_speed)

def face_difference(plus_flux, minus_flux, cells, axis_at, stride):

    def window(values, offset):
        return lax.slice_in_dim(values, offset * stride, (offset + cells + 1) * stride, axis=axis_at)
    upwind = (2.0 * window(plus_flux, 0) - 13.0 * window(plus_flux, 1) + 47.0 * window(plus_flux, 2) + 27.0 * window(plus_flux, 3) - 3.0 * window(plus_flux, 4)) / 60.0
    downwind = (-3.0 * window(minus_flux, 1) + 27.0 * window(minus_flux, 2) + 47.0 * window(minus_flux, 3) - 13.0 * window(minus_flux, 4) + 2.0 * window(minus_flux, 5)) / 60.0
    face_sum = upwind + downwind
    return lax.slice_in_dim(face_sum, stride, (cells + 1) * stride, axis=axis_at) - lax.slice_in_dim(face_sum, 0, cells * stride, axis=axis_at)

def stretch(index_rows, total_rows):
    growth = jnp.exp(STRETCH_RATE * (index_rows + 0.5) / total_rows)
    denominator = math.exp(STRETCH_RATE) - 1.0
    return ((growth - 1.0) / denominator, STRETCH_RATE * growth / (total_rows * denominator))

def split_pair(fluxes, speeds, conserved):
    return (0.5 * (fluxes + speeds * conserved), 0.5 * (fluxes - speeds * conserved))

def stream_part(conserved_x, height_ext, spacing_rows, planes):
    columns = conserved_x.shape[1] - 6
    specific_volume_inverse, vel_x, vel_y, vel_z, thermodynamic_stress, sound_speed = primitives(conserved_x)
    metric = SPAN_STEP * jnp.tile(height_ext, (1, conserved_x.shape[2] // planes)) * spacing_rows[None, :]
    fluxes = jnp.stack([conserved_x[1], conserved_x[1] * vel_x + thermodynamic_stress, conserved_x[2] * vel_x, conserved_x[3] * vel_x, (conserved_x[4] + thermodynamic_stress) * vel_x, conserved_x[5] * vel_x]) * metric
    speeds = (jnp.abs(vel_x) + sound_speed) * metric
    plus_flux, minus_flux = split_pair(fluxes, speeds, conserved_x)
    return face_difference(plus_flux, minus_flux, columns, 1, 1)

def normal_part(conserved_y, slope_x, slope_z, shock_rate, eta_rows, planes):
    copies = conserved_y.shape[2] // planes
    row_count = copies - 6
    specific_volume_inverse, vel_x, vel_y, vel_z, thermodynamic_stress, sound_speed = primitives(conserved_y)
    face_area = STREAM_STEP * SPAN_STEP
    metric_x = -face_area * eta_rows[None, :] * jnp.tile(slope_x, (1, copies))
    metric_z = -face_area * eta_rows[None, :] * jnp.tile(slope_z, (1, copies))
    metric_t = -face_area * eta_rows[None, :] * jnp.tile(shock_rate, (1, copies))
    contra = metric_t + metric_x * vel_x + face_area * vel_y + metric_z * vel_z
    fluxes = jnp.stack([conserved_y[0] * contra, conserved_y[1] * contra + metric_x * thermodynamic_stress, conserved_y[2] * contra + face_area * thermodynamic_stress, conserved_y[3] * contra + metric_z * thermodynamic_stress, (conserved_y[4] + thermodynamic_stress) * contra - metric_t * thermodynamic_stress, conserved_y[5] * contra])
    speeds = jnp.abs(contra) + sound_speed * jnp.sqrt(metric_x * metric_x + face_area * face_area + metric_z * metric_z)
    plus_flux, minus_flux = split_pair(fluxes, speeds, conserved_y)
    return face_difference(plus_flux, minus_flux, row_count, 2, planes)

def span_part(conserved, height, spacing_rows, planes):
    specific_volume_inverse, vel_x, vel_y, vel_z, thermodynamic_stress, sound_speed = primitives(conserved)
    metric = STREAM_STEP * jnp.tile(height, (1, conserved.shape[2] // planes)) * spacing_rows[None, :]
    fluxes = jnp.stack([conserved[3], conserved[1] * vel_z, conserved[2] * vel_z, conserved[3] * vel_z + thermodynamic_stress, (conserved[4] + thermodynamic_stress) * vel_z, conserved[5] * vel_z]) * metric
    speeds = (jnp.abs(vel_z) + sound_speed) * metric
    plus_flux, minus_flux = split_pair(fluxes, speeds, conserved)
    upwind = (2.0 * zshift(plus_flux, 2, planes) - 13.0 * zshift(plus_flux, 1, planes) + 47.0 * plus_flux + 27.0 * zshift(plus_flux, -1, planes) - 3.0 * zshift(plus_flux, -2, planes)) / 60.0
    downwind = (-3.0 * zshift(minus_flux, 1, planes) + 27.0 * minus_flux + 47.0 * zshift(minus_flux, -1, planes) - 13.0 * zshift(minus_flux, -2, planes) + 2.0 * zshift(minus_flux, -3, planes)) / 60.0
    face_sum = upwind + downwind
    return face_sum - zshift(face_sum, 1, planes)

def relaxation(conserved):
    specific_volume_inverse, vel_x, vel_y, vel_z, thermodynamic_stress, sound_speed = primitives(conserved)
    heavy_particle_kelvin = thermodynamic_stress / specific_volume_inverse
    oscillator_balanced_share = CHARACTER_KELVIN / (jnp.exp(CHARACTER_KELVIN / heavy_particle_kelvin) - 1.0)
    landau_teller_source = thermodynamic_stress / (LANDAU_TELLER * jnp.exp(WHITE_LAW_FACTOR * jnp.exp(-jnp.log(heavy_particle_kelvin) / 3.0)))
    return specific_volume_inverse * (oscillator_balanced_share - conserved[5] / specific_volume_inverse) * landau_teller_source

def slopes(height_ext, planes):
    columns = height_ext.shape[0] - 6
    slope_x = (height_ext[1:columns + 1] - 8.0 * height_ext[2:columns + 2] + 8.0 * height_ext[4:columns + 4] - height_ext[5:columns + 5]) / (12.0 * STREAM_STEP)
    height = height_ext[3:columns + 3]
    slope_z = (zshift(height, 2, planes) - 8.0 * zshift(height, 1, planes) + 8.0 * zshift(height, -1, planes) - zshift(height, -2, planes)) / (12.0 * SPAN_STEP)
    return (slope_x, slope_z)

def shock_speed(top_row, slope_x, slope_z):
    specific_volume_inverse, vel_x, vel_y, vel_z, thermodynamic_stress, sound_speed = primitives(top_row)
    tilt_norm = jnp.sqrt(1.0 + slope_x * slope_x + slope_z * slope_z)
    normal = (vel_y - vel_x * slope_x - vel_z * slope_z) / tilt_norm
    sine_sq = slope_x * slope_x / (tilt_norm * tilt_norm)
    jump_pressure = FREE_PRESSURE * (1.0 + 2.0 * HEAT_RATIO / (HEAT_RATIO + 1.0) * (FREE_MACH * FREE_MACH * sine_sq - 1.0))
    return tilt_norm * (normal + (jump_pressure - thermodynamic_stress) / (specific_volume_inverse * sound_speed))

def wall_ghosts(first_rows, blowing, planes):
    mirror = jnp.concatenate([first_rows[..., 2 * planes:3 * planes], first_rows[..., planes:2 * planes], first_rows[..., 0:planes]], axis=-1)
    blown_y = 2.0 * jnp.tile(blowing, (1, 3)) - mirror[2]
    stagnation_enthalpy_sum = mirror[4] + 0.5 * (blown_y * blown_y - mirror[2] * mirror[2]) / mirror[0]
    return jnp.stack([mirror[0], mirror[1], blown_y, mirror[3], stagnation_enthalpy_sum, mirror[5]])

def advance(conserved, conserved_x, conserved_y, height_ext, slope_x, slope_z, shock_rate, first_row, total_rows, planes):
    columns = conserved.shape[1]
    row_count = conserved.shape[2] // planes
    local_rows = (first_row + jnp.arange(row_count, dtype=jnp.int32)).astype(jnp.float32)
    eta_local, spacing_local = stretch(local_rows, total_rows)
    spacing_rows = jnp.repeat(spacing_local, planes)
    outer_rows = (first_row - 3 + jnp.arange(row_count + 6, dtype=jnp.int32)).astype(jnp.float32)
    eta_outer = stretch(outer_rows, total_rows)[0]
    eta_rows = jnp.repeat(eta_outer, planes)
    height = height_ext[3:columns + 3]
    divergence = stream_part(conserved_x, height_ext, spacing_rows, planes) + normal_part(conserved_y, slope_x, slope_z, shock_rate, eta_rows, planes) + span_part(conserved, height, spacing_rows, planes)
    height_rows = jnp.tile(height, (1, row_count))
    rate_rows = jnp.tile(shock_rate, (1, row_count))
    volume = STREAM_STEP * SPAN_STEP * height_rows * spacing_rows[None, :]
    change = -divergence / volume - conserved * (rate_rows / height_rows)
    change = jnp.concatenate([change[:5], (change[5] + relaxation(conserved))[None]], axis=0)
    return conserved + COURANT / total_rows * change

def reference(state, shock_height, wall_segment, segment_level, blow_table):
    planes = NZ
    length = NY * NZ
    height_ext = jnp.pad(shock_height, ((3, 3), (0, 0)), mode='edge')
    slope_x, slope_z = slopes(height_ext, planes)
    shock_rate = shock_speed(state[:, :, length - planes:], slope_x, slope_z)
    shock_new = shock_height + COURANT / NY * shock_rate
    blowing = blow_table[segment_level[wall_segment]]
    padded = jnp.pad(state, ((0, 0), (3, 3), (0, 0)), mode='edge')
    zero_idx = jnp.zeros((), jnp.int32)

    def block_step(block_at, result):
        start_col = (block_at * CX).astype(jnp.int32)
        conserved_x = lax.dynamic_slice(padded, (zero_idx, start_col, zero_idx), (6, CX + 6, length))
        conserved = conserved_x[:, 3:CX + 3]
        ext_height = lax.dynamic_slice(height_ext, (start_col, zero_idx), (CX + 6, planes))
        block_sx = lax.dynamic_slice(slope_x, (start_col, zero_idx), (CX, planes))
        block_sz = lax.dynamic_slice(slope_z, (start_col, zero_idx), (CX, planes))
        block_rate = lax.dynamic_slice(shock_rate, (start_col, zero_idx), (CX, planes))
        block_blow = lax.dynamic_slice(blowing, (start_col, zero_idx), (CX, planes))
        conserved_y = jnp.concatenate([wall_ghosts(conserved[..., :3 * planes], block_blow, planes), conserved, jnp.tile(conserved[..., length - planes:], (1, 1, 3))], axis=2)
        updated = advance(conserved, conserved_x, conserved_y, ext_height, block_sx, block_sz, block_rate, 0, NY, planes)
        return lax.dynamic_update_slice(result, updated, (zero_idx, start_col, zero_idx))
    state_new = lax.fori_loop(0, N_GX, block_step, jnp.zeros_like(state))
    return (state_new, shock_new)
```

```python
import math

import jax
import jax.numpy as jnp
from jax import lax
from jax.sharding import PartitionSpec as P

HEAT_RATIO = 1.4
STREAM_STEP = 0.05
SPAN_STEP = 0.05
STRETCH_RATE = 2.0
CHARACTER_KELVIN = 3.0
WHITE_LAW_FACTOR = 1.0
LANDAU_TELLER = 0.002
FREE_PRESSURE = 0.1
FREE_MACH = 6.0
COURANT = 0.05


def padded(block, sides, width):
    for axis, dim in sides:
        count = lax.axis_size(axis)
        forward = [(i, i + 1) for i in range(count - 1)]
        backward = [(target, source) for source, target in forward]
        low = lax.ppermute(
            lax.slice_in_dim(block, block.shape[dim] - width, None, axis=dim), axis, forward
        )
        high = lax.ppermute(lax.slice_in_dim(block, 0, width, axis=dim), axis, backward)
        block = jnp.concatenate([low, block, high], axis=dim)
    return block


def broadcast(array, axis, root):
    count = lax.axis_size(axis)
    index = lax.axis_index(axis)
    holders = [root]
    while len(holders) < count:
        waiting = [i for i in range(count) if i not in holders]
        pairs = list(zip(holders, waiting))
        received = lax.ppermute(array, axis, pairs)
        targets = jnp.zeros((), jnp.bool_)
        for _, target in pairs:
            targets = targets | (index == target)
        array = jnp.where(targets, received, array)
        holders = holders + [target for _, target in pairs]
    return array


def zshift(values, offset, planes):
    length = values.shape[-1]
    plane_at = jnp.arange(length, dtype=jnp.int32) % planes
    if offset > 0:
        return jnp.where(
            plane_at >= offset,
            jnp.roll(values, offset, axis=-1),
            jnp.roll(values, offset - planes, axis=-1),
        )
    return jnp.where(
        plane_at < planes + offset,
        jnp.roll(values, offset, axis=-1),
        jnp.roll(values, offset + planes, axis=-1),
    )


def primitives(conserved):
    specific_volume_inverse = conserved[0]
    vel_x = conserved[1] / specific_volume_inverse
    vel_y = conserved[2] / specific_volume_inverse
    vel_z = conserved[3] / specific_volume_inverse
    thermodynamic_stress = (HEAT_RATIO - 1.0) * (
        conserved[4]
        - 0.5 * (conserved[1] * vel_x + conserved[2] * vel_y + conserved[3] * vel_z)
        - conserved[5]
    )
    sound_speed = jnp.sqrt(HEAT_RATIO * thermodynamic_stress / specific_volume_inverse)
    return (specific_volume_inverse, vel_x, vel_y, vel_z, thermodynamic_stress, sound_speed)


def face_difference(plus_flux, minus_flux, cells, axis_at, stride):

    def window(values, offset):
        return lax.slice_in_dim(
            values, offset * stride, (offset + cells + 1) * stride, axis=axis_at
        )

    upwind = (
        2.0 * window(plus_flux, 0)
        - 13.0 * window(plus_flux, 1)
        + 47.0 * window(plus_flux, 2)
        + 27.0 * window(plus_flux, 3)
        - 3.0 * window(plus_flux, 4)
    ) / 60.0
    downwind = (
        -3.0 * window(minus_flux, 1)
        + 27.0 * window(minus_flux, 2)
        + 47.0 * window(minus_flux, 3)
        - 13.0 * window(minus_flux, 4)
        + 2.0 * window(minus_flux, 5)
    ) / 60.0
    face_sum = upwind + downwind
    return lax.slice_in_dim(
        face_sum, stride, (cells + 1) * stride, axis=axis_at
    ) - lax.slice_in_dim(face_sum, 0, cells * stride, axis=axis_at)


def stretch(index_rows, total_rows):
    growth = jnp.exp(STRETCH_RATE * (index_rows + 0.5) / total_rows)
    denominator = math.exp(STRETCH_RATE) - 1.0
    return ((growth - 1.0) / denominator, STRETCH_RATE * growth / (total_rows * denominator))


def split_pair(fluxes, speeds, conserved):
    return (0.5 * (fluxes + speeds * conserved), 0.5 * (fluxes - speeds * conserved))


def stream_part(conserved_x, height_ext, spacing_rows, planes):
    columns = conserved_x.shape[1] - 6
    specific_volume_inverse, vel_x, vel_y, vel_z, thermodynamic_stress, sound_speed = primitives(
        conserved_x
    )
    metric = (
        SPAN_STEP
        * jnp.tile(height_ext, (1, conserved_x.shape[2] // planes))
        * spacing_rows[None, :]
    )
    fluxes = (
        jnp.stack(
            [
                conserved_x[1],
                conserved_x[1] * vel_x + thermodynamic_stress,
                conserved_x[2] * vel_x,
                conserved_x[3] * vel_x,
                (conserved_x[4] + thermodynamic_stress) * vel_x,
                conserved_x[5] * vel_x,
            ]
        )
        * metric
    )
    speeds = (jnp.abs(vel_x) + sound_speed) * metric
    plus_flux, minus_flux = split_pair(fluxes, speeds, conserved_x)
    return face_difference(plus_flux, minus_flux, columns, 1, 1)


def normal_part(conserved_y, slope_x, slope_z, shock_rate, eta_rows, planes):
    copies = conserved_y.shape[2] // planes
    row_count = copies - 6
    specific_volume_inverse, vel_x, vel_y, vel_z, thermodynamic_stress, sound_speed = primitives(
        conserved_y
    )
    face_area = STREAM_STEP * SPAN_STEP
    metric_x = -face_area * eta_rows[None, :] * jnp.tile(slope_x, (1, copies))
    metric_z = -face_area * eta_rows[None, :] * jnp.tile(slope_z, (1, copies))
    metric_t = -face_area * eta_rows[None, :] * jnp.tile(shock_rate, (1, copies))
    contra = metric_t + metric_x * vel_x + face_area * vel_y + metric_z * vel_z
    fluxes = jnp.stack(
        [
            conserved_y[0] * contra,
            conserved_y[1] * contra + metric_x * thermodynamic_stress,
            conserved_y[2] * contra + face_area * thermodynamic_stress,
            conserved_y[3] * contra + metric_z * thermodynamic_stress,
            (conserved_y[4] + thermodynamic_stress) * contra - metric_t * thermodynamic_stress,
            conserved_y[5] * contra,
        ]
    )
    speeds = jnp.abs(contra) + sound_speed * jnp.sqrt(
        metric_x * metric_x + face_area * face_area + metric_z * metric_z
    )
    plus_flux, minus_flux = split_pair(fluxes, speeds, conserved_y)
    return face_difference(plus_flux, minus_flux, row_count, 2, planes)


def span_part(conserved, height, spacing_rows, planes):
    specific_volume_inverse, vel_x, vel_y, vel_z, thermodynamic_stress, sound_speed = primitives(
        conserved
    )
    metric = (
        STREAM_STEP * jnp.tile(height, (1, conserved.shape[2] // planes)) * spacing_rows[None, :]
    )
    fluxes = (
        jnp.stack(
            [
                conserved[3],
                conserved[1] * vel_z,
                conserved[2] * vel_z,
                conserved[3] * vel_z + thermodynamic_stress,
                (conserved[4] + thermodynamic_stress) * vel_z,
                conserved[5] * vel_z,
            ]
        )
        * metric
    )
    speeds = (jnp.abs(vel_z) + sound_speed) * metric
    plus_flux, minus_flux = split_pair(fluxes, speeds, conserved)
    upwind = (
        2.0 * zshift(plus_flux, 2, planes)
        - 13.0 * zshift(plus_flux, 1, planes)
        + 47.0 * plus_flux
        + 27.0 * zshift(plus_flux, -1, planes)
        - 3.0 * zshift(plus_flux, -2, planes)
    ) / 60.0
    downwind = (
        -3.0 * zshift(minus_flux, 1, planes)
        + 27.0 * minus_flux
        + 47.0 * zshift(minus_flux, -1, planes)
        - 13.0 * zshift(minus_flux, -2, planes)
        + 2.0 * zshift(minus_flux, -3, planes)
    ) / 60.0
    face_sum = upwind + downwind
    return face_sum - zshift(face_sum, 1, planes)


def relaxation(conserved):
    specific_volume_inverse, vel_x, vel_y, vel_z, thermodynamic_stress, sound_speed = primitives(
        conserved
    )
    heavy_particle_kelvin = thermodynamic_stress / specific_volume_inverse
    oscillator_balanced_share = CHARACTER_KELVIN / (
        jnp.exp(CHARACTER_KELVIN / heavy_particle_kelvin) - 1.0
    )
    landau_teller_source = thermodynamic_stress / (
        LANDAU_TELLER * jnp.exp(WHITE_LAW_FACTOR * jnp.exp(-jnp.log(heavy_particle_kelvin) / 3.0))
    )
    return (
        specific_volume_inverse
        * (oscillator_balanced_share - conserved[5] / specific_volume_inverse)
        * landau_teller_source
    )


def slopes(height_ext, planes):
    columns = height_ext.shape[0] - 6
    slope_x = (
        height_ext[1 : columns + 1]
        - 8.0 * height_ext[2 : columns + 2]
        + 8.0 * height_ext[4 : columns + 4]
        - height_ext[5 : columns + 5]
    ) / (12.0 * STREAM_STEP)
    height = height_ext[3 : columns + 3]
    slope_z = (
        zshift(height, 2, planes)
        - 8.0 * zshift(height, 1, planes)
        + 8.0 * zshift(height, -1, planes)
        - zshift(height, -2, planes)
    ) / (12.0 * SPAN_STEP)
    return (slope_x, slope_z)


def shock_speed(top_row, slope_x, slope_z):
    specific_volume_inverse, vel_x, vel_y, vel_z, thermodynamic_stress, sound_speed = primitives(
        top_row
    )
    tilt_norm = jnp.sqrt(1.0 + slope_x * slope_x + slope_z * slope_z)
    normal = (vel_y - vel_x * slope_x - vel_z * slope_z) / tilt_norm
    sine_sq = slope_x * slope_x / (tilt_norm * tilt_norm)
    jump_pressure = FREE_PRESSURE * (
        1.0 + 2.0 * HEAT_RATIO / (HEAT_RATIO + 1.0) * (FREE_MACH * FREE_MACH * sine_sq - 1.0)
    )
    return tilt_norm * (
        normal + (jump_pressure - thermodynamic_stress) / (specific_volume_inverse * sound_speed)
    )


def wall_ghosts(first_rows, blowing, planes):
    mirror = jnp.concatenate(
        [
            first_rows[..., 2 * planes : 3 * planes],
            first_rows[..., planes : 2 * planes],
            first_rows[..., 0:planes],
        ],
        axis=-1,
    )
    blown_y = 2.0 * jnp.tile(blowing, (1, 3)) - mirror[2]
    stagnation_enthalpy_sum = (
        mirror[4] + 0.5 * (blown_y * blown_y - mirror[2] * mirror[2]) / mirror[0]
    )
    return jnp.stack([mirror[0], mirror[1], blown_y, mirror[3], stagnation_enthalpy_sum, mirror[5]])


def advance(
    conserved,
    conserved_x,
    conserved_y,
    height_ext,
    slope_x,
    slope_z,
    shock_rate,
    first_row,
    total_rows,
    planes,
):
    columns = conserved.shape[1]
    row_count = conserved.shape[2] // planes
    local_rows = (first_row + jnp.arange(row_count, dtype=jnp.int32)).astype(jnp.float32)
    eta_local, spacing_local = stretch(local_rows, total_rows)
    spacing_rows = jnp.repeat(spacing_local, planes)
    outer_rows = (first_row - 3 + jnp.arange(row_count + 6, dtype=jnp.int32)).astype(jnp.float32)
    eta_outer = stretch(outer_rows, total_rows)[0]
    eta_rows = jnp.repeat(eta_outer, planes)
    height = height_ext[3 : columns + 3]
    divergence = (
        stream_part(conserved_x, height_ext, spacing_rows, planes)
        + normal_part(conserved_y, slope_x, slope_z, shock_rate, eta_rows, planes)
        + span_part(conserved, height, spacing_rows, planes)
    )
    height_rows = jnp.tile(height, (1, row_count))
    rate_rows = jnp.tile(shock_rate, (1, row_count))
    volume = STREAM_STEP * SPAN_STEP * height_rows * spacing_rows[None, :]
    change = -divergence / volume - conserved * (rate_rows / height_rows)
    change = jnp.concatenate([change[:5], (change[5] + relaxation(conserved))[None]], axis=0)
    return conserved + COURANT / total_rows * change


def edge_fill(values, axis_at, cells, device_at, devices):
    positions = jnp.arange(cells + 6, dtype=jnp.int32)
    processor_arrangement = [1] * values.ndim
    processor_arrangement[axis_at] = cells + 6
    positions = positions.reshape(processor_arrangement)
    leading = lax.slice_in_dim(values, 3, 4, axis=axis_at)
    trailing = lax.slice_in_dim(values, cells + 2, cells + 3, axis=axis_at)
    values = jnp.where((device_at == 0) & (positions < 3), leading, values)
    return jnp.where((device_at == devices - 1) & (positions >= cells + 3), trailing, values)


def wall_flux(wall_segment, segment_level, blow_table):
    seg_hit = wall_segment[:, None] == jnp.arange(segment_level.shape[0], dtype=jnp.int32)[None, :]
    levels = jnp.sum(jnp.where(seg_hit, segment_level[None, :], 0), axis=1)
    level_hit = levels[:, None] == jnp.arange(blow_table.shape[0], dtype=jnp.int32)[None, :]
    return jnp.sum(jnp.where(level_hit[:, :, None], blow_table[None, :, :], 0.0), axis=1)


def shards(state, shock_height, wall_segment, segment_level, blow_table):
    planes = blow_table.shape[1]
    columns = state.shape[1]
    length = state.shape[2]
    row_count = length // planes
    col_devs = lax.axis_size("gx")
    row_devs = lax.axis_size("gy")
    col_dev = lax.axis_index("gx")
    row_dev = lax.axis_index("gy")
    total_rows = row_count * row_devs
    conserved_x = padded(state, (("gx", 1),), 3)
    height_ext = padded(shock_height, (("gx", 0),), 3)
    conserved_x = edge_fill(conserved_x, 1, columns, col_dev, col_devs)
    height_ext = edge_fill(height_ext, 0, columns, col_dev, col_devs)
    slope_x, slope_z = slopes(height_ext, planes)
    top_row = broadcast(state[:, :, length - planes :], "gy", row_devs - 1)
    shock_rate = shock_speed(top_row, slope_x, slope_z)
    blowing = wall_flux(wall_segment, segment_level, blow_table)
    halo_y = padded(state, (("gy", 2),), 3 * planes)
    ghost_below = jnp.where(
        row_dev == 0,
        wall_ghosts(state[..., : 3 * planes], blowing, planes),
        halo_y[..., : 3 * planes],
    )
    ghost_above = jnp.where(
        row_dev == row_devs - 1,
        jnp.tile(state[..., length - planes :], (1, 1, 3)),
        halo_y[..., length + 3 * planes :],
    )
    conserved_y = jnp.concatenate([ghost_below, state, ghost_above], axis=2)
    state_new = advance(
        state,
        conserved_x,
        conserved_y,
        height_ext,
        slope_x,
        slope_z,
        shock_rate,
        row_dev * row_count,
        total_rows,
        planes,
    )
    shock_new = shock_height + COURANT / total_rows * shock_rate
    return (state_new, shock_new)


def solution(mesh):
    in_specs = (P(None, "gx", "gy"), P("gx", None), P("gx"), P(), P())
    out_specs = (P(None, "gx", "gy"), P("gx", None))
    return jax.shard_map(shards, mesh=mesh, in_specs=in_specs, out_specs=out_specs, check_vma=False)
```

```python
import math

import jax
import jax.numpy as jnp
from jax import lax
from jax.experimental import pallas as pl
from jax.experimental.pallas import tpu as pltpu
from jax.sharding import PartitionSpec as P

HEAT_RATIO = 1.4
STREAM_STEP = 0.05
SPAN_STEP = 0.05
STRETCH_RATE = 2.0
CHARACTER_KELVIN = 3.0
WHITE_LAW_FACTOR = 1.0
LANDAU_TELLER = 0.002
FREE_PRESSURE = 0.1
FREE_MACH = 6.0
COURANT = 0.05


PLUS_WEIGHTS = (-2.0, 15.0, -60.0, 20.0, 30.0, -3.0, 0.0)
MINUS_WEIGHTS = (0.0, 3.0, -30.0, -20.0, 60.0, -15.0, 2.0)
CHUNK = 256
PAD = 128


def kernel_primitives(q):
    inverse = 1.0 / q[0]
    vel_x = q[1] * inverse
    vel_y = q[2] * inverse
    vel_z = q[3] * inverse
    stress = (HEAT_RATIO - 1.0) * (q[4] - 0.5 * (q[1] * vel_x + q[2] * vel_y + q[3] * vel_z) - q[5])
    sound = jnp.sqrt(HEAT_RATIO * stress * inverse)
    return inverse, vel_x, vel_y, vel_z, stress, sound


def combined(plus, minus, t):
    a = PLUS_WEIGHTS[t + 3]
    b = MINUS_WEIGHTS[t + 3]
    if a == 0.0:
        return b * minus
    if b == 0.0:
        return a * plus
    return a * plus + b * minus


def make_kernel(columns, length, planes, dt):
    width = CHUNK + 2 * PAD
    face_area = STREAM_STEP * SPAN_STEP

    def kernel(qx_ref, qy_ref, hx_ref, hz_ref, sx_ref, sz_ref, rt_ref, rh_ref, s_ref, eta_ref,
               out_ref, px_ref, mx_ref):
        lane = lax.broadcasted_iota(jnp.int32, (columns, CHUNK), 1) % planes

        def body(k, carry):
            o = pl.multiple_of(k * CHUNK, CHUNK)
            spacing = s_ref[:, pl.ds(o, CHUNK)]
            xa = [qx_ref[c, :, pl.ds(o, CHUNK)] for c in range(6)]
            inverse, vel_x, vel_y, vel_z, stress, sound = kernel_primitives(xa)
            metric = STREAM_STEP * hx_ref[...] * spacing
            fluxes = [xa[1], xa[1] * vel_x + stress, xa[2] * vel_x, xa[3] * vel_x,
                      (xa[4] + stress) * vel_x, xa[5] * vel_x]
            speed = (jnp.abs(vel_x) + sound) * metric
            for c in range(6):
                f = fluxes[c] * metric
                px_ref[c] = 0.5 * (f + speed * xa[c])
                mx_ref[c] = 0.5 * (f - speed * xa[c])
            div = []
            for c in range(6):
                acc = None
                for t in range(-3, 4):
                    term = None
                    a = PLUS_WEIGHTS[t + 3]
                    b = MINUS_WEIGHTS[t + 3]
                    if a != 0.0:
                        term = a * px_ref[c, pl.ds(t + 3, columns), :]
                    if b != 0.0:
                        mterm = b * mx_ref[c, pl.ds(t + 3, columns), :]
                        term = mterm if term is None else term + mterm
                    acc = term if acc is None else acc + term
                div.append(acc)
            ya = [qy_ref[c, :, pl.ds(o, width)] for c in range(6)]
            inverse, vel_x, vel_y, vel_z, stress, sound = kernel_primitives(ya)
            eta = eta_ref[:, pl.ds(o, width)]
            scaled = -face_area * eta
            metric_x = scaled * sx_ref[...]
            metric_z = scaled * sz_ref[...]
            metric_t = scaled * rt_ref[...]
            contra = metric_t + metric_x * vel_x + face_area * vel_y + metric_z * vel_z
            fluxes = [ya[0] * contra, ya[1] * contra + metric_x * stress,
                      ya[2] * contra + face_area * stress, ya[3] * contra + metric_z * stress,
                      (ya[4] + stress) * contra - metric_t * stress, ya[5] * contra]
            speed = jnp.abs(contra) + sound * jnp.sqrt(
                metric_x * metric_x + face_area * face_area + metric_z * metric_z)
            for c in range(6):
                plus = 0.5 * (fluxes[c] + speed * ya[c])
                minus = 0.5 * (fluxes[c] - speed * ya[c])
                acc = None
                for t in range(-3, 4):
                    term = combined(plus, minus, t)
                    if t != 0:
                        term = pltpu.roll(term, (-planes * t) % width, 1)
                    acc = term if acc is None else acc + term
                div[c] = div[c] + acc[:, PAD:PAD + CHUNK]
            q = [v[:, PAD:PAD + CHUNK] for v in ya]
            inverse = inverse[:, PAD:PAD + CHUNK]
            vel_x = vel_x[:, PAD:PAD + CHUNK]
            vel_z = vel_z[:, PAD:PAD + CHUNK]
            stress = stress[:, PAD:PAD + CHUNK]
            sound = sound[:, PAD:PAD + CHUNK]
            height = hz_ref[...]
            metric = STREAM_STEP * height * spacing
            fluxes = [q[3], q[1] * vel_z, q[2] * vel_z, q[3] * vel_z + stress,
                      (q[4] + stress) * vel_z, q[5] * vel_z]
            speed = (jnp.abs(vel_z) + sound) * metric
            for c in range(6):
                f = fluxes[c] * metric
                plus = 0.5 * (f + speed * q[c])
                minus = 0.5 * (f - speed * q[c])
                acc = None
                for t in range(-3, 4):
                    term = combined(plus, minus, t)
                    if t > 0:
                        term = jnp.where(lane < planes - t, pltpu.roll(term, CHUNK - t, 1),
                                         pltpu.roll(term, planes - t, 1))
                    elif t < 0:
                        term = jnp.where(lane >= -t, pltpu.roll(term, -t, 1),
                                         pltpu.roll(term, (CHUNK - planes - t) % CHUNK, 1))
                    acc = term if acc is None else acc + term
                div[c] = div[c] + acc
            kelvin = stress * inverse
            balanced = CHARACTER_KELVIN / (jnp.exp(CHARACTER_KELVIN / kelvin) - 1.0)
            teller = stress / (LANDAU_TELLER * jnp.exp(
                WHITE_LAW_FACTOR * jnp.exp(-jnp.log(kelvin) / 3.0)))
            source = q[0] * (balanced - q[5] * inverse) * teller
            volume = face_area * height * spacing
            ratio = rh_ref[...]
            for c in range(6):
                change = -(div[c] * (1.0 / 60.0)) / volume - q[c] * ratio
                if c == 5:
                    change = change + source
                out_ref[c, :, pl.ds(o, CHUNK)] = q[c] + dt * change
            return carry

        lax.fori_loop(0, length // CHUNK, body, 0)

    return kernel


def update(qx, qy, hx, hz, sx, sz, rt, rh, s_lane, eta_lane, planes, dt, interpret=False):
    columns = hz.shape[0]
    length = s_lane.shape[1]
    kern = make_kernel(columns, length, planes, dt)
    rows_x = qx.shape[1]
    return pl.pallas_call(
        kern,
        out_shape=jax.ShapeDtypeStruct((6, columns, length), jnp.float32),
        scratch_shapes=[pltpu.VMEM((6, rows_x, CHUNK), jnp.float32),
                        pltpu.VMEM((6, rows_x, CHUNK), jnp.float32)],
        interpret=interpret,
    )(qx, qy, hx, hz, sx, sz, rt, rh, s_lane, eta_lane)


def padded(block, sides, width):
    for axis, dim in sides:
        count = lax.axis_size(axis)
        forward = [(i, i + 1) for i in range(count - 1)]
        backward = [(target, source) for source, target in forward]
        low = lax.ppermute(
            lax.slice_in_dim(block, block.shape[dim] - width, None, axis=dim), axis, forward
        )
        high = lax.ppermute(lax.slice_in_dim(block, 0, width, axis=dim), axis, backward)
        block = jnp.concatenate([low, block, high], axis=dim)
    return block


def broadcast(array, axis, root):
    count = lax.axis_size(axis)
    index = lax.axis_index(axis)
    holders = [root]
    while len(holders) < count:
        waiting = [i for i in range(count) if i not in holders]
        pairs = list(zip(holders, waiting))
        received = lax.ppermute(array, axis, pairs)
        targets = jnp.zeros((), jnp.bool_)
        for _, target in pairs:
            targets = targets | (index == target)
        array = jnp.where(targets, received, array)
        holders = holders + [target for _, target in pairs]
    return array


def zshift(values, offset, planes):
    length = values.shape[-1]
    plane_at = jnp.arange(length, dtype=jnp.int32) % planes
    if offset > 0:
        return jnp.where(
            plane_at >= offset,
            jnp.roll(values, offset, axis=-1),
            jnp.roll(values, offset - planes, axis=-1),
        )
    return jnp.where(
        plane_at < planes + offset,
        jnp.roll(values, offset, axis=-1),
        jnp.roll(values, offset + planes, axis=-1),
    )


def primitives(conserved):
    specific_volume_inverse = conserved[0]
    vel_x = conserved[1] / specific_volume_inverse
    vel_y = conserved[2] / specific_volume_inverse
    vel_z = conserved[3] / specific_volume_inverse
    thermodynamic_stress = (HEAT_RATIO - 1.0) * (
        conserved[4]
        - 0.5 * (conserved[1] * vel_x + conserved[2] * vel_y + conserved[3] * vel_z)
        - conserved[5]
    )
    sound_speed = jnp.sqrt(HEAT_RATIO * thermodynamic_stress / specific_volume_inverse)
    return (specific_volume_inverse, vel_x, vel_y, vel_z, thermodynamic_stress, sound_speed)


def face_difference(plus_flux, minus_flux, cells, axis_at, stride):

    def window(values, offset):
        return lax.slice_in_dim(
            values, offset * stride, (offset + cells + 1) * stride, axis=axis_at
        )

    upwind = (
        2.0 * window(plus_flux, 0)
        - 13.0 * window(plus_flux, 1)
        + 47.0 * window(plus_flux, 2)
        + 27.0 * window(plus_flux, 3)
        - 3.0 * window(plus_flux, 4)
    ) / 60.0
    downwind = (
        -3.0 * window(minus_flux, 1)
        + 27.0 * window(minus_flux, 2)
        + 47.0 * window(minus_flux, 3)
        - 13.0 * window(minus_flux, 4)
        + 2.0 * window(minus_flux, 5)
    ) / 60.0
    face_sum = upwind + downwind
    return lax.slice_in_dim(
        face_sum, stride, (cells + 1) * stride, axis=axis_at
    ) - lax.slice_in_dim(face_sum, 0, cells * stride, axis=axis_at)


def stretch(index_rows, total_rows):
    growth = jnp.exp(STRETCH_RATE * (index_rows + 0.5) / total_rows)
    denominator = math.exp(STRETCH_RATE) - 1.0
    return ((growth - 1.0) / denominator, STRETCH_RATE * growth / (total_rows * denominator))


def split_pair(fluxes, speeds, conserved):
    return (0.5 * (fluxes + speeds * conserved), 0.5 * (fluxes - speeds * conserved))


def stream_part(conserved_x, height_ext, spacing_rows, planes):
    columns = conserved_x.shape[1] - 6
    specific_volume_inverse, vel_x, vel_y, vel_z, thermodynamic_stress, sound_speed = primitives(
        conserved_x
    )
    metric = (
        SPAN_STEP
        * jnp.tile(height_ext, (1, conserved_x.shape[2] // planes))
        * spacing_rows[None, :]
    )
    fluxes = (
        jnp.stack(
            [
                conserved_x[1],
                conserved_x[1] * vel_x + thermodynamic_stress,
                conserved_x[2] * vel_x,
                conserved_x[3] * vel_x,
                (conserved_x[4] + thermodynamic_stress) * vel_x,
                conserved_x[5] * vel_x,
            ]
        )
        * metric
    )
    speeds = (jnp.abs(vel_x) + sound_speed) * metric
    plus_flux, minus_flux = split_pair(fluxes, speeds, conserved_x)
    return face_difference(plus_flux, minus_flux, columns, 1, 1)


def normal_part(conserved_y, slope_x, slope_z, shock_rate, eta_rows, planes):
    copies = conserved_y.shape[2] // planes
    row_count = copies - 6
    specific_volume_inverse, vel_x, vel_y, vel_z, thermodynamic_stress, sound_speed = primitives(
        conserved_y
    )
    face_area = STREAM_STEP * SPAN_STEP
    metric_x = -face_area * eta_rows[None, :] * jnp.tile(slope_x, (1, copies))
    metric_z = -face_area * eta_rows[None, :] * jnp.tile(slope_z, (1, copies))
    metric_t = -face_area * eta_rows[None, :] * jnp.tile(shock_rate, (1, copies))
    contra = metric_t + metric_x * vel_x + face_area * vel_y + metric_z * vel_z
    fluxes = jnp.stack(
        [
            conserved_y[0] * contra,
            conserved_y[1] * contra + metric_x * thermodynamic_stress,
            conserved_y[2] * contra + face_area * thermodynamic_stress,
            conserved_y[3] * contra + metric_z * thermodynamic_stress,
            (conserved_y[4] + thermodynamic_stress) * contra - metric_t * thermodynamic_stress,
            conserved_y[5] * contra,
        ]
    )
    speeds = jnp.abs(contra) + sound_speed * jnp.sqrt(
        metric_x * metric_x + face_area * face_area + metric_z * metric_z
    )
    plus_flux, minus_flux = split_pair(fluxes, speeds, conserved_y)
    return face_difference(plus_flux, minus_flux, row_count, 2, planes)


def span_part(conserved, height, spacing_rows, planes):
    specific_volume_inverse, vel_x, vel_y, vel_z, thermodynamic_stress, sound_speed = primitives(
        conserved
    )
    metric = (
        STREAM_STEP * jnp.tile(height, (1, conserved.shape[2] // planes)) * spacing_rows[None, :]
    )
    fluxes = (
        jnp.stack(
            [
                conserved[3],
                conserved[1] * vel_z,
                conserved[2] * vel_z,
                conserved[3] * vel_z + thermodynamic_stress,
                (conserved[4] + thermodynamic_stress) * vel_z,
                conserved[5] * vel_z,
            ]
        )
        * metric
    )
    speeds = (jnp.abs(vel_z) + sound_speed) * metric
    plus_flux, minus_flux = split_pair(fluxes, speeds, conserved)
    upwind = (
        2.0 * zshift(plus_flux, 2, planes)
        - 13.0 * zshift(plus_flux, 1, planes)
        + 47.0 * plus_flux
        + 27.0 * zshift(plus_flux, -1, planes)
        - 3.0 * zshift(plus_flux, -2, planes)
    ) / 60.0
    downwind = (
        -3.0 * zshift(minus_flux, 1, planes)
        + 27.0 * minus_flux
        + 47.0 * zshift(minus_flux, -1, planes)
        - 13.0 * zshift(minus_flux, -2, planes)
        + 2.0 * zshift(minus_flux, -3, planes)
    ) / 60.0
    face_sum = upwind + downwind
    return face_sum - zshift(face_sum, 1, planes)


def relaxation(conserved):
    specific_volume_inverse, vel_x, vel_y, vel_z, thermodynamic_stress, sound_speed = primitives(
        conserved
    )
    heavy_particle_kelvin = thermodynamic_stress / specific_volume_inverse
    oscillator_balanced_share = CHARACTER_KELVIN / (
        jnp.exp(CHARACTER_KELVIN / heavy_particle_kelvin) - 1.0
    )
    landau_teller_source = thermodynamic_stress / (
        LANDAU_TELLER * jnp.exp(WHITE_LAW_FACTOR * jnp.exp(-jnp.log(heavy_particle_kelvin) / 3.0))
    )
    return (
        specific_volume_inverse
        * (oscillator_balanced_share - conserved[5] / specific_volume_inverse)
        * landau_teller_source
    )


def slopes(height_ext, planes):
    columns = height_ext.shape[0] - 6
    slope_x = (
        height_ext[1 : columns + 1]
        - 8.0 * height_ext[2 : columns + 2]
        + 8.0 * height_ext[4 : columns + 4]
        - height_ext[5 : columns + 5]
    ) / (12.0 * STREAM_STEP)
    height = height_ext[3 : columns + 3]
    slope_z = (
        zshift(height, 2, planes)
        - 8.0 * zshift(height, 1, planes)
        + 8.0 * zshift(height, -1, planes)
        - zshift(height, -2, planes)
    ) / (12.0 * SPAN_STEP)
    return (slope_x, slope_z)


def shock_speed(top_row, slope_x, slope_z):
    specific_volume_inverse, vel_x, vel_y, vel_z, thermodynamic_stress, sound_speed = primitives(
        top_row
    )
    tilt_norm = jnp.sqrt(1.0 + slope_x * slope_x + slope_z * slope_z)
    normal = (vel_y - vel_x * slope_x - vel_z * slope_z) / tilt_norm
    sine_sq = slope_x * slope_x / (tilt_norm * tilt_norm)
    jump_pressure = FREE_PRESSURE * (
        1.0 + 2.0 * HEAT_RATIO / (HEAT_RATIO + 1.0) * (FREE_MACH * FREE_MACH * sine_sq - 1.0)
    )
    return tilt_norm * (
        normal + (jump_pressure - thermodynamic_stress) / (specific_volume_inverse * sound_speed)
    )


def wall_ghosts(first_rows, blowing, planes):
    mirror = jnp.concatenate(
        [
            first_rows[..., 2 * planes : 3 * planes],
            first_rows[..., planes : 2 * planes],
            first_rows[..., 0:planes],
        ],
        axis=-1,
    )
    blown_y = 2.0 * jnp.tile(blowing, (1, 3)) - mirror[2]
    stagnation_enthalpy_sum = (
        mirror[4] + 0.5 * (blown_y * blown_y - mirror[2] * mirror[2]) / mirror[0]
    )
    return jnp.stack([mirror[0], mirror[1], blown_y, mirror[3], stagnation_enthalpy_sum, mirror[5]])


def advance(
    conserved,
    conserved_x,
    conserved_y,
    height_ext,
    slope_x,
    slope_z,
    shock_rate,
    first_row,
    total_rows,
    planes,
):
    columns = conserved.shape[1]
    row_count = conserved.shape[2] // planes
    local_rows = (first_row + jnp.arange(row_count, dtype=jnp.int32)).astype(jnp.float32)
    eta_local, spacing_local = stretch(local_rows, total_rows)
    spacing_rows = jnp.repeat(spacing_local, planes)
    outer_rows = (first_row - 3 + jnp.arange(row_count + 6, dtype=jnp.int32)).astype(jnp.float32)
    eta_outer = stretch(outer_rows, total_rows)[0]
    eta_rows = jnp.repeat(eta_outer, planes)
    height = height_ext[3 : columns + 3]
    divergence = (
        stream_part(conserved_x, height_ext, spacing_rows, planes)
        + normal_part(conserved_y, slope_x, slope_z, shock_rate, eta_rows, planes)
        + span_part(conserved, height, spacing_rows, planes)
    )
    height_rows = jnp.tile(height, (1, row_count))
    rate_rows = jnp.tile(shock_rate, (1, row_count))
    volume = STREAM_STEP * SPAN_STEP * height_rows * spacing_rows[None, :]
    change = -divergence / volume - conserved * (rate_rows / height_rows)
    change = jnp.concatenate([change[:5], (change[5] + relaxation(conserved))[None]], axis=0)
    return conserved + COURANT / total_rows * change


def edge_fill(values, axis_at, cells, device_at, devices):
    positions = jnp.arange(cells + 6, dtype=jnp.int32)
    processor_arrangement = [1] * values.ndim
    processor_arrangement[axis_at] = cells + 6
    positions = positions.reshape(processor_arrangement)
    leading = lax.slice_in_dim(values, 3, 4, axis=axis_at)
    trailing = lax.slice_in_dim(values, cells + 2, cells + 3, axis=axis_at)
    values = jnp.where((device_at == 0) & (positions < 3), leading, values)
    return jnp.where((device_at == devices - 1) & (positions >= cells + 3), trailing, values)


def wall_flux(wall_segment, segment_level, blow_table):
    seg_hit = wall_segment[:, None] == jnp.arange(segment_level.shape[0], dtype=jnp.int32)[None, :]
    levels = jnp.sum(jnp.where(seg_hit, segment_level[None, :], 0), axis=1)
    level_hit = levels[:, None] == jnp.arange(blow_table.shape[0], dtype=jnp.int32)[None, :]
    return jnp.sum(jnp.where(level_hit[:, :, None], blow_table[None, :, :], 0.0), axis=1)


def shards(state, shock_height, wall_segment, segment_level, blow_table):
    planes = blow_table.shape[1]
    columns = state.shape[1]
    length = state.shape[2]
    row_count = length // planes
    col_devs = lax.axis_size("gx")
    row_devs = lax.axis_size("gy")
    col_dev = lax.axis_index("gx")
    row_dev = lax.axis_index("gy")
    total_rows = row_count * row_devs
    conserved_x = padded(state, (("gx", 1),), 3)
    height_ext = padded(shock_height, (("gx", 0),), 3)
    conserved_x = edge_fill(conserved_x, 1, columns, col_dev, col_devs)
    height_ext = edge_fill(height_ext, 0, columns, col_dev, col_devs)
    slope_x, slope_z = slopes(height_ext, planes)
    top_row = broadcast(state[:, :, length - planes :], "gy", row_devs - 1)
    shock_rate = shock_speed(top_row, slope_x, slope_z)
    blowing = wall_flux(wall_segment, segment_level, blow_table)
    halo_y = padded(state, (("gy", 2),), 3 * planes)
    ghost_below = jnp.where(
        row_dev == 0,
        wall_ghosts(state[..., : 3 * planes], blowing, planes),
        halo_y[..., : 3 * planes],
    )
    ghost_above = jnp.where(
        row_dev == row_devs - 1,
        jnp.tile(state[..., length - planes :], (1, 1, 3)),
        halo_y[..., length + 3 * planes :],
    )
    conserved_y = jnp.concatenate(
        [ghost_below[..., :planes], ghost_below, state, ghost_above, ghost_above[..., -planes:]], axis=2
    )
    conserved_x = jnp.concatenate([conserved_x, conserved_x[:, -2:]], axis=1)
    width = CHUNK + 2 * PAD
    height = height_ext[3 : columns + 3]
    first_row = row_dev * row_count
    local_rows = (first_row + jnp.arange(row_count, dtype=jnp.int32)).astype(jnp.float32)
    spacing_lane = jnp.repeat(stretch(local_rows, total_rows)[1], planes)[None, :]
    outer_rows = (first_row - 4 + jnp.arange(row_count + 8, dtype=jnp.int32)).astype(jnp.float32)
    eta_lane = jnp.repeat(stretch(outer_rows, total_rows)[0], planes)[None, :]
    height_x = jnp.tile(jnp.concatenate([height_ext, height_ext[-2:]], axis=0), (1, CHUNK // planes))
    state_new = update(
        conserved_x,
        conserved_y,
        height_x,
        jnp.tile(height, (1, CHUNK // planes)),
        jnp.tile(slope_x, (1, width // planes)),
        jnp.tile(slope_z, (1, width // planes)),
        jnp.tile(shock_rate, (1, width // planes)),
        jnp.tile(shock_rate / height, (1, CHUNK // planes)),
        spacing_lane,
        eta_lane,
        planes,
        COURANT / total_rows,
    )
    shock_new = shock_height + COURANT / total_rows * shock_rate
    return (state_new, shock_new)


def solution(mesh):
    in_specs = (P(None, "gx", "gy"), P("gx", None), P("gx"), P(), P())
    out_specs = (P(None, "gx", "gy"), P("gx", None))
    return jax.shard_map(shards, mesh=mesh, in_specs=in_specs, out_specs=out_specs, check_vma=False)
```

```python
import math

import jax
import jax.numpy as jnp
from jax import lax
from jax.experimental import pallas as pl
from jax.experimental.pallas import tpu as pltpu
from jax.sharding import PartitionSpec as P

HEAT_RATIO = 1.4
STREAM_STEP = 0.05
SPAN_STEP = 0.05
STRETCH_RATE = 2.0
CHARACTER_KELVIN = 3.0
WHITE_LAW_FACTOR = 1.0
LANDAU_TELLER = 0.002
FREE_PRESSURE = 0.1
FREE_MACH = 6.0
COURANT = 0.05

PLUS_WEIGHTS = (-2.0, 15.0, -60.0, 20.0, 30.0, -3.0, 0.0)
MINUS_WEIGHTS = (0.0, 3.0, -30.0, -20.0, 60.0, -15.0, 2.0)
CHUNK = 256
PAD = 128
HALO = 3
XPAD = 8
LANES = 128


def kernel_primitives(q):
    inverse = 1.0 / q[0]
    vel_x = q[1] * inverse
    vel_y = q[2] * inverse
    vel_z = q[3] * inverse
    stress = (HEAT_RATIO - 1.0) * (q[4] - 0.5 * (q[1] * vel_x + q[2] * vel_y + q[3] * vel_z) - q[5])
    sound = jnp.sqrt(HEAT_RATIO * stress * inverse)
    return inverse, vel_x, vel_y, vel_z, stress, sound


def combined(plus, minus, t):
    a = PLUS_WEIGHTS[t + 3]
    b = MINUS_WEIGHTS[t + 3]
    if a == 0.0:
        return b * minus
    if b == 0.0:
        return a * plus
    return a * plus + b * minus


def lane_tile(values, width):
    return jnp.concatenate([values] * (width // values.shape[-1]), axis=-1)


def stretch_factors(rows, total_rows):
    growth = jnp.exp(STRETCH_RATE * (rows + 0.5) / total_rows)
    denominator = math.exp(STRETCH_RATE) - 1.0
    return (growth - 1.0) / denominator, STRETCH_RATE * growth / (total_rows * denominator)


def make_kernel(columns, length, planes, total_rows, dt):
    width = CHUNK + 2 * PAD
    face_area = STREAM_STEP * SPAN_STEP
    xrows = columns + 2 * XPAD

    def kernel(flags_ref, state_ref, xlo_ref, xhi_ref, ylo_ref, yhi_ref, geo_ref,
               out_ref, qx_ref, qy_ref, px_ref, mx_ref):
        first_row = flags_ref[0]
        for c in range(6):
            qx_ref[c, 0:XPAD, :] = state_ref[c, 0:XPAD, :]
            qx_ref[c, XPAD:XPAD + columns, :] = state_ref[c]
            qx_ref[c, XPAD + columns:, :] = state_ref[c, columns - XPAD:, :]
            qx_ref[c, XPAD - HALO:XPAD, :] = xlo_ref[c]
            qx_ref[c, XPAD + columns:XPAD + columns + HALO, :] = xhi_ref[c]
            qy_ref[c, :, 0:PAD] = ylo_ref[c]
            qy_ref[c, :, PAD:PAD + length] = state_ref[c]
            qy_ref[c, :, PAD + length:] = yhi_ref[c]

        @pl.when(flags_ref[1] == 1)
        def _():
            for c in range(6):
                qx_ref[c, XPAD - HALO:XPAD, :] = jnp.broadcast_to(state_ref[c, 0:1, :], (HALO, length))

        @pl.when(flags_ref[2] == 1)
        def _():
            for c in range(6):
                qx_ref[c, XPAD + columns:XPAD + columns + HALO, :] = jnp.broadcast_to(
                    state_ref[c, columns - 1:columns, :], (HALO, length))

        height_x = lane_tile(geo_ref[0:xrows, :], CHUNK)
        slope_x = lane_tile(geo_ref[xrows:xrows + columns, :], width)
        slope_z = lane_tile(geo_ref[xrows + columns:xrows + 2 * columns, :], width)
        rate = lane_tile(geo_ref[xrows + 2 * columns:xrows + 3 * columns, :], width)
        ratio = lane_tile(geo_ref[xrows + 3 * columns:xrows + 4 * columns, :], CHUNK)
        height = lane_tile(geo_ref[xrows + 4 * columns:xrows + 5 * columns, :], CHUNK)
        lane = lax.broadcasted_iota(jnp.int32, (columns, CHUNK), 1) % planes
        lane_in = lax.broadcasted_iota(jnp.int32, (1, CHUNK), 1)
        lane_out = lax.broadcasted_iota(jnp.int32, (1, width), 1)

        def body(k, carry):
            o = pl.multiple_of(k * CHUNK, CHUNK)
            rows_in = (first_row + (o + lane_in) // planes).astype(jnp.float32)
            spacing = stretch_factors(rows_in, total_rows)[1]
            rows_out = (first_row - PAD // planes + (o + lane_out) // planes).astype(jnp.float32)
            eta = stretch_factors(rows_out, total_rows)[0]
            xa = [qx_ref[c, :, pl.ds(o, CHUNK)] for c in range(6)]
            inverse, vel_x, vel_y, vel_z, stress, sound = kernel_primitives(xa)
            metric = STREAM_STEP * height_x * spacing
            fluxes = [xa[1], xa[1] * vel_x + stress, xa[2] * vel_x, xa[3] * vel_x,
                      (xa[4] + stress) * vel_x, xa[5] * vel_x]
            speed = (jnp.abs(vel_x) + sound) * metric
            for c in range(6):
                f = fluxes[c] * metric
                px_ref[c] = 0.5 * (f + speed * xa[c])
                mx_ref[c] = 0.5 * (f - speed * xa[c])
            div = []
            for c in range(6):
                acc = None
                for t in range(-3, 4):
                    term = None
                    a = PLUS_WEIGHTS[t + 3]
                    b = MINUS_WEIGHTS[t + 3]
                    if a != 0.0:
                        term = a * px_ref[c, pl.ds(XPAD + t, columns), :]
                    if b != 0.0:
                        mterm = b * mx_ref[c, pl.ds(XPAD + t, columns), :]
                        term = mterm if term is None else term + mterm
                    acc = term if acc is None else acc + term
                div.append(acc)
            ya = [qy_ref[c, :, pl.ds(o, width)] for c in range(6)]
            inverse, vel_x, vel_y, vel_z, stress, sound = kernel_primitives(ya)
            scaled = -face_area * eta
            metric_x = scaled * slope_x
            metric_z = scaled * slope_z
            metric_t = scaled * rate
            contra = metric_t + metric_x * vel_x + face_area * vel_y + metric_z * vel_z
            fluxes = [ya[0] * contra, ya[1] * contra + metric_x * stress,
                      ya[2] * contra + face_area * stress, ya[3] * contra + metric_z * stress,
                      (ya[4] + stress) * contra - metric_t * stress, ya[5] * contra]
            speed = jnp.abs(contra) + sound * jnp.sqrt(
                metric_x * metric_x + face_area * face_area + metric_z * metric_z)
            for c in range(6):
                plus = 0.5 * (fluxes[c] + speed * ya[c])
                minus = 0.5 * (fluxes[c] - speed * ya[c])
                acc = None
                for t in range(-3, 4):
                    term = combined(plus, minus, t)
                    if t != 0:
                        term = pltpu.roll(term, (-planes * t) % width, 1)
                    acc = term if acc is None else acc + term
                div[c] = div[c] + acc[:, PAD:PAD + CHUNK]
            q = [v[:, PAD:PAD + CHUNK] for v in ya]
            inverse = inverse[:, PAD:PAD + CHUNK]
            vel_z = vel_z[:, PAD:PAD + CHUNK]
            stress = stress[:, PAD:PAD + CHUNK]
            sound = sound[:, PAD:PAD + CHUNK]
            metric = STREAM_STEP * height * spacing
            fluxes = [q[3], q[1] * vel_z, q[2] * vel_z, q[3] * vel_z + stress,
                      (q[4] + stress) * vel_z, q[5] * vel_z]
            speed = (jnp.abs(vel_z) + sound) * metric
            for c in range(6):
                f = fluxes[c] * metric
                plus = 0.5 * (f + speed * q[c])
                minus = 0.5 * (f - speed * q[c])
                acc = None
                for t in range(-3, 4):
                    term = combined(plus, minus, t)
                    if t > 0:
                        term = jnp.where(lane < planes - t, pltpu.roll(term, CHUNK - t, 1),
                                         pltpu.roll(term, planes - t, 1))
                    elif t < 0:
                        term = jnp.where(lane >= -t, pltpu.roll(term, -t, 1),
                                         pltpu.roll(term, (CHUNK - planes - t) % CHUNK, 1))
                    acc = term if acc is None else acc + term
                div[c] = div[c] + acc
            kelvin = stress * inverse
            balanced = CHARACTER_KELVIN / (jnp.exp(CHARACTER_KELVIN / kelvin) - 1.0)
            teller = stress / (LANDAU_TELLER * jnp.exp(
                WHITE_LAW_FACTOR * jnp.exp(-jnp.log(kelvin) / 3.0)))
            source = q[0] * (balanced - q[5] * inverse) * teller
            volume = face_area * height * spacing
            for c in range(6):
                change = -(div[c] * (1.0 / 60.0)) / volume - q[c] * ratio
                if c == 5:
                    change = change + source
                out_ref[c, :, pl.ds(o, CHUNK)] = q[c] + dt * change
            return carry

        lax.fori_loop(0, length // CHUNK, body, 0)

    return kernel


def update(flags, state, xlo, xhi, ylo, yhi, geo, planes, total_rows, dt):
    columns = state.shape[1]
    length = state.shape[2]
    kern = make_kernel(columns, length, planes, total_rows, dt)
    vmem = pl.BlockSpec(memory_space=pltpu.VMEM)
    return pl.pallas_call(
        kern,
        out_shape=jax.ShapeDtypeStruct((6, columns, length), jnp.float32),
        in_specs=[pl.BlockSpec(memory_space=pltpu.SMEM)] + [vmem] * 6,
        out_specs=vmem,
        scratch_shapes=[
            pltpu.VMEM((6, columns + 2 * XPAD, length), jnp.float32),
            pltpu.VMEM((6, columns, length + 2 * PAD), jnp.float32),
            pltpu.VMEM((6, columns + 2 * XPAD, CHUNK), jnp.float32),
            pltpu.VMEM((6, columns + 2 * XPAD, CHUNK), jnp.float32),
        ],
    )(flags, state, xlo, xhi, ylo, yhi, geo)


def shifted(block, axis, forward, cyclic=False):
    count = lax.axis_size(axis)
    pairs = [(i, i + 1) for i in range(count - 1)]
    if cyclic and count > 1:
        pairs.append((count - 1, 0))
    if not forward:
        pairs = [(target, source) for source, target in pairs]
    return lax.ppermute(block, axis, pairs)


def broadcast(array, axis, holders):
    count = lax.axis_size(axis)
    index = lax.axis_index(axis)
    while len(holders) < count:
        waiting = [i for i in range(count) if i not in holders]
        pairs = list(zip(holders, waiting))
        received = lax.ppermute(array, axis, pairs)
        targets = jnp.zeros((), jnp.bool_)
        for _, target in pairs:
            targets = targets | (index == target)
        array = jnp.where(targets, received, array)
        holders = holders + [target for _, target in pairs]
    return array


def zshift(values, offset, planes):
    length = values.shape[-1]
    plane_at = jnp.arange(length, dtype=jnp.int32) % planes
    if offset > 0:
        return jnp.where(
            plane_at >= offset,
            jnp.roll(values, offset, axis=-1),
            jnp.roll(values, offset - planes, axis=-1),
        )
    return jnp.where(
        plane_at < planes + offset,
        jnp.roll(values, offset, axis=-1),
        jnp.roll(values, offset + planes, axis=-1),
    )


def primitives(conserved):
    specific_volume_inverse = conserved[0]
    vel_x = conserved[1] / specific_volume_inverse
    vel_y = conserved[2] / specific_volume_inverse
    vel_z = conserved[3] / specific_volume_inverse
    thermodynamic_stress = (HEAT_RATIO - 1.0) * (
        conserved[4]
        - 0.5 * (conserved[1] * vel_x + conserved[2] * vel_y + conserved[3] * vel_z)
        - conserved[5]
    )
    sound_speed = jnp.sqrt(HEAT_RATIO * thermodynamic_stress / specific_volume_inverse)
    return (specific_volume_inverse, vel_x, vel_y, vel_z, thermodynamic_stress, sound_speed)


def slopes(height_ext, planes):
    columns = height_ext.shape[0] - 6
    slope_x = (
        height_ext[1 : columns + 1]
        - 8.0 * height_ext[2 : columns + 2]
        + 8.0 * height_ext[4 : columns + 4]
        - height_ext[5 : columns + 5]
    ) / (12.0 * STREAM_STEP)
    height = height_ext[3 : columns + 3]
    slope_z = (
        zshift(height, 2, planes)
        - 8.0 * zshift(height, 1, planes)
        + 8.0 * zshift(height, -1, planes)
        - zshift(height, -2, planes)
    ) / (12.0 * SPAN_STEP)
    return (slope_x, slope_z)


def shock_speed(top_row, slope_x, slope_z):
    specific_volume_inverse, vel_x, vel_y, vel_z, thermodynamic_stress, sound_speed = primitives(
        top_row
    )
    tilt_norm = jnp.sqrt(1.0 + slope_x * slope_x + slope_z * slope_z)
    normal = (vel_y - vel_x * slope_x - vel_z * slope_z) / tilt_norm
    sine_sq = slope_x * slope_x / (tilt_norm * tilt_norm)
    jump_pressure = FREE_PRESSURE * (
        1.0 + 2.0 * HEAT_RATIO / (HEAT_RATIO + 1.0) * (FREE_MACH * FREE_MACH * sine_sq - 1.0)
    )
    return tilt_norm * (
        normal + (jump_pressure - thermodynamic_stress) / (specific_volume_inverse * sound_speed)
    )


def wall_ghosts(first_rows, blowing, planes):
    mirror = jnp.concatenate(
        [
            first_rows[..., 2 * planes : 3 * planes],
            first_rows[..., planes : 2 * planes],
            first_rows[..., 0:planes],
        ],
        axis=-1,
    )
    blown_y = 2.0 * jnp.tile(blowing, (1, 3)) - mirror[2]
    stagnation_enthalpy_sum = (
        mirror[4] + 0.5 * (blown_y * blown_y - mirror[2] * mirror[2]) / mirror[0]
    )
    return jnp.stack([mirror[0], mirror[1], blown_y, mirror[3], stagnation_enthalpy_sum, mirror[5]])


def wall_flux(wall_segment, segment_level, blow_table):
    seg_hit = wall_segment[:, None] == jnp.arange(segment_level.shape[0], dtype=jnp.int32)[None, :]
    levels = jnp.sum(jnp.where(seg_hit, segment_level[None, :], 0), axis=1)
    level_hit = levels[:, None] == jnp.arange(blow_table.shape[0], dtype=jnp.int32)[None, :]
    return jnp.sum(jnp.where(level_hit[:, :, None], blow_table[None, :, :], 0.0), axis=1)


def replicate_lanes(small, planes):
    pick = (
        jnp.arange(LANES, dtype=jnp.int32)[None, :] % planes
        == jnp.arange(planes, dtype=jnp.int32)[:, None]
    ).astype(jnp.float32)
    return jnp.dot(small, pick, precision=lax.Precision.HIGHEST, preferred_element_type=jnp.float32)


def shards(state, shock_height, wall_segment, segment_level, blow_table):
    planes = blow_table.shape[1]
    columns = state.shape[1]
    length = state.shape[2]
    row_count = length // planes
    col_devs = lax.axis_size("gx")
    row_devs = lax.axis_size("gy")
    col_dev = lax.axis_index("gx")
    row_dev = lax.axis_index("gy")
    total_rows = row_count * row_devs
    band = HALO * planes

    def pack(cols, heights):
        extra = jnp.zeros((1, HALO, length), jnp.float32)
        extra = lax.dynamic_update_slice(extra, heights[None], (0, 0, 0))
        return jnp.concatenate([cols, extra], axis=0)

    from_low = shifted(pack(state[:, columns - HALO :], shock_height[columns - HALO :]), "gx", True)
    from_high = shifted(pack(state[:, :HALO], shock_height[:HALO]), "gx", False)
    below = shifted(state[..., length - band :], "gy", True, cyclic=True)
    above = shifted(state[..., :band], "gy", False)

    low_height = jnp.where(
        col_dev == 0, jnp.broadcast_to(shock_height[:1], (HALO, planes)), from_low[6, :, :planes]
    )
    high_height = jnp.where(
        col_dev == col_devs - 1,
        jnp.broadcast_to(shock_height[columns - 1 :], (HALO, planes)),
        from_high[6, :, :planes],
    )
    height_ext = jnp.concatenate([low_height, shock_height, high_height], axis=0)
    slope_x, slope_z = slopes(height_ext, planes)

    top_seed = jnp.where(
        row_dev == row_devs - 1, state[..., length - planes :], below[..., band - planes :]
    )
    top_row = broadcast(top_seed, "gy", [row_devs - 1, 0] if row_devs > 1 else [0])
    shock_rate = shock_speed(top_row, slope_x, slope_z)

    blowing = wall_flux(wall_segment, segment_level, blow_table)
    ghost_below = jnp.where(row_dev == 0, wall_ghosts(state[..., :band], blowing, planes), below)
    ghost_above = jnp.where(
        row_dev == row_devs - 1, jnp.tile(state[..., length - planes :], (1, 1, HALO)), above
    )
    ylo = jnp.concatenate([ghost_below[..., : PAD - band], ghost_below], axis=2)
    yhi = jnp.concatenate([ghost_above, ghost_above[..., band - (PAD - band) :]], axis=2)

    height = shock_height
    xrows = columns + 2 * XPAD
    height_x = jnp.concatenate(
        [
            jnp.broadcast_to(height_ext[:1], (XPAD - HALO, planes)),
            height_ext,
            jnp.broadcast_to(height_ext[-1:], (XPAD - HALO, planes)),
        ],
        axis=0,
    )
    small = jnp.concatenate(
        [height_x, slope_x, slope_z, shock_rate, shock_rate / height, height], axis=0
    )
    geo = replicate_lanes(small, planes)
    flags = jnp.stack(
        [
            (row_dev * row_count).astype(jnp.int32),
            (col_dev == 0).astype(jnp.int32),
            (col_dev == col_devs - 1).astype(jnp.int32),
            jnp.zeros((), jnp.int32),
        ]
    )
    state_new = update(
        flags,
        state,
        from_low,
        from_high,
        ylo,
        yhi,
        geo,
        planes,
        total_rows,
        COURANT / total_rows,
    )
    shock_new = shock_height + COURANT / total_rows * shock_rate
    return (state_new, shock_new)


def solution(mesh):
    in_specs = (P(None, "gx", "gy"), P("gx", None), P("gx"), P(), P())
    out_specs = (P(None, "gx", "gy"), P("gx", None))
    return jax.shard_map(shards, mesh=mesh, in_specs=in_specs, out_specs=out_specs, check_vma=False)
```

```python
import math

import jax
import jax.numpy as jnp
from jax import lax
from jax.experimental import pallas as pl
from jax.experimental.pallas import tpu as pltpu
from jax.sharding import PartitionSpec as P

HEAT_RATIO = 1.4
STREAM_STEP = 0.05
SPAN_STEP = 0.05
STRETCH_RATE = 2.0
CHARACTER_KELVIN = 3.0
WHITE_LAW_FACTOR = 1.0
LANDAU_TELLER = 0.002
FREE_PRESSURE = 0.1
FREE_MACH = 6.0
COURANT = 0.05

PLUS_WEIGHTS = (-2.0, 15.0, -60.0, 20.0, 30.0, -3.0, 0.0)
MINUS_WEIGHTS = (0.0, 3.0, -30.0, -20.0, 60.0, -15.0, 2.0)
CHUNK = 256
PAD = 128
HALO = 3
XPAD = 8
LANES = 128


def kernel_primitives(q):
    inverse = 1.0 / q[0]
    vel_x = q[1] * inverse
    vel_y = q[2] * inverse
    vel_z = q[3] * inverse
    stress = (HEAT_RATIO - 1.0) * (q[4] - 0.5 * (q[1] * vel_x + q[2] * vel_y + q[3] * vel_z) - q[5])
    sound = jnp.sqrt(HEAT_RATIO * stress * inverse)
    return inverse, vel_x, vel_y, vel_z, stress, sound


def combined(plus, minus, t):
    a = PLUS_WEIGHTS[t + 3]
    b = MINUS_WEIGHTS[t + 3]
    if a == 0.0:
        return b * minus
    if b == 0.0:
        return a * plus
    return a * plus + b * minus


def lane_tile(values, width):
    return jnp.concatenate([values] * (width // values.shape[-1]), axis=-1)


def stretch_factors(rows, total_rows):
    growth = jnp.exp(STRETCH_RATE * (rows + 0.5) / total_rows)
    denominator = math.exp(STRETCH_RATE) - 1.0
    return (growth - 1.0) / denominator, STRETCH_RATE * growth / (total_rows * denominator)


def make_kernel(columns, length, planes, total_rows, dt):
    width = CHUNK + 2 * PAD
    face_area = STREAM_STEP * SPAN_STEP
    xrows = columns + 2 * XPAD

    def kernel(flags_ref, state_ref, xlo_ref, xhi_ref, ylo_ref, yhi_ref, geo_ref,
               out_ref, qx_ref, qy_ref, px_ref, mx_ref):
        first_row = flags_ref[0]
        for c in range(6):
            qx_ref[c, 0:XPAD, :] = state_ref[c, 0:XPAD, :]
            qx_ref[c, XPAD:XPAD + columns, :] = state_ref[c]
            qx_ref[c, XPAD + columns:, :] = state_ref[c, columns - XPAD:, :]
            qx_ref[c, XPAD - HALO:XPAD, :] = xlo_ref[c]
            qx_ref[c, XPAD + columns:XPAD + columns + HALO, :] = xhi_ref[c]
            qy_ref[c, :, 0:PAD] = ylo_ref[c]
            qy_ref[c, :, PAD:PAD + length] = state_ref[c]
            qy_ref[c, :, PAD + length:] = yhi_ref[c]

        @pl.when(flags_ref[1] == 1)
        def _():
            for c in range(6):
                qx_ref[c, XPAD - HALO:XPAD, :] = jnp.broadcast_to(state_ref[c, 0:1, :], (HALO, length))

        @pl.when(flags_ref[2] == 1)
        def _():
            for c in range(6):
                qx_ref[c, XPAD + columns:XPAD + columns + HALO, :] = jnp.broadcast_to(
                    state_ref[c, columns - 1:columns, :], (HALO, length))

        height_x = lane_tile(geo_ref[0:xrows, :], CHUNK)
        slope_x = lane_tile(geo_ref[xrows:xrows + columns, :], width)
        slope_z = lane_tile(geo_ref[xrows + columns:xrows + 2 * columns, :], width)
        rate = lane_tile(geo_ref[xrows + 2 * columns:xrows + 3 * columns, :], width)
        ratio = lane_tile(geo_ref[xrows + 3 * columns:xrows + 4 * columns, :], CHUNK)
        height = lane_tile(geo_ref[xrows + 4 * columns:xrows + 5 * columns, :], CHUNK)
        lane = lax.broadcasted_iota(jnp.int32, (columns, CHUNK), 1) % planes
        lane_in = lax.broadcasted_iota(jnp.int32, (1, CHUNK), 1)
        lane_out = lax.broadcasted_iota(jnp.int32, (1, width), 1)

        def body(k, carry):
            o = pl.multiple_of(k * CHUNK, CHUNK)
            rows_in = (first_row + (o + lane_in) // planes).astype(jnp.float32)
            spacing = stretch_factors(rows_in, total_rows)[1]
            rows_out = (first_row - PAD // planes + (o + lane_out) // planes).astype(jnp.float32)
            eta = stretch_factors(rows_out, total_rows)[0]
            xa = [qx_ref[c, :, pl.ds(o, CHUNK)] for c in range(6)]
            inverse, vel_x, vel_y, vel_z, stress, sound = kernel_primitives(xa)
            metric = STREAM_STEP * height_x * spacing
            fluxes = [xa[1], xa[1] * vel_x + stress, xa[2] * vel_x, xa[3] * vel_x,
                      (xa[4] + stress) * vel_x, xa[5] * vel_x]
            speed = (jnp.abs(vel_x) + sound) * metric
            for c in range(6):
                f = fluxes[c] * metric
                px_ref[c] = 0.5 * (f + speed * xa[c])
                mx_ref[c] = 0.5 * (f - speed * xa[c])
            div = []
            for c in range(6):
                acc = None
                for t in range(-3, 4):
                    term = None
                    a = PLUS_WEIGHTS[t + 3]
                    b = MINUS_WEIGHTS[t + 3]
                    if a != 0.0:
                        term = a * px_ref[c, pl.ds(XPAD + t, columns), :]
                    if b != 0.0:
                        mterm = b * mx_ref[c, pl.ds(XPAD + t, columns), :]
                        term = mterm if term is None else term + mterm
                    acc = term if acc is None else acc + term
                div.append(acc)
            ya = [qy_ref[c, :, pl.ds(o, width)] for c in range(6)]
            inverse, vel_x, vel_y, vel_z, stress, sound = kernel_primitives(ya)
            scaled = -face_area * eta
            metric_x = scaled * slope_x
            metric_z = scaled * slope_z
            metric_t = scaled * rate
            contra = metric_t + metric_x * vel_x + face_area * vel_y + metric_z * vel_z
            fluxes = [ya[0] * contra, ya[1] * contra + metric_x * stress,
                      ya[2] * contra + face_area * stress, ya[3] * contra + metric_z * stress,
                      (ya[4] + stress) * contra - metric_t * stress, ya[5] * contra]
            speed = jnp.abs(contra) + sound * jnp.sqrt(
                metric_x * metric_x + face_area * face_area + metric_z * metric_z)
            for c in range(6):
                plus = 0.5 * (fluxes[c] + speed * ya[c])
                minus = 0.5 * (fluxes[c] - speed * ya[c])
                acc = None
                for t in range(-3, 4):
                    term = combined(plus, minus, t)
                    if t != 0:
                        term = pltpu.roll(term, (-planes * t) % width, 1)
                    acc = term if acc is None else acc + term
                div[c] = div[c] + acc[:, PAD:PAD + CHUNK]
            q = [v[:, PAD:PAD + CHUNK] for v in ya]
            inverse = inverse[:, PAD:PAD + CHUNK]
            vel_z = vel_z[:, PAD:PAD + CHUNK]
            stress = stress[:, PAD:PAD + CHUNK]
            sound = sound[:, PAD:PAD + CHUNK]
            metric = STREAM_STEP * height * spacing
            fluxes = [q[3], q[1] * vel_z, q[2] * vel_z, q[3] * vel_z + stress,
                      (q[4] + stress) * vel_z, q[5] * vel_z]
            speed = (jnp.abs(vel_z) + sound) * metric
            for c in range(6):
                f = fluxes[c] * metric
                plus = 0.5 * (f + speed * q[c])
                minus = 0.5 * (f - speed * q[c])
                acc = None
                for t in range(-3, 4):
                    term = combined(plus, minus, t)
                    if t > 0:
                        term = jnp.where(lane < planes - t, pltpu.roll(term, CHUNK - t, 1),
                                         pltpu.roll(term, planes - t, 1))
                    elif t < 0:
                        term = jnp.where(lane >= -t, pltpu.roll(term, -t, 1),
                                         pltpu.roll(term, (CHUNK - planes - t) % CHUNK, 1))
                    acc = term if acc is None else acc + term
                div[c] = div[c] + acc
            kelvin = stress * inverse
            balanced = CHARACTER_KELVIN / (jnp.exp(CHARACTER_KELVIN / kelvin) - 1.0)
            teller = stress / (LANDAU_TELLER * jnp.exp(
                WHITE_LAW_FACTOR * jnp.exp(-jnp.log(kelvin) / 3.0)))
            source = q[0] * (balanced - q[5] * inverse) * teller
            volume = face_area * height * spacing
            for c in range(6):
                change = -(div[c] * (1.0 / 60.0)) / volume - q[c] * ratio
                if c == 5:
                    change = change + source
                out_ref[c, :, pl.ds(o, CHUNK)] = q[c] + dt * change
            return carry

        lax.fori_loop(0, length // CHUNK, body, 0)

    return kernel


def update(flags, state, xlo, xhi, ylo, yhi, geo, planes, total_rows, dt):
    columns = state.shape[1]
    length = state.shape[2]
    kern = make_kernel(columns, length, planes, total_rows, dt)
    vmem = pl.BlockSpec(memory_space=pltpu.VMEM)
    return pl.pallas_call(
        kern,
        out_shape=jax.ShapeDtypeStruct((6, columns, length), jnp.float32),
        in_specs=[pl.BlockSpec(memory_space=pltpu.SMEM)] + [vmem] * 6,
        out_specs=vmem,
        scratch_shapes=[
            pltpu.VMEM((6, columns + 2 * XPAD, length), jnp.float32),
            pltpu.VMEM((6, columns, length + 2 * PAD), jnp.float32),
            pltpu.VMEM((6, columns + 2 * XPAD, CHUNK), jnp.float32),
            pltpu.VMEM((6, columns + 2 * XPAD, CHUNK), jnp.float32),
        ],
    )(flags, state, xlo, xhi, ylo, yhi, geo)


def shifted(block, axis, forward, cyclic=False):
    count = lax.axis_size(axis)
    pairs = [(i, i + 1) for i in range(count - 1)]
    if cyclic and count > 1:
        pairs.append((count - 1, 0))
    if not forward:
        pairs = [(target, source) for source, target in pairs]
    return lax.ppermute(block, axis, pairs)


def broadcast(array, axis, holders):
    count = lax.axis_size(axis)
    index = lax.axis_index(axis)
    while len(holders) < count:
        waiting = [i for i in range(count) if i not in holders]
        pairs = list(zip(holders, waiting))
        received = lax.ppermute(array, axis, pairs)
        targets = jnp.zeros((), jnp.bool_)
        for _, target in pairs:
            targets = targets | (index == target)
        array = jnp.where(targets, received, array)
        holders = holders + [target for _, target in pairs]
    return array


def zshift(values, offset, planes):
    length = values.shape[-1]
    plane_at = jnp.arange(length, dtype=jnp.int32) % planes
    if offset > 0:
        return jnp.where(
            plane_at >= offset,
            jnp.roll(values, offset, axis=-1),
            jnp.roll(values, offset - planes, axis=-1),
        )
    return jnp.where(
        plane_at < planes + offset,
        jnp.roll(values, offset, axis=-1),
        jnp.roll(values, offset + planes, axis=-1),
    )


def primitives(conserved):
    specific_volume_inverse = conserved[0]
    vel_x = conserved[1] / specific_volume_inverse
    vel_y = conserved[2] / specific_volume_inverse
    vel_z = conserved[3] / specific_volume_inverse
    thermodynamic_stress = (HEAT_RATIO - 1.0) * (
        conserved[4]
        - 0.5 * (conserved[1] * vel_x + conserved[2] * vel_y + conserved[3] * vel_z)
        - conserved[5]
    )
    sound_speed = jnp.sqrt(HEAT_RATIO * thermodynamic_stress / specific_volume_inverse)
    return (specific_volume_inverse, vel_x, vel_y, vel_z, thermodynamic_stress, sound_speed)


def slopes(height_ext, planes):
    columns = height_ext.shape[0] - 6
    slope_x = (
        height_ext[1 : columns + 1]
        - 8.0 * height_ext[2 : columns + 2]
        + 8.0 * height_ext[4 : columns + 4]
        - height_ext[5 : columns + 5]
    ) / (12.0 * STREAM_STEP)
    height = height_ext[3 : columns + 3]
    slope_z = (
        zshift(height, 2, planes)
        - 8.0 * zshift(height, 1, planes)
        + 8.0 * zshift(height, -1, planes)
        - zshift(height, -2, planes)
    ) / (12.0 * SPAN_STEP)
    return (slope_x, slope_z)


def shock_speed(top_row, slope_x, slope_z):
    specific_volume_inverse, vel_x, vel_y, vel_z, thermodynamic_stress, sound_speed = primitives(
        top_row
    )
    tilt_norm = jnp.sqrt(1.0 + slope_x * slope_x + slope_z * slope_z)
    normal = (vel_y - vel_x * slope_x - vel_z * slope_z) / tilt_norm
    sine_sq = slope_x * slope_x / (tilt_norm * tilt_norm)
    jump_pressure = FREE_PRESSURE * (
        1.0 + 2.0 * HEAT_RATIO / (HEAT_RATIO + 1.0) * (FREE_MACH * FREE_MACH * sine_sq - 1.0)
    )
    return tilt_norm * (
        normal + (jump_pressure - thermodynamic_stress) / (specific_volume_inverse * sound_speed)
    )


def wall_ghosts(first_rows, blowing, planes):
    mirror = jnp.concatenate(
        [
            first_rows[..., 2 * planes : 3 * planes],
            first_rows[..., planes : 2 * planes],
            first_rows[..., 0:planes],
        ],
        axis=-1,
    )
    blown_y = 2.0 * jnp.tile(blowing, (1, 3)) - mirror[2]
    stagnation_enthalpy_sum = (
        mirror[4] + 0.5 * (blown_y * blown_y - mirror[2] * mirror[2]) / mirror[0]
    )
    return jnp.stack([mirror[0], mirror[1], blown_y, mirror[3], stagnation_enthalpy_sum, mirror[5]])


def wall_flux(wall_segment, segment_level, blow_table):
    seg_hit = wall_segment[:, None] == jnp.arange(segment_level.shape[0], dtype=jnp.int32)[None, :]
    levels = jnp.sum(jnp.where(seg_hit, segment_level[None, :], 0), axis=1)
    level_hit = levels[:, None] == jnp.arange(blow_table.shape[0], dtype=jnp.int32)[None, :]
    return jnp.sum(jnp.where(level_hit[:, :, None], blow_table[None, :, :], 0.0), axis=1)


def replicate_lanes(small, planes):
    pick = (
        jnp.arange(LANES, dtype=jnp.int32)[None, :] % planes
        == jnp.arange(planes, dtype=jnp.int32)[:, None]
    ).astype(jnp.float32)
    return jnp.dot(small, pick, precision=lax.Precision.HIGHEST, preferred_element_type=jnp.float32)


def shards(state, shock_height, wall_segment, segment_level, blow_table):
    planes = blow_table.shape[1]
    columns = state.shape[1]
    length = state.shape[2]
    row_count = length // planes
    col_devs = lax.axis_size("gx")
    row_devs = lax.axis_size("gy")
    col_dev = lax.axis_index("gx")
    row_dev = lax.axis_index("gy")
    total_rows = row_count * row_devs
    band = HALO * planes

    def pack(cols, heights):
        extra = jnp.zeros((1, HALO, length), jnp.float32)
        extra = lax.dynamic_update_slice(extra, heights[None], (0, 0, 0))
        return jnp.concatenate([cols, extra], axis=0)

    from_low = shifted(pack(state[:, columns - HALO :], shock_height[columns - HALO :]), "gx", True)
    from_high = shifted(pack(state[:, :HALO], shock_height[:HALO]), "gx", False)
    below = shifted(state[..., length - band :], "gy", True, cyclic=True)
    above = shifted(state[..., :band], "gy", False)

    low_height = jnp.where(
        col_dev == 0, jnp.broadcast_to(shock_height[:1], (HALO, planes)), from_low[6, :, :planes]
    )
    high_height = jnp.where(
        col_dev == col_devs - 1,
        jnp.broadcast_to(shock_height[columns - 1 :], (HALO, planes)),
        from_high[6, :, :planes],
    )
    height_ext = jnp.concatenate([low_height, shock_height, high_height], axis=0)
    slope_x, slope_z = slopes(height_ext, planes)

    top_copies = jnp.broadcast_to(state[None, ..., length - planes :], (row_devs, 6, columns, planes))
    top_row = lax.all_to_all(top_copies, "gy", 0, 0)[row_devs - 1]
    shock_rate = shock_speed(top_row, slope_x, slope_z)

    blowing = wall_flux(wall_segment, segment_level, blow_table)
    ghost_below = jnp.where(row_dev == 0, wall_ghosts(state[..., :band], blowing, planes), below)
    ghost_above = jnp.where(
        row_dev == row_devs - 1, jnp.tile(state[..., length - planes :], (1, 1, HALO)), above
    )
    ylo = jnp.concatenate([ghost_below[..., : PAD - band], ghost_below], axis=2)
    yhi = jnp.concatenate([ghost_above, ghost_above[..., band - (PAD - band) :]], axis=2)

    height = shock_height
    xrows = columns + 2 * XPAD
    height_x = jnp.concatenate(
        [
            jnp.broadcast_to(height_ext[:1], (XPAD - HALO, planes)),
            height_ext,
            jnp.broadcast_to(height_ext[-1:], (XPAD - HALO, planes)),
        ],
        axis=0,
    )
    small = jnp.concatenate(
        [height_x, slope_x, slope_z, shock_rate, shock_rate / height, height], axis=0
    )
    geo = replicate_lanes(small, planes)
    flags = jnp.stack(
        [
            (row_dev * row_count).astype(jnp.int32),
            (col_dev == 0).astype(jnp.int32),
            (col_dev == col_devs - 1).astype(jnp.int32),
            jnp.zeros((), jnp.int32),
        ]
    )
    state_new = update(
        flags,
        state,
        from_low,
        from_high,
        ylo,
        yhi,
        geo,
        planes,
        total_rows,
        COURANT / total_rows,
    )
    shock_new = shock_height + COURANT / total_rows * shock_rate
    return (state_new, shock_new)


def solution(mesh):
    in_specs = (P(None, "gx", "gy"), P("gx", None), P("gx"), P(), P())
    out_specs = (P(None, "gx", "gy"), P("gx", None))
    return jax.shard_map(shards, mesh=mesh, in_specs=in_specs, out_specs=out_specs, check_vma=False)
```

```python
import math

import jax
import jax.numpy as jnp
from jax import lax
from jax.experimental import pallas as pl
from jax.experimental.pallas import tpu as pltpu
from jax.sharding import PartitionSpec as P

HEAT_RATIO = 1.4
STREAM_STEP = 0.05
SPAN_STEP = 0.05
STRETCH_RATE = 2.0
CHARACTER_KELVIN = 3.0
WHITE_LAW_FACTOR = 1.0
LANDAU_TELLER = 0.002
FREE_PRESSURE = 0.1
FREE_MACH = 6.0
COURANT = 0.05

PLUS_WEIGHTS = (-2.0, 15.0, -60.0, 20.0, 30.0, -3.0, 0.0)
MINUS_WEIGHTS = (0.0, 3.0, -30.0, -20.0, 60.0, -15.0, 2.0)
CHUNK = 256
PAD = 128
HALO = 3
XPAD = 8
LANES = 128


def kernel_primitives(q):
    inverse = 1.0 / q[0]
    vel_x = q[1] * inverse
    vel_y = q[2] * inverse
    vel_z = q[3] * inverse
    stress = (HEAT_RATIO - 1.0) * (q[4] - 0.5 * (q[1] * vel_x + q[2] * vel_y + q[3] * vel_z) - q[5])
    sound = jnp.sqrt(HEAT_RATIO * stress * inverse)
    return inverse, vel_x, vel_y, vel_z, stress, sound


def combined(plus, minus, t):
    a = PLUS_WEIGHTS[t + 3]
    b = MINUS_WEIGHTS[t + 3]
    if a == 0.0:
        return b * minus
    if b == 0.0:
        return a * plus
    return a * plus + b * minus


def lane_tile(values, width):
    return jnp.concatenate([values] * (width // values.shape[-1]), axis=-1)


def stretch_factors(rows, total_rows):
    growth = jnp.exp(STRETCH_RATE * (rows + 0.5) / total_rows)
    denominator = math.exp(STRETCH_RATE) - 1.0
    return (growth - 1.0) / denominator, STRETCH_RATE * growth / (total_rows * denominator)


def make_kernel(columns, length, planes, total_rows, dt):
    width = CHUNK + 2 * PAD
    face_area = STREAM_STEP * SPAN_STEP
    xrows = columns + 2 * XPAD

    def kernel(state_ref, xlo_ref, xhi_ref, yhalo_ref, geo_ref,
               out_ref, qx_ref, qy_ref, px_ref, mx_ref):
        col_dev = lax.axis_index("gx")
        first_row = lax.axis_index("gy") * (length // planes)
        for c in range(6):
            qx_ref[c, 0:XPAD, :] = state_ref[c, 0:XPAD, :]
            qx_ref[c, XPAD:XPAD + columns, :] = state_ref[c]
            qx_ref[c, XPAD + columns:, :] = state_ref[c, columns - XPAD:, :]
            qx_ref[c, XPAD - HALO:XPAD, :] = xlo_ref[c]
            qx_ref[c, XPAD + columns:XPAD + columns + HALO, :] = xhi_ref[c]
            qy_ref[c, :, 0:PAD] = yhalo_ref[0, c]
            qy_ref[c, :, PAD:PAD + length] = state_ref[c]
            qy_ref[c, :, PAD + length:] = yhalo_ref[1, c, :, 0:PAD]

        @pl.when(col_dev == 0)
        def _():
            for c in range(6):
                qx_ref[c, XPAD - HALO:XPAD, :] = jnp.broadcast_to(state_ref[c, 0:1, :], (HALO, length))

        @pl.when(col_dev == lax.axis_size("gx") - 1)
        def _():
            for c in range(6):
                qx_ref[c, XPAD + columns:XPAD + columns + HALO, :] = jnp.broadcast_to(
                    state_ref[c, columns - 1:columns, :], (HALO, length))

        height_x = lane_tile(geo_ref[0:xrows, :], CHUNK)
        slope_x = lane_tile(geo_ref[xrows:xrows + columns, :], width)
        slope_z = lane_tile(geo_ref[xrows + columns:xrows + 2 * columns, :], width)
        rate = lane_tile(geo_ref[xrows + 2 * columns:xrows + 3 * columns, :], width)
        ratio = lane_tile(geo_ref[xrows + 3 * columns:xrows + 4 * columns, :], CHUNK)
        height = lane_tile(geo_ref[xrows + 4 * columns:xrows + 5 * columns, :], CHUNK)
        lane = lax.broadcasted_iota(jnp.int32, (columns, CHUNK), 1) % planes
        lane_in = lax.broadcasted_iota(jnp.int32, (1, CHUNK), 1)
        lane_out = lax.broadcasted_iota(jnp.int32, (1, width), 1)

        def body(k, carry):
            o = pl.multiple_of(k * CHUNK, CHUNK)
            rows_in = (first_row + (o + lane_in) // planes).astype(jnp.float32)
            spacing = stretch_factors(rows_in, total_rows)[1]
            rows_out = (first_row - PAD // planes + (o + lane_out) // planes).astype(jnp.float32)
            eta = stretch_factors(rows_out, total_rows)[0]
            xa = [qx_ref[c, :, pl.ds(o, CHUNK)] for c in range(6)]
            inverse, vel_x, vel_y, vel_z, stress, sound = kernel_primitives(xa)
            metric = STREAM_STEP * height_x * spacing
            fluxes = [xa[1], xa[1] * vel_x + stress, xa[2] * vel_x, xa[3] * vel_x,
                      (xa[4] + stress) * vel_x, xa[5] * vel_x]
            speed = (jnp.abs(vel_x) + sound) * metric
            for c in range(6):
                f = fluxes[c] * metric
                px_ref[c] = 0.5 * (f + speed * xa[c])
                mx_ref[c] = 0.5 * (f - speed * xa[c])
            div = []
            for c in range(6):
                acc = None
                for t in range(-3, 4):
                    term = None
                    a = PLUS_WEIGHTS[t + 3]
                    b = MINUS_WEIGHTS[t + 3]
                    if a != 0.0:
                        term = a * px_ref[c, pl.ds(XPAD + t, columns), :]
                    if b != 0.0:
                        mterm = b * mx_ref[c, pl.ds(XPAD + t, columns), :]
                        term = mterm if term is None else term + mterm
                    acc = term if acc is None else acc + term
                div.append(acc)
            ya = [qy_ref[c, :, pl.ds(o, width)] for c in range(6)]
            inverse, vel_x, vel_y, vel_z, stress, sound = kernel_primitives(ya)
            scaled = -face_area * eta
            metric_x = scaled * slope_x
            metric_z = scaled * slope_z
            metric_t = scaled * rate
            contra = metric_t + metric_x * vel_x + face_area * vel_y + metric_z * vel_z
            fluxes = [ya[0] * contra, ya[1] * contra + metric_x * stress,
                      ya[2] * contra + face_area * stress, ya[3] * contra + metric_z * stress,
                      (ya[4] + stress) * contra - metric_t * stress, ya[5] * contra]
            speed = jnp.abs(contra) + sound * jnp.sqrt(
                metric_x * metric_x + face_area * face_area + metric_z * metric_z)
            for c in range(6):
                plus = 0.5 * (fluxes[c] + speed * ya[c])
                minus = 0.5 * (fluxes[c] - speed * ya[c])
                acc = None
                for t in range(-3, 4):
                    term = combined(plus, minus, t)
                    if t != 0:
                        term = pltpu.roll(term, (-planes * t) % width, 1)
                    acc = term if acc is None else acc + term
                div[c] = div[c] + acc[:, PAD:PAD + CHUNK]
            q = [v[:, PAD:PAD + CHUNK] for v in ya]
            inverse = inverse[:, PAD:PAD + CHUNK]
            vel_z = vel_z[:, PAD:PAD + CHUNK]
            stress = stress[:, PAD:PAD + CHUNK]
            sound = sound[:, PAD:PAD + CHUNK]
            metric = STREAM_STEP * height * spacing
            fluxes = [q[3], q[1] * vel_z, q[2] * vel_z, q[3] * vel_z + stress,
                      (q[4] + stress) * vel_z, q[5] * vel_z]
            speed = (jnp.abs(vel_z) + sound) * metric
            for c in range(6):
                f = fluxes[c] * metric
                plus = 0.5 * (f + speed * q[c])
                minus = 0.5 * (f - speed * q[c])
                acc = None
                for t in range(-3, 4):
                    term = combined(plus, minus, t)
                    if t > 0:
                        term = jnp.where(lane < planes - t, pltpu.roll(term, CHUNK - t, 1),
                                         pltpu.roll(term, planes - t, 1))
                    elif t < 0:
                        term = jnp.where(lane >= -t, pltpu.roll(term, -t, 1),
                                         pltpu.roll(term, (CHUNK - planes - t) % CHUNK, 1))
                    acc = term if acc is None else acc + term
                div[c] = div[c] + acc
            kelvin = stress * inverse
            balanced = CHARACTER_KELVIN / (jnp.exp(CHARACTER_KELVIN / kelvin) - 1.0)
            teller = stress / (LANDAU_TELLER * jnp.exp(
                WHITE_LAW_FACTOR * jnp.exp(-jnp.log(kelvin) / 3.0)))
            source = q[0] * (balanced - q[5] * inverse) * teller
            volume = face_area * height * spacing
            for c in range(6):
                change = -(div[c] * (1.0 / 60.0)) / volume - q[c] * ratio
                if c == 5:
                    change = change + source
                out_ref[c, :, pl.ds(o, CHUNK)] = q[c] + dt * change
            return carry

        lax.fori_loop(0, length // CHUNK, body, 0)

    return kernel


def update(state, xlo, xhi, yhalo, geo, planes, total_rows, dt):
    columns = state.shape[1]
    length = state.shape[2]
    kern = make_kernel(columns, length, planes, total_rows, dt)
    vmem = pl.BlockSpec(memory_space=pltpu.VMEM)
    return pl.pallas_call(
        kern,
        out_shape=jax.ShapeDtypeStruct((6, columns, length), jnp.float32),
        in_specs=[vmem] * 5,
        out_specs=vmem,
        scratch_shapes=[
            pltpu.VMEM((6, columns + 2 * XPAD, length), jnp.float32),
            pltpu.VMEM((6, columns, length + 2 * PAD), jnp.float32),
            pltpu.VMEM((6, columns + 2 * XPAD, CHUNK), jnp.float32),
            pltpu.VMEM((6, columns + 2 * XPAD, CHUNK), jnp.float32),
        ],
    )(state, xlo, xhi, yhalo, geo)


def shifted(block, axis, forward, cyclic=False):
    count = lax.axis_size(axis)
    pairs = [(i, i + 1) for i in range(count - 1)]
    if cyclic and count > 1:
        pairs.append((count - 1, 0))
    if not forward:
        pairs = [(target, source) for source, target in pairs]
    return lax.ppermute(block, axis, pairs)


def broadcast(array, axis, holders, fanouts):
    count = lax.axis_size(axis)
    index = lax.axis_index(axis)
    for fanout in fanouts:
        if len(holders) >= count:
            break
        waiting = [i for i in range(count) if i not in holders]
        targets = jnp.zeros((), jnp.bool_)
        arrived = array
        reached = []
        for _ in range(fanout):
            pairs = list(zip(holders, waiting))
            waiting = waiting[len(pairs) :]
            if not pairs:
                break
            received = lax.ppermute(array, axis, pairs)
            hit = jnp.zeros((), jnp.bool_)
            for _, target in pairs:
                hit = hit | (index == target)
            arrived = jnp.where(hit, received, arrived)
            reached = reached + [target for _, target in pairs]
        array = arrived
        holders = holders + reached
    return array


def zshift(values, offset, planes):
    length = values.shape[-1]
    plane_at = jnp.arange(length, dtype=jnp.int32) % planes
    if offset > 0:
        return jnp.where(
            plane_at >= offset,
            jnp.roll(values, offset, axis=-1),
            jnp.roll(values, offset - planes, axis=-1),
        )
    return jnp.where(
        plane_at < planes + offset,
        jnp.roll(values, offset, axis=-1),
        jnp.roll(values, offset + planes, axis=-1),
    )


def primitives(conserved):
    specific_volume_inverse = conserved[0]
    vel_x = conserved[1] / specific_volume_inverse
    vel_y = conserved[2] / specific_volume_inverse
    vel_z = conserved[3] / specific_volume_inverse
    thermodynamic_stress = (HEAT_RATIO - 1.0) * (
        conserved[4]
        - 0.5 * (conserved[1] * vel_x + conserved[2] * vel_y + conserved[3] * vel_z)
        - conserved[5]
    )
    sound_speed = jnp.sqrt(HEAT_RATIO * thermodynamic_stress / specific_volume_inverse)
    return (specific_volume_inverse, vel_x, vel_y, vel_z, thermodynamic_stress, sound_speed)


def slopes(height_ext, planes):
    columns = height_ext.shape[0] - 6
    slope_x = (
        height_ext[1 : columns + 1]
        - 8.0 * height_ext[2 : columns + 2]
        + 8.0 * height_ext[4 : columns + 4]
        - height_ext[5 : columns + 5]
    ) / (12.0 * STREAM_STEP)
    height = height_ext[3 : columns + 3]
    slope_z = (
        zshift(height, 2, planes)
        - 8.0 * zshift(height, 1, planes)
        + 8.0 * zshift(height, -1, planes)
        - zshift(height, -2, planes)
    ) / (12.0 * SPAN_STEP)
    return (slope_x, slope_z)


def shock_speed(top_row, slope_x, slope_z):
    specific_volume_inverse, vel_x, vel_y, vel_z, thermodynamic_stress, sound_speed = primitives(
        top_row
    )
    tilt_norm = jnp.sqrt(1.0 + slope_x * slope_x + slope_z * slope_z)
    normal = (vel_y - vel_x * slope_x - vel_z * slope_z) / tilt_norm
    sine_sq = slope_x * slope_x / (tilt_norm * tilt_norm)
    jump_pressure = FREE_PRESSURE * (
        1.0 + 2.0 * HEAT_RATIO / (HEAT_RATIO + 1.0) * (FREE_MACH * FREE_MACH * sine_sq - 1.0)
    )
    return tilt_norm * (
        normal + (jump_pressure - thermodynamic_stress) / (specific_volume_inverse * sound_speed)
    )


def wall_ghosts(first_rows, blowing, planes):
    mirror = jnp.concatenate(
        [
            first_rows[..., 2 * planes : 3 * planes],
            first_rows[..., planes : 2 * planes],
            first_rows[..., 0:planes],
        ],
        axis=-1,
    )
    blown_y = 2.0 * jnp.tile(blowing, (1, 3)) - mirror[2]
    stagnation_enthalpy_sum = (
        mirror[4] + 0.5 * (blown_y * blown_y - mirror[2] * mirror[2]) / mirror[0]
    )
    return jnp.stack([mirror[0], mirror[1], blown_y, mirror[3], stagnation_enthalpy_sum, mirror[5]])


def wall_flux(wall_segment, segment_level, blow_table):
    seg_hit = wall_segment[:, None] == jnp.arange(segment_level.shape[0], dtype=jnp.int32)[None, :]
    levels = jnp.sum(jnp.where(seg_hit, segment_level[None, :], 0), axis=1)
    level_hit = levels[:, None] == jnp.arange(blow_table.shape[0], dtype=jnp.int32)[None, :]
    return jnp.sum(jnp.where(level_hit[:, :, None], blow_table[None, :, :], 0.0), axis=1)


def replicate_lanes(small, planes):
    pick = (
        jnp.arange(LANES, dtype=jnp.int32)[None, :] % planes
        == jnp.arange(planes, dtype=jnp.int32)[:, None]
    ).astype(jnp.float32)
    return jnp.dot(small, pick, precision=lax.Precision.HIGHEST, preferred_element_type=jnp.float32)


def shards(state, shock_height, wall_segment, segment_level, blow_table):
    planes = blow_table.shape[1]
    columns = state.shape[1]
    length = state.shape[2]
    row_count = length // planes
    col_devs = lax.axis_size("gx")
    row_devs = lax.axis_size("gy")
    col_dev = lax.axis_index("gx")
    row_dev = lax.axis_index("gy")
    total_rows = row_count * row_devs
    band = HALO * planes

    def pack(cols, heights):
        extra = jnp.zeros((1, HALO, length), jnp.float32)
        extra = lax.dynamic_update_slice(extra, heights[None], (0, 0, 0))
        return jnp.concatenate([cols, extra], axis=0)

    from_low = shifted(pack(state[:, columns - HALO :], shock_height[columns - HALO :]), "gx", True)
    from_high = shifted(pack(state[:, :HALO], shock_height[:HALO]), "gx", False)
    below = shifted(state[..., length - band :], "gy", True, cyclic=True)
    above = shifted(
        jnp.concatenate([state[..., :band], state[..., length - planes :]], axis=2), "gy", False
    )

    low_height = jnp.where(
        col_dev == 0, jnp.broadcast_to(shock_height[:1], (HALO, planes)), from_low[6, :, :planes]
    )
    high_height = jnp.where(
        col_dev == col_devs - 1,
        jnp.broadcast_to(shock_height[columns - 1 :], (HALO, planes)),
        from_high[6, :, :planes],
    )
    height_ext = jnp.concatenate([low_height, shock_height, high_height], axis=0)
    slope_x, slope_z = slopes(height_ext, planes)

    top_seed = jnp.where(
        row_dev == row_devs - 1,
        state[..., length - planes :],
        jnp.where(row_dev == 0, below[..., band - planes :], above[..., band:]),
    )
    seeded = sorted({row_devs - 1, 0, max(row_devs - 2, 0)}, reverse=True)
    top_row = broadcast(top_seed, "gy", seeded, (2, 1, 1, 1, 1))
    shock_rate = shock_speed(top_row, slope_x, slope_z)

    blowing = wall_flux(wall_segment, segment_level, blow_table)
    ghost_below = jnp.where(row_dev == 0, wall_ghosts(state[..., :band], blowing, planes), below)
    ghost_above = jnp.where(
        row_dev == row_devs - 1, jnp.tile(state[..., length - planes :], (1, 1, HALO + 1)), above
    )
    yhalo = jnp.stack([jnp.concatenate([ghost_below[..., : PAD - band], ghost_below], axis=2), ghost_above])

    height = shock_height
    xrows = columns + 2 * XPAD
    height_x = jnp.concatenate(
        [
            jnp.broadcast_to(height_ext[:1], (XPAD - HALO, planes)),
            height_ext,
            jnp.broadcast_to(height_ext[-1:], (XPAD - HALO, planes)),
        ],
        axis=0,
    )
    small = jnp.concatenate(
        [height_x, slope_x, slope_z, shock_rate, shock_rate / height, height], axis=0
    )
    geo = replicate_lanes(small, planes)
    state_new = update(
        state,
        from_low,
        from_high,
        yhalo,
        geo,
        planes,
        total_rows,
        COURANT / total_rows,
    )
    shock_new = shock_height + COURANT / total_rows * shock_rate
    return (state_new, shock_new)


def solution(mesh):
    in_specs = (P(None, "gx", "gy"), P("gx", None), P("gx"), P(), P())
    out_specs = (P(None, "gx", "gy"), P("gx", None))
    return jax.shard_map(shards, mesh=mesh, in_specs=in_specs, out_specs=out_specs, check_vma=False)
```

```python
import math

import jax
import jax.numpy as jnp
from jax import lax
from jax.experimental import pallas as pl
from jax.experimental.pallas import tpu as pltpu
from jax.sharding import PartitionSpec as P

HEAT_RATIO = 1.4
STREAM_STEP = 0.05
SPAN_STEP = 0.05
STRETCH_RATE = 2.0
CHARACTER_KELVIN = 3.0
WHITE_LAW_FACTOR = 1.0
LANDAU_TELLER = 0.002
FREE_PRESSURE = 0.1
FREE_MACH = 6.0
COURANT = 0.05

PLUS_WEIGHTS = (-2.0, 15.0, -60.0, 20.0, 30.0, -3.0, 0.0)
MINUS_WEIGHTS = (0.0, 3.0, -30.0, -20.0, 60.0, -15.0, 2.0)
CHUNK = 512
PAD = 128
HALO = 3
XPAD = 3
LANES = 128


def kernel_primitives(q):
    inverse = 1.0 / q[0]
    vel_x = q[1] * inverse
    vel_y = q[2] * inverse
    vel_z = q[3] * inverse
    stress = (HEAT_RATIO - 1.0) * (q[4] - 0.5 * (q[1] * vel_x + q[2] * vel_y + q[3] * vel_z) - q[5])
    sound = jnp.sqrt(HEAT_RATIO * stress * inverse)
    return inverse, vel_x, vel_y, vel_z, stress, sound


def combined(plus, minus, t):
    a = PLUS_WEIGHTS[t + 3]
    b = MINUS_WEIGHTS[t + 3]
    if a == 0.0:
        return b * minus
    if b == 0.0:
        return a * plus
    return a * plus + b * minus


def lane_tile(values, width):
    return jnp.concatenate([values] * (width // values.shape[-1]), axis=-1)


def stretch_factors(rows, total_rows):
    growth = jnp.exp(STRETCH_RATE * (rows + 0.5) / total_rows)
    denominator = math.exp(STRETCH_RATE) - 1.0
    return (growth - 1.0) / denominator, STRETCH_RATE * growth / (total_rows * denominator)


def make_kernel(columns, length, planes, total_rows, dt):
    width = CHUNK + 2 * PAD
    face_area = STREAM_STEP * SPAN_STEP
    xrows = columns + 2 * XPAD + 2

    def kernel(state_ref, xlo_ref, xhi_ref, yhalo_ref, geo_ref,
               out_ref, qx_ref, qy_ref, px_ref, mx_ref):
        col_dev = lax.axis_index("gx")
        first_row = lax.axis_index("gy") * (length // planes)
        for c in range(6):
            qx_ref[c, XPAD:XPAD + columns, :] = state_ref[c]
            qx_ref[c, XPAD + columns + HALO:, :] = state_ref[c, 2 * columns + 2 * XPAD - xrows:columns, :]
            qx_ref[c, 0:HALO, :] = xlo_ref[c]
            qx_ref[c, XPAD + columns:XPAD + columns + HALO, :] = xhi_ref[c]
            qy_ref[c, :, 0:PAD] = yhalo_ref[0, c]
            qy_ref[c, :, PAD:PAD + length] = state_ref[c]
            qy_ref[c, :, PAD + length:] = yhalo_ref[1, c, :, 0:PAD]

        @pl.when(col_dev == 0)
        def _():
            for c in range(6):
                qx_ref[c, XPAD - HALO:XPAD, :] = jnp.broadcast_to(state_ref[c, 0:1, :], (HALO, length))

        @pl.when(col_dev == lax.axis_size("gx") - 1)
        def _():
            for c in range(6):
                qx_ref[c, XPAD + columns:XPAD + columns + HALO, :] = jnp.broadcast_to(
                    state_ref[c, columns - 1:columns, :], (HALO, length))

        height_x = lane_tile(geo_ref[0:xrows, :], CHUNK)
        slope_x = lane_tile(geo_ref[xrows:xrows + columns, :], width)
        slope_z = lane_tile(geo_ref[xrows + columns:xrows + 2 * columns, :], width)
        rate = lane_tile(geo_ref[xrows + 2 * columns:xrows + 3 * columns, :], width)
        ratio = lane_tile(geo_ref[xrows + 3 * columns:xrows + 4 * columns, :], CHUNK)
        height = lane_tile(geo_ref[xrows + 4 * columns:xrows + 5 * columns, :], CHUNK)
        lane = lax.broadcasted_iota(jnp.int32, (columns, CHUNK), 1) % planes
        lane_in = lax.broadcasted_iota(jnp.int32, (1, CHUNK), 1)
        lane_out = lax.broadcasted_iota(jnp.int32, (1, width), 1)

        def body(k, carry):
            o = pl.multiple_of(k * CHUNK, CHUNK)
            rows_in = (first_row + (o + lane_in) // planes).astype(jnp.float32)
            spacing = stretch_factors(rows_in, total_rows)[1]
            rows_out = (first_row - PAD // planes + (o + lane_out) // planes).astype(jnp.float32)
            eta = stretch_factors(rows_out, total_rows)[0]
            xa = [qx_ref[c, :, pl.ds(o, CHUNK)] for c in range(6)]
            inverse, vel_x, vel_y, vel_z, stress, sound = kernel_primitives(xa)
            metric = STREAM_STEP * height_x * spacing
            fluxes = [xa[1], xa[1] * vel_x + stress, xa[2] * vel_x, xa[3] * vel_x,
                      (xa[4] + stress) * vel_x, xa[5] * vel_x]
            speed = (jnp.abs(vel_x) + sound) * metric
            for c in range(6):
                f = fluxes[c] * metric
                px_ref[c] = 0.5 * (f + speed * xa[c])
                mx_ref[c] = 0.5 * (f - speed * xa[c])
            div = []
            for c in range(6):
                acc = None
                for t in range(-3, 4):
                    term = None
                    a = PLUS_WEIGHTS[t + 3]
                    b = MINUS_WEIGHTS[t + 3]
                    if a != 0.0:
                        term = a * px_ref[c, pl.ds(XPAD + t, columns), :]
                    if b != 0.0:
                        mterm = b * mx_ref[c, pl.ds(XPAD + t, columns), :]
                        term = mterm if term is None else term + mterm
                    acc = term if acc is None else acc + term
                div.append(acc)
            ya = [qy_ref[c, :, pl.ds(o, width)] for c in range(6)]
            inverse, vel_x, vel_y, vel_z, stress, sound = kernel_primitives(ya)
            scaled = -face_area * eta
            metric_x = scaled * slope_x
            metric_z = scaled * slope_z
            metric_t = scaled * rate
            contra = metric_t + metric_x * vel_x + face_area * vel_y + metric_z * vel_z
            fluxes = [ya[0] * contra, ya[1] * contra + metric_x * stress,
                      ya[2] * contra + face_area * stress, ya[3] * contra + metric_z * stress,
                      (ya[4] + stress) * contra - metric_t * stress, ya[5] * contra]
            speed = jnp.abs(contra) + sound * jnp.sqrt(
                metric_x * metric_x + face_area * face_area + metric_z * metric_z)
            for c in range(6):
                plus = 0.5 * (fluxes[c] + speed * ya[c])
                minus = 0.5 * (fluxes[c] - speed * ya[c])
                acc = None
                for t in range(-3, 4):
                    term = combined(plus, minus, t)
                    if t != 0:
                        term = pltpu.roll(term, (-planes * t) % width, 1)
                    acc = term if acc is None else acc + term
                div[c] = div[c] + acc[:, PAD:PAD + CHUNK]
            q = [v[:, PAD:PAD + CHUNK] for v in ya]
            inverse = inverse[:, PAD:PAD + CHUNK]
            vel_z = vel_z[:, PAD:PAD + CHUNK]
            stress = stress[:, PAD:PAD + CHUNK]
            sound = sound[:, PAD:PAD + CHUNK]
            metric = STREAM_STEP * height * spacing
            fluxes = [q[3], q[1] * vel_z, q[2] * vel_z, q[3] * vel_z + stress,
                      (q[4] + stress) * vel_z, q[5] * vel_z]
            speed = (jnp.abs(vel_z) + sound) * metric
            for c in range(6):
                f = fluxes[c] * metric
                plus = 0.5 * (f + speed * q[c])
                minus = 0.5 * (f - speed * q[c])
                acc = None
                for t in range(-3, 4):
                    term = combined(plus, minus, t)
                    if t > 0:
                        term = jnp.where(lane < planes - t, pltpu.roll(term, CHUNK - t, 1),
                                         pltpu.roll(term, planes - t, 1))
                    elif t < 0:
                        term = jnp.where(lane >= -t, pltpu.roll(term, -t, 1),
                                         pltpu.roll(term, (CHUNK - planes - t) % CHUNK, 1))
                    acc = term if acc is None else acc + term
                div[c] = div[c] + acc
            kelvin = stress * inverse
            balanced = CHARACTER_KELVIN / (jnp.exp(CHARACTER_KELVIN / kelvin) - 1.0)
            teller = stress / (LANDAU_TELLER * jnp.exp(
                WHITE_LAW_FACTOR * jnp.exp(-jnp.log(kelvin) / 3.0)))
            source = q[0] * (balanced - q[5] * inverse) * teller
            volume = face_area * height * spacing
            for c in range(6):
                change = -(div[c] * (1.0 / 60.0)) / volume - q[c] * ratio
                if c == 5:
                    change = change + source
                out_ref[c, :, pl.ds(o, CHUNK)] = q[c] + dt * change
            return carry

        lax.fori_loop(0, length // CHUNK, body, 0)

    return kernel


def update(state, xlo, xhi, yhalo, geo, planes, total_rows, dt):
    columns = state.shape[1]
    length = state.shape[2]
    kern = make_kernel(columns, length, planes, total_rows, dt)
    vmem = pl.BlockSpec(memory_space=pltpu.VMEM)
    return pl.pallas_call(
        kern,
        out_shape=jax.ShapeDtypeStruct((6, columns, length), jnp.float32),
        in_specs=[vmem] * 5,
        out_specs=vmem,
        scratch_shapes=[
            pltpu.VMEM((6, columns + 2 * XPAD + 2, length), jnp.float32),
            pltpu.VMEM((6, columns, length + 2 * PAD), jnp.float32),
            pltpu.VMEM((6, columns + 2 * XPAD + 2, CHUNK), jnp.float32),
            pltpu.VMEM((6, columns + 2 * XPAD + 2, CHUNK), jnp.float32),
        ],
    )(state, xlo, xhi, yhalo, geo)


def shifted(block, axis, forward, cyclic=False):
    count = lax.axis_size(axis)
    pairs = [(i, i + 1) for i in range(count - 1)]
    if cyclic and count > 1:
        pairs.append((count - 1, 0))
    if not forward:
        pairs = [(target, source) for source, target in pairs]
    return lax.ppermute(block, axis, pairs)


def broadcast(array, axis, holders, fanouts):
    count = lax.axis_size(axis)
    index = lax.axis_index(axis)
    for fanout in fanouts:
        if len(holders) >= count:
            break
        waiting = [i for i in range(count) if i not in holders]
        targets = jnp.zeros((), jnp.bool_)
        arrived = array
        reached = []
        for _ in range(fanout):
            pairs = list(zip(holders, waiting))
            waiting = waiting[len(pairs) :]
            if not pairs:
                break
            received = lax.ppermute(array, axis, pairs)
            hit = jnp.zeros((), jnp.bool_)
            for _, target in pairs:
                hit = hit | (index == target)
            arrived = jnp.where(hit, received, arrived)
            reached = reached + [target for _, target in pairs]
        array = arrived
        holders = holders + reached
    return array


def zshift(values, offset, planes):
    length = values.shape[-1]
    plane_at = jnp.arange(length, dtype=jnp.int32) % planes
    if offset > 0:
        return jnp.where(
            plane_at >= offset,
            jnp.roll(values, offset, axis=-1),
            jnp.roll(values, offset - planes, axis=-1),
        )
    return jnp.where(
        plane_at < planes + offset,
        jnp.roll(values, offset, axis=-1),
        jnp.roll(values, offset + planes, axis=-1),
    )


def primitives(conserved):
    specific_volume_inverse = conserved[0]
    vel_x = conserved[1] / specific_volume_inverse
    vel_y = conserved[2] / specific_volume_inverse
    vel_z = conserved[3] / specific_volume_inverse
    thermodynamic_stress = (HEAT_RATIO - 1.0) * (
        conserved[4]
        - 0.5 * (conserved[1] * vel_x + conserved[2] * vel_y + conserved[3] * vel_z)
        - conserved[5]
    )
    sound_speed = jnp.sqrt(HEAT_RATIO * thermodynamic_stress / specific_volume_inverse)
    return (specific_volume_inverse, vel_x, vel_y, vel_z, thermodynamic_stress, sound_speed)


def slopes(height_ext, planes):
    columns = height_ext.shape[0] - 6
    slope_x = (
        height_ext[1 : columns + 1]
        - 8.0 * height_ext[2 : columns + 2]
        + 8.0 * height_ext[4 : columns + 4]
        - height_ext[5 : columns + 5]
    ) / (12.0 * STREAM_STEP)
    height = height_ext[3 : columns + 3]
    slope_z = (
        zshift(height, 2, planes)
        - 8.0 * zshift(height, 1, planes)
        + 8.0 * zshift(height, -1, planes)
        - zshift(height, -2, planes)
    ) / (12.0 * SPAN_STEP)
    return (slope_x, slope_z)


def shock_speed(top_row, slope_x, slope_z):
    specific_volume_inverse, vel_x, vel_y, vel_z, thermodynamic_stress, sound_speed = primitives(
        top_row
    )
    tilt_norm = jnp.sqrt(1.0 + slope_x * slope_x + slope_z * slope_z)
    normal = (vel_y - vel_x * slope_x - vel_z * slope_z) / tilt_norm
    sine_sq = slope_x * slope_x / (tilt_norm * tilt_norm)
    jump_pressure = FREE_PRESSURE * (
        1.0 + 2.0 * HEAT_RATIO / (HEAT_RATIO + 1.0) * (FREE_MACH * FREE_MACH * sine_sq - 1.0)
    )
    return tilt_norm * (
        normal + (jump_pressure - thermodynamic_stress) / (specific_volume_inverse * sound_speed)
    )


def wall_ghosts(first_rows, blowing, planes):
    mirror = jnp.concatenate(
        [
            first_rows[..., 2 * planes : 3 * planes],
            first_rows[..., planes : 2 * planes],
            first_rows[..., 0:planes],
        ],
        axis=-1,
    )
    blown_y = 2.0 * jnp.tile(blowing, (1, 3)) - mirror[2]
    stagnation_enthalpy_sum = (
        mirror[4] + 0.5 * (blown_y * blown_y - mirror[2] * mirror[2]) / mirror[0]
    )
    return jnp.stack([mirror[0], mirror[1], blown_y, mirror[3], stagnation_enthalpy_sum, mirror[5]])


def wall_flux(wall_segment, segment_level, blow_table):
    seg_hit = wall_segment[:, None] == jnp.arange(segment_level.shape[0], dtype=jnp.int32)[None, :]
    levels = jnp.sum(jnp.where(seg_hit, segment_level[None, :], 0), axis=1)
    level_hit = levels[:, None] == jnp.arange(blow_table.shape[0], dtype=jnp.int32)[None, :]
    return jnp.sum(jnp.where(level_hit[:, :, None], blow_table[None, :, :], 0.0), axis=1)


def replicate_lanes(small, planes):
    pick = (
        jnp.arange(LANES, dtype=jnp.int32)[None, :] % planes
        == jnp.arange(planes, dtype=jnp.int32)[:, None]
    ).astype(jnp.float32)
    return jnp.dot(small, pick, precision=lax.Precision.HIGHEST, preferred_element_type=jnp.float32)


def shards(state, shock_height, wall_segment, segment_level, blow_table):
    planes = blow_table.shape[1]
    columns = state.shape[1]
    length = state.shape[2]
    row_count = length // planes
    col_devs = lax.axis_size("gx")
    row_devs = lax.axis_size("gy")
    col_dev = lax.axis_index("gx")
    row_dev = lax.axis_index("gy")
    total_rows = row_count * row_devs
    band = HALO * planes

    def pack(cols, heights):
        extra = jnp.zeros((1, HALO, length), jnp.float32)
        extra = lax.dynamic_update_slice(extra, heights[None], (0, 0, 0))
        return jnp.concatenate([cols, extra], axis=0)

    from_low = shifted(pack(state[:, columns - HALO :], shock_height[columns - HALO :]), "gx", True)
    from_high = shifted(pack(state[:, :HALO], shock_height[:HALO]), "gx", False)
    below = shifted(state[..., length - band :], "gy", True, cyclic=True)
    above = shifted(
        jnp.concatenate([state[..., :band], state[..., length - planes :]], axis=2), "gy", False
    )

    low_height = jnp.where(
        col_dev == 0, jnp.broadcast_to(shock_height[:1], (HALO, planes)), from_low[6, :, :planes]
    )
    high_height = jnp.where(
        col_dev == col_devs - 1,
        jnp.broadcast_to(shock_height[columns - 1 :], (HALO, planes)),
        from_high[6, :, :planes],
    )
    height_ext = jnp.concatenate([low_height, shock_height, high_height], axis=0)
    slope_x, slope_z = slopes(height_ext, planes)

    top_seed = jnp.where(
        row_dev == row_devs - 1,
        state[..., length - planes :],
        jnp.where(row_dev == 0, below[..., band - planes :], above[..., band:]),
    )
    seeded = sorted({row_devs - 1, 0, max(row_devs - 2, 0)}, reverse=True)
    top_row = broadcast(top_seed, "gy", seeded, (2, 1, 1, 1, 1))
    shock_rate = shock_speed(top_row, slope_x, slope_z)

    blowing = wall_flux(wall_segment, segment_level, blow_table)
    ghost_below = jnp.where(row_dev == 0, wall_ghosts(state[..., :band], blowing, planes), below)
    ghost_above = jnp.where(
        row_dev == row_devs - 1, jnp.tile(state[..., length - planes :], (1, 1, HALO + 1)), above
    )
    yhalo = jnp.stack([jnp.concatenate([ghost_below[..., : PAD - band], ghost_below], axis=2), ghost_above])

    height = shock_height
    height_x = jnp.concatenate([height_ext, jnp.broadcast_to(height_ext[-1:], (2, planes))], axis=0)
    small = jnp.concatenate(
        [height_x, slope_x, slope_z, shock_rate, shock_rate / height, height], axis=0
    )
    geo = replicate_lanes(small, planes)
    state_new = update(
        state,
        from_low,
        from_high,
        yhalo,
        geo,
        planes,
        total_rows,
        COURANT / total_rows,
    )
    shock_new = shock_height + COURANT / total_rows * shock_rate
    return (state_new, shock_new)


def solution(mesh):
    in_specs = (P(None, "gx", "gy"), P("gx", None), P("gx"), P(), P())
    out_specs = (P(None, "gx", "gy"), P("gx", None))
    return jax.shard_map(shards, mesh=mesh, in_specs=in_specs, out_specs=out_specs, check_vma=False)
```

```python
import math

import jax
import jax.numpy as jnp
from jax import lax
from jax.experimental import pallas as pl
from jax.experimental.pallas import tpu as pltpu
from jax.sharding import PartitionSpec as P

HEAT_RATIO = 1.4
STREAM_STEP = 0.05
SPAN_STEP = 0.05
STRETCH_RATE = 2.0
CHARACTER_KELVIN = 3.0
WHITE_LAW_FACTOR = 1.0
LANDAU_TELLER = 0.002
FREE_PRESSURE = 0.1
FREE_MACH = 6.0
COURANT = 0.05

PLUS_WEIGHTS = (-2.0, 15.0, -60.0, 20.0, 30.0, -3.0, 0.0)
MINUS_WEIGHTS = (0.0, 3.0, -30.0, -20.0, 60.0, -15.0, 2.0)
CHUNK = 512
PAD = 128
HALO = 3
XPAD = 3
LANES = 128


def kernel_primitives(q):
    inverse = 1.0 / q[0]
    vel_x = q[1] * inverse
    vel_y = q[2] * inverse
    vel_z = q[3] * inverse
    stress = (HEAT_RATIO - 1.0) * (q[4] - 0.5 * (q[1] * vel_x + q[2] * vel_y + q[3] * vel_z) - q[5])
    sound = jnp.sqrt(HEAT_RATIO * stress * inverse)
    return inverse, vel_x, vel_y, vel_z, stress, sound


def combined(plus, minus, t):
    a = PLUS_WEIGHTS[t + 3]
    b = MINUS_WEIGHTS[t + 3]
    if a == 0.0:
        return b * minus
    if b == 0.0:
        return a * plus
    return a * plus + b * minus


def lane_tile(values, width):
    return jnp.concatenate([values] * (width // values.shape[-1]), axis=-1)


def stretch_factors(rows, total_rows):
    growth = jnp.exp(STRETCH_RATE * (rows + 0.5) / total_rows)
    denominator = math.exp(STRETCH_RATE) - 1.0
    return (growth - 1.0) / denominator, STRETCH_RATE * growth / (total_rows * denominator)


def stream_kernel(columns, length, planes, total_rows, dt):
    face_area = STREAM_STEP * SPAN_STEP
    xrows = columns + 2 * XPAD + 2

    def kernel(state_ref, xlo_ref, xhi_ref, geo_ref, out_ref, qx_ref, px_ref, mx_ref):
        col_dev = lax.axis_index("gx")
        first_row = lax.axis_index("gy") * (length // planes)
        for c in range(6):
            qx_ref[c, XPAD:XPAD + columns, :] = state_ref[c]
            qx_ref[c, XPAD + columns + HALO:, :] = state_ref[c, 2 * columns + 2 * XPAD - xrows:columns, :]
            qx_ref[c, 0:HALO, :] = xlo_ref[c]
            qx_ref[c, XPAD + columns:XPAD + columns + HALO, :] = xhi_ref[c]

        @pl.when(col_dev == 0)
        def _():
            for c in range(6):
                qx_ref[c, XPAD - HALO:XPAD, :] = jnp.broadcast_to(state_ref[c, 0:1, :], (HALO, length))

        @pl.when(col_dev == lax.axis_size("gx") - 1)
        def _():
            for c in range(6):
                qx_ref[c, XPAD + columns:XPAD + columns + HALO, :] = jnp.broadcast_to(
                    state_ref[c, columns - 1:columns, :], (HALO, length))

        height_x = lane_tile(geo_ref[0:xrows, :], CHUNK)
        height = lane_tile(geo_ref[xrows:xrows + columns, :], CHUNK)
        lane = lax.broadcasted_iota(jnp.int32, (columns, CHUNK), 1) % planes
        lane_in = lax.broadcasted_iota(jnp.int32, (1, CHUNK), 1)

        def body(k, carry):
            o = pl.multiple_of(k * CHUNK, CHUNK)
            rows_in = (first_row + (o + lane_in) // planes).astype(jnp.float32)
            spacing = stretch_factors(rows_in, total_rows)[1]
            xa = [qx_ref[c, :, pl.ds(o, CHUNK)] for c in range(6)]
            inverse, vel_x, vel_y, vel_z, stress, sound = kernel_primitives(xa)
            metric = STREAM_STEP * height_x * spacing
            fluxes = [xa[1], xa[1] * vel_x + stress, xa[2] * vel_x, xa[3] * vel_x,
                      (xa[4] + stress) * vel_x, xa[5] * vel_x]
            speed = (jnp.abs(vel_x) + sound) * metric
            for c in range(6):
                f = fluxes[c] * metric
                px_ref[c] = 0.5 * (f + speed * xa[c])
                mx_ref[c] = 0.5 * (f - speed * xa[c])
            div = []
            for c in range(6):
                acc = None
                for t in range(-3, 4):
                    term = None
                    a = PLUS_WEIGHTS[t + 3]
                    b = MINUS_WEIGHTS[t + 3]
                    if a != 0.0:
                        term = a * px_ref[c, pl.ds(XPAD + t, columns), :]
                    if b != 0.0:
                        mterm = b * mx_ref[c, pl.ds(XPAD + t, columns), :]
                        term = mterm if term is None else term + mterm
                    acc = term if acc is None else acc + term
                div.append(acc)
            q = [state_ref[c, :, pl.ds(o, CHUNK)] for c in range(6)]
            inverse, vel_x, vel_y, vel_z, stress, sound = kernel_primitives(q)
            metric = STREAM_STEP * height * spacing
            fluxes = [q[3], q[1] * vel_z, q[2] * vel_z, q[3] * vel_z + stress,
                      (q[4] + stress) * vel_z, q[5] * vel_z]
            speed = (jnp.abs(vel_z) + sound) * metric
            for c in range(6):
                f = fluxes[c] * metric
                plus = 0.5 * (f + speed * q[c])
                minus = 0.5 * (f - speed * q[c])
                acc = None
                for t in range(-3, 4):
                    term = combined(plus, minus, t)
                    if t > 0:
                        term = jnp.where(lane < planes - t, pltpu.roll(term, CHUNK - t, 1),
                                         pltpu.roll(term, planes - t, 1))
                    elif t < 0:
                        term = jnp.where(lane >= -t, pltpu.roll(term, -t, 1),
                                         pltpu.roll(term, (CHUNK - planes - t) % CHUNK, 1))
                    acc = term if acc is None else acc + term
                div[c] = div[c] + acc
            kelvin = stress * inverse
            balanced = CHARACTER_KELVIN / (jnp.exp(CHARACTER_KELVIN / kelvin) - 1.0)
            teller = stress / (LANDAU_TELLER * jnp.exp(
                WHITE_LAW_FACTOR * jnp.exp(-jnp.log(kelvin) / 3.0)))
            source = q[0] * (balanced - q[5] * inverse) * teller
            volume = face_area * height * spacing
            for c in range(6):
                change = -(div[c] * (1.0 / 60.0)) / volume
                if c == 5:
                    change = change + source
                out_ref[c, :, pl.ds(o, CHUNK)] = q[c] + dt * change
            return carry

        lax.fori_loop(0, length // CHUNK, body, 0)

    return kernel


def normal_kernel(columns, length, planes, total_rows, dt):
    width = CHUNK + 2 * PAD
    face_area = STREAM_STEP * SPAN_STEP

    def kernel(state_ref, yhalo_ref, geo_ref, part_ref, out_ref, qy_ref):
        first_row = lax.axis_index("gy") * (length // planes)
        for c in range(6):
            qy_ref[c, :, 0:PAD] = yhalo_ref[0, c]
            qy_ref[c, :, PAD:PAD + length] = state_ref[c]
            qy_ref[c, :, PAD + length:] = yhalo_ref[1, c]

        slope_x = lane_tile(geo_ref[0:columns, :], width)
        slope_z = lane_tile(geo_ref[columns:2 * columns, :], width)
        rate = lane_tile(geo_ref[2 * columns:3 * columns, :], width)
        ratio = lane_tile(geo_ref[3 * columns:4 * columns, :], CHUNK)
        height = lane_tile(geo_ref[4 * columns:5 * columns, :], CHUNK)
        lane_in = lax.broadcasted_iota(jnp.int32, (1, CHUNK), 1)
        lane_out = lax.broadcasted_iota(jnp.int32, (1, width), 1)

        def body(k, carry):
            o = pl.multiple_of(k * CHUNK, CHUNK)
            rows_in = (first_row + (o + lane_in) // planes).astype(jnp.float32)
            spacing = stretch_factors(rows_in, total_rows)[1]
            rows_out = (first_row - PAD // planes + (o + lane_out) // planes).astype(jnp.float32)
            eta = stretch_factors(rows_out, total_rows)[0]
            ya = [qy_ref[c, :, pl.ds(o, width)] for c in range(6)]
            inverse, vel_x, vel_y, vel_z, stress, sound = kernel_primitives(ya)
            scaled = -face_area * eta
            metric_x = scaled * slope_x
            metric_z = scaled * slope_z
            metric_t = scaled * rate
            contra = metric_t + metric_x * vel_x + face_area * vel_y + metric_z * vel_z
            fluxes = [ya[0] * contra, ya[1] * contra + metric_x * stress,
                      ya[2] * contra + face_area * stress, ya[3] * contra + metric_z * stress,
                      (ya[4] + stress) * contra - metric_t * stress, ya[5] * contra]
            speed = jnp.abs(contra) + sound * jnp.sqrt(
                metric_x * metric_x + face_area * face_area + metric_z * metric_z)
            volume = face_area * height * spacing
            for c in range(6):
                plus = 0.5 * (fluxes[c] + speed * ya[c])
                minus = 0.5 * (fluxes[c] - speed * ya[c])
                acc = None
                for t in range(-3, 4):
                    term = combined(plus, minus, t)
                    if t != 0:
                        term = pltpu.roll(term, (-planes * t) % width, 1)
                    acc = term if acc is None else acc + term
                div = acc[:, PAD:PAD + CHUNK]
                q = ya[c][:, PAD:PAD + CHUNK]
                change = -(div * (1.0 / 60.0)) / volume - q * ratio
                out_ref[c, :, pl.ds(o, CHUNK)] = part_ref[c, :, pl.ds(o, CHUNK)] + dt * change
            return carry

        lax.fori_loop(0, length // CHUNK, body, 0)

    return kernel


def stream_update(state, xlo, xhi, geo, planes, total_rows, dt):
    columns = state.shape[1]
    length = state.shape[2]
    vmem = pl.BlockSpec(memory_space=pltpu.VMEM)
    cells = 6 * columns * length
    return pl.pallas_call(
        stream_kernel(columns, length, planes, total_rows, dt),
        out_shape=jax.ShapeDtypeStruct((6, columns, length), jnp.float32),
        in_specs=[vmem] * 4,
        out_specs=vmem,
        scratch_shapes=[
            pltpu.VMEM((6, columns + 2 * XPAD + 2, length), jnp.float32),
            pltpu.VMEM((6, columns + 2 * XPAD + 2, CHUNK), jnp.float32),
            pltpu.VMEM((6, columns + 2 * XPAD + 2, CHUNK), jnp.float32),
        ],
        cost_estimate=pl.CostEstimate(flops=150 * cells, transcendentals=cells, bytes_accessed=12 * cells),
    )(state, xlo, xhi, geo)


def normal_update(state, yhalo, geo, part, planes, total_rows, dt):
    columns = state.shape[1]
    length = state.shape[2]
    vmem = pl.BlockSpec(memory_space=pltpu.VMEM)
    cells = 6 * columns * length
    return pl.pallas_call(
        normal_kernel(columns, length, planes, total_rows, dt),
        out_shape=jax.ShapeDtypeStruct((6, columns, length), jnp.float32),
        in_specs=[vmem] * 4,
        out_specs=vmem,
        input_output_aliases={3: 0},
        scratch_shapes=[pltpu.VMEM((6, columns, length + 2 * PAD), jnp.float32)],
        cost_estimate=pl.CostEstimate(flops=150 * cells, transcendentals=cells, bytes_accessed=12 * cells),
    )(state, yhalo, geo, part)


def shifted(block, axis, forward, cyclic=False):
    count = lax.axis_size(axis)
    pairs = [(i, i + 1) for i in range(count - 1)]
    if cyclic and count > 1:
        pairs.append((count - 1, 0))
    if not forward:
        pairs = [(target, source) for source, target in pairs]
    return lax.ppermute(block, axis, pairs)


def broadcast(array, axis, holders, fanouts):
    count = lax.axis_size(axis)
    index = lax.axis_index(axis)
    for fanout in fanouts:
        if len(holders) >= count:
            break
        waiting = [i for i in range(count) if i not in holders]
        targets = jnp.zeros((), jnp.bool_)
        arrived = array
        reached = []
        for _ in range(fanout):
            pairs = list(zip(holders, waiting))
            waiting = waiting[len(pairs) :]
            if not pairs:
                break
            received = lax.ppermute(array, axis, pairs)
            hit = jnp.zeros((), jnp.bool_)
            for _, target in pairs:
                hit = hit | (index == target)
            arrived = jnp.where(hit, received, arrived)
            reached = reached + [target for _, target in pairs]
        array = arrived
        holders = holders + reached
    return array


def zshift(values, offset, planes):
    length = values.shape[-1]
    plane_at = jnp.arange(length, dtype=jnp.int32) % planes
    if offset > 0:
        return jnp.where(
            plane_at >= offset,
            jnp.roll(values, offset, axis=-1),
            jnp.roll(values, offset - planes, axis=-1),
        )
    return jnp.where(
        plane_at < planes + offset,
        jnp.roll(values, offset, axis=-1),
        jnp.roll(values, offset + planes, axis=-1),
    )


def primitives(conserved):
    specific_volume_inverse = conserved[0]
    vel_x = conserved[1] / specific_volume_inverse
    vel_y = conserved[2] / specific_volume_inverse
    vel_z = conserved[3] / specific_volume_inverse
    thermodynamic_stress = (HEAT_RATIO - 1.0) * (
        conserved[4]
        - 0.5 * (conserved[1] * vel_x + conserved[2] * vel_y + conserved[3] * vel_z)
        - conserved[5]
    )
    sound_speed = jnp.sqrt(HEAT_RATIO * thermodynamic_stress / specific_volume_inverse)
    return (specific_volume_inverse, vel_x, vel_y, vel_z, thermodynamic_stress, sound_speed)


def slopes(height_ext, planes):
    columns = height_ext.shape[0] - 6
    slope_x = (
        height_ext[1 : columns + 1]
        - 8.0 * height_ext[2 : columns + 2]
        + 8.0 * height_ext[4 : columns + 4]
        - height_ext[5 : columns + 5]
    ) / (12.0 * STREAM_STEP)
    height = height_ext[3 : columns + 3]
    slope_z = (
        zshift(height, 2, planes)
        - 8.0 * zshift(height, 1, planes)
        + 8.0 * zshift(height, -1, planes)
        - zshift(height, -2, planes)
    ) / (12.0 * SPAN_STEP)
    return (slope_x, slope_z)


def shock_speed(top_row, slope_x, slope_z):
    specific_volume_inverse, vel_x, vel_y, vel_z, thermodynamic_stress, sound_speed = primitives(
        top_row
    )
    tilt_norm = jnp.sqrt(1.0 + slope_x * slope_x + slope_z * slope_z)
    normal = (vel_y - vel_x * slope_x - vel_z * slope_z) / tilt_norm
    sine_sq = slope_x * slope_x / (tilt_norm * tilt_norm)
    jump_pressure = FREE_PRESSURE * (
        1.0 + 2.0 * HEAT_RATIO / (HEAT_RATIO + 1.0) * (FREE_MACH * FREE_MACH * sine_sq - 1.0)
    )
    return tilt_norm * (
        normal + (jump_pressure - thermodynamic_stress) / (specific_volume_inverse * sound_speed)
    )


def wall_ghosts(first_rows, blowing, planes):
    mirror = jnp.concatenate(
        [
            first_rows[..., 2 * planes : 3 * planes],
            first_rows[..., planes : 2 * planes],
            first_rows[..., 0:planes],
        ],
        axis=-1,
    )
    blown_y = 2.0 * jnp.tile(blowing, (1, 3)) - mirror[2]
    stagnation_enthalpy_sum = (
        mirror[4] + 0.5 * (blown_y * blown_y - mirror[2] * mirror[2]) / mirror[0]
    )
    return jnp.stack([mirror[0], mirror[1], blown_y, mirror[3], stagnation_enthalpy_sum, mirror[5]])


def wall_flux(wall_segment, segment_level, blow_table):
    seg_hit = wall_segment[:, None] == jnp.arange(segment_level.shape[0], dtype=jnp.int32)[None, :]
    levels = jnp.sum(jnp.where(seg_hit, segment_level[None, :], 0), axis=1)
    level_hit = levels[:, None] == jnp.arange(blow_table.shape[0], dtype=jnp.int32)[None, :]
    return jnp.sum(jnp.where(level_hit[:, :, None], blow_table[None, :, :], 0.0), axis=1)


def replicate_lanes(small, planes):
    pick = (
        jnp.arange(LANES, dtype=jnp.int32)[None, :] % planes
        == jnp.arange(planes, dtype=jnp.int32)[:, None]
    ).astype(jnp.float32)
    return jnp.dot(small, pick, precision=lax.Precision.HIGHEST, preferred_element_type=jnp.float32)


def shards(state, shock_height, wall_segment, segment_level, blow_table):
    planes = blow_table.shape[1]
    columns = state.shape[1]
    length = state.shape[2]
    row_count = length // planes
    col_devs = lax.axis_size("gx")
    row_devs = lax.axis_size("gy")
    col_dev = lax.axis_index("gx")
    row_dev = lax.axis_index("gy")
    total_rows = row_count * row_devs
    band = HALO * planes

    def pack(cols, heights):
        extra = jnp.zeros((1, HALO, length), jnp.float32)
        extra = lax.dynamic_update_slice(extra, heights[None], (0, 0, 0))
        return jnp.concatenate([cols, extra], axis=0)

    from_low = shifted(pack(state[:, columns - HALO :], shock_height[columns - HALO :]), "gx", True)
    from_high = shifted(pack(state[:, :HALO], shock_height[:HALO]), "gx", False)
    below = shifted(state[..., length - band :], "gy", True, cyclic=True)
    above = shifted(
        jnp.concatenate([state[..., :band], state[..., length - planes :]], axis=2), "gy", False
    )

    low_height = jnp.where(
        col_dev == 0, jnp.broadcast_to(shock_height[:1], (HALO, planes)), from_low[6, :, :planes]
    )
    high_height = jnp.where(
        col_dev == col_devs - 1,
        jnp.broadcast_to(shock_height[columns - 1 :], (HALO, planes)),
        from_high[6, :, :planes],
    )
    height_ext = jnp.concatenate([low_height, shock_height, high_height], axis=0)
    slope_x, slope_z = slopes(height_ext, planes)

    top_seed = jnp.where(
        row_dev == row_devs - 1,
        state[..., length - planes :],
        jnp.where(row_dev == 0, below[..., band - planes :], above[..., band:]),
    )
    seeded = sorted({row_devs - 1, 0, max(row_devs - 2, 0)}, reverse=True)
    height_x = jnp.concatenate([height_ext, jnp.broadcast_to(height_ext[-1:], (2, planes))], axis=0)
    geo_x = replicate_lanes(jnp.concatenate([height_x, shock_height], axis=0), planes)
    part = stream_update(state, from_low, from_high, geo_x, planes, total_rows, COURANT / total_rows)
    top_seed, part = lax.optimization_barrier((top_seed, part))
    top_row = broadcast(top_seed, "gy", seeded, (2, 1, 1, 1, 1))
    shock_rate = shock_speed(top_row, slope_x, slope_z)

    blowing = wall_flux(wall_segment, segment_level, blow_table)
    ghost_below = jnp.where(row_dev == 0, wall_ghosts(state[..., :band], blowing, planes), below)
    ghost_above = jnp.where(
        row_dev == row_devs - 1, jnp.tile(state[..., length - planes :], (1, 1, HALO + 1)), above
    )
    yhalo = jnp.stack([jnp.concatenate([ghost_below[..., : PAD - band], ghost_below], axis=2), ghost_above])

    height = shock_height
    small = jnp.concatenate([slope_x, slope_z, shock_rate, shock_rate / height, height], axis=0)
    geo = replicate_lanes(small, planes)
    state_new = normal_update(state, yhalo, geo, part, planes, total_rows, COURANT / total_rows)
    shock_new = shock_height + COURANT / total_rows * shock_rate
    return (state_new, shock_new)


def solution(mesh):
    in_specs = (P(None, "gx", "gy"), P("gx", None), P("gx"), P(), P())
    out_specs = (P(None, "gx", "gy"), P("gx", None))
    return jax.shard_map(shards, mesh=mesh, in_specs=in_specs, out_specs=out_specs, check_vma=False)
```

```python
import math

import jax
import jax.numpy as jnp
from jax import lax
from jax.experimental import pallas as pl
from jax.experimental.pallas import tpu as pltpu
from jax.sharding import PartitionSpec as P

HEAT_RATIO = 1.4
STREAM_STEP = 0.05
SPAN_STEP = 0.05
STRETCH_RATE = 2.0
CHARACTER_KELVIN = 3.0
WHITE_LAW_FACTOR = 1.0
LANDAU_TELLER = 0.002
FREE_PRESSURE = 0.1
FREE_MACH = 6.0
COURANT = 0.05

PLUS_WEIGHTS = (-2.0, 15.0, -60.0, 20.0, 30.0, -3.0, 0.0)
MINUS_WEIGHTS = (0.0, 3.0, -30.0, -20.0, 60.0, -15.0, 2.0)
CHUNK = 512
PAD = 128
HALO = 3
XPAD = 3
LANES = 128


def kernel_primitives(q):
    inverse = 1.0 / q[0]
    vel_x = q[1] * inverse
    vel_y = q[2] * inverse
    vel_z = q[3] * inverse
    stress = (HEAT_RATIO - 1.0) * (q[4] - 0.5 * (q[1] * vel_x + q[2] * vel_y + q[3] * vel_z) - q[5])
    sound = jnp.sqrt(HEAT_RATIO * stress * inverse)
    return inverse, vel_x, vel_y, vel_z, stress, sound


def combined(plus, minus, t):
    a = PLUS_WEIGHTS[t + 3]
    b = MINUS_WEIGHTS[t + 3]
    if a == 0.0:
        return b * minus
    if b == 0.0:
        return a * plus
    return a * plus + b * minus


def lane_tile(values, width):
    return jnp.concatenate([values] * (width // values.shape[-1]), axis=-1)


def stretch_factors(rows, total_rows):
    growth = jnp.exp(STRETCH_RATE * (rows + 0.5) / total_rows)
    denominator = math.exp(STRETCH_RATE) - 1.0
    return (growth - 1.0) / denominator, STRETCH_RATE * growth / (total_rows * denominator)


def make_kernel(columns, length, planes, total_rows, dt):
    width = CHUNK + 2 * PAD
    face_area = STREAM_STEP * SPAN_STEP
    xrows = columns + 2 * XPAD + 2

    def kernel(state_ref, xlo_ref, xhi_ref, yhalo_ref, geo_ref,
               out_ref, qx_ref, qy_ref, px_ref, mx_ref):
        col_dev = lax.axis_index("gx")
        first_row = lax.axis_index("gy") * (length // planes)
        for c in range(6):
            qx_ref[c, XPAD:XPAD + columns, :] = state_ref[c]
            qx_ref[c, XPAD + columns + HALO:, :] = state_ref[c, 2 * columns + 2 * XPAD - xrows:columns, :]
            qx_ref[c, 0:HALO, :] = xlo_ref[c]
            qx_ref[c, XPAD + columns:XPAD + columns + HALO, :] = xhi_ref[c]
            qy_ref[c, :, 0:PAD] = yhalo_ref[0, c]
            qy_ref[c, :, PAD:PAD + length] = state_ref[c]
            qy_ref[c, :, PAD + length:] = yhalo_ref[1, c, :, 0:PAD]

        @pl.when(col_dev == 0)
        def _():
            for c in range(6):
                qx_ref[c, XPAD - HALO:XPAD, :] = jnp.broadcast_to(state_ref[c, 0:1, :], (HALO, length))

        @pl.when(col_dev == lax.axis_size("gx") - 1)
        def _():
            for c in range(6):
                qx_ref[c, XPAD + columns:XPAD + columns + HALO, :] = jnp.broadcast_to(
                    state_ref[c, columns - 1:columns, :], (HALO, length))

        height_x = lane_tile(geo_ref[0:xrows, :], CHUNK)
        slope_x = lane_tile(geo_ref[xrows:xrows + columns, :], width)
        slope_z = lane_tile(geo_ref[xrows + columns:xrows + 2 * columns, :], width)
        rate = lane_tile(geo_ref[xrows + 2 * columns:xrows + 3 * columns, :], width)
        ratio = lane_tile(geo_ref[xrows + 3 * columns:xrows + 4 * columns, :], CHUNK)
        height = lane_tile(geo_ref[xrows + 4 * columns:xrows + 5 * columns, :], CHUNK)
        lane = lax.broadcasted_iota(jnp.int32, (columns, CHUNK), 1) % planes
        lane_in = lax.broadcasted_iota(jnp.int32, (1, CHUNK), 1)
        lane_out = lax.broadcasted_iota(jnp.int32, (1, width), 1)

        def body(k, carry):
            o = pl.multiple_of(k * CHUNK, CHUNK)
            rows_in = (first_row + (o + lane_in) // planes).astype(jnp.float32)
            spacing = stretch_factors(rows_in, total_rows)[1]
            rows_out = (first_row - PAD // planes + (o + lane_out) // planes).astype(jnp.float32)
            eta = stretch_factors(rows_out, total_rows)[0]
            xa = [qx_ref[c, :, pl.ds(o, CHUNK)] for c in range(6)]
            inverse, vel_x, vel_y, vel_z, stress, sound = kernel_primitives(xa)
            metric = STREAM_STEP * height_x * spacing
            fluxes = [xa[1], xa[1] * vel_x + stress, xa[2] * vel_x, xa[3] * vel_x,
                      (xa[4] + stress) * vel_x, xa[5] * vel_x]
            speed = (jnp.abs(vel_x) + sound) * metric
            for c in range(6):
                f = fluxes[c] * metric
                px_ref[c] = 0.5 * (f + speed * xa[c])
                mx_ref[c] = 0.5 * (f - speed * xa[c])
            div = []
            for c in range(6):
                acc = None
                for t in range(-3, 4):
                    term = None
                    a = PLUS_WEIGHTS[t + 3]
                    b = MINUS_WEIGHTS[t + 3]
                    if a != 0.0:
                        term = a * px_ref[c, pl.ds(XPAD + t, columns), :]
                    if b != 0.0:
                        mterm = b * mx_ref[c, pl.ds(XPAD + t, columns), :]
                        term = mterm if term is None else term + mterm
                    acc = term if acc is None else acc + term
                div.append(acc)
            ya = [qy_ref[c, :, pl.ds(o, width)] for c in range(6)]
            inverse, vel_x, vel_y, vel_z, stress, sound = kernel_primitives(ya)
            scaled = -face_area * eta
            metric_x = scaled * slope_x
            metric_z = scaled * slope_z
            metric_t = scaled * rate
            contra = metric_t + metric_x * vel_x + face_area * vel_y + metric_z * vel_z
            fluxes = [ya[0] * contra, ya[1] * contra + metric_x * stress,
                      ya[2] * contra + face_area * stress, ya[3] * contra + metric_z * stress,
                      (ya[4] + stress) * contra - metric_t * stress, ya[5] * contra]
            speed = jnp.abs(contra) + sound * jnp.sqrt(
                metric_x * metric_x + face_area * face_area + metric_z * metric_z)
            for c in range(6):
                plus = 0.5 * (fluxes[c] + speed * ya[c])
                minus = 0.5 * (fluxes[c] - speed * ya[c])
                acc = None
                for t in range(-3, 4):
                    term = combined(plus, minus, t)
                    if t != 0:
                        term = pltpu.roll(term, (-planes * t) % width, 1)
                    acc = term if acc is None else acc + term
                div[c] = div[c] + acc[:, PAD:PAD + CHUNK]
            q = [v[:, PAD:PAD + CHUNK] for v in ya]
            inverse = inverse[:, PAD:PAD + CHUNK]
            vel_z = vel_z[:, PAD:PAD + CHUNK]
            stress = stress[:, PAD:PAD + CHUNK]
            sound = sound[:, PAD:PAD + CHUNK]
            metric = STREAM_STEP * height * spacing
            fluxes = [q[3], q[1] * vel_z, q[2] * vel_z, q[3] * vel_z + stress,
                      (q[4] + stress) * vel_z, q[5] * vel_z]
            speed = (jnp.abs(vel_z) + sound) * metric
            for c in range(6):
                f = fluxes[c] * metric
                plus = 0.5 * (f + speed * q[c])
                minus = 0.5 * (f - speed * q[c])
                acc = None
                for t in range(-3, 4):
                    term = combined(plus, minus, t)
                    if t > 0:
                        term = jnp.where(lane < planes - t, pltpu.roll(term, CHUNK - t, 1),
                                         pltpu.roll(term, planes - t, 1))
                    elif t < 0:
                        term = jnp.where(lane >= -t, pltpu.roll(term, -t, 1),
                                         pltpu.roll(term, (CHUNK - planes - t) % CHUNK, 1))
                    acc = term if acc is None else acc + term
                div[c] = div[c] + acc
            kelvin = stress * inverse
            balanced = CHARACTER_KELVIN / (jnp.exp(CHARACTER_KELVIN / kelvin) - 1.0)
            teller = stress / (LANDAU_TELLER * jnp.exp(
                WHITE_LAW_FACTOR * jnp.exp(-jnp.log(kelvin) / 3.0)))
            source = q[0] * (balanced - q[5] * inverse) * teller
            volume = face_area * height * spacing
            for c in range(6):
                change = -(div[c] * (1.0 / 60.0)) / volume - q[c] * ratio
                if c == 5:
                    change = change + source
                out_ref[c, :, pl.ds(o, CHUNK)] = q[c] + dt * change
            return carry

        lax.fori_loop(0, length // CHUNK, body, 0)

    return kernel


def update(state, xlo, xhi, yhalo, geo, planes, total_rows, dt):
    columns = state.shape[1]
    length = state.shape[2]
    kern = make_kernel(columns, length, planes, total_rows, dt)
    vmem = pl.BlockSpec(memory_space=pltpu.VMEM)
    return pl.pallas_call(
        kern,
        out_shape=jax.ShapeDtypeStruct((6, columns, length), jnp.float32),
        in_specs=[vmem] * 5,
        out_specs=vmem,
        scratch_shapes=[
            pltpu.VMEM((6, columns + 2 * XPAD + 2, length), jnp.float32),
            pltpu.VMEM((6, columns, length + 2 * PAD), jnp.float32),
            pltpu.VMEM((6, columns + 2 * XPAD + 2, CHUNK), jnp.float32),
            pltpu.VMEM((6, columns + 2 * XPAD + 2, CHUNK), jnp.float32),
        ],
    )(state, xlo, xhi, yhalo, geo)


def shifted(block, axis, forward, cyclic=False):
    count = lax.axis_size(axis)
    pairs = [(i, i + 1) for i in range(count - 1)]
    if cyclic and count > 1:
        pairs.append((count - 1, 0))
    if not forward:
        pairs = [(target, source) for source, target in pairs]
    return lax.ppermute(block, axis, pairs)


def broadcast(array, axis, holders, fanouts):
    count = lax.axis_size(axis)
    index = lax.axis_index(axis)
    for fanout in fanouts:
        if len(holders) >= count:
            break
        waiting = [i for i in range(count) if i not in holders]
        targets = jnp.zeros((), jnp.bool_)
        arrived = array
        reached = []
        for _ in range(fanout):
            pairs = list(zip(holders, waiting))
            waiting = waiting[len(pairs) :]
            if not pairs:
                break
            received = lax.ppermute(array, axis, pairs)
            hit = jnp.zeros((), jnp.bool_)
            for _, target in pairs:
                hit = hit | (index == target)
            arrived = jnp.where(hit, received, arrived)
            reached = reached + [target for _, target in pairs]
        array = arrived
        holders = holders + reached
    return array


def zshift(values, offset, planes):
    length = values.shape[-1]
    plane_at = jnp.arange(length, dtype=jnp.int32) % planes
    if offset > 0:
        return jnp.where(
            plane_at >= offset,
            jnp.roll(values, offset, axis=-1),
            jnp.roll(values, offset - planes, axis=-1),
        )
    return jnp.where(
        plane_at < planes + offset,
        jnp.roll(values, offset, axis=-1),
        jnp.roll(values, offset + planes, axis=-1),
    )


def primitives(conserved):
    specific_volume_inverse = conserved[0]
    vel_x = conserved[1] / specific_volume_inverse
    vel_y = conserved[2] / specific_volume_inverse
    vel_z = conserved[3] / specific_volume_inverse
    thermodynamic_stress = (HEAT_RATIO - 1.0) * (
        conserved[4]
        - 0.5 * (conserved[1] * vel_x + conserved[2] * vel_y + conserved[3] * vel_z)
        - conserved[5]
    )
    sound_speed = jnp.sqrt(HEAT_RATIO * thermodynamic_stress / specific_volume_inverse)
    return (specific_volume_inverse, vel_x, vel_y, vel_z, thermodynamic_stress, sound_speed)


def slopes(height_ext, planes):
    columns = height_ext.shape[0] - 6
    slope_x = (
        height_ext[1 : columns + 1]
        - 8.0 * height_ext[2 : columns + 2]
        + 8.0 * height_ext[4 : columns + 4]
        - height_ext[5 : columns + 5]
    ) / (12.0 * STREAM_STEP)
    height = height_ext[3 : columns + 3]
    slope_z = (
        zshift(height, 2, planes)
        - 8.0 * zshift(height, 1, planes)
        + 8.0 * zshift(height, -1, planes)
        - zshift(height, -2, planes)
    ) / (12.0 * SPAN_STEP)
    return (slope_x, slope_z)


def shock_speed(top_row, slope_x, slope_z):
    specific_volume_inverse, vel_x, vel_y, vel_z, thermodynamic_stress, sound_speed = primitives(
        top_row
    )
    tilt_norm = jnp.sqrt(1.0 + slope_x * slope_x + slope_z * slope_z)
    normal = (vel_y - vel_x * slope_x - vel_z * slope_z) / tilt_norm
    sine_sq = slope_x * slope_x / (tilt_norm * tilt_norm)
    jump_pressure = FREE_PRESSURE * (
        1.0 + 2.0 * HEAT_RATIO / (HEAT_RATIO + 1.0) * (FREE_MACH * FREE_MACH * sine_sq - 1.0)
    )
    return tilt_norm * (
        normal + (jump_pressure - thermodynamic_stress) / (specific_volume_inverse * sound_speed)
    )


def wall_ghosts(first_rows, blowing, planes):
    mirror = jnp.concatenate(
        [
            first_rows[..., 2 * planes : 3 * planes],
            first_rows[..., planes : 2 * planes],
            first_rows[..., 0:planes],
        ],
        axis=-1,
    )
    blown_y = 2.0 * jnp.tile(blowing, (1, 3)) - mirror[2]
    stagnation_enthalpy_sum = (
        mirror[4] + 0.5 * (blown_y * blown_y - mirror[2] * mirror[2]) / mirror[0]
    )
    return jnp.stack([mirror[0], mirror[1], blown_y, mirror[3], stagnation_enthalpy_sum, mirror[5]])


def wall_flux(wall_segment, segment_level, blow_table):
    seg_hit = wall_segment[:, None] == jnp.arange(segment_level.shape[0], dtype=jnp.int32)[None, :]
    levels = jnp.sum(jnp.where(seg_hit, segment_level[None, :], 0), axis=1)
    level_hit = levels[:, None] == jnp.arange(blow_table.shape[0], dtype=jnp.int32)[None, :]
    return jnp.sum(jnp.where(level_hit[:, :, None], blow_table[None, :, :], 0.0), axis=1)


def replicate_lanes(small, planes):
    pick = (
        jnp.arange(LANES, dtype=jnp.int32)[None, :] % planes
        == jnp.arange(planes, dtype=jnp.int32)[:, None]
    ).astype(jnp.float32)
    return jnp.dot(small, pick, precision=lax.Precision.HIGHEST, preferred_element_type=jnp.float32)


def shards(state, shock_height, wall_segment, segment_level, blow_table):
    planes = blow_table.shape[1]
    columns = state.shape[1]
    length = state.shape[2]
    row_count = length // planes
    col_devs = lax.axis_size("gx")
    row_devs = lax.axis_size("gy")
    col_dev = lax.axis_index("gx")
    row_dev = lax.axis_index("gy")
    total_rows = row_count * row_devs
    band = HALO * planes

    def pack(cols, heights):
        extra = jnp.zeros((1, HALO, length), jnp.float32)
        extra = lax.dynamic_update_slice(extra, heights[None], (0, 0, 0))
        return jnp.concatenate([cols, extra], axis=0)

    top_row = broadcast(state[..., length - planes :], "gy", [row_devs - 1], (1, 2, 2, 2, 2))
    low_cols, high_cols, low_rows, high_rows, top_row = lax.optimization_barrier(
        (state[:, columns - HALO :], state[:, :HALO], state[..., length - band :], state[..., :band], top_row)
    )
    from_low = shifted(pack(low_cols, shock_height[columns - HALO :]), "gx", True)
    from_high = shifted(pack(high_cols, shock_height[:HALO]), "gx", False)
    below = shifted(low_rows, "gy", True)
    above = shifted(high_rows, "gy", False)

    low_height = jnp.where(
        col_dev == 0, jnp.broadcast_to(shock_height[:1], (HALO, planes)), from_low[6, :, :planes]
    )
    high_height = jnp.where(
        col_dev == col_devs - 1,
        jnp.broadcast_to(shock_height[columns - 1 :], (HALO, planes)),
        from_high[6, :, :planes],
    )
    height_ext = jnp.concatenate([low_height, shock_height, high_height], axis=0)
    slope_x, slope_z = slopes(height_ext, planes)

    shock_rate = shock_speed(top_row, slope_x, slope_z)

    blowing = wall_flux(wall_segment, segment_level, blow_table)
    ghost_below = jnp.where(row_dev == 0, wall_ghosts(state[..., :band], blowing, planes), below)
    ghost_above = jnp.where(
        row_dev == row_devs - 1, jnp.tile(state[..., length - planes :], (1, 1, HALO)), above
    )
    yhalo = jnp.stack(
        [
            jnp.concatenate([ghost_below[..., : PAD - band], ghost_below], axis=2),
            jnp.concatenate([ghost_above, ghost_above[..., band - (PAD - band) :]], axis=2),
        ]
    )

    height = shock_height
    height_x = jnp.concatenate([height_ext, jnp.broadcast_to(height_ext[-1:], (2, planes))], axis=0)
    small = jnp.concatenate(
        [height_x, slope_x, slope_z, shock_rate, shock_rate / height, height], axis=0
    )
    geo = replicate_lanes(small, planes)
    state_new = update(
        state,
        from_low,
        from_high,
        yhalo,
        geo,
        planes,
        total_rows,
        COURANT / total_rows,
    )
    shock_new = shock_height + COURANT / total_rows * shock_rate
    return (state_new, shock_new)


def solution(mesh):
    in_specs = (P(None, "gx", "gy"), P("gx", None), P("gx"), P(), P())
    out_specs = (P(None, "gx", "gy"), P("gx", None))
    return jax.shard_map(shards, mesh=mesh, in_specs=in_specs, out_specs=out_specs, check_vma=False)
```

```python
import math

import jax
import jax.numpy as jnp
from jax import lax
from jax.experimental import pallas as pl
from jax.experimental.pallas import tpu as pltpu
from jax.sharding import PartitionSpec as P

HEAT_RATIO = 1.4
STREAM_STEP = 0.05
SPAN_STEP = 0.05
STRETCH_RATE = 2.0
CHARACTER_KELVIN = 3.0
WHITE_LAW_FACTOR = 1.0
LANDAU_TELLER = 0.002
FREE_PRESSURE = 0.1
FREE_MACH = 6.0
COURANT = 0.05

FLUX_WEIGHTS = (45.0, -9.0, 1.0)
SPEED_WEIGHTS = (20.0, -15.0, 6.0, -1.0)
CHUNK = 512
PAD = 128
HALO = 3
XPAD = 8
LANES = 128


def kernel_primitives(q):
    inverse = 1.0 / q[0]
    vel_x = q[1] * inverse
    vel_y = q[2] * inverse
    vel_z = q[3] * inverse
    stress = (HEAT_RATIO - 1.0) * (q[4] - 0.5 * (q[1] * vel_x + q[2] * vel_y + q[3] * vel_z) - q[5])
    sound = jnp.sqrt(HEAT_RATIO * stress * inverse)
    return inverse, vel_x, vel_y, vel_z, stress, sound


def pair_terms(flux, damped, t):
    odd = FLUX_WEIGHTS[t - 1]
    even = SPEED_WEIGHTS[t]
    odd_part = flux if odd == 1.0 else odd * flux
    if even == -1.0:
        return odd_part - damped, -(odd_part + damped)
    even_part = even * damped
    return even_part + odd_part, even_part - odd_part


def lane_tile(values, width):
    return jnp.concatenate([values] * (width // values.shape[-1]), axis=-1)


def stretch_factors(rows, total_rows):
    growth = jnp.exp(STRETCH_RATE * (rows + 0.5) / total_rows)
    denominator = math.exp(STRETCH_RATE) - 1.0
    return (growth - 1.0) / denominator, STRETCH_RATE * growth / (total_rows * denominator)


def make_kernel(columns, length, planes, total_rows, dt):
    width = CHUNK + 2 * PAD
    face_area = STREAM_STEP * SPAN_STEP
    xrows = columns + 2 * XPAD

    def kernel(state_ref, xlo_ref, xhi_ref, yhalo_ref, geo_ref,
               out_ref, qx_ref, qy_ref, pair_ref):
        col_dev = lax.axis_index("gx")
        first_row = lax.axis_index("gy") * (length // planes)
        for c in range(6):
            qx_ref[c, 0:XPAD, :] = state_ref[c, 0:XPAD, :]
            qx_ref[c, XPAD:XPAD + columns, :] = state_ref[c]
            qx_ref[c, XPAD + columns:, :] = state_ref[c, columns - XPAD:, :]
            qx_ref[c, XPAD - HALO:XPAD, :] = xlo_ref[c]
            qx_ref[c, XPAD + columns:XPAD + columns + HALO, :] = xhi_ref[c]
            qy_ref[c, :, 0:PAD] = yhalo_ref[0, c]
            qy_ref[c, :, PAD:PAD + length] = state_ref[c]
            qy_ref[c, :, PAD + length:] = yhalo_ref[1, c, :, 0:PAD]

        @pl.when(col_dev == 0)
        def _():
            for c in range(6):
                qx_ref[c, XPAD - HALO:XPAD, :] = jnp.broadcast_to(state_ref[c, 0:1, :], (HALO, length))

        @pl.when(col_dev == lax.axis_size("gx") - 1)
        def _():
            for c in range(6):
                qx_ref[c, XPAD + columns:XPAD + columns + HALO, :] = jnp.broadcast_to(
                    state_ref[c, columns - 1:columns, :], (HALO, length))

        height_x = lane_tile(geo_ref[0:xrows, :], CHUNK)
        slope_x = lane_tile(geo_ref[xrows:xrows + columns, :], width)
        slope_z = lane_tile(geo_ref[xrows + columns:xrows + 2 * columns, :], width)
        rate = lane_tile(geo_ref[xrows + 2 * columns:xrows + 3 * columns, :], width)
        ratio = lane_tile(geo_ref[xrows + 3 * columns:xrows + 4 * columns, :], CHUNK)
        height = lane_tile(geo_ref[xrows + 4 * columns:xrows + 5 * columns, :], CHUNK)
        lane = lax.broadcasted_iota(jnp.int32, (columns, CHUNK), 1) % planes
        lane_in = lax.broadcasted_iota(jnp.int32, (1, CHUNK), 1)
        lane_out = lax.broadcasted_iota(jnp.int32, (1, width), 1)

        def body(k, carry):
            o = pl.multiple_of(k * CHUNK, CHUNK)
            rows_in = (first_row + (o + lane_in) // planes).astype(jnp.float32)
            spacing = stretch_factors(rows_in, total_rows)[1]
            rows_out = (first_row - PAD // planes + (o + lane_out) // planes).astype(jnp.float32)
            eta = stretch_factors(rows_out, total_rows)[0]
            xa = [qx_ref[c, :, pl.ds(o, CHUNK)] for c in range(6)]
            inverse, vel_x, vel_y, vel_z, stress, sound = kernel_primitives(xa)
            metric = STREAM_STEP * height_x * spacing
            fluxes = [xa[1], xa[1] * vel_x + stress, xa[2] * vel_x, xa[3] * vel_x,
                      (xa[4] + stress) * vel_x, xa[5] * vel_x]
            speed = (jnp.abs(vel_x) + sound) * metric
            div = []
            for c in range(6):
                flux = fluxes[c] * metric
                damped = speed * xa[c]
                for t in range(1, 4):
                    up, down = pair_terms(flux, damped, t)
                    pair_ref[c, 2 * t - 2] = up
                    pair_ref[c, 2 * t - 1] = down
                acc = SPEED_WEIGHTS[0] * damped[XPAD:XPAD + columns]
                for t in range(1, 4):
                    acc = acc + pair_ref[c, 2 * t - 2, pl.ds(XPAD + t, columns), :]
                    acc = acc + pair_ref[c, 2 * t - 1, pl.ds(XPAD - t, columns), :]
                div.append(acc)
            ya = [qy_ref[c, :, pl.ds(o, width)] for c in range(6)]
            inverse, vel_x, vel_y, vel_z, stress, sound = kernel_primitives(ya)
            scaled = -face_area * eta
            metric_x = scaled * slope_x
            metric_z = scaled * slope_z
            metric_t = scaled * rate
            contra = metric_t + metric_x * vel_x + face_area * vel_y + metric_z * vel_z
            fluxes = [ya[0] * contra, ya[1] * contra + metric_x * stress,
                      ya[2] * contra + face_area * stress, ya[3] * contra + metric_z * stress,
                      (ya[4] + stress) * contra - metric_t * stress, ya[5] * contra]
            speed = jnp.abs(contra) + sound * jnp.sqrt(
                metric_x * metric_x + face_area * face_area + metric_z * metric_z)
            for c in range(6):
                damped = speed * ya[c]
                acc = SPEED_WEIGHTS[0] * damped
                for t in range(1, 4):
                    up, down = pair_terms(fluxes[c], damped, t)
                    acc = acc + pltpu.roll(up, (-planes * t) % width, 1) + pltpu.roll(down, planes * t, 1)
                div[c] = div[c] + acc[:, PAD:PAD + CHUNK]
            q = [v[:, PAD:PAD + CHUNK] for v in ya]
            inverse = inverse[:, PAD:PAD + CHUNK]
            vel_z = vel_z[:, PAD:PAD + CHUNK]
            stress = stress[:, PAD:PAD + CHUNK]
            sound = sound[:, PAD:PAD + CHUNK]
            metric = STREAM_STEP * height * spacing
            fluxes = [q[3], q[1] * vel_z, q[2] * vel_z, q[3] * vel_z + stress,
                      (q[4] + stress) * vel_z, q[5] * vel_z]
            speed = (jnp.abs(vel_z) + sound) * metric
            for c in range(6):
                damped = speed * q[c]
                acc = SPEED_WEIGHTS[0] * damped
                for t in range(1, 4):
                    up, down = pair_terms(fluxes[c] * metric, damped, t)
                    up = jnp.where(lane < planes - t, pltpu.roll(up, CHUNK - t, 1),
                                   pltpu.roll(up, planes - t, 1))
                    down = jnp.where(lane >= t, pltpu.roll(down, t, 1),
                                     pltpu.roll(down, CHUNK - planes + t, 1))
                    acc = acc + up + down
                div[c] = div[c] + acc
            kelvin = stress * inverse
            balanced = CHARACTER_KELVIN / (jnp.exp(CHARACTER_KELVIN / kelvin) - 1.0)
            teller = stress / (LANDAU_TELLER * jnp.exp(
                WHITE_LAW_FACTOR * jnp.exp(-jnp.log(kelvin) / 3.0)))
            source = q[0] * (balanced - q[5] * inverse) * teller
            scale = 1.0 / (60.0 * (face_area * height * spacing))
            for c in range(6):
                change = -(div[c] * scale) - q[c] * ratio
                if c == 5:
                    change = change + source
                out_ref[c, :, pl.ds(o, CHUNK)] = q[c] + dt * change
            return carry

        lax.fori_loop(0, length // CHUNK, body, 0)

    return kernel


def update(state, xlo, xhi, yhalo, geo, planes, total_rows, dt):
    columns = state.shape[1]
    length = state.shape[2]
    kern = make_kernel(columns, length, planes, total_rows, dt)
    vmem = pl.BlockSpec(memory_space=pltpu.VMEM)
    return pl.pallas_call(
        kern,
        out_shape=jax.ShapeDtypeStruct((6, columns, length), jnp.float32),
        in_specs=[vmem] * 5,
        out_specs=vmem,
        scratch_shapes=[
            pltpu.VMEM((6, columns + 2 * XPAD, length), jnp.float32),
            pltpu.VMEM((6, columns, length + 2 * PAD), jnp.float32),
            pltpu.VMEM((6, 6, columns + 2 * XPAD, CHUNK), jnp.float32),
        ],
    )(state, xlo, xhi, yhalo, geo)


def shifted(block, axis, forward, cyclic=False):
    count = lax.axis_size(axis)
    pairs = [(i, i + 1) for i in range(count - 1)]
    if cyclic and count > 1:
        pairs.append((count - 1, 0))
    if not forward:
        pairs = [(target, source) for source, target in pairs]
    return lax.ppermute(block, axis, pairs)


def broadcast(array, axis, holders, fanouts):
    count = lax.axis_size(axis)
    index = lax.axis_index(axis)
    for fanout in fanouts:
        if len(holders) >= count:
            break
        waiting = [i for i in range(count) if i not in holders]
        targets = jnp.zeros((), jnp.bool_)
        arrived = array
        reached = []
        for _ in range(fanout):
            pairs = list(zip(holders, waiting))
            waiting = waiting[len(pairs) :]
            if not pairs:
                break
            received = lax.ppermute(array, axis, pairs)
            hit = jnp.zeros((), jnp.bool_)
            for _, target in pairs:
                hit = hit | (index == target)
            arrived = jnp.where(hit, received, arrived)
            reached = reached + [target for _, target in pairs]
        array = arrived
        holders = holders + reached
    return array


def zshift(values, offset, planes):
    length = values.shape[-1]
    plane_at = jnp.arange(length, dtype=jnp.int32) % planes
    if offset > 0:
        return jnp.where(
            plane_at >= offset,
            jnp.roll(values, offset, axis=-1),
            jnp.roll(values, offset - planes, axis=-1),
        )
    return jnp.where(
        plane_at < planes + offset,
        jnp.roll(values, offset, axis=-1),
        jnp.roll(values, offset + planes, axis=-1),
    )


def primitives(conserved):
    specific_volume_inverse = conserved[0]
    vel_x = conserved[1] / specific_volume_inverse
    vel_y = conserved[2] / specific_volume_inverse
    vel_z = conserved[3] / specific_volume_inverse
    thermodynamic_stress = (HEAT_RATIO - 1.0) * (
        conserved[4]
        - 0.5 * (conserved[1] * vel_x + conserved[2] * vel_y + conserved[3] * vel_z)
        - conserved[5]
    )
    sound_speed = jnp.sqrt(HEAT_RATIO * thermodynamic_stress / specific_volume_inverse)
    return (specific_volume_inverse, vel_x, vel_y, vel_z, thermodynamic_stress, sound_speed)


def slopes(height_ext, planes):
    columns = height_ext.shape[0] - 6
    slope_x = (
        height_ext[1 : columns + 1]
        - 8.0 * height_ext[2 : columns + 2]
        + 8.0 * height_ext[4 : columns + 4]
        - height_ext[5 : columns + 5]
    ) / (12.0 * STREAM_STEP)
    height = height_ext[3 : columns + 3]
    slope_z = (
        zshift(height, 2, planes)
        - 8.0 * zshift(height, 1, planes)
        + 8.0 * zshift(height, -1, planes)
        - zshift(height, -2, planes)
    ) / (12.0 * SPAN_STEP)
    return (slope_x, slope_z)


def shock_speed(top_row, slope_x, slope_z):
    specific_volume_inverse, vel_x, vel_y, vel_z, thermodynamic_stress, sound_speed = primitives(
        top_row
    )
    tilt_norm = jnp.sqrt(1.0 + slope_x * slope_x + slope_z * slope_z)
    normal = (vel_y - vel_x * slope_x - vel_z * slope_z) / tilt_norm
    sine_sq = slope_x * slope_x / (tilt_norm * tilt_norm)
    jump_pressure = FREE_PRESSURE * (
        1.0 + 2.0 * HEAT_RATIO / (HEAT_RATIO + 1.0) * (FREE_MACH * FREE_MACH * sine_sq - 1.0)
    )
    return tilt_norm * (
        normal + (jump_pressure - thermodynamic_stress) / (specific_volume_inverse * sound_speed)
    )


def wall_ghosts(first_rows, blowing, planes):
    mirror = jnp.concatenate(
        [
            first_rows[..., 2 * planes : 3 * planes],
            first_rows[..., planes : 2 * planes],
            first_rows[..., 0:planes],
        ],
        axis=-1,
    )
    blown_y = 2.0 * jnp.tile(blowing, (1, 3)) - mirror[2]
    stagnation_enthalpy_sum = (
        mirror[4] + 0.5 * (blown_y * blown_y - mirror[2] * mirror[2]) / mirror[0]
    )
    return jnp.stack([mirror[0], mirror[1], blown_y, mirror[3], stagnation_enthalpy_sum, mirror[5]])


def wall_flux(wall_segment, segment_level, blow_table):
    seg_hit = wall_segment[:, None] == jnp.arange(segment_level.shape[0], dtype=jnp.int32)[None, :]
    levels = jnp.sum(jnp.where(seg_hit, segment_level[None, :], 0), axis=1)
    level_hit = levels[:, None] == jnp.arange(blow_table.shape[0], dtype=jnp.int32)[None, :]
    return jnp.sum(jnp.where(level_hit[:, :, None], blow_table[None, :, :], 0.0), axis=1)


def replicate_lanes(small, planes):
    pick = (
        jnp.arange(LANES, dtype=jnp.int32)[None, :] % planes
        == jnp.arange(planes, dtype=jnp.int32)[:, None]
    ).astype(jnp.float32)
    return jnp.dot(small, pick, precision=lax.Precision.HIGHEST, preferred_element_type=jnp.float32)


def shards(state, shock_height, wall_segment, segment_level, blow_table):
    planes = blow_table.shape[1]
    columns = state.shape[1]
    length = state.shape[2]
    row_count = length // planes
    col_devs = lax.axis_size("gx")
    row_devs = lax.axis_size("gy")
    col_dev = lax.axis_index("gx")
    row_dev = lax.axis_index("gy")
    total_rows = row_count * row_devs
    band = HALO * planes

    def pack(cols, heights):
        extra = jnp.zeros((1, HALO, length), jnp.float32)
        extra = lax.dynamic_update_slice(extra, heights[None], (0, 0, 0))
        return jnp.concatenate([cols, extra], axis=0)

    from_low = shifted(pack(state[:, columns - HALO :], shock_height[columns - HALO :]), "gx", True)
    from_high = shifted(pack(state[:, :HALO], shock_height[:HALO]), "gx", False)
    below = shifted(state[..., length - band :], "gy", True, cyclic=True)
    above = shifted(
        jnp.concatenate([state[..., :band], state[..., length - planes :]], axis=2), "gy", False
    )

    low_height = jnp.where(
        col_dev == 0, jnp.broadcast_to(shock_height[:1], (HALO, planes)), from_low[6, :, :planes]
    )
    high_height = jnp.where(
        col_dev == col_devs - 1,
        jnp.broadcast_to(shock_height[columns - 1 :], (HALO, planes)),
        from_high[6, :, :planes],
    )
    height_ext = jnp.concatenate([low_height, shock_height, high_height], axis=0)
    slope_x, slope_z = slopes(height_ext, planes)

    top_seed = jnp.where(
        row_dev == row_devs - 1,
        state[..., length - planes :],
        jnp.where(row_dev == 0, below[..., band - planes :], above[..., band:]),
    )
    seeded = sorted({row_devs - 1, 0, max(row_devs - 2, 0)}, reverse=True)
    top_row = broadcast(top_seed, "gy", seeded, (2, 1, 1, 1, 1))
    shock_rate = shock_speed(top_row, slope_x, slope_z)

    blowing = wall_flux(wall_segment, segment_level, blow_table)
    ghost_below = jnp.where(row_dev == 0, wall_ghosts(state[..., :band], blowing, planes), below)
    ghost_above = jnp.where(
        row_dev == row_devs - 1, jnp.tile(state[..., length - planes :], (1, 1, HALO + 1)), above
    )
    yhalo = jnp.stack([jnp.concatenate([ghost_below[..., : PAD - band], ghost_below], axis=2), ghost_above])

    height = shock_height
    height_x = jnp.concatenate(
        [
            jnp.broadcast_to(height_ext[:1], (XPAD - HALO, planes)),
            height_ext,
            jnp.broadcast_to(height_ext[-1:], (XPAD - HALO, planes)),
        ],
        axis=0,
    )
    small = jnp.concatenate(
        [height_x, slope_x, slope_z, shock_rate, shock_rate / height, height], axis=0
    )
    geo = replicate_lanes(small, planes)
    state_new = update(
        state,
        from_low,
        from_high,
        yhalo,
        geo,
        planes,
        total_rows,
        COURANT / total_rows,
    )
    shock_new = shock_height + COURANT / total_rows * shock_rate
    return (state_new, shock_new)


def solution(mesh):
    in_specs = (P(None, "gx", "gy"), P("gx", None), P("gx"), P(), P())
    out_specs = (P(None, "gx", "gy"), P("gx", None))
    return jax.shard_map(shards, mesh=mesh, in_specs=in_specs, out_specs=out_specs, check_vma=False)
```

```python
import math

import jax
import jax.numpy as jnp
from jax import lax
from jax.experimental import pallas as pl
from jax.experimental.pallas import tpu as pltpu
from jax.sharding import PartitionSpec as P

HEAT_RATIO = 1.4
STREAM_STEP = 0.05
SPAN_STEP = 0.05
STRETCH_RATE = 2.0
CHARACTER_KELVIN = 3.0
WHITE_LAW_FACTOR = 1.0
LANDAU_TELLER = 0.002
FREE_PRESSURE = 0.1
FREE_MACH = 6.0
COURANT = 0.05

FLUX_WEIGHTS = (45.0, -9.0, 1.0)
SPEED_WEIGHTS = (20.0, -15.0, 6.0, -1.0)
CHUNK = 512
PAD = 128
HALO = 3
XPAD = 8
LANES = 128


def kernel_primitives(q):
    inverse = 1.0 / q[0]
    vel_x = q[1] * inverse
    vel_y = q[2] * inverse
    vel_z = q[3] * inverse
    stress = (HEAT_RATIO - 1.0) * (q[4] - 0.5 * (q[1] * vel_x + q[2] * vel_y + q[3] * vel_z) - q[5])
    sound = jnp.sqrt(HEAT_RATIO * stress * inverse)
    return inverse, vel_x, vel_y, vel_z, stress, sound


def pair_terms(flux, damped, t):
    odd = FLUX_WEIGHTS[t - 1]
    even = SPEED_WEIGHTS[t]
    odd_part = flux if odd == 1.0 else odd * flux
    if even == -1.0:
        return odd_part - damped, -(odd_part + damped)
    even_part = even * damped
    return even_part + odd_part, even_part - odd_part


def lane_tile(values, width):
    return jnp.concatenate([values] * (width // values.shape[-1]), axis=-1)


def stretch_factors(rows, total_rows):
    growth = jnp.exp(STRETCH_RATE * (rows + 0.5) / total_rows)
    denominator = math.exp(STRETCH_RATE) - 1.0
    return (growth - 1.0) / denominator, STRETCH_RATE * growth / (total_rows * denominator)


def make_kernel(columns, length, planes, total_rows, dt):
    width = CHUNK + 2 * PAD
    face_area = STREAM_STEP * SPAN_STEP
    xrows = columns + 2 * XPAD

    def kernel(state_ref, xlo_ref, xhi_ref, yhalo_ref, geo_ref,
               out_ref, qx_ref, qy_ref, pair_ref):
        col_dev = lax.axis_index("gx")
        first_row = lax.axis_index("gy") * (length // planes)
        for c in range(6):
            qx_ref[c, 0:XPAD, :] = state_ref[c, 0:XPAD, :]
            qx_ref[c, XPAD:XPAD + columns, :] = state_ref[c]
            qx_ref[c, XPAD + columns:, :] = state_ref[c, columns - XPAD:, :]
            qx_ref[c, XPAD - HALO:XPAD, :] = xlo_ref[c]
            qx_ref[c, XPAD + columns:XPAD + columns + HALO, :] = xhi_ref[c]
            qy_ref[c, :, 0:PAD] = yhalo_ref[0, c]
            qy_ref[c, :, PAD:PAD + length] = state_ref[c]
            qy_ref[c, :, PAD + length:] = yhalo_ref[1, c, :, 0:PAD]

        @pl.when(col_dev == 0)
        def _():
            for c in range(6):
                qx_ref[c, XPAD - HALO:XPAD, :] = jnp.broadcast_to(state_ref[c, 0:1, :], (HALO, length))

        @pl.when(col_dev == lax.axis_size("gx") - 1)
        def _():
            for c in range(6):
                qx_ref[c, XPAD + columns:XPAD + columns + HALO, :] = jnp.broadcast_to(
                    state_ref[c, columns - 1:columns, :], (HALO, length))

        height_x = lane_tile(geo_ref[0:xrows, :], CHUNK)
        slope_x = lane_tile(geo_ref[xrows:xrows + columns, :], width)
        slope_z = lane_tile(geo_ref[xrows + columns:xrows + 2 * columns, :], width)
        rate = lane_tile(geo_ref[xrows + 2 * columns:xrows + 3 * columns, :], width)
        ratio = lane_tile(geo_ref[xrows + 3 * columns:xrows + 4 * columns, :], CHUNK)
        height = lane_tile(geo_ref[xrows + 4 * columns:xrows + 5 * columns, :], CHUNK)
        lane = lax.broadcasted_iota(jnp.int32, (columns, CHUNK), 1) % planes
        lane_in = lax.broadcasted_iota(jnp.int32, (1, CHUNK), 1)
        lane_out = lax.broadcasted_iota(jnp.int32, (1, width), 1)

        def body(k, carry):
            o = pl.multiple_of(k * CHUNK, CHUNK)
            rows_in = (first_row + (o + lane_in) // planes).astype(jnp.float32)
            spacing = stretch_factors(rows_in, total_rows)[1]
            rows_out = (first_row - PAD // planes + (o + lane_out) // planes).astype(jnp.float32)
            eta = stretch_factors(rows_out, total_rows)[0]
            xa = [qx_ref[c, :, pl.ds(o, CHUNK)] for c in range(6)]
            inverse, vel_x, vel_y, vel_z, stress, sound = kernel_primitives(xa)
            metric = STREAM_STEP * height_x * spacing
            fluxes = [xa[1], xa[1] * vel_x + stress, xa[2] * vel_x, xa[3] * vel_x,
                      (xa[4] + stress) * vel_x, xa[5] * vel_x]
            speed = (jnp.abs(vel_x) + sound) * metric
            div = []
            for c in range(6):
                flux = fluxes[c] * metric
                damped = speed * xa[c]
                for t in range(1, 4):
                    up, down = pair_terms(flux, damped, t)
                    pair_ref[c, 2 * t - 2] = up
                    pair_ref[c, 2 * t - 1] = down
                acc = SPEED_WEIGHTS[0] * damped[XPAD:XPAD + columns]
                for t in range(1, 4):
                    acc = acc + pair_ref[c, 2 * t - 2, pl.ds(XPAD + t, columns), :]
                    acc = acc + pair_ref[c, 2 * t - 1, pl.ds(XPAD - t, columns), :]
                div.append(acc)
            ya = [qy_ref[c, :, pl.ds(o, width)] for c in range(6)]
            inverse, vel_x, vel_y, vel_z, stress, sound = kernel_primitives(ya)
            scaled = -face_area * eta
            metric_x = scaled * slope_x
            metric_z = scaled * slope_z
            metric_t = scaled * rate
            contra = metric_t + metric_x * vel_x + face_area * vel_y + metric_z * vel_z
            fluxes = [ya[0] * contra, ya[1] * contra + metric_x * stress,
                      ya[2] * contra + face_area * stress, ya[3] * contra + metric_z * stress,
                      (ya[4] + stress) * contra - metric_t * stress, ya[5] * contra]
            speed = jnp.abs(contra) + sound * jnp.sqrt(
                metric_x * metric_x + face_area * face_area + metric_z * metric_z)
            for c in range(6):
                damped = speed * ya[c]
                acc = SPEED_WEIGHTS[0] * damped
                for t in range(1, 4):
                    up, down = pair_terms(fluxes[c], damped, t)
                    acc = acc + pltpu.roll(up, (-planes * t) % width, 1) + pltpu.roll(down, planes * t, 1)
                div[c] = div[c] + acc[:, PAD:PAD + CHUNK]
            q = [v[:, PAD:PAD + CHUNK] for v in ya]
            inverse = inverse[:, PAD:PAD + CHUNK]
            vel_z = vel_z[:, PAD:PAD + CHUNK]
            stress = stress[:, PAD:PAD + CHUNK]
            sound = sound[:, PAD:PAD + CHUNK]
            metric = STREAM_STEP * height * spacing
            fluxes = [q[3], q[1] * vel_z, q[2] * vel_z, q[3] * vel_z + stress,
                      (q[4] + stress) * vel_z, q[5] * vel_z]
            speed = (jnp.abs(vel_z) + sound) * metric
            for c in range(6):
                damped = speed * q[c]
                acc = SPEED_WEIGHTS[0] * damped
                for t in range(1, 4):
                    up, down = pair_terms(fluxes[c] * metric, damped, t)
                    up = jnp.where(lane < planes - t, pltpu.roll(up, CHUNK - t, 1),
                                   pltpu.roll(up, planes - t, 1))
                    down = jnp.where(lane >= t, pltpu.roll(down, t, 1),
                                     pltpu.roll(down, CHUNK - planes + t, 1))
                    acc = acc + up + down
                div[c] = div[c] + acc
            kelvin = stress * inverse
            balanced = CHARACTER_KELVIN / (jnp.exp(CHARACTER_KELVIN / kelvin) - 1.0)
            teller = stress / (LANDAU_TELLER * jnp.exp(
                WHITE_LAW_FACTOR * jnp.exp(-jnp.log(kelvin) / 3.0)))
            source = q[0] * (balanced - q[5] * inverse) * teller
            scale = 1.0 / (60.0 * (face_area * height * spacing))
            for c in range(6):
                change = -(div[c] * scale) - q[c] * ratio
                if c == 5:
                    change = change + source
                out_ref[c, :, pl.ds(o, CHUNK)] = q[c] + dt * change
            return carry

        lax.fori_loop(0, length // CHUNK, body, 0)

    return kernel


def update(state, xlo, xhi, yhalo, geo, planes, total_rows, dt):
    columns = state.shape[1]
    length = state.shape[2]
    kern = make_kernel(columns, length, planes, total_rows, dt)
    vmem = pl.BlockSpec(memory_space=pltpu.VMEM)
    return pl.pallas_call(
        kern,
        out_shape=jax.ShapeDtypeStruct((6, columns, length), jnp.float32),
        in_specs=[vmem] * 5,
        out_specs=vmem,
        scratch_shapes=[
            pltpu.VMEM((6, columns + 2 * XPAD, length), jnp.float32),
            pltpu.VMEM((6, columns, length + 2 * PAD), jnp.float32),
            pltpu.VMEM((6, 6, columns + 2 * XPAD, CHUNK), jnp.float32),
        ],
    )(state, xlo, xhi, yhalo, geo)


def shifted(block, axis, forward, cyclic=False):
    count = lax.axis_size(axis)
    pairs = [(i, i + 1) for i in range(count - 1)]
    if cyclic and count > 1:
        pairs.append((count - 1, 0))
    if not forward:
        pairs = [(target, source) for source, target in pairs]
    return lax.ppermute(block, axis, pairs)


def broadcast(array, axis, holders, fanouts, tied=None):
    count = lax.axis_size(axis)
    index = lax.axis_index(axis)
    for step, fanout in enumerate(fanouts):
        if step == 1 and tied is not None:
            array, tied = lax.optimization_barrier((array, tied))
        if len(holders) >= count:
            break
        waiting = [i for i in range(count) if i not in holders]
        targets = jnp.zeros((), jnp.bool_)
        arrived = array
        reached = []
        for _ in range(fanout):
            pairs = list(zip(holders, waiting))
            waiting = waiting[len(pairs) :]
            if not pairs:
                break
            received = lax.ppermute(array, axis, pairs)
            hit = jnp.zeros((), jnp.bool_)
            for _, target in pairs:
                hit = hit | (index == target)
            arrived = jnp.where(hit, received, arrived)
            reached = reached + [target for _, target in pairs]
        array = arrived
        holders = holders + reached
    return array, tied


def zshift(values, offset, planes):
    length = values.shape[-1]
    plane_at = jnp.arange(length, dtype=jnp.int32) % planes
    if offset > 0:
        return jnp.where(
            plane_at >= offset,
            jnp.roll(values, offset, axis=-1),
            jnp.roll(values, offset - planes, axis=-1),
        )
    return jnp.where(
        plane_at < planes + offset,
        jnp.roll(values, offset, axis=-1),
        jnp.roll(values, offset + planes, axis=-1),
    )


def primitives(conserved):
    specific_volume_inverse = conserved[0]
    vel_x = conserved[1] / specific_volume_inverse
    vel_y = conserved[2] / specific_volume_inverse
    vel_z = conserved[3] / specific_volume_inverse
    thermodynamic_stress = (HEAT_RATIO - 1.0) * (
        conserved[4]
        - 0.5 * (conserved[1] * vel_x + conserved[2] * vel_y + conserved[3] * vel_z)
        - conserved[5]
    )
    sound_speed = jnp.sqrt(HEAT_RATIO * thermodynamic_stress / specific_volume_inverse)
    return (specific_volume_inverse, vel_x, vel_y, vel_z, thermodynamic_stress, sound_speed)


def slopes(height_ext, planes):
    columns = height_ext.shape[0] - 6
    slope_x = (
        height_ext[1 : columns + 1]
        - 8.0 * height_ext[2 : columns + 2]
        + 8.0 * height_ext[4 : columns + 4]
        - height_ext[5 : columns + 5]
    ) / (12.0 * STREAM_STEP)
    height = height_ext[3 : columns + 3]
    slope_z = (
        zshift(height, 2, planes)
        - 8.0 * zshift(height, 1, planes)
        + 8.0 * zshift(height, -1, planes)
        - zshift(height, -2, planes)
    ) / (12.0 * SPAN_STEP)
    return (slope_x, slope_z)


def shock_speed(top_row, slope_x, slope_z):
    specific_volume_inverse, vel_x, vel_y, vel_z, thermodynamic_stress, sound_speed = primitives(
        top_row
    )
    tilt_norm = jnp.sqrt(1.0 + slope_x * slope_x + slope_z * slope_z)
    normal = (vel_y - vel_x * slope_x - vel_z * slope_z) / tilt_norm
    sine_sq = slope_x * slope_x / (tilt_norm * tilt_norm)
    jump_pressure = FREE_PRESSURE * (
        1.0 + 2.0 * HEAT_RATIO / (HEAT_RATIO + 1.0) * (FREE_MACH * FREE_MACH * sine_sq - 1.0)
    )
    return tilt_norm * (
        normal + (jump_pressure - thermodynamic_stress) / (specific_volume_inverse * sound_speed)
    )


def wall_ghosts(first_rows, blowing, planes):
    mirror = jnp.concatenate(
        [
            first_rows[..., 2 * planes : 3 * planes],
            first_rows[..., planes : 2 * planes],
            first_rows[..., 0:planes],
        ],
        axis=-1,
    )
    blown_y = 2.0 * jnp.tile(blowing, (1, 3)) - mirror[2]
    stagnation_enthalpy_sum = (
        mirror[4] + 0.5 * (blown_y * blown_y - mirror[2] * mirror[2]) / mirror[0]
    )
    return jnp.stack([mirror[0], mirror[1], blown_y, mirror[3], stagnation_enthalpy_sum, mirror[5]])


def wall_flux(wall_segment, segment_level, blow_table):
    seg_hit = wall_segment[:, None] == jnp.arange(segment_level.shape[0], dtype=jnp.int32)[None, :]
    levels = jnp.sum(jnp.where(seg_hit, segment_level[None, :], 0), axis=1)
    level_hit = levels[:, None] == jnp.arange(blow_table.shape[0], dtype=jnp.int32)[None, :]
    return jnp.sum(jnp.where(level_hit[:, :, None], blow_table[None, :, :], 0.0), axis=1)


def replicate_lanes(small, planes):
    pick = (
        jnp.arange(LANES, dtype=jnp.int32)[None, :] % planes
        == jnp.arange(planes, dtype=jnp.int32)[:, None]
    ).astype(jnp.float32)
    return jnp.dot(small, pick, precision=lax.Precision.HIGHEST, preferred_element_type=jnp.float32)


def shards(state, shock_height, wall_segment, segment_level, blow_table):
    planes = blow_table.shape[1]
    columns = state.shape[1]
    length = state.shape[2]
    row_count = length // planes
    col_devs = lax.axis_size("gx")
    row_devs = lax.axis_size("gy")
    col_dev = lax.axis_index("gx")
    row_dev = lax.axis_index("gy")
    total_rows = row_count * row_devs
    band = HALO * planes

    def pack(cols, heights):
        extra = jnp.zeros((1, HALO, length), jnp.float32)
        extra = lax.dynamic_update_slice(extra, heights[None], (0, 0, 0))
        return jnp.concatenate([cols, extra], axis=0)

    below = shifted(state[..., length - band :], "gy", True, cyclic=True)
    above = shifted(
        jnp.concatenate([state[..., :band], state[..., length - planes :]], axis=2), "gy", False
    )

    top_seed = jnp.where(
        row_dev == row_devs - 1,
        state[..., length - planes :],
        jnp.where(row_dev == 0, below[..., band - planes :], above[..., band:]),
    )
    seeded = sorted({row_devs - 1, 0, max(row_devs - 2, 0)}, reverse=True)
    sends = (
        pack(state[:, columns - HALO :], shock_height[columns - HALO :]),
        pack(state[:, :HALO], shock_height[:HALO]),
    )
    top_row, sends = broadcast(top_seed, "gy", seeded, (2, 1, 1, 1, 1), sends)
    from_low = shifted(sends[0], "gx", True)
    from_high = shifted(sends[1], "gx", False)
    low_height = jnp.where(
        col_dev == 0, jnp.broadcast_to(shock_height[:1], (HALO, planes)), from_low[6, :, :planes]
    )
    high_height = jnp.where(
        col_dev == col_devs - 1,
        jnp.broadcast_to(shock_height[columns - 1 :], (HALO, planes)),
        from_high[6, :, :planes],
    )
    height_ext = jnp.concatenate([low_height, shock_height, high_height], axis=0)
    slope_x, slope_z = slopes(height_ext, planes)

    shock_rate = shock_speed(top_row, slope_x, slope_z)

    blowing = wall_flux(wall_segment, segment_level, blow_table)
    ghost_below = jnp.where(row_dev == 0, wall_ghosts(state[..., :band], blowing, planes), below)
    ghost_above = jnp.where(
        row_dev == row_devs - 1, jnp.tile(state[..., length - planes :], (1, 1, HALO + 1)), above
    )
    yhalo = jnp.stack([jnp.concatenate([ghost_below[..., : PAD - band], ghost_below], axis=2), ghost_above])

    height = shock_height
    height_x = jnp.concatenate(
        [
            jnp.broadcast_to(height_ext[:1], (XPAD - HALO, planes)),
            height_ext,
            jnp.broadcast_to(height_ext[-1:], (XPAD - HALO, planes)),
        ],
        axis=0,
    )
    small = jnp.concatenate(
        [height_x, slope_x, slope_z, shock_rate, shock_rate / height, height], axis=0
    )
    geo = replicate_lanes(small, planes)
    state_new = update(
        state,
        from_low,
        from_high,
        yhalo,
        geo,
        planes,
        total_rows,
        COURANT / total_rows,
    )
    shock_new = shock_height + COURANT / total_rows * shock_rate
    return (state_new, shock_new)


def solution(mesh):
    in_specs = (P(None, "gx", "gy"), P("gx", None), P("gx"), P(), P())
    out_specs = (P(None, "gx", "gy"), P("gx", None))
    return jax.shard_map(shards, mesh=mesh, in_specs=in_specs, out_specs=out_specs, check_vma=False)
```

```python
import math

import jax
import jax.numpy as jnp
from jax import lax
from jax.experimental import pallas as pl
from jax.experimental.pallas import tpu as pltpu
from jax.sharding import PartitionSpec as P

HEAT_RATIO = 1.4
STREAM_STEP = 0.05
SPAN_STEP = 0.05
STRETCH_RATE = 2.0
CHARACTER_KELVIN = 3.0
WHITE_LAW_FACTOR = 1.0
LANDAU_TELLER = 0.002
FREE_PRESSURE = 0.1
FREE_MACH = 6.0
COURANT = 0.05

FLUX_WEIGHTS = (45.0, -9.0, 1.0)
SPEED_WEIGHTS = (20.0, -15.0, 6.0, -1.0)
CHUNK = 512
PAD = 128
HALO = 3
XPAD = 8
LANES = 128


def kernel_primitives(q):
    inverse = 1.0 / q[0]
    vel_x = q[1] * inverse
    vel_y = q[2] * inverse
    vel_z = q[3] * inverse
    stress = (HEAT_RATIO - 1.0) * (q[4] - 0.5 * (q[1] * vel_x + q[2] * vel_y + q[3] * vel_z) - q[5])
    sound = jnp.sqrt(HEAT_RATIO * stress * inverse)
    return inverse, vel_x, vel_y, vel_z, stress, sound


def pair_terms(flux, damped, t):
    odd = FLUX_WEIGHTS[t - 1]
    even = SPEED_WEIGHTS[t]
    odd_part = flux if odd == 1.0 else odd * flux
    if even == -1.0:
        return odd_part - damped, -(odd_part + damped)
    even_part = even * damped
    return even_part + odd_part, even_part - odd_part


def lane_tile(values, width):
    return jnp.concatenate([values] * (width // values.shape[-1]), axis=-1)


def stretch_factors(rows, total_rows):
    growth = jnp.exp(STRETCH_RATE * (rows + 0.5) / total_rows)
    denominator = math.exp(STRETCH_RATE) - 1.0
    return (growth - 1.0) / denominator, STRETCH_RATE * growth / (total_rows * denominator)


def make_kernel(columns, length, planes, total_rows, dt):
    width = CHUNK + 2 * PAD
    face_area = STREAM_STEP * SPAN_STEP
    xrows = columns + 2 * XPAD

    def kernel(state_ref, xlo_ref, xhi_ref, yhalo_ref, geo_ref, top_ref, height_ref,
               out_ref, shock_ref, qx_ref, qy_ref, pair_ref):
        col_dev = lax.axis_index("gx")
        first_row = lax.axis_index("gy") * (length // planes)
        for c in range(6):
            qx_ref[c, 0:XPAD, :] = state_ref[c, 0:XPAD, :]
            qx_ref[c, XPAD:XPAD + columns, :] = state_ref[c]
            qx_ref[c, XPAD + columns:, :] = state_ref[c, columns - XPAD:, :]
            qx_ref[c, XPAD - HALO:XPAD, :] = xlo_ref[c]
            qx_ref[c, XPAD + columns:XPAD + columns + HALO, :] = xhi_ref[c]
            qy_ref[c, :, 0:PAD] = yhalo_ref[0, c]
            qy_ref[c, :, PAD:PAD + length] = state_ref[c]
            qy_ref[c, :, PAD + length:] = yhalo_ref[1, c, :, 0:PAD]

        @pl.when(col_dev == 0)
        def _():
            for c in range(6):
                qx_ref[c, XPAD - HALO:XPAD, :] = jnp.broadcast_to(state_ref[c, 0:1, :], (HALO, length))

        @pl.when(col_dev == lax.axis_size("gx") - 1)
        def _():
            for c in range(6):
                qx_ref[c, XPAD + columns:XPAD + columns + HALO, :] = jnp.broadcast_to(
                    state_ref[c, columns - 1:columns, :], (HALO, length))

        height_x = lane_tile(geo_ref[0:xrows, :], CHUNK)
        slope_x_row = geo_ref[xrows:xrows + columns, :]
        slope_z_row = geo_ref[xrows + columns:xrows + 2 * columns, :]
        height_row = geo_ref[xrows + 2 * columns:xrows + 3 * columns, :]
        group = lax.broadcasted_iota(jnp.int32, (columns, LANES), 1) // planes
        top = []
        for c in range(6):
            held = top_ref[c]
            spread = jnp.where(group == 0, pltpu.roll(held, planes, 1),
                               jnp.where(group == 1, pltpu.roll(held, 2 * planes, 1),
                                         jnp.where(group == 2, pltpu.roll(held, 3 * planes, 1), held)))
            top.append(spread)
        rate_row = shock_speed(top, slope_x_row, slope_z_row)
        shock_ref[...] = height_ref[...] + dt * rate_row[:, 0:planes]
        slope_x = lane_tile(slope_x_row, width)
        slope_z = lane_tile(slope_z_row, width)
        rate = lane_tile(rate_row, width)
        ratio = lane_tile(rate_row / height_row, CHUNK)
        height = lane_tile(height_row, CHUNK)
        lane = lax.broadcasted_iota(jnp.int32, (columns, CHUNK), 1) % planes
        lane_in = lax.broadcasted_iota(jnp.int32, (1, CHUNK), 1)
        lane_out = lax.broadcasted_iota(jnp.int32, (1, width), 1)

        def body(k, carry):
            o = pl.multiple_of(k * CHUNK, CHUNK)
            rows_in = (first_row + (o + lane_in) // planes).astype(jnp.float32)
            spacing = stretch_factors(rows_in, total_rows)[1]
            rows_out = (first_row - PAD // planes + (o + lane_out) // planes).astype(jnp.float32)
            eta = stretch_factors(rows_out, total_rows)[0]
            xa = [qx_ref[c, :, pl.ds(o, CHUNK)] for c in range(6)]
            inverse, vel_x, vel_y, vel_z, stress, sound = kernel_primitives(xa)
            metric = STREAM_STEP * height_x * spacing
            fluxes = [xa[1], xa[1] * vel_x + stress, xa[2] * vel_x, xa[3] * vel_x,
                      (xa[4] + stress) * vel_x, xa[5] * vel_x]
            speed = (jnp.abs(vel_x) + sound) * metric
            div = []
            for c in range(6):
                flux = fluxes[c] * metric
                damped = speed * xa[c]
                for t in range(1, 4):
                    up, down = pair_terms(flux, damped, t)
                    pair_ref[c, 2 * t - 2] = up
                    pair_ref[c, 2 * t - 1] = down
                acc = SPEED_WEIGHTS[0] * damped[XPAD:XPAD + columns]
                for t in range(1, 4):
                    acc = acc + pair_ref[c, 2 * t - 2, pl.ds(XPAD + t, columns), :]
                    acc = acc + pair_ref[c, 2 * t - 1, pl.ds(XPAD - t, columns), :]
                div.append(acc)
            ya = [qy_ref[c, :, pl.ds(o, width)] for c in range(6)]
            inverse, vel_x, vel_y, vel_z, stress, sound = kernel_primitives(ya)
            scaled = -face_area * eta
            metric_x = scaled * slope_x
            metric_z = scaled * slope_z
            metric_t = scaled * rate
            contra = metric_t + metric_x * vel_x + face_area * vel_y + metric_z * vel_z
            fluxes = [ya[0] * contra, ya[1] * contra + metric_x * stress,
                      ya[2] * contra + face_area * stress, ya[3] * contra + metric_z * stress,
                      (ya[4] + stress) * contra - metric_t * stress, ya[5] * contra]
            speed = jnp.abs(contra) + sound * jnp.sqrt(
                metric_x * metric_x + face_area * face_area + metric_z * metric_z)
            for c in range(6):
                damped = speed * ya[c]
                acc = SPEED_WEIGHTS[0] * damped
                for t in range(1, 4):
                    up, down = pair_terms(fluxes[c], damped, t)
                    acc = acc + pltpu.roll(up, (-planes * t) % width, 1) + pltpu.roll(down, planes * t, 1)
                div[c] = div[c] + acc[:, PAD:PAD + CHUNK]
            q = [v[:, PAD:PAD + CHUNK] for v in ya]
            inverse = inverse[:, PAD:PAD + CHUNK]
            vel_z = vel_z[:, PAD:PAD + CHUNK]
            stress = stress[:, PAD:PAD + CHUNK]
            sound = sound[:, PAD:PAD + CHUNK]
            metric = STREAM_STEP * height * spacing
            fluxes = [q[3], q[1] * vel_z, q[2] * vel_z, q[3] * vel_z + stress,
                      (q[4] + stress) * vel_z, q[5] * vel_z]
            speed = (jnp.abs(vel_z) + sound) * metric
            for c in range(6):
                damped = speed * q[c]
                acc = SPEED_WEIGHTS[0] * damped
                for t in range(1, 4):
                    up, down = pair_terms(fluxes[c] * metric, damped, t)
                    up = jnp.where(lane < planes - t, pltpu.roll(up, CHUNK - t, 1),
                                   pltpu.roll(up, planes - t, 1))
                    down = jnp.where(lane >= t, pltpu.roll(down, t, 1),
                                     pltpu.roll(down, CHUNK - planes + t, 1))
                    acc = acc + up + down
                div[c] = div[c] + acc
            kelvin = stress * inverse
            balanced = CHARACTER_KELVIN / (jnp.exp(CHARACTER_KELVIN / kelvin) - 1.0)
            teller = stress / (LANDAU_TELLER * jnp.exp(
                WHITE_LAW_FACTOR * jnp.exp(-jnp.log(kelvin) / 3.0)))
            source = q[0] * (balanced - q[5] * inverse) * teller
            scale = 1.0 / (60.0 * (face_area * height * spacing))
            for c in range(6):
                change = -(div[c] * scale) - q[c] * ratio
                if c == 5:
                    change = change + source
                out_ref[c, :, pl.ds(o, CHUNK)] = q[c] + dt * change
            return carry

        lax.fori_loop(0, length // CHUNK, body, 0)

    return kernel


def update(state, xlo, xhi, yhalo, geo, top, height, planes, total_rows, dt):
    columns = state.shape[1]
    length = state.shape[2]
    kern = make_kernel(columns, length, planes, total_rows, dt)
    vmem = pl.BlockSpec(memory_space=pltpu.VMEM)
    return pl.pallas_call(
        kern,
        out_shape=(
            jax.ShapeDtypeStruct((6, columns, length), jnp.float32),
            jax.ShapeDtypeStruct((columns, planes), jnp.float32),
        ),
        in_specs=[vmem] * 7,
        out_specs=(vmem, vmem),
        scratch_shapes=[
            pltpu.VMEM((6, columns + 2 * XPAD, length), jnp.float32),
            pltpu.VMEM((6, columns, length + 2 * PAD), jnp.float32),
            pltpu.VMEM((6, 6, columns + 2 * XPAD, CHUNK), jnp.float32),
        ],
    )(state, xlo, xhi, yhalo, geo, top, height)


def shifted(block, axis, forward, cyclic=False):
    count = lax.axis_size(axis)
    pairs = [(i, i + 1) for i in range(count - 1)]
    if cyclic and count > 1:
        pairs.append((count - 1, 0))
    if not forward:
        pairs = [(target, source) for source, target in pairs]
    return lax.ppermute(block, axis, pairs)


def broadcast(array, axis, holders, fanouts):
    count = lax.axis_size(axis)
    index = lax.axis_index(axis)
    for fanout in fanouts:
        if len(holders) >= count:
            break
        waiting = [i for i in range(count) if i not in holders]
        targets = jnp.zeros((), jnp.bool_)
        arrived = array
        reached = []
        for _ in range(fanout):
            pairs = list(zip(holders, waiting))
            waiting = waiting[len(pairs) :]
            if not pairs:
                break
            received = lax.ppermute(array, axis, pairs)
            hit = jnp.zeros((), jnp.bool_)
            for _, target in pairs:
                hit = hit | (index == target)
            arrived = jnp.where(hit, received, arrived)
            reached = reached + [target for _, target in pairs]
        array = arrived
        holders = holders + reached
    return array


def zshift(values, offset, planes):
    length = values.shape[-1]
    plane_at = jnp.arange(length, dtype=jnp.int32) % planes
    if offset > 0:
        return jnp.where(
            plane_at >= offset,
            jnp.roll(values, offset, axis=-1),
            jnp.roll(values, offset - planes, axis=-1),
        )
    return jnp.where(
        plane_at < planes + offset,
        jnp.roll(values, offset, axis=-1),
        jnp.roll(values, offset + planes, axis=-1),
    )


def primitives(conserved):
    specific_volume_inverse = conserved[0]
    vel_x = conserved[1] / specific_volume_inverse
    vel_y = conserved[2] / specific_volume_inverse
    vel_z = conserved[3] / specific_volume_inverse
    thermodynamic_stress = (HEAT_RATIO - 1.0) * (
        conserved[4]
        - 0.5 * (conserved[1] * vel_x + conserved[2] * vel_y + conserved[3] * vel_z)
        - conserved[5]
    )
    sound_speed = jnp.sqrt(HEAT_RATIO * thermodynamic_stress / specific_volume_inverse)
    return (specific_volume_inverse, vel_x, vel_y, vel_z, thermodynamic_stress, sound_speed)


def slopes(height_ext, planes):
    columns = height_ext.shape[0] - 6
    slope_x = (
        height_ext[1 : columns + 1]
        - 8.0 * height_ext[2 : columns + 2]
        + 8.0 * height_ext[4 : columns + 4]
        - height_ext[5 : columns + 5]
    ) / (12.0 * STREAM_STEP)
    height = height_ext[3 : columns + 3]
    slope_z = (
        zshift(height, 2, planes)
        - 8.0 * zshift(height, 1, planes)
        + 8.0 * zshift(height, -1, planes)
        - zshift(height, -2, planes)
    ) / (12.0 * SPAN_STEP)
    return (slope_x, slope_z)


def shock_speed(top_row, slope_x, slope_z):
    specific_volume_inverse, vel_x, vel_y, vel_z, thermodynamic_stress, sound_speed = primitives(
        top_row
    )
    tilt_norm = jnp.sqrt(1.0 + slope_x * slope_x + slope_z * slope_z)
    normal = (vel_y - vel_x * slope_x - vel_z * slope_z) / tilt_norm
    sine_sq = slope_x * slope_x / (tilt_norm * tilt_norm)
    jump_pressure = FREE_PRESSURE * (
        1.0 + 2.0 * HEAT_RATIO / (HEAT_RATIO + 1.0) * (FREE_MACH * FREE_MACH * sine_sq - 1.0)
    )
    return tilt_norm * (
        normal + (jump_pressure - thermodynamic_stress) / (specific_volume_inverse * sound_speed)
    )


def wall_ghosts(first_rows, blowing, planes):
    mirror = jnp.concatenate(
        [
            first_rows[..., 2 * planes : 3 * planes],
            first_rows[..., planes : 2 * planes],
            first_rows[..., 0:planes],
        ],
        axis=-1,
    )
    blown_y = 2.0 * jnp.tile(blowing, (1, 3)) - mirror[2]
    stagnation_enthalpy_sum = (
        mirror[4] + 0.5 * (blown_y * blown_y - mirror[2] * mirror[2]) / mirror[0]
    )
    return jnp.stack([mirror[0], mirror[1], blown_y, mirror[3], stagnation_enthalpy_sum, mirror[5]])


def wall_flux(wall_segment, segment_level, blow_table):
    seg_hit = wall_segment[:, None] == jnp.arange(segment_level.shape[0], dtype=jnp.int32)[None, :]
    levels = jnp.sum(jnp.where(seg_hit, segment_level[None, :], 0), axis=1)
    level_hit = levels[:, None] == jnp.arange(blow_table.shape[0], dtype=jnp.int32)[None, :]
    return jnp.sum(jnp.where(level_hit[:, :, None], blow_table[None, :, :], 0.0), axis=1)


def replicate_lanes(small, planes):
    pick = (
        jnp.arange(LANES, dtype=jnp.int32)[None, :] % planes
        == jnp.arange(planes, dtype=jnp.int32)[:, None]
    ).astype(jnp.float32)
    return jnp.dot(small, pick, precision=lax.Precision.HIGHEST, preferred_element_type=jnp.float32)


def shards(state, shock_height, wall_segment, segment_level, blow_table):
    planes = blow_table.shape[1]
    columns = state.shape[1]
    length = state.shape[2]
    row_count = length // planes
    col_devs = lax.axis_size("gx")
    row_devs = lax.axis_size("gy")
    col_dev = lax.axis_index("gx")
    row_dev = lax.axis_index("gy")
    total_rows = row_count * row_devs
    band = HALO * planes

    def pack(cols, heights):
        extra = jnp.zeros((1, HALO, length), jnp.float32)
        extra = lax.dynamic_update_slice(extra, heights[None], (0, 0, 0))
        return jnp.concatenate([cols, extra], axis=0)

    from_low = shifted(pack(state[:, columns - HALO :], shock_height[columns - HALO :]), "gx", True)
    from_high = shifted(pack(state[:, :HALO], shock_height[:HALO]), "gx", False)
    plane_lane = jnp.arange(PAD, dtype=jnp.int32)[None, None, :]
    top_block = state[..., length - PAD :]
    below = shifted(top_block, "gy", True, cyclic=True)
    above = shifted(jnp.where(plane_lane < band, state[..., :PAD], top_block), "gy", False)
    low_height = jnp.where(
        col_dev == 0, jnp.broadcast_to(shock_height[:1], (HALO, planes)), from_low[6, :, :planes]
    )
    high_height = jnp.where(
        col_dev == col_devs - 1,
        jnp.broadcast_to(shock_height[columns - 1 :], (HALO, planes)),
        from_high[6, :, :planes],
    )
    height_ext = jnp.concatenate([low_height, shock_height, high_height], axis=0)
    slope_x, slope_z = slopes(height_ext, planes)

    top_seed = jnp.where(row_dev == row_devs - 1, top_block, jnp.where(row_dev == 0, below, above))
    seeded = sorted({row_devs - 1, 0, max(row_devs - 2, 0)}, reverse=True)
    top_held = broadcast(top_seed, "gy", seeded, (2, 1, 1, 1, 1))

    blowing = wall_flux(wall_segment, segment_level, blow_table)
    wall_block = wall_ghosts(state[..., :band], blowing, planes)
    ghost_below = jnp.where(
        row_dev == 0, jnp.concatenate([wall_block[..., : PAD - band], wall_block], axis=2), below
    )
    ghost_above = jnp.where(
        row_dev == row_devs - 1, jnp.tile(state[..., length - planes :], (1, 1, PAD // planes)), above
    )
    yhalo = jnp.stack([ghost_below, ghost_above])

    height = shock_height
    height_x = jnp.concatenate(
        [
            jnp.broadcast_to(height_ext[:1], (XPAD - HALO, planes)),
            height_ext,
            jnp.broadcast_to(height_ext[-1:], (XPAD - HALO, planes)),
        ],
        axis=0,
    )
    small = jnp.concatenate([height_x, slope_x, slope_z, height], axis=0)
    geo = replicate_lanes(small, planes)
    state_new, shock_new = update(
        state,
        from_low,
        from_high,
        yhalo,
        geo,
        top_held,
        shock_height,
        planes,
        total_rows,
        COURANT / total_rows,
    )
    return (state_new, shock_new)


def solution(mesh):
    in_specs = (P(None, "gx", "gy"), P("gx", None), P("gx"), P(), P())
    out_specs = (P(None, "gx", "gy"), P("gx", None))
    return jax.shard_map(shards, mesh=mesh, in_specs=in_specs, out_specs=out_specs, check_vma=False)
```

```python
import math

import jax
import jax.numpy as jnp
from jax import lax
from jax.experimental import pallas as pl
from jax.experimental.pallas import tpu as pltpu
from jax.sharding import PartitionSpec as P

HEAT_RATIO = 1.4
STREAM_STEP = 0.05
SPAN_STEP = 0.05
STRETCH_RATE = 2.0
CHARACTER_KELVIN = 3.0
WHITE_LAW_FACTOR = 1.0
LANDAU_TELLER = 0.002
FREE_PRESSURE = 0.1
FREE_MACH = 6.0
COURANT = 0.05

FLUX_WEIGHTS = (45.0, -9.0, 1.0)
SPEED_WEIGHTS = (20.0, -15.0, 6.0, -1.0)
CHUNK = 512
PAD = 128
HALO = 3
XPAD = 8
LANES = 128


def kernel_primitives(q):
    inverse = 1.0 / q[0]
    vel_x = q[1] * inverse
    vel_y = q[2] * inverse
    vel_z = q[3] * inverse
    stress = (HEAT_RATIO - 1.0) * (q[4] - 0.5 * (q[1] * vel_x + q[2] * vel_y + q[3] * vel_z) - q[5])
    sound = jnp.sqrt(HEAT_RATIO * stress * inverse)
    return inverse, vel_x, vel_y, vel_z, stress, sound


def pair_terms(flux, damped, t):
    odd = FLUX_WEIGHTS[t - 1]
    even = SPEED_WEIGHTS[t]
    odd_part = flux if odd == 1.0 else odd * flux
    if even == -1.0:
        return odd_part - damped, -(odd_part + damped)
    even_part = even * damped
    return even_part + odd_part, even_part - odd_part


def lane_tile(values, width):
    return jnp.concatenate([values] * (width // values.shape[-1]), axis=-1)


def stretch_factors(rows, total_rows):
    growth = jnp.exp(STRETCH_RATE * (rows + 0.5) / total_rows)
    denominator = math.exp(STRETCH_RATE) - 1.0
    return (growth - 1.0) / denominator, STRETCH_RATE * growth / (total_rows * denominator)


def make_kernel(columns, length, planes, total_rows, dt, targets):
    width = CHUNK + 2 * PAD
    face_area = STREAM_STEP * SPAN_STEP
    xrows = columns + 2 * XPAD

    def kernel(state_ref, xlo_ref, xhi_ref, yhalo_ref, geo_ref, before_ref, last_ref, height_ref,
               out_ref, shock_ref, qx_ref, qy_ref, pair_ref):
        col_dev = lax.axis_index("gx")
        first_row = lax.axis_index("gy") * (length // planes)
        for c in range(6):
            qx_ref[c, 0:XPAD, :] = state_ref[c, 0:XPAD, :]
            qx_ref[c, XPAD:XPAD + columns, :] = state_ref[c]
            qx_ref[c, XPAD + columns:, :] = state_ref[c, columns - XPAD:, :]
            qx_ref[c, XPAD - HALO:XPAD, :] = xlo_ref[c]
            qx_ref[c, XPAD + columns:XPAD + columns + HALO, :] = xhi_ref[c]
            qy_ref[c, :, 0:PAD] = yhalo_ref[0, c]
            qy_ref[c, :, PAD:PAD + length] = state_ref[c]
            qy_ref[c, :, PAD + length:] = yhalo_ref[1, c, :, 0:PAD]

        @pl.when(col_dev == 0)
        def _():
            for c in range(6):
                qx_ref[c, XPAD - HALO:XPAD, :] = jnp.broadcast_to(state_ref[c, 0:1, :], (HALO, length))

        @pl.when(col_dev == lax.axis_size("gx") - 1)
        def _():
            for c in range(6):
                qx_ref[c, XPAD + columns:XPAD + columns + HALO, :] = jnp.broadcast_to(
                    state_ref[c, columns - 1:columns, :], (HALO, length))

        height_x = lane_tile(geo_ref[0:xrows, :], CHUNK)
        slope_x_row = geo_ref[xrows:xrows + columns, :]
        slope_z_row = geo_ref[xrows + columns:xrows + 2 * columns, :]
        height_row = geo_ref[xrows + 2 * columns:xrows + 3 * columns, :]
        group = lax.broadcasted_iota(jnp.int32, (columns, LANES), 1) // planes
        top = []
        row_dev = lax.axis_index("gy")
        hit = jnp.zeros((columns, LANES), jnp.bool_)
        for target in targets:
            hit = hit | (row_dev == target)
        for c in range(6):
            held = jnp.where(hit, last_ref[c], before_ref[c])
            spread = jnp.where(group == 0, pltpu.roll(held, planes, 1),
                               jnp.where(group == 1, pltpu.roll(held, 2 * planes, 1),
                                         jnp.where(group == 2, pltpu.roll(held, 3 * planes, 1), held)))
            top.append(spread)
        rate_row = shock_speed(top, slope_x_row, slope_z_row)
        shock_ref[...] = height_ref[...] + dt * rate_row[:, 0:planes]
        slope_x = lane_tile(slope_x_row, width)
        slope_z = lane_tile(slope_z_row, width)
        rate = lane_tile(rate_row, width)
        ratio = lane_tile(rate_row / height_row, CHUNK)
        height = lane_tile(height_row, CHUNK)
        lane = lax.broadcasted_iota(jnp.int32, (columns, CHUNK), 1) % planes
        lane_in = lax.broadcasted_iota(jnp.int32, (1, CHUNK), 1)
        lane_out = lax.broadcasted_iota(jnp.int32, (1, width), 1)

        def body(k, carry):
            o = pl.multiple_of(k * CHUNK, CHUNK)
            rows_in = (first_row + (o + lane_in) // planes).astype(jnp.float32)
            spacing = stretch_factors(rows_in, total_rows)[1]
            rows_out = (first_row - PAD // planes + (o + lane_out) // planes).astype(jnp.float32)
            eta = stretch_factors(rows_out, total_rows)[0]
            xa = [qx_ref[c, :, pl.ds(o, CHUNK)] for c in range(6)]
            inverse, vel_x, vel_y, vel_z, stress, sound = kernel_primitives(xa)
            metric = STREAM_STEP * height_x * spacing
            fluxes = [xa[1], xa[1] * vel_x + stress, xa[2] * vel_x, xa[3] * vel_x,
                      (xa[4] + stress) * vel_x, xa[5] * vel_x]
            speed = (jnp.abs(vel_x) + sound) * metric
            div = []
            for c in range(6):
                flux = fluxes[c] * metric
                damped = speed * xa[c]
                for t in range(1, 4):
                    up, down = pair_terms(flux, damped, t)
                    pair_ref[c, 2 * t - 2] = up
                    pair_ref[c, 2 * t - 1] = down
                acc = SPEED_WEIGHTS[0] * damped[XPAD:XPAD + columns]
                for t in range(1, 4):
                    acc = acc + pair_ref[c, 2 * t - 2, pl.ds(XPAD + t, columns), :]
                    acc = acc + pair_ref[c, 2 * t - 1, pl.ds(XPAD - t, columns), :]
                div.append(acc)
            ya = [qy_ref[c, :, pl.ds(o, width)] for c in range(6)]
            inverse, vel_x, vel_y, vel_z, stress, sound = kernel_primitives(ya)
            scaled = -face_area * eta
            metric_x = scaled * slope_x
            metric_z = scaled * slope_z
            metric_t = scaled * rate
            contra = metric_t + metric_x * vel_x + face_area * vel_y + metric_z * vel_z
            fluxes = [ya[0] * contra, ya[1] * contra + metric_x * stress,
                      ya[2] * contra + face_area * stress, ya[3] * contra + metric_z * stress,
                      (ya[4] + stress) * contra - metric_t * stress, ya[5] * contra]
            speed = jnp.abs(contra) + sound * jnp.sqrt(
                metric_x * metric_x + face_area * face_area + metric_z * metric_z)
            for c in range(6):
                damped = speed * ya[c]
                acc = SPEED_WEIGHTS[0] * damped
                for t in range(1, 4):
                    up, down = pair_terms(fluxes[c], damped, t)
                    acc = acc + pltpu.roll(up, (-planes * t) % width, 1) + pltpu.roll(down, planes * t, 1)
                div[c] = div[c] + acc[:, PAD:PAD + CHUNK]
            q = [v[:, PAD:PAD + CHUNK] for v in ya]
            inverse = inverse[:, PAD:PAD + CHUNK]
            vel_z = vel_z[:, PAD:PAD + CHUNK]
            stress = stress[:, PAD:PAD + CHUNK]
            sound = sound[:, PAD:PAD + CHUNK]
            metric = STREAM_STEP * height * spacing
            fluxes = [q[3], q[1] * vel_z, q[2] * vel_z, q[3] * vel_z + stress,
                      (q[4] + stress) * vel_z, q[5] * vel_z]
            speed = (jnp.abs(vel_z) + sound) * metric
            for c in range(6):
                damped = speed * q[c]
                acc = SPEED_WEIGHTS[0] * damped
                for t in range(1, 4):
                    up, down = pair_terms(fluxes[c] * metric, damped, t)
                    up = jnp.where(lane < planes - t, pltpu.roll(up, CHUNK - t, 1),
                                   pltpu.roll(up, planes - t, 1))
                    down = jnp.where(lane >= t, pltpu.roll(down, t, 1),
                                     pltpu.roll(down, CHUNK - planes + t, 1))
                    acc = acc + up + down
                div[c] = div[c] + acc
            kelvin = stress * inverse
            balanced = CHARACTER_KELVIN / (jnp.exp(CHARACTER_KELVIN / kelvin) - 1.0)
            teller = stress / (LANDAU_TELLER * jnp.exp(
                WHITE_LAW_FACTOR * jnp.exp(-jnp.log(kelvin) / 3.0)))
            source = q[0] * (balanced - q[5] * inverse) * teller
            scale = 1.0 / (60.0 * (face_area * height * spacing))
            for c in range(6):
                change = -(div[c] * scale) - q[c] * ratio
                if c == 5:
                    change = change + source
                out_ref[c, :, pl.ds(o, CHUNK)] = q[c] + dt * change
            return carry

        lax.fori_loop(0, length // CHUNK, body, 0)

    return kernel


def update(state, xlo, xhi, yhalo, geo, top_before, top_last, height, targets, planes, total_rows, dt):
    columns = state.shape[1]
    length = state.shape[2]
    kern = make_kernel(columns, length, planes, total_rows, dt, targets)
    vmem = pl.BlockSpec(memory_space=pltpu.VMEM)
    return pl.pallas_call(
        kern,
        out_shape=(
            jax.ShapeDtypeStruct((6, columns, length), jnp.float32),
            jax.ShapeDtypeStruct((columns, planes), jnp.float32),
        ),
        in_specs=[vmem] * 8,
        out_specs=(vmem, vmem),
        scratch_shapes=[
            pltpu.VMEM((6, columns + 2 * XPAD, length), jnp.float32),
            pltpu.VMEM((6, columns, length + 2 * PAD), jnp.float32),
            pltpu.VMEM((6, 6, columns + 2 * XPAD, CHUNK), jnp.float32),
        ],
    )(state, xlo, xhi, yhalo, geo, top_before, top_last, height)


def shifted(block, axis, forward, cyclic=False):
    count = lax.axis_size(axis)
    pairs = [(i, i + 1) for i in range(count - 1)]
    if cyclic and count > 1:
        pairs.append((count - 1, 0))
    if not forward:
        pairs = [(target, source) for source, target in pairs]
    return lax.ppermute(block, axis, pairs)


def broadcast(array, axis, holders, fanouts):
    count = lax.axis_size(axis)
    index = lax.axis_index(axis)
    last = (array, array, [])
    for fanout in fanouts:
        if len(holders) >= count:
            break
        waiting = [i for i in range(count) if i not in holders]
        targets = jnp.zeros((), jnp.bool_)
        arrived = array
        reached = []
        for _ in range(fanout):
            pairs = list(zip(holders, waiting))
            waiting = waiting[len(pairs) :]
            if not pairs:
                break
            received = lax.ppermute(array, axis, pairs)
            last = (arrived, received, [target for _, target in pairs])
            hit = jnp.zeros((), jnp.bool_)
            for _, target in pairs:
                hit = hit | (index == target)
            arrived = jnp.where(hit, received, arrived)
            reached = reached + [target for _, target in pairs]
        array = arrived
        holders = holders + reached
    return last


def zshift(values, offset, planes):
    length = values.shape[-1]
    plane_at = jnp.arange(length, dtype=jnp.int32) % planes
    if offset > 0:
        return jnp.where(
            plane_at >= offset,
            jnp.roll(values, offset, axis=-1),
            jnp.roll(values, offset - planes, axis=-1),
        )
    return jnp.where(
        plane_at < planes + offset,
        jnp.roll(values, offset, axis=-1),
        jnp.roll(values, offset + planes, axis=-1),
    )


def primitives(conserved):
    specific_volume_inverse = conserved[0]
    vel_x = conserved[1] / specific_volume_inverse
    vel_y = conserved[2] / specific_volume_inverse
    vel_z = conserved[3] / specific_volume_inverse
    thermodynamic_stress = (HEAT_RATIO - 1.0) * (
        conserved[4]
        - 0.5 * (conserved[1] * vel_x + conserved[2] * vel_y + conserved[3] * vel_z)
        - conserved[5]
    )
    sound_speed = jnp.sqrt(HEAT_RATIO * thermodynamic_stress / specific_volume_inverse)
    return (specific_volume_inverse, vel_x, vel_y, vel_z, thermodynamic_stress, sound_speed)


def slopes(height_ext, planes):
    columns = height_ext.shape[0] - 6
    slope_x = (
        height_ext[1 : columns + 1]
        - 8.0 * height_ext[2 : columns + 2]
        + 8.0 * height_ext[4 : columns + 4]
        - height_ext[5 : columns + 5]
    ) / (12.0 * STREAM_STEP)
    height = height_ext[3 : columns + 3]
    slope_z = (
        zshift(height, 2, planes)
        - 8.0 * zshift(height, 1, planes)
        + 8.0 * zshift(height, -1, planes)
        - zshift(height, -2, planes)
    ) / (12.0 * SPAN_STEP)
    return (slope_x, slope_z)


def shock_speed(top_row, slope_x, slope_z):
    specific_volume_inverse, vel_x, vel_y, vel_z, thermodynamic_stress, sound_speed = primitives(
        top_row
    )
    tilt_norm = jnp.sqrt(1.0 + slope_x * slope_x + slope_z * slope_z)
    normal = (vel_y - vel_x * slope_x - vel_z * slope_z) / tilt_norm
    sine_sq = slope_x * slope_x / (tilt_norm * tilt_norm)
    jump_pressure = FREE_PRESSURE * (
        1.0 + 2.0 * HEAT_RATIO / (HEAT_RATIO + 1.0) * (FREE_MACH * FREE_MACH * sine_sq - 1.0)
    )
    return tilt_norm * (
        normal + (jump_pressure - thermodynamic_stress) / (specific_volume_inverse * sound_speed)
    )


def wall_ghosts(first_rows, blowing, planes):
    mirror = jnp.concatenate(
        [
            first_rows[..., 2 * planes : 3 * planes],
            first_rows[..., planes : 2 * planes],
            first_rows[..., 0:planes],
        ],
        axis=-1,
    )
    blown_y = 2.0 * jnp.tile(blowing, (1, 3)) - mirror[2]
    stagnation_enthalpy_sum = (
        mirror[4] + 0.5 * (blown_y * blown_y - mirror[2] * mirror[2]) / mirror[0]
    )
    return jnp.stack([mirror[0], mirror[1], blown_y, mirror[3], stagnation_enthalpy_sum, mirror[5]])


def wall_flux(wall_segment, segment_level, blow_table):
    seg_hit = wall_segment[:, None] == jnp.arange(segment_level.shape[0], dtype=jnp.int32)[None, :]
    levels = jnp.sum(jnp.where(seg_hit, segment_level[None, :], 0), axis=1)
    level_hit = levels[:, None] == jnp.arange(blow_table.shape[0], dtype=jnp.int32)[None, :]
    return jnp.sum(jnp.where(level_hit[:, :, None], blow_table[None, :, :], 0.0), axis=1)


def replicate_lanes(small, planes):
    pick = (
        jnp.arange(LANES, dtype=jnp.int32)[None, :] % planes
        == jnp.arange(planes, dtype=jnp.int32)[:, None]
    ).astype(jnp.float32)
    return jnp.dot(small, pick, precision=lax.Precision.HIGHEST, preferred_element_type=jnp.float32)


def shards(state, shock_height, wall_segment, segment_level, blow_table):
    planes = blow_table.shape[1]
    columns = state.shape[1]
    length = state.shape[2]
    row_count = length // planes
    col_devs = lax.axis_size("gx")
    row_devs = lax.axis_size("gy")
    col_dev = lax.axis_index("gx")
    row_dev = lax.axis_index("gy")
    total_rows = row_count * row_devs
    band = HALO * planes

    def pack(cols, heights):
        extra = jnp.zeros((1, HALO, length), jnp.float32)
        extra = lax.dynamic_update_slice(extra, heights[None], (0, 0, 0))
        return jnp.concatenate([cols, extra], axis=0)

    from_low = shifted(pack(state[:, columns - HALO :], shock_height[columns - HALO :]), "gx", True)
    from_high = shifted(pack(state[:, :HALO], shock_height[:HALO]), "gx", False)
    plane_lane = jnp.arange(PAD, dtype=jnp.int32)[None, None, :]
    top_block = state[..., length - PAD :]
    below = shifted(top_block, "gy", True, cyclic=True)
    above = shifted(jnp.where(plane_lane < band, state[..., :PAD], top_block), "gy", False)
    low_height = jnp.where(
        col_dev == 0, jnp.broadcast_to(shock_height[:1], (HALO, planes)), from_low[6, :, :planes]
    )
    high_height = jnp.where(
        col_dev == col_devs - 1,
        jnp.broadcast_to(shock_height[columns - 1 :], (HALO, planes)),
        from_high[6, :, :planes],
    )
    height_ext = jnp.concatenate([low_height, shock_height, high_height], axis=0)
    slope_x, slope_z = slopes(height_ext, planes)

    top_seed = jnp.where(row_dev == row_devs - 1, top_block, jnp.where(row_dev == 0, below, above))
    seeded = sorted({row_devs - 1, 0, max(row_devs - 2, 0)}, reverse=True)
    top_before, top_last, last_targets = broadcast(top_seed, "gy", seeded, (2, 1, 1, 1, 1))

    blowing = wall_flux(wall_segment, segment_level, blow_table)
    wall_block = wall_ghosts(state[..., :band], blowing, planes)
    ghost_below = jnp.where(
        row_dev == 0, jnp.concatenate([wall_block[..., : PAD - band], wall_block], axis=2), below
    )
    ghost_above = jnp.where(
        row_dev == row_devs - 1, jnp.tile(state[..., length - planes :], (1, 1, PAD // planes)), above
    )
    yhalo = jnp.stack([ghost_below, ghost_above])

    height = shock_height
    height_x = jnp.concatenate(
        [
            jnp.broadcast_to(height_ext[:1], (XPAD - HALO, planes)),
            height_ext,
            jnp.broadcast_to(height_ext[-1:], (XPAD - HALO, planes)),
        ],
        axis=0,
    )
    small = jnp.concatenate([height_x, slope_x, slope_z, height], axis=0)
    geo = replicate_lanes(small, planes)
    state_new, shock_new = update(
        state,
        from_low,
        from_high,
        yhalo,
        geo,
        top_before,
        top_last,
        shock_height,
        tuple(last_targets),
        planes,
        total_rows,
        COURANT / total_rows,
    )
    return (state_new, shock_new)


def solution(mesh):
    in_specs = (P(None, "gx", "gy"), P("gx", None), P("gx"), P(), P())
    out_specs = (P(None, "gx", "gy"), P("gx", None))
    return jax.shard_map(shards, mesh=mesh, in_specs=in_specs, out_specs=out_specs, check_vma=False)
```

```python
import math

import jax
import jax.numpy as jnp
from jax import lax
from jax.experimental import pallas as pl
from jax.experimental.pallas import tpu as pltpu
from jax.sharding import PartitionSpec as P

HEAT_RATIO = 1.4
STREAM_STEP = 0.05
SPAN_STEP = 0.05
STRETCH_RATE = 2.0
CHARACTER_KELVIN = 3.0
WHITE_LAW_FACTOR = 1.0
LANDAU_TELLER = 0.002
FREE_PRESSURE = 0.1
FREE_MACH = 6.0
COURANT = 0.05

FLUX_WEIGHTS = (45.0, -9.0, 1.0)
SPEED_WEIGHTS = (20.0, -15.0, 6.0, -1.0)
CHUNK = 512
PAD = 128
HALO = 3
XPAD = 8
LANES = 128


def kernel_primitives(q):
    inverse = 1.0 / q[0]
    vel_x = q[1] * inverse
    vel_y = q[2] * inverse
    vel_z = q[3] * inverse
    stress = (HEAT_RATIO - 1.0) * (q[4] - 0.5 * (q[1] * vel_x + q[2] * vel_y + q[3] * vel_z) - q[5])
    sound = jnp.sqrt(HEAT_RATIO * stress * inverse)
    return inverse, vel_x, vel_y, vel_z, stress, sound


def pair_terms(flux, damped, t):
    odd = FLUX_WEIGHTS[t - 1]
    even = SPEED_WEIGHTS[t]
    odd_part = flux if odd == 1.0 else odd * flux
    if even == -1.0:
        return odd_part - damped, -(odd_part + damped)
    even_part = even * damped
    return even_part + odd_part, even_part - odd_part


def lane_tile(values, width):
    return jnp.concatenate([values] * (width // values.shape[-1]), axis=-1)


def stretch_factors(rows, total_rows):
    growth = jnp.exp(STRETCH_RATE * (rows + 0.5) / total_rows)
    denominator = math.exp(STRETCH_RATE) - 1.0
    return (growth - 1.0) / denominator, STRETCH_RATE * growth / (total_rows * denominator)


def make_kernel(columns, length, planes, total_rows, dt, targets):
    width = CHUNK + 2 * PAD
    face_area = STREAM_STEP * SPAN_STEP
    xrows = columns + 2 * XPAD

    def kernel(state_ref, xlo_ref, xhi_ref, yhalo_ref, geo_ref, before_ref, last_ref, height_ref,
               out_ref, shock_ref, qx_ref, qy_ref, pair_ref):
        col_dev = lax.axis_index("gx")
        first_row = lax.axis_index("gy") * (length // planes)
        for c in range(6):
            qx_ref[c, 0:XPAD, :] = state_ref[c, 0:XPAD, :]
            qx_ref[c, XPAD:XPAD + columns, :] = state_ref[c]
            qx_ref[c, XPAD + columns:, :] = state_ref[c, columns - XPAD:, :]
            qx_ref[c, XPAD - HALO:XPAD, :] = xlo_ref[c]
            qx_ref[c, XPAD + columns:XPAD + columns + HALO, :] = xhi_ref[c]
            qy_ref[c, :, 0:PAD] = yhalo_ref[0, c]
            qy_ref[c, :, PAD:PAD + length] = state_ref[c]
            qy_ref[c, :, PAD + length:] = yhalo_ref[1, c, :, 0:PAD]

        @pl.when(col_dev == 0)
        def _():
            for c in range(6):
                qx_ref[c, XPAD - HALO:XPAD, :] = jnp.broadcast_to(state_ref[c, 0:1, :], (HALO, length))

        @pl.when(col_dev == lax.axis_size("gx") - 1)
        def _():
            for c in range(6):
                qx_ref[c, XPAD + columns:XPAD + columns + HALO, :] = jnp.broadcast_to(
                    state_ref[c, columns - 1:columns, :], (HALO, length))

        height_x = lane_tile(geo_ref[0:xrows, :], CHUNK)
        slope_x_row = geo_ref[xrows:xrows + columns, :]
        slope_z_row = geo_ref[xrows + columns:xrows + 2 * columns, :]
        height_row = geo_ref[xrows + 2 * columns:xrows + 3 * columns, :]
        group = lax.broadcasted_iota(jnp.int32, (columns, LANES), 1) // planes
        top = []
        row_dev = lax.axis_index("gy")
        hit = jnp.zeros((columns, LANES), jnp.bool_)
        for target in targets:
            hit = hit | (row_dev == target)
        for c in range(6):
            held = jnp.where(hit, last_ref[c], before_ref[c])
            spread = jnp.where(group == 0, pltpu.roll(held, planes, 1),
                               jnp.where(group == 1, pltpu.roll(held, 2 * planes, 1),
                                         jnp.where(group == 2, pltpu.roll(held, 3 * planes, 1), held)))
            top.append(spread)
        rate_row = shock_speed(top, slope_x_row, slope_z_row)
        shock_ref[...] = height_ref[...] + dt * rate_row[:, 0:planes]
        slope_x = lane_tile(slope_x_row, width)
        slope_z = lane_tile(slope_z_row, width)
        rate = lane_tile(rate_row, width)
        ratio = lane_tile(rate_row / height_row, CHUNK)
        height = lane_tile(height_row, CHUNK)
        lane = lax.broadcasted_iota(jnp.int32, (columns, CHUNK), 1) % planes
        lane_in = lax.broadcasted_iota(jnp.int32, (1, CHUNK), 1)
        lane_out = lax.broadcasted_iota(jnp.int32, (1, width), 1)

        def body(k, carry):
            o = pl.multiple_of(k * CHUNK, CHUNK)
            rows_in = (first_row + (o + lane_in) // planes).astype(jnp.float32)
            spacing = stretch_factors(rows_in, total_rows)[1]
            rows_out = (first_row - PAD // planes + (o + lane_out) // planes).astype(jnp.float32)
            eta = stretch_factors(rows_out, total_rows)[0]
            xa = [qx_ref[c, :, pl.ds(o, CHUNK)] for c in range(6)]
            inverse, vel_x, vel_y, vel_z, stress, sound = kernel_primitives(xa)
            metric = STREAM_STEP * height_x * spacing
            fluxes = [xa[1], xa[1] * vel_x + stress, xa[2] * vel_x, xa[3] * vel_x,
                      (xa[4] + stress) * vel_x, xa[5] * vel_x]
            speed = (jnp.abs(vel_x) + sound) * metric
            div = []
            for c in range(6):
                flux = fluxes[c] * metric
                damped = speed * xa[c]
                for t in range(1, 4):
                    up, down = pair_terms(flux, damped, t)
                    pair_ref[c, 2 * t - 2] = up
                    pair_ref[c, 2 * t - 1] = down
                acc = SPEED_WEIGHTS[0] * damped[XPAD:XPAD + columns]
                for t in range(1, 4):
                    acc = acc + pair_ref[c, 2 * t - 2, pl.ds(XPAD + t, columns), :]
                    acc = acc + pair_ref[c, 2 * t - 1, pl.ds(XPAD - t, columns), :]
                div.append(acc)
            ya = [qy_ref[c, :, pl.ds(o, width)] for c in range(6)]
            inverse, vel_x, vel_y, vel_z, stress, sound = kernel_primitives(ya)
            scaled = -face_area * eta
            metric_x = scaled * slope_x
            metric_z = scaled * slope_z
            metric_t = scaled * rate
            contra = metric_t + metric_x * vel_x + face_area * vel_y + metric_z * vel_z
            fluxes = [ya[0] * contra, ya[1] * contra + metric_x * stress,
                      ya[2] * contra + face_area * stress, ya[3] * contra + metric_z * stress,
                      (ya[4] + stress) * contra - metric_t * stress, ya[5] * contra]
            speed = jnp.abs(contra) + sound * jnp.sqrt(
                metric_x * metric_x + face_area * face_area + metric_z * metric_z)
            for c in range(6):
                damped = speed * ya[c]
                acc = SPEED_WEIGHTS[0] * damped
                for t in range(1, 4):
                    up, down = pair_terms(fluxes[c], damped, t)
                    acc = acc + pltpu.roll(up, (-planes * t) % width, 1) + pltpu.roll(down, planes * t, 1)
                div[c] = div[c] + acc[:, PAD:PAD + CHUNK]
            q = [v[:, PAD:PAD + CHUNK] for v in ya]
            inverse = inverse[:, PAD:PAD + CHUNK]
            vel_z = vel_z[:, PAD:PAD + CHUNK]
            stress = stress[:, PAD:PAD + CHUNK]
            sound = sound[:, PAD:PAD + CHUNK]
            metric = STREAM_STEP * height * spacing
            fluxes = [q[3], q[1] * vel_z, q[2] * vel_z, q[3] * vel_z + stress,
                      (q[4] + stress) * vel_z, q[5] * vel_z]
            speed = (jnp.abs(vel_z) + sound) * metric
            for c in range(6):
                damped = speed * q[c]
                acc = SPEED_WEIGHTS[0] * damped
                for t in range(1, 4):
                    up, down = pair_terms(fluxes[c] * metric, damped, t)
                    up = jnp.where(lane < planes - t, pltpu.roll(up, CHUNK - t, 1),
                                   pltpu.roll(up, planes - t, 1))
                    down = jnp.where(lane >= t, pltpu.roll(down, t, 1),
                                     pltpu.roll(down, CHUNK - planes + t, 1))
                    acc = acc + up + down
                div[c] = div[c] + acc
            kelvin = stress * inverse
            balanced = CHARACTER_KELVIN / (jnp.exp(CHARACTER_KELVIN / kelvin) - 1.0)
            teller = stress / (LANDAU_TELLER * jnp.exp(
                WHITE_LAW_FACTOR * jnp.exp(-jnp.log(kelvin) / 3.0)))
            source = q[0] * (balanced - q[5] * inverse) * teller
            scale = 1.0 / (60.0 * (face_area * height * spacing))
            for c in range(6):
                change = -(div[c] * scale) - q[c] * ratio
                if c == 5:
                    change = change + source
                out_ref[c, :, pl.ds(o, CHUNK)] = q[c] + dt * change
            return carry

        lax.fori_loop(0, length // CHUNK, body, 0)

    return kernel


def update(state, xlo, xhi, yhalo, geo, top_before, top_last, height, targets, planes, total_rows, dt):
    columns = state.shape[1]
    length = state.shape[2]
    kern = make_kernel(columns, length, planes, total_rows, dt, targets)
    vmem = pl.BlockSpec(memory_space=pltpu.VMEM)
    return pl.pallas_call(
        kern,
        out_shape=(
            jax.ShapeDtypeStruct((6, columns, length), jnp.float32),
            jax.ShapeDtypeStruct((columns, planes), jnp.float32),
        ),
        in_specs=[vmem] * 8,
        out_specs=(vmem, vmem),
        scratch_shapes=[
            pltpu.VMEM((6, columns + 2 * XPAD, length), jnp.float32),
            pltpu.VMEM((6, columns, length + 2 * PAD), jnp.float32),
            pltpu.VMEM((6, 6, columns + 2 * XPAD, CHUNK), jnp.float32),
        ],
    )(state, xlo, xhi, yhalo, geo, top_before, top_last, height)


def shifted(block, axis, forward, cyclic=False):
    count = lax.axis_size(axis)
    pairs = [(i, i + 1) for i in range(count - 1)]
    if cyclic and count > 1:
        pairs.append((count - 1, 0))
    if not forward:
        pairs = [(target, source) for source, target in pairs]
    return lax.ppermute(block, axis, pairs)


def broadcast(array, axis, holders, fanouts):
    count = lax.axis_size(axis)
    index = lax.axis_index(axis)
    last = (array, array, [])
    for fanout in fanouts:
        if len(holders) >= count:
            break
        waiting = [i for i in range(count) if i not in holders]
        targets = jnp.zeros((), jnp.bool_)
        arrived = array
        reached = []
        for _ in range(fanout):
            pairs = list(zip(holders, waiting))
            waiting = waiting[len(pairs) :]
            if not pairs:
                break
            received = lax.ppermute(array, axis, pairs)
            last = (arrived, received, [target for _, target in pairs])
            hit = jnp.zeros((), jnp.bool_)
            for _, target in pairs:
                hit = hit | (index == target)
            arrived = jnp.where(hit, received, arrived)
            reached = reached + [target for _, target in pairs]
        array = arrived
        holders = holders + reached
    return last


def zshift(values, offset, planes):
    length = values.shape[-1]
    plane_at = jnp.arange(length, dtype=jnp.int32) % planes
    if offset > 0:
        return jnp.where(
            plane_at >= offset,
            jnp.roll(values, offset, axis=-1),
            jnp.roll(values, offset - planes, axis=-1),
        )
    return jnp.where(
        plane_at < planes + offset,
        jnp.roll(values, offset, axis=-1),
        jnp.roll(values, offset + planes, axis=-1),
    )


def primitives(conserved):
    specific_volume_inverse = conserved[0]
    vel_x = conserved[1] / specific_volume_inverse
    vel_y = conserved[2] / specific_volume_inverse
    vel_z = conserved[3] / specific_volume_inverse
    thermodynamic_stress = (HEAT_RATIO - 1.0) * (
        conserved[4]
        - 0.5 * (conserved[1] * vel_x + conserved[2] * vel_y + conserved[3] * vel_z)
        - conserved[5]
    )
    sound_speed = jnp.sqrt(HEAT_RATIO * thermodynamic_stress / specific_volume_inverse)
    return (specific_volume_inverse, vel_x, vel_y, vel_z, thermodynamic_stress, sound_speed)


def slopes(height_ext, planes):
    columns = height_ext.shape[0] - 6
    slope_x = (
        height_ext[1 : columns + 1]
        - 8.0 * height_ext[2 : columns + 2]
        + 8.0 * height_ext[4 : columns + 4]
        - height_ext[5 : columns + 5]
    ) / (12.0 * STREAM_STEP)
    height = height_ext[3 : columns + 3]
    slope_z = (
        zshift(height, 2, planes)
        - 8.0 * zshift(height, 1, planes)
        + 8.0 * zshift(height, -1, planes)
        - zshift(height, -2, planes)
    ) / (12.0 * SPAN_STEP)
    return (slope_x, slope_z)


def shock_speed(top_row, slope_x, slope_z):
    specific_volume_inverse, vel_x, vel_y, vel_z, thermodynamic_stress, sound_speed = primitives(
        top_row
    )
    tilt_norm = jnp.sqrt(1.0 + slope_x * slope_x + slope_z * slope_z)
    normal = (vel_y - vel_x * slope_x - vel_z * slope_z) / tilt_norm
    sine_sq = slope_x * slope_x / (tilt_norm * tilt_norm)
    jump_pressure = FREE_PRESSURE * (
        1.0 + 2.0 * HEAT_RATIO / (HEAT_RATIO + 1.0) * (FREE_MACH * FREE_MACH * sine_sq - 1.0)
    )
    return tilt_norm * (
        normal + (jump_pressure - thermodynamic_stress) / (specific_volume_inverse * sound_speed)
    )


def wall_ghosts(first_rows, blowing, planes):
    mirror = jnp.concatenate(
        [
            first_rows[..., 2 * planes : 3 * planes],
            first_rows[..., planes : 2 * planes],
            first_rows[..., 0:planes],
        ],
        axis=-1,
    )
    blown_y = 2.0 * jnp.tile(blowing, (1, 3)) - mirror[2]
    stagnation_enthalpy_sum = (
        mirror[4] + 0.5 * (blown_y * blown_y - mirror[2] * mirror[2]) / mirror[0]
    )
    return jnp.stack([mirror[0], mirror[1], blown_y, mirror[3], stagnation_enthalpy_sum, mirror[5]])


def wall_flux(wall_segment, segment_level, blow_table):
    seg_hit = wall_segment[:, None] == jnp.arange(segment_level.shape[0], dtype=jnp.int32)[None, :]
    levels = jnp.sum(jnp.where(seg_hit, segment_level[None, :], 0), axis=1)
    level_hit = levels[:, None] == jnp.arange(blow_table.shape[0], dtype=jnp.int32)[None, :]
    return jnp.sum(jnp.where(level_hit[:, :, None], blow_table[None, :, :], 0.0), axis=1)


def replicate_lanes(small, planes):
    pick = (
        jnp.arange(LANES, dtype=jnp.int32)[None, :] % planes
        == jnp.arange(planes, dtype=jnp.int32)[:, None]
    ).astype(jnp.float32)
    return jnp.dot(small, pick, precision=lax.Precision.HIGHEST, preferred_element_type=jnp.float32)


def shards(state, shock_height, wall_segment, segment_level, blow_table):
    planes = blow_table.shape[1]
    columns = state.shape[1]
    length = state.shape[2]
    row_count = length // planes
    col_devs = lax.axis_size("gx")
    row_devs = lax.axis_size("gy")
    col_dev = lax.axis_index("gx")
    row_dev = lax.axis_index("gy")
    total_rows = row_count * row_devs
    band = HALO * planes

    def pack(cols, heights):
        extra = jnp.zeros((1, HALO, length), jnp.float32)
        extra = lax.dynamic_update_slice(extra, heights[None], (0, 0, 0))
        return jnp.concatenate([cols, extra], axis=0)

    from_low = shifted(pack(state[:, columns - HALO :], shock_height[columns - HALO :]), "gx", True)
    from_high = shifted(pack(state[:, :HALO], shock_height[:HALO]), "gx", False)
    plane_lane = jnp.arange(PAD, dtype=jnp.int32)[None, None, :]
    top_block = state[..., length - PAD :]
    below = shifted(top_block, "gy", True, cyclic=True)
    above = shifted(jnp.where(plane_lane < band, state[..., :PAD], top_block), "gy", False)
    low_height = jnp.where(
        col_dev == 0, jnp.broadcast_to(shock_height[:1], (HALO, planes)), from_low[6, :, :planes]
    )
    high_height = jnp.where(
        col_dev == col_devs - 1,
        jnp.broadcast_to(shock_height[columns - 1 :], (HALO, planes)),
        from_high[6, :, :planes],
    )
    height_ext = jnp.concatenate([low_height, shock_height, high_height], axis=0)
    slope_x, slope_z = slopes(height_ext, planes)

    top_seed = jnp.where(row_dev == row_devs - 1, top_block, jnp.where(row_dev == 0, below, above))
    top_seed, below, above = lax.optimization_barrier((top_seed, below, above))
    seeded = sorted({row_devs - 1, 0, max(row_devs - 2, 0)}, reverse=True)
    top_before, top_last, last_targets = broadcast(top_seed, "gy", seeded, (2, 1, 1, 1, 1))

    blowing = wall_flux(wall_segment, segment_level, blow_table)
    wall_block = wall_ghosts(state[..., :band], blowing, planes)
    ghost_below = jnp.where(
        row_dev == 0, jnp.concatenate([wall_block[..., : PAD - band], wall_block], axis=2), below
    )
    ghost_above = jnp.where(
        row_dev == row_devs - 1, jnp.tile(state[..., length - planes :], (1, 1, PAD // planes)), above
    )
    yhalo = jnp.stack([ghost_below, ghost_above])

    height = shock_height
    height_x = jnp.concatenate(
        [
            jnp.broadcast_to(height_ext[:1], (XPAD - HALO, planes)),
            height_ext,
            jnp.broadcast_to(height_ext[-1:], (XPAD - HALO, planes)),
        ],
        axis=0,
    )
    small = jnp.concatenate([height_x, slope_x, slope_z, height], axis=0)
    geo = replicate_lanes(small, planes)
    state_new, shock_new = update(
        state,
        from_low,
        from_high,
        yhalo,
        geo,
        top_before,
        top_last,
        shock_height,
        tuple(last_targets),
        planes,
        total_rows,
        COURANT / total_rows,
    )
    return (state_new, shock_new)


def solution(mesh):
    in_specs = (P(None, "gx", "gy"), P("gx", None), P("gx"), P(), P())
    out_specs = (P(None, "gx", "gy"), P("gx", None))
    return jax.shard_map(shards, mesh=mesh, in_specs=in_specs, out_specs=out_specs, check_vma=False)
```

```python
import math

import jax
import jax.numpy as jnp
from jax import lax
from jax.experimental import pallas as pl
from jax.experimental.pallas import tpu as pltpu
from jax.sharding import PartitionSpec as P

HEAT_RATIO = 1.4
STREAM_STEP = 0.05
SPAN_STEP = 0.05
STRETCH_RATE = 2.0
CHARACTER_KELVIN = 3.0
WHITE_LAW_FACTOR = 1.0
LANDAU_TELLER = 0.002
FREE_PRESSURE = 0.1
FREE_MACH = 6.0
COURANT = 0.05

FLUX_WEIGHTS = (45.0, -9.0, 1.0)
SPEED_WEIGHTS = (20.0, -15.0, 6.0, -1.0)
CHUNK = 512
PAD = 128
HALO = 3
XPAD = 8
LANES = 128


def kernel_primitives(q):
    inverse = 1.0 / q[0]
    vel_x = q[1] * inverse
    vel_y = q[2] * inverse
    vel_z = q[3] * inverse
    stress = (HEAT_RATIO - 1.0) * (q[4] - 0.5 * (q[1] * vel_x + q[2] * vel_y + q[3] * vel_z) - q[5])
    sound = jnp.sqrt(HEAT_RATIO * stress * inverse)
    return inverse, vel_x, vel_y, vel_z, stress, sound


def pair_terms(flux, damped, t):
    odd = FLUX_WEIGHTS[t - 1]
    even = SPEED_WEIGHTS[t]
    odd_part = flux if odd == 1.0 else odd * flux
    if even == -1.0:
        return odd_part - damped, -(odd_part + damped)
    even_part = even * damped
    return even_part + odd_part, even_part - odd_part


def lane_tile(values, width):
    return jnp.concatenate([values] * (width // values.shape[-1]), axis=-1)


def stretch_factors(rows, total_rows):
    growth = jnp.exp(STRETCH_RATE * (rows + 0.5) / total_rows)
    denominator = math.exp(STRETCH_RATE) - 1.0
    return (growth - 1.0) / denominator, STRETCH_RATE * growth / (total_rows * denominator)


def make_kernel(columns, length, planes, total_rows, dt, targets):
    width = CHUNK + 2 * PAD
    face_area = STREAM_STEP * SPAN_STEP
    xrows = columns + 2 * XPAD

    def kernel(state_ref, xlo_ref, xhi_ref, yhalo_ref, geo_ref, before_ref, last_ref, height_ref,
               out_ref, shock_ref, qy_ref, pair_ref):
        col_dev = lax.axis_index("gx")
        first_row = lax.axis_index("gy") * (length // planes)
        for c in range(6):
            qy_ref[c, :, 0:PAD] = yhalo_ref[0, c]
            qy_ref[c, :, PAD:PAD + length] = state_ref[c]
            qy_ref[c, :, PAD + length:] = yhalo_ref[1, c]
        first_col = col_dev == 0
        last_col = col_dev == lax.axis_size("gx") - 1

        height_x = lane_tile(geo_ref[0:xrows, :], CHUNK)
        slope_x_row = geo_ref[xrows:xrows + columns, :]
        slope_z_row = geo_ref[xrows + columns:xrows + 2 * columns, :]
        height_row = geo_ref[xrows + 2 * columns:xrows + 3 * columns, :]
        group = lax.broadcasted_iota(jnp.int32, (columns, LANES), 1) // planes
        top = []
        row_dev = lax.axis_index("gy")
        hit = jnp.zeros((columns, LANES), jnp.bool_)
        for target in targets:
            hit = hit | (row_dev == target)
        for c in range(6):
            held = jnp.where(hit, last_ref[c], before_ref[c])
            spread = jnp.where(group == 0, pltpu.roll(held, planes, 1),
                               jnp.where(group == 1, pltpu.roll(held, 2 * planes, 1),
                                         jnp.where(group == 2, pltpu.roll(held, 3 * planes, 1), held)))
            top.append(spread)
        rate_row = shock_speed(top, slope_x_row, slope_z_row)
        shock_ref[...] = height_ref[...] + dt * rate_row[:, 0:planes]
        slope_x = lane_tile(slope_x_row, width)
        slope_z = lane_tile(slope_z_row, width)
        rate = lane_tile(rate_row, width)
        ratio = lane_tile(rate_row / height_row, CHUNK)
        height = lane_tile(height_row, CHUNK)
        lane = lax.broadcasted_iota(jnp.int32, (columns, CHUNK), 1) % planes
        lane_in = lax.broadcasted_iota(jnp.int32, (1, CHUNK), 1)
        lane_out = lax.broadcasted_iota(jnp.int32, (1, width), 1)

        def body(k, carry):
            o = pl.multiple_of(k * CHUNK, CHUNK)
            rows_in = (first_row + (o + lane_in) // planes).astype(jnp.float32)
            spacing = stretch_factors(rows_in, total_rows)[1]
            rows_out = (first_row - PAD // planes + (o + lane_out) // planes).astype(jnp.float32)
            eta = stretch_factors(rows_out, total_rows)[0]
            xa = []
            for c in range(6):
                mid = state_ref[c, :, pl.ds(o, CHUNK)]
                low = jnp.where(first_col, jnp.broadcast_to(mid[0:1], (XPAD, CHUNK)),
                                xlo_ref[c, :, pl.ds(o, CHUNK)])
                high = jnp.where(last_col, jnp.broadcast_to(mid[columns - 1:columns], (XPAD, CHUNK)),
                                 xhi_ref[c, :, pl.ds(o, CHUNK)])
                xa.append(jnp.concatenate([low, mid, high], axis=0))
            inverse, vel_x, vel_y, vel_z, stress, sound = kernel_primitives(xa)
            metric = STREAM_STEP * height_x * spacing
            fluxes = [xa[1], xa[1] * vel_x + stress, xa[2] * vel_x, xa[3] * vel_x,
                      (xa[4] + stress) * vel_x, xa[5] * vel_x]
            speed = (jnp.abs(vel_x) + sound) * metric
            div = []
            for c in range(6):
                flux = fluxes[c] * metric
                damped = speed * xa[c]
                for t in range(1, 4):
                    up, down = pair_terms(flux, damped, t)
                    pair_ref[c, 2 * t - 2] = up
                    pair_ref[c, 2 * t - 1] = down
                acc = SPEED_WEIGHTS[0] * damped[XPAD:XPAD + columns]
                for t in range(1, 4):
                    acc = acc + pair_ref[c, 2 * t - 2, pl.ds(XPAD + t, columns), :]
                    acc = acc + pair_ref[c, 2 * t - 1, pl.ds(XPAD - t, columns), :]
                div.append(acc)
            ya = [qy_ref[c, :, pl.ds(o, width)] for c in range(6)]
            inverse, vel_x, vel_y, vel_z, stress, sound = kernel_primitives(ya)
            scaled = -face_area * eta
            metric_x = scaled * slope_x
            metric_z = scaled * slope_z
            metric_t = scaled * rate
            contra = metric_t + metric_x * vel_x + face_area * vel_y + metric_z * vel_z
            fluxes = [ya[0] * contra, ya[1] * contra + metric_x * stress,
                      ya[2] * contra + face_area * stress, ya[3] * contra + metric_z * stress,
                      (ya[4] + stress) * contra - metric_t * stress, ya[5] * contra]
            speed = jnp.abs(contra) + sound * jnp.sqrt(
                metric_x * metric_x + face_area * face_area + metric_z * metric_z)
            for c in range(6):
                damped = speed * ya[c]
                acc = SPEED_WEIGHTS[0] * damped
                for t in range(1, 4):
                    up, down = pair_terms(fluxes[c], damped, t)
                    acc = acc + pltpu.roll(up, (-planes * t) % width, 1) + pltpu.roll(down, planes * t, 1)
                div[c] = div[c] + acc[:, PAD:PAD + CHUNK]
            q = [v[:, PAD:PAD + CHUNK] for v in ya]
            inverse = inverse[:, PAD:PAD + CHUNK]
            vel_z = vel_z[:, PAD:PAD + CHUNK]
            stress = stress[:, PAD:PAD + CHUNK]
            sound = sound[:, PAD:PAD + CHUNK]
            metric = STREAM_STEP * height * spacing
            fluxes = [q[3], q[1] * vel_z, q[2] * vel_z, q[3] * vel_z + stress,
                      (q[4] + stress) * vel_z, q[5] * vel_z]
            speed = (jnp.abs(vel_z) + sound) * metric
            for c in range(6):
                damped = speed * q[c]
                acc = SPEED_WEIGHTS[0] * damped
                for t in range(1, 4):
                    up, down = pair_terms(fluxes[c] * metric, damped, t)
                    up = jnp.where(lane < planes - t, pltpu.roll(up, CHUNK - t, 1),
                                   pltpu.roll(up, planes - t, 1))
                    down = jnp.where(lane >= t, pltpu.roll(down, t, 1),
                                     pltpu.roll(down, CHUNK - planes + t, 1))
                    acc = acc + up + down
                div[c] = div[c] + acc
            kelvin = stress * inverse
            balanced = CHARACTER_KELVIN / (jnp.exp(CHARACTER_KELVIN / kelvin) - 1.0)
            teller = stress / (LANDAU_TELLER * jnp.exp(
                WHITE_LAW_FACTOR * jnp.exp(-jnp.log(kelvin) / 3.0)))
            source = q[0] * (balanced - q[5] * inverse) * teller
            scale = 1.0 / (60.0 * (face_area * height * spacing))
            for c in range(6):
                change = -(div[c] * scale) - q[c] * ratio
                if c == 5:
                    change = change + source
                out_ref[c, :, pl.ds(o, CHUNK)] = q[c] + dt * change
            return carry

        lax.fori_loop(0, length // CHUNK, body, 0)

    return kernel


def update(state, xlo, xhi, yhalo, geo, top_before, top_last, height, targets, planes, total_rows, dt):
    columns = state.shape[1]
    length = state.shape[2]
    kern = make_kernel(columns, length, planes, total_rows, dt, targets)
    vmem = pl.BlockSpec(memory_space=pltpu.VMEM)
    return pl.pallas_call(
        kern,
        out_shape=(
            jax.ShapeDtypeStruct((6, columns, length), jnp.float32),
            jax.ShapeDtypeStruct((columns, planes), jnp.float32),
        ),
        in_specs=[vmem] * 8,
        out_specs=(vmem, vmem),
        scratch_shapes=[
            pltpu.VMEM((6, columns, length + 2 * PAD), jnp.float32),
            pltpu.VMEM((6, 6, columns + 2 * XPAD, CHUNK), jnp.float32),
        ],
    )(state, xlo, xhi, yhalo, geo, top_before, top_last, height)


def shifted(block, axis, forward, cyclic=False):
    count = lax.axis_size(axis)
    pairs = [(i, i + 1) for i in range(count - 1)]
    if cyclic and count > 1:
        pairs.append((count - 1, 0))
    if not forward:
        pairs = [(target, source) for source, target in pairs]
    return lax.ppermute(block, axis, pairs)


def broadcast(array, axis, holders, fanouts):
    count = lax.axis_size(axis)
    index = lax.axis_index(axis)
    last = (array, array, [])
    for fanout in fanouts:
        if len(holders) >= count:
            break
        waiting = [i for i in range(count) if i not in holders]
        targets = jnp.zeros((), jnp.bool_)
        arrived = array
        reached = []
        for _ in range(fanout):
            pairs = list(zip(holders, waiting))
            waiting = waiting[len(pairs) :]
            if not pairs:
                break
            received = lax.ppermute(array, axis, pairs)
            last = (arrived, received, [target for _, target in pairs])
            hit = jnp.zeros((), jnp.bool_)
            for _, target in pairs:
                hit = hit | (index == target)
            arrived = jnp.where(hit, received, arrived)
            reached = reached + [target for _, target in pairs]
        array = arrived
        holders = holders + reached
    return last


def zshift(values, offset, planes):
    length = values.shape[-1]
    plane_at = jnp.arange(length, dtype=jnp.int32) % planes
    if offset > 0:
        return jnp.where(
            plane_at >= offset,
            jnp.roll(values, offset, axis=-1),
            jnp.roll(values, offset - planes, axis=-1),
        )
    return jnp.where(
        plane_at < planes + offset,
        jnp.roll(values, offset, axis=-1),
        jnp.roll(values, offset + planes, axis=-1),
    )


def primitives(conserved):
    specific_volume_inverse = conserved[0]
    vel_x = conserved[1] / specific_volume_inverse
    vel_y = conserved[2] / specific_volume_inverse
    vel_z = conserved[3] / specific_volume_inverse
    thermodynamic_stress = (HEAT_RATIO - 1.0) * (
        conserved[4]
        - 0.5 * (conserved[1] * vel_x + conserved[2] * vel_y + conserved[3] * vel_z)
        - conserved[5]
    )
    sound_speed = jnp.sqrt(HEAT_RATIO * thermodynamic_stress / specific_volume_inverse)
    return (specific_volume_inverse, vel_x, vel_y, vel_z, thermodynamic_stress, sound_speed)


def slopes(height_ext, planes):
    columns = height_ext.shape[0] - 6
    slope_x = (
        height_ext[1 : columns + 1]
        - 8.0 * height_ext[2 : columns + 2]
        + 8.0 * height_ext[4 : columns + 4]
        - height_ext[5 : columns + 5]
    ) / (12.0 * STREAM_STEP)
    height = height_ext[3 : columns + 3]
    slope_z = (
        zshift(height, 2, planes)
        - 8.0 * zshift(height, 1, planes)
        + 8.0 * zshift(height, -1, planes)
        - zshift(height, -2, planes)
    ) / (12.0 * SPAN_STEP)
    return (slope_x, slope_z)


def shock_speed(top_row, slope_x, slope_z):
    specific_volume_inverse, vel_x, vel_y, vel_z, thermodynamic_stress, sound_speed = primitives(
        top_row
    )
    tilt_norm = jnp.sqrt(1.0 + slope_x * slope_x + slope_z * slope_z)
    normal = (vel_y - vel_x * slope_x - vel_z * slope_z) / tilt_norm
    sine_sq = slope_x * slope_x / (tilt_norm * tilt_norm)
    jump_pressure = FREE_PRESSURE * (
        1.0 + 2.0 * HEAT_RATIO / (HEAT_RATIO + 1.0) * (FREE_MACH * FREE_MACH * sine_sq - 1.0)
    )
    return tilt_norm * (
        normal + (jump_pressure - thermodynamic_stress) / (specific_volume_inverse * sound_speed)
    )


def wall_ghosts(first_rows, blowing, planes):
    mirror = jnp.concatenate(
        [
            first_rows[..., 2 * planes : 3 * planes],
            first_rows[..., planes : 2 * planes],
            first_rows[..., 0:planes],
        ],
        axis=-1,
    )
    blown_y = 2.0 * jnp.tile(blowing, (1, 3)) - mirror[2]
    stagnation_enthalpy_sum = (
        mirror[4] + 0.5 * (blown_y * blown_y - mirror[2] * mirror[2]) / mirror[0]
    )
    return jnp.stack([mirror[0], mirror[1], blown_y, mirror[3], stagnation_enthalpy_sum, mirror[5]])


def wall_flux(wall_segment, segment_level, blow_table):
    seg_hit = wall_segment[:, None] == jnp.arange(segment_level.shape[0], dtype=jnp.int32)[None, :]
    levels = jnp.sum(jnp.where(seg_hit, segment_level[None, :], 0), axis=1)
    level_hit = levels[:, None] == jnp.arange(blow_table.shape[0], dtype=jnp.int32)[None, :]
    return jnp.sum(jnp.where(level_hit[:, :, None], blow_table[None, :, :], 0.0), axis=1)


def replicate_lanes(small, planes):
    pick = (
        jnp.arange(LANES, dtype=jnp.int32)[None, :] % planes
        == jnp.arange(planes, dtype=jnp.int32)[:, None]
    ).astype(jnp.float32)
    return jnp.dot(small, pick, precision=lax.Precision.HIGHEST, preferred_element_type=jnp.float32)


def shards(state, shock_height, wall_segment, segment_level, blow_table):
    planes = blow_table.shape[1]
    columns = state.shape[1]
    length = state.shape[2]
    row_count = length // planes
    col_devs = lax.axis_size("gx")
    row_devs = lax.axis_size("gy")
    col_dev = lax.axis_index("gx")
    row_dev = lax.axis_index("gy")
    total_rows = row_count * row_devs
    band = HALO * planes

    from_low = shifted(
        lax.dynamic_update_slice(state[:, columns - XPAD :], shock_height[columns - HALO :][None], (0, 0, 0)),
        "gx",
        True,
    )
    from_high = shifted(
        lax.dynamic_update_slice(state[:, :XPAD], shock_height[:HALO][None], (0, XPAD - HALO, 0)),
        "gx",
        False,
    )
    plane_lane = jnp.arange(PAD, dtype=jnp.int32)[None, None, :]
    top_block = state[..., length - PAD :]
    below = shifted(top_block, "gy", True, cyclic=True)
    above = shifted(jnp.where(plane_lane < band, state[..., :PAD], top_block), "gy", False)
    low_height = jnp.where(
        col_dev == 0, jnp.broadcast_to(shock_height[:1], (HALO, planes)), from_low[0, :HALO, :planes]
    )
    high_height = jnp.where(
        col_dev == col_devs - 1,
        jnp.broadcast_to(shock_height[columns - 1 :], (HALO, planes)),
        from_high[0, XPAD - HALO :, :planes],
    )
    height_ext = jnp.concatenate([low_height, shock_height, high_height], axis=0)
    slope_x, slope_z = slopes(height_ext, planes)

    top_seed = jnp.where(row_dev == row_devs - 1, top_block, jnp.where(row_dev == 0, below, above))
    top_seed, below, above = lax.optimization_barrier((top_seed, below, above))
    seeded = sorted({row_devs - 1, 0, max(row_devs - 2, 0)}, reverse=True)
    top_before, top_last, last_targets = broadcast(top_seed, "gy", seeded, (2, 1, 1, 1, 1))

    blowing = wall_flux(wall_segment, segment_level, blow_table)
    wall_block = wall_ghosts(state[..., :band], blowing, planes)
    ghost_below = jnp.where(
        row_dev == 0, jnp.concatenate([wall_block[..., : PAD - band], wall_block], axis=2), below
    )
    ghost_above = jnp.where(
        row_dev == row_devs - 1, jnp.tile(state[..., length - planes :], (1, 1, PAD // planes)), above
    )
    yhalo = jnp.stack([ghost_below, ghost_above])

    height = shock_height
    height_x = jnp.concatenate(
        [
            jnp.broadcast_to(height_ext[:1], (XPAD - HALO, planes)),
            height_ext,
            jnp.broadcast_to(height_ext[-1:], (XPAD - HALO, planes)),
        ],
        axis=0,
    )
    small = jnp.concatenate([height_x, slope_x, slope_z, height], axis=0)
    geo = replicate_lanes(small, planes)
    state_new, shock_new = update(
        state,
        from_low,
        from_high,
        yhalo,
        geo,
        top_before,
        top_last,
        shock_height,
        tuple(last_targets),
        planes,
        total_rows,
        COURANT / total_rows,
    )
    return (state_new, shock_new)


def solution(mesh):
    in_specs = (P(None, "gx", "gy"), P("gx", None), P("gx"), P(), P())
    out_specs = (P(None, "gx", "gy"), P("gx", None))
    return jax.shard_map(shards, mesh=mesh, in_specs=in_specs, out_specs=out_specs, check_vma=False)
```

```python
import math

import jax
import jax.numpy as jnp
from jax import lax
from jax.experimental import pallas as pl
from jax.experimental.pallas import tpu as pltpu
from jax.sharding import PartitionSpec as P

HEAT_RATIO = 1.4
STREAM_STEP = 0.05
SPAN_STEP = 0.05
STRETCH_RATE = 2.0
CHARACTER_KELVIN = 3.0
WHITE_LAW_FACTOR = 1.0
LANDAU_TELLER = 0.002
FREE_PRESSURE = 0.1
FREE_MACH = 6.0
COURANT = 0.05

FLUX_WEIGHTS = (45.0, -9.0, 1.0)
SPEED_WEIGHTS = (20.0, -15.0, 6.0, -1.0)
CHUNK = 512
PAD = 128
HALO = 3
XPAD = 8
LANES = 128


def kernel_primitives(q):
    inverse = 1.0 / q[0]
    vel_x = q[1] * inverse
    vel_y = q[2] * inverse
    vel_z = q[3] * inverse
    stress = (HEAT_RATIO - 1.0) * (q[4] - 0.5 * (q[1] * vel_x + q[2] * vel_y + q[3] * vel_z) - q[5])
    sound = jnp.sqrt(HEAT_RATIO * stress * inverse)
    return inverse, vel_x, vel_y, vel_z, stress, sound


def pair_terms(flux, damped, t):
    odd = FLUX_WEIGHTS[t - 1]
    even = SPEED_WEIGHTS[t]
    odd_part = flux if odd == 1.0 else odd * flux
    if even == -1.0:
        return odd_part - damped, -(odd_part + damped)
    even_part = even * damped
    return even_part + odd_part, even_part - odd_part


def lane_tile(values, width):
    return jnp.concatenate([values] * (width // values.shape[-1]), axis=-1)


def stretch_factors(rows, total_rows):
    growth = jnp.exp(STRETCH_RATE * (rows + 0.5) / total_rows)
    denominator = math.exp(STRETCH_RATE) - 1.0
    return (growth - 1.0) / denominator, STRETCH_RATE * growth / (total_rows * denominator)


def make_kernel(columns, length, planes, total_rows, dt, targets):
    width = CHUNK + 2 * PAD
    face_area = STREAM_STEP * SPAN_STEP
    xrows = columns + 2 * XPAD

    def kernel(state_ref, xlo_ref, xhi_ref, yhalo_ref, geo_ref, before_ref, last_ref, height_ref,
               out_ref, shock_ref, qx_ref, qy_ref, pair_ref):
        col_dev = lax.axis_index("gx")
        first_row = lax.axis_index("gy") * (length // planes)
        for c in range(6):
            qx_ref[c, 0:XPAD, :] = state_ref[c, 0:XPAD, :]
            qx_ref[c, XPAD:XPAD + columns, :] = state_ref[c]
            qx_ref[c, XPAD + columns:, :] = state_ref[c, columns - XPAD:, :]
            qx_ref[c, XPAD - HALO:XPAD, :] = xlo_ref[c]
            qx_ref[c, XPAD + columns:XPAD + columns + HALO, :] = xhi_ref[c]
            qy_ref[c, :, 0:PAD] = yhalo_ref[0, c]
            qy_ref[c, :, PAD:PAD + length] = state_ref[c]
            qy_ref[c, :, PAD + length:] = yhalo_ref[1, c, :, 0:PAD]

        @pl.when(col_dev == 0)
        def _():
            for c in range(6):
                qx_ref[c, XPAD - HALO:XPAD, :] = jnp.broadcast_to(state_ref[c, 0:1, :], (HALO, length))

        @pl.when(col_dev == lax.axis_size("gx") - 1)
        def _():
            for c in range(6):
                qx_ref[c, XPAD + columns:XPAD + columns + HALO, :] = jnp.broadcast_to(
                    state_ref[c, columns - 1:columns, :], (HALO, length))

        height_x = lane_tile(geo_ref[0:xrows, :], CHUNK)
        slope_x_row = geo_ref[xrows:xrows + columns, :]
        slope_z_row = geo_ref[xrows + columns:xrows + 2 * columns, :]
        height_row = geo_ref[xrows + 2 * columns:xrows + 3 * columns, :]
        group = lax.broadcasted_iota(jnp.int32, (columns, LANES), 1) // planes
        top = []
        row_dev = lax.axis_index("gy")
        hit = jnp.zeros((columns, LANES), jnp.bool_)
        for target in targets:
            hit = hit | (row_dev == target)
        for c in range(6):
            held = jnp.where(hit, last_ref[c], before_ref[c])
            spread = jnp.where(group == 0, pltpu.roll(held, planes, 1),
                               jnp.where(group == 1, pltpu.roll(held, 2 * planes, 1),
                                         jnp.where(group == 2, pltpu.roll(held, 3 * planes, 1), held)))
            top.append(spread)
        rate_row = shock_speed(top, slope_x_row, slope_z_row)
        shock_ref[...] = height_ref[...] + dt * rate_row[:, 0:planes]
        slope_x = lane_tile(slope_x_row, width)
        slope_z = lane_tile(slope_z_row, width)
        rate = lane_tile(rate_row, width)
        ratio = lane_tile(rate_row / height_row, CHUNK)
        height = lane_tile(height_row, CHUNK)
        lane = lax.broadcasted_iota(jnp.int32, (columns, CHUNK), 1) % planes
        lane_in = lax.broadcasted_iota(jnp.int32, (1, CHUNK), 1)
        lane_out = lax.broadcasted_iota(jnp.int32, (1, width), 1)

        def body(k, carry):
            o = pl.multiple_of(k * CHUNK, CHUNK)
            rows_in = (first_row + (o + lane_in) // planes).astype(jnp.float32)
            spacing = stretch_factors(rows_in, total_rows)[1]
            rows_out = (first_row - PAD // planes + (o + lane_out) // planes).astype(jnp.float32)
            eta = stretch_factors(rows_out, total_rows)[0]
            xa = [qx_ref[c, :, pl.ds(o, CHUNK)] for c in range(6)]
            inverse, vel_x, vel_y, vel_z, stress, sound = kernel_primitives(xa)
            metric = STREAM_STEP * height_x * spacing
            fluxes = [xa[1], xa[1] * vel_x + stress, xa[2] * vel_x, xa[3] * vel_x,
                      (xa[4] + stress) * vel_x, xa[5] * vel_x]
            speed = (jnp.abs(vel_x) + sound) * metric
            div = []
            for c in range(6):
                flux = fluxes[c] * metric
                damped = speed * xa[c]
                for t in range(1, 4):
                    up, down = pair_terms(flux, damped, t)
                    pair_ref[c, 2 * t - 2] = up
                    pair_ref[c, 2 * t - 1] = down
                acc = SPEED_WEIGHTS[0] * damped[XPAD:XPAD + columns]
                for t in range(1, 4):
                    acc = acc + pair_ref[c, 2 * t - 2, pl.ds(XPAD + t, columns), :]
                    acc = acc + pair_ref[c, 2 * t - 1, pl.ds(XPAD - t, columns), :]
                div.append(acc)
            ya = [qy_ref[c, :, pl.ds(o, width)] for c in range(6)]
            inverse, vel_x, vel_y, vel_z, stress, sound = kernel_primitives(ya)
            scaled = -face_area * eta
            metric_x = scaled * slope_x
            metric_z = scaled * slope_z
            metric_t = scaled * rate
            contra = metric_t + metric_x * vel_x + face_area * vel_y + metric_z * vel_z
            fluxes = [ya[0] * contra, ya[1] * contra + metric_x * stress,
                      ya[2] * contra + face_area * stress, ya[3] * contra + metric_z * stress,
                      (ya[4] + stress) * contra - metric_t * stress, ya[5] * contra]
            speed = jnp.abs(contra) + sound * jnp.sqrt(
                metric_x * metric_x + face_area * face_area + metric_z * metric_z)
            for c in range(6):
                damped = speed * ya[c]
                acc = SPEED_WEIGHTS[0] * damped
                for t in range(1, 4):
                    up, down = pair_terms(fluxes[c], damped, t)
                    acc = acc + pltpu.roll(up, (-planes * t) % width, 1) + pltpu.roll(down, planes * t, 1)
                div[c] = div[c] + acc[:, PAD:PAD + CHUNK]
            q = [v[:, PAD:PAD + CHUNK] for v in ya]
            inverse = inverse[:, PAD:PAD + CHUNK]
            vel_z = vel_z[:, PAD:PAD + CHUNK]
            stress = stress[:, PAD:PAD + CHUNK]
            sound = sound[:, PAD:PAD + CHUNK]
            metric = STREAM_STEP * height * spacing
            fluxes = [q[3], q[1] * vel_z, q[2] * vel_z, q[3] * vel_z + stress,
                      (q[4] + stress) * vel_z, q[5] * vel_z]
            speed = (jnp.abs(vel_z) + sound) * metric
            for c in range(6):
                damped = speed * q[c]
                acc = SPEED_WEIGHTS[0] * damped
                for t in range(1, 4):
                    up, down = pair_terms(fluxes[c] * metric, damped, t)
                    up = jnp.where(lane < planes - t, pltpu.roll(up, CHUNK - t, 1),
                                   pltpu.roll(up, planes - t, 1))
                    down = jnp.where(lane >= t, pltpu.roll(down, t, 1),
                                     pltpu.roll(down, CHUNK - planes + t, 1))
                    acc = acc + up + down
                div[c] = div[c] + acc
            kelvin = stress * inverse
            balanced = CHARACTER_KELVIN / (jnp.exp(CHARACTER_KELVIN / kelvin) - 1.0)
            teller = stress / (LANDAU_TELLER * jnp.exp(
                WHITE_LAW_FACTOR * jnp.exp(-jnp.log(kelvin) / 3.0)))
            source = q[0] * (balanced - q[5] * inverse) * teller
            scale = 1.0 / (60.0 * (face_area * height * spacing))
            for c in range(6):
                change = -(div[c] * scale) - q[c] * ratio
                if c == 5:
                    change = change + source
                out_ref[c, :, pl.ds(o, CHUNK)] = q[c] + dt * change
            return carry

        lax.fori_loop(0, length // CHUNK, body, 0)

    return kernel


def update(state, xlo, xhi, yhalo, geo, top_before, top_last, height, targets, planes, total_rows, dt):
    columns = state.shape[1]
    length = state.shape[2]
    kern = make_kernel(columns, length, planes, total_rows, dt, targets)
    vmem = pl.BlockSpec(memory_space=pltpu.VMEM)
    return pl.pallas_call(
        kern,
        out_shape=(
            jax.ShapeDtypeStruct((6, columns, length), jnp.float32),
            jax.ShapeDtypeStruct((columns, planes), jnp.float32),
        ),
        in_specs=[vmem] * 8,
        out_specs=(vmem, vmem),
        scratch_shapes=[
            pltpu.VMEM((6, columns + 2 * XPAD, length), jnp.float32),
            pltpu.VMEM((6, columns, length + 2 * PAD), jnp.float32),
            pltpu.VMEM((6, 6, columns + 2 * XPAD, CHUNK), jnp.float32),
        ],
    )(state, xlo, xhi, yhalo, geo, top_before, top_last, height)


def shifted(block, axis, forward, cyclic=False):
    count = lax.axis_size(axis)
    pairs = [(i, i + 1) for i in range(count - 1)]
    if cyclic and count > 1:
        pairs.append((count - 1, 0))
    if not forward:
        pairs = [(target, source) for source, target in pairs]
    return lax.ppermute(block, axis, pairs)


def broadcast(array, axis, holders, fanouts):
    count = lax.axis_size(axis)
    index = lax.axis_index(axis)
    last = (array, array, [])
    for fanout in fanouts:
        if len(holders) >= count:
            break
        waiting = [i for i in range(count) if i not in holders]
        targets = jnp.zeros((), jnp.bool_)
        arrived = array
        reached = []
        for _ in range(fanout):
            pairs = list(zip(holders, waiting))
            waiting = waiting[len(pairs) :]
            if not pairs:
                break
            received = lax.ppermute(array, axis, pairs)
            last = (arrived, received, [target for _, target in pairs])
            hit = jnp.zeros((), jnp.bool_)
            for _, target in pairs:
                hit = hit | (index == target)
            arrived = jnp.where(hit, received, arrived)
            reached = reached + [target for _, target in pairs]
        array = arrived
        holders = holders + reached
    return last


def zshift(values, offset, planes):
    length = values.shape[-1]
    plane_at = jnp.arange(length, dtype=jnp.int32) % planes
    if offset > 0:
        return jnp.where(
            plane_at >= offset,
            jnp.roll(values, offset, axis=-1),
            jnp.roll(values, offset - planes, axis=-1),
        )
    return jnp.where(
        plane_at < planes + offset,
        jnp.roll(values, offset, axis=-1),
        jnp.roll(values, offset + planes, axis=-1),
    )


def primitives(conserved):
    specific_volume_inverse = conserved[0]
    vel_x = conserved[1] / specific_volume_inverse
    vel_y = conserved[2] / specific_volume_inverse
    vel_z = conserved[3] / specific_volume_inverse
    thermodynamic_stress = (HEAT_RATIO - 1.0) * (
        conserved[4]
        - 0.5 * (conserved[1] * vel_x + conserved[2] * vel_y + conserved[3] * vel_z)
        - conserved[5]
    )
    sound_speed = jnp.sqrt(HEAT_RATIO * thermodynamic_stress / specific_volume_inverse)
    return (specific_volume_inverse, vel_x, vel_y, vel_z, thermodynamic_stress, sound_speed)


def slopes(height_ext, planes):
    columns = height_ext.shape[0] - 6
    slope_x = (
        height_ext[1 : columns + 1]
        - 8.0 * height_ext[2 : columns + 2]
        + 8.0 * height_ext[4 : columns + 4]
        - height_ext[5 : columns + 5]
    ) / (12.0 * STREAM_STEP)
    height = height_ext[3 : columns + 3]
    slope_z = (
        zshift(height, 2, planes)
        - 8.0 * zshift(height, 1, planes)
        + 8.0 * zshift(height, -1, planes)
        - zshift(height, -2, planes)
    ) / (12.0 * SPAN_STEP)
    return (slope_x, slope_z)


def shock_speed(top_row, slope_x, slope_z):
    specific_volume_inverse, vel_x, vel_y, vel_z, thermodynamic_stress, sound_speed = primitives(
        top_row
    )
    tilt_norm = jnp.sqrt(1.0 + slope_x * slope_x + slope_z * slope_z)
    normal = (vel_y - vel_x * slope_x - vel_z * slope_z) / tilt_norm
    sine_sq = slope_x * slope_x / (tilt_norm * tilt_norm)
    jump_pressure = FREE_PRESSURE * (
        1.0 + 2.0 * HEAT_RATIO / (HEAT_RATIO + 1.0) * (FREE_MACH * FREE_MACH * sine_sq - 1.0)
    )
    return tilt_norm * (
        normal + (jump_pressure - thermodynamic_stress) / (specific_volume_inverse * sound_speed)
    )


def wall_ghosts(first_rows, blowing, planes):
    mirror = jnp.concatenate(
        [
            first_rows[..., 2 * planes : 3 * planes],
            first_rows[..., planes : 2 * planes],
            first_rows[..., 0:planes],
        ],
        axis=-1,
    )
    blown_y = 2.0 * jnp.tile(blowing, (1, 3)) - mirror[2]
    stagnation_enthalpy_sum = (
        mirror[4] + 0.5 * (blown_y * blown_y - mirror[2] * mirror[2]) / mirror[0]
    )
    return jnp.stack([mirror[0], mirror[1], blown_y, mirror[3], stagnation_enthalpy_sum, mirror[5]])


def wall_flux(wall_segment, segment_level, blow_table):
    seg_hit = wall_segment[:, None] == jnp.arange(segment_level.shape[0], dtype=jnp.int32)[None, :]
    levels = jnp.sum(jnp.where(seg_hit, segment_level[None, :], 0), axis=1)
    level_hit = levels[:, None] == jnp.arange(blow_table.shape[0], dtype=jnp.int32)[None, :]
    return jnp.sum(jnp.where(level_hit[:, :, None], blow_table[None, :, :], 0.0), axis=1)


def replicate_lanes(small, planes):
    pick = (
        jnp.arange(LANES, dtype=jnp.int32)[None, :] % planes
        == jnp.arange(planes, dtype=jnp.int32)[:, None]
    ).astype(jnp.float32)
    return jnp.dot(small, pick, precision=lax.Precision.HIGHEST, preferred_element_type=jnp.float32)


def shards(state, shock_height, wall_segment, segment_level, blow_table):
    planes = blow_table.shape[1]
    columns = state.shape[1]
    length = state.shape[2]
    row_count = length // planes
    col_devs = lax.axis_size("gx")
    row_devs = lax.axis_size("gy")
    col_dev = lax.axis_index("gx")
    row_dev = lax.axis_index("gy")
    total_rows = row_count * row_devs
    band = HALO * planes

    def pack(cols, heights):
        extra = jnp.zeros((1, HALO, length), jnp.float32)
        extra = lax.dynamic_update_slice(extra, heights[None], (0, 0, 0))
        return jnp.concatenate([cols, extra], axis=0)

    from_low = shifted(pack(state[:, columns - HALO :], shock_height[columns - HALO :]), "gx", True)
    from_high = shifted(pack(state[:, :HALO], shock_height[:HALO]), "gx", False)
    plane_lane = jnp.arange(PAD, dtype=jnp.int32)[None, None, :]
    top_block = state[..., length - PAD :]
    below = shifted(top_block, "gy", True, cyclic=True)
    above = shifted(jnp.where(plane_lane < band, state[..., :PAD], top_block), "gy", False)
    low_height = jnp.where(
        col_dev == 0, jnp.broadcast_to(shock_height[:1], (HALO, planes)), from_low[6, :, :planes]
    )
    high_height = jnp.where(
        col_dev == col_devs - 1,
        jnp.broadcast_to(shock_height[columns - 1 :], (HALO, planes)),
        from_high[6, :, :planes],
    )
    height_ext = jnp.concatenate([low_height, shock_height, high_height], axis=0)
    slope_x, slope_z = slopes(height_ext, planes)

    top_seed = jnp.where(row_dev == row_devs - 1, top_block, jnp.where(row_dev == 0, below, above))
    top_seed, below, above = lax.optimization_barrier((top_seed, below, above))
    seeded = sorted({row_devs - 1, 0, max(row_devs - 2, 0)}, reverse=True)
    top_before, top_last, last_targets = broadcast(top_seed, "gy", seeded, (5, 5, 5, 5))

    blowing = wall_flux(wall_segment, segment_level, blow_table)
    wall_block = wall_ghosts(state[..., :band], blowing, planes)
    ghost_below = jnp.where(
        row_dev == 0, jnp.concatenate([wall_block[..., : PAD - band], wall_block], axis=2), below
    )
    ghost_above = jnp.where(
        row_dev == row_devs - 1, jnp.tile(state[..., length - planes :], (1, 1, PAD // planes)), above
    )
    yhalo = jnp.stack([ghost_below, ghost_above])

    height = shock_height
    height_x = jnp.concatenate(
        [
            jnp.broadcast_to(height_ext[:1], (XPAD - HALO, planes)),
            height_ext,
            jnp.broadcast_to(height_ext[-1:], (XPAD - HALO, planes)),
        ],
        axis=0,
    )
    small = jnp.concatenate([height_x, slope_x, slope_z, height], axis=0)
    geo = replicate_lanes(small, planes)
    state_new, shock_new = update(
        state,
        from_low,
        from_high,
        yhalo,
        geo,
        top_before,
        top_last,
        shock_height,
        tuple(last_targets),
        planes,
        total_rows,
        COURANT / total_rows,
    )
    return (state_new, shock_new)


def solution(mesh):
    in_specs = (P(None, "gx", "gy"), P("gx", None), P("gx"), P(), P())
    out_specs = (P(None, "gx", "gy"), P("gx", None))
    return jax.shard_map(shards, mesh=mesh, in_specs=in_specs, out_specs=out_specs, check_vma=False)
```

```python
import math

import jax
import jax.numpy as jnp
from jax import lax
from jax.experimental import pallas as pl
from jax.experimental.pallas import tpu as pltpu
from jax.sharding import PartitionSpec as P

HEAT_RATIO = 1.4
STREAM_STEP = 0.05
SPAN_STEP = 0.05
STRETCH_RATE = 2.0
CHARACTER_KELVIN = 3.0
WHITE_LAW_FACTOR = 1.0
LANDAU_TELLER = 0.002
FREE_PRESSURE = 0.1
FREE_MACH = 6.0
COURANT = 0.05

FLUX_WEIGHTS = (45.0, -9.0, 1.0)
SPEED_WEIGHTS = (20.0, -15.0, 6.0, -1.0)
CHUNK = 512
PAD = 128
HALO = 3
XPAD = 8
LANES = 128


def kernel_primitives(q):
    inverse = 1.0 / q[0]
    vel_x = q[1] * inverse
    vel_y = q[2] * inverse
    vel_z = q[3] * inverse
    stress = (HEAT_RATIO - 1.0) * (q[4] - 0.5 * (q[1] * vel_x + q[2] * vel_y + q[3] * vel_z) - q[5])
    sound = jnp.sqrt(HEAT_RATIO * stress * inverse)
    return inverse, vel_x, vel_y, vel_z, stress, sound


def pair_terms(flux, damped, t):
    odd = FLUX_WEIGHTS[t - 1]
    even = SPEED_WEIGHTS[t]
    odd_part = flux if odd == 1.0 else odd * flux
    if even == -1.0:
        return odd_part - damped, -(odd_part + damped)
    even_part = even * damped
    return even_part + odd_part, even_part - odd_part


def lane_tile(values, width):
    return jnp.concatenate([values] * (width // values.shape[-1]), axis=-1)


def stretch_factors(rows, total_rows):
    growth = jnp.exp(STRETCH_RATE * (rows + 0.5) / total_rows)
    denominator = math.exp(STRETCH_RATE) - 1.0
    return (growth - 1.0) / denominator, STRETCH_RATE * growth / (total_rows * denominator)


def make_kernel(columns, length, planes, total_rows, dt, targets):
    width = CHUNK + 2 * PAD
    face_area = STREAM_STEP * SPAN_STEP
    xrows = columns + 2 * XPAD

    def kernel(state_ref, xlo_ref, xhi_ref, below_ref, above_ref, geo_ref, before_ref, last_ref,
               height_ref, out_ref, shock_ref, qx_ref, qy_ref, pair_ref):
        col_dev = lax.axis_index("gx")
        first_row = lax.axis_index("gy") * (length // planes)
        for c in range(6):
            qx_ref[c, 0:XPAD, :] = state_ref[c, 0:XPAD, :]
            qx_ref[c, XPAD:XPAD + columns, :] = state_ref[c]
            qx_ref[c, XPAD + columns:, :] = state_ref[c, columns - XPAD:, :]
            qx_ref[c, XPAD - HALO:XPAD, :] = xlo_ref[c]
            qx_ref[c, XPAD + columns:XPAD + columns + HALO, :] = xhi_ref[c]
            qy_ref[c, :, 0:PAD] = below_ref[c]
            qy_ref[c, :, PAD:PAD + length] = state_ref[c]
            qy_ref[c, :, PAD + length:] = above_ref[c]

        @pl.when(col_dev == 0)
        def _():
            for c in range(6):
                qx_ref[c, XPAD - HALO:XPAD, :] = jnp.broadcast_to(state_ref[c, 0:1, :], (HALO, length))

        @pl.when(col_dev == lax.axis_size("gx") - 1)
        def _():
            for c in range(6):
                qx_ref[c, XPAD + columns:XPAD + columns + HALO, :] = jnp.broadcast_to(
                    state_ref[c, columns - 1:columns, :], (HALO, length))

        height_x = lane_tile(geo_ref[0:xrows, :], CHUNK)
        slope_x_row = geo_ref[xrows:xrows + columns, :]
        slope_z_row = geo_ref[xrows + columns:xrows + 2 * columns, :]
        height_row = geo_ref[xrows + 2 * columns:xrows + 3 * columns, :]
        group = lax.broadcasted_iota(jnp.int32, (columns, LANES), 1) // planes

        @pl.when(lax.axis_index("gy") == 0)
        def _():
            mirror = []
            for c in range(6):
                rows = state_ref[c, :, 0:LANES]
                mirror.append(jnp.where(group == 2, pltpu.roll(rows, planes, 1),
                                        pltpu.roll(rows, 3 * planes, 1)))
            blown_y = 2.0 * geo_ref[xrows + 3 * columns:xrows + 4 * columns, :] - mirror[2]
            energy = mirror[4] + 0.5 * (blown_y * blown_y - mirror[2] * mirror[2]) / mirror[0]
            ghosts = [mirror[0], mirror[1], blown_y, mirror[3], energy, mirror[5]]
            for c in range(6):
                qy_ref[c, :, 0:PAD] = ghosts[c]

        @pl.when(lax.axis_index("gy") == lax.axis_size("gy") - 1)
        def _():
            for c in range(6):
                rows = state_ref[c, :, length - LANES:]
                qy_ref[c, :, PAD + length:] = jnp.where(
                    group == 0, pltpu.roll(rows, planes, 1),
                    jnp.where(group == 1, pltpu.roll(rows, 2 * planes, 1),
                              jnp.where(group == 2, pltpu.roll(rows, 3 * planes, 1), rows)))
        top = []
        row_dev = lax.axis_index("gy")
        hit = jnp.zeros((columns, LANES), jnp.bool_)
        for target in targets:
            hit = hit | (row_dev == target)
        for c in range(6):
            held = jnp.where(hit, last_ref[c], before_ref[c])
            spread = jnp.where(group == 0, pltpu.roll(held, planes, 1),
                               jnp.where(group == 1, pltpu.roll(held, 2 * planes, 1),
                                         jnp.where(group == 2, pltpu.roll(held, 3 * planes, 1), held)))
            top.append(spread)
        rate_row = shock_speed(top, slope_x_row, slope_z_row)
        shock_ref[...] = height_ref[...] + dt * rate_row[:, 0:planes]
        slope_x = lane_tile(slope_x_row, width)
        slope_z = lane_tile(slope_z_row, width)
        rate = lane_tile(rate_row, width)
        ratio = lane_tile(rate_row / height_row, CHUNK)
        height = lane_tile(height_row, CHUNK)
        lane = lax.broadcasted_iota(jnp.int32, (columns, CHUNK), 1) % planes
        lane_in = lax.broadcasted_iota(jnp.int32, (1, CHUNK), 1)
        lane_out = lax.broadcasted_iota(jnp.int32, (1, width), 1)

        def body(k, carry):
            o = pl.multiple_of(k * CHUNK, CHUNK)
            rows_in = (first_row + (o + lane_in) // planes).astype(jnp.float32)
            spacing = stretch_factors(rows_in, total_rows)[1]
            rows_out = (first_row - PAD // planes + (o + lane_out) // planes).astype(jnp.float32)
            eta = stretch_factors(rows_out, total_rows)[0]
            xa = [qx_ref[c, :, pl.ds(o, CHUNK)] for c in range(6)]
            inverse, vel_x, vel_y, vel_z, stress, sound = kernel_primitives(xa)
            metric = STREAM_STEP * height_x * spacing
            fluxes = [xa[1], xa[1] * vel_x + stress, xa[2] * vel_x, xa[3] * vel_x,
                      (xa[4] + stress) * vel_x, xa[5] * vel_x]
            speed = (jnp.abs(vel_x) + sound) * metric
            div = []
            for c in range(6):
                flux = fluxes[c] * metric
                damped = speed * xa[c]
                for t in range(1, 4):
                    up, down = pair_terms(flux, damped, t)
                    pair_ref[c, 2 * t - 2] = up
                    pair_ref[c, 2 * t - 1] = down
                acc = SPEED_WEIGHTS[0] * damped[XPAD:XPAD + columns]
                for t in range(1, 4):
                    acc = acc + pair_ref[c, 2 * t - 2, pl.ds(XPAD + t, columns), :]
                    acc = acc + pair_ref[c, 2 * t - 1, pl.ds(XPAD - t, columns), :]
                div.append(acc)
            ya = [qy_ref[c, :, pl.ds(o, width)] for c in range(6)]
            inverse, vel_x, vel_y, vel_z, stress, sound = kernel_primitives(ya)
            scaled = -face_area * eta
            metric_x = scaled * slope_x
            metric_z = scaled * slope_z
            metric_t = scaled * rate
            contra = metric_t + metric_x * vel_x + face_area * vel_y + metric_z * vel_z
            fluxes = [ya[0] * contra, ya[1] * contra + metric_x * stress,
                      ya[2] * contra + face_area * stress, ya[3] * contra + metric_z * stress,
                      (ya[4] + stress) * contra - metric_t * stress, ya[5] * contra]
            speed = jnp.abs(contra) + sound * jnp.sqrt(
                metric_x * metric_x + face_area * face_area + metric_z * metric_z)
            for c in range(6):
                damped = speed * ya[c]
                acc = SPEED_WEIGHTS[0] * damped
                for t in range(1, 4):
                    up, down = pair_terms(fluxes[c], damped, t)
                    acc = acc + pltpu.roll(up, (-planes * t) % width, 1) + pltpu.roll(down, planes * t, 1)
                div[c] = div[c] + acc[:, PAD:PAD + CHUNK]
            q = [v[:, PAD:PAD + CHUNK] for v in ya]
            inverse = inverse[:, PAD:PAD + CHUNK]
            vel_z = vel_z[:, PAD:PAD + CHUNK]
            stress = stress[:, PAD:PAD + CHUNK]
            sound = sound[:, PAD:PAD + CHUNK]
            metric = STREAM_STEP * height * spacing
            fluxes = [q[3], q[1] * vel_z, q[2] * vel_z, q[3] * vel_z + stress,
                      (q[4] + stress) * vel_z, q[5] * vel_z]
            speed = (jnp.abs(vel_z) + sound) * metric
            for c in range(6):
                damped = speed * q[c]
                acc = SPEED_WEIGHTS[0] * damped
                for t in range(1, 4):
                    up, down = pair_terms(fluxes[c] * metric, damped, t)
                    up = jnp.where(lane < planes - t, pltpu.roll(up, CHUNK - t, 1),
                                   pltpu.roll(up, planes - t, 1))
                    down = jnp.where(lane >= t, pltpu.roll(down, t, 1),
                                     pltpu.roll(down, CHUNK - planes + t, 1))
                    acc = acc + up + down
                div[c] = div[c] + acc
            kelvin = stress * inverse
            balanced = CHARACTER_KELVIN / (jnp.exp(CHARACTER_KELVIN / kelvin) - 1.0)
            teller = stress / (LANDAU_TELLER * jnp.exp(
                WHITE_LAW_FACTOR * jnp.exp(-jnp.log(kelvin) / 3.0)))
            source = q[0] * (balanced - q[5] * inverse) * teller
            scale = 1.0 / (60.0 * (face_area * height * spacing))
            for c in range(6):
                change = -(div[c] * scale) - q[c] * ratio
                if c == 5:
                    change = change + source
                out_ref[c, :, pl.ds(o, CHUNK)] = q[c] + dt * change
            return carry

        lax.fori_loop(0, length // CHUNK, body, 0)

    return kernel


def update(state, xlo, xhi, below, above, geo, top_before, top_last, height, targets, planes, total_rows,
           dt):
    columns = state.shape[1]
    length = state.shape[2]
    kern = make_kernel(columns, length, planes, total_rows, dt, targets)
    vmem = pl.BlockSpec(memory_space=pltpu.VMEM)
    return pl.pallas_call(
        kern,
        out_shape=(
            jax.ShapeDtypeStruct((6, columns, length), jnp.float32),
            jax.ShapeDtypeStruct((columns, planes), jnp.float32),
        ),
        in_specs=[vmem] * 9,
        out_specs=(vmem, vmem),
        scratch_shapes=[
            pltpu.VMEM((6, columns + 2 * XPAD, length), jnp.float32),
            pltpu.VMEM((6, columns, length + 2 * PAD), jnp.float32),
            pltpu.VMEM((6, 6, columns + 2 * XPAD, CHUNK), jnp.float32),
        ],
    )(state, xlo, xhi, below, above, geo, top_before, top_last, height)


def shifted(block, axis, forward, cyclic=False):
    count = lax.axis_size(axis)
    pairs = [(i, i + 1) for i in range(count - 1)]
    if cyclic and count > 1:
        pairs.append((count - 1, 0))
    if not forward:
        pairs = [(target, source) for source, target in pairs]
    return lax.ppermute(block, axis, pairs)


def broadcast(array, axis, holders, fanouts):
    count = lax.axis_size(axis)
    index = lax.axis_index(axis)
    last = (array, array, [])
    for fanout in fanouts:
        if len(holders) >= count:
            break
        waiting = [i for i in range(count) if i not in holders]
        targets = jnp.zeros((), jnp.bool_)
        arrived = array
        reached = []
        for _ in range(fanout):
            pairs = list(zip(holders, waiting))
            waiting = waiting[len(pairs) :]
            if not pairs:
                break
            received = lax.ppermute(array, axis, pairs)
            last = (arrived, received, [target for _, target in pairs])
            hit = jnp.zeros((), jnp.bool_)
            for _, target in pairs:
                hit = hit | (index == target)
            arrived = jnp.where(hit, received, arrived)
            reached = reached + [target for _, target in pairs]
        array = arrived
        holders = holders + reached
    return last


def zshift(values, offset, planes):
    length = values.shape[-1]
    plane_at = jnp.arange(length, dtype=jnp.int32) % planes
    if offset > 0:
        return jnp.where(
            plane_at >= offset,
            jnp.roll(values, offset, axis=-1),
            jnp.roll(values, offset - planes, axis=-1),
        )
    return jnp.where(
        plane_at < planes + offset,
        jnp.roll(values, offset, axis=-1),
        jnp.roll(values, offset + planes, axis=-1),
    )


def primitives(conserved):
    specific_volume_inverse = conserved[0]
    vel_x = conserved[1] / specific_volume_inverse
    vel_y = conserved[2] / specific_volume_inverse
    vel_z = conserved[3] / specific_volume_inverse
    thermodynamic_stress = (HEAT_RATIO - 1.0) * (
        conserved[4]
        - 0.5 * (conserved[1] * vel_x + conserved[2] * vel_y + conserved[3] * vel_z)
        - conserved[5]
    )
    sound_speed = jnp.sqrt(HEAT_RATIO * thermodynamic_stress / specific_volume_inverse)
    return (specific_volume_inverse, vel_x, vel_y, vel_z, thermodynamic_stress, sound_speed)


def slopes(height_ext, planes):
    columns = height_ext.shape[0] - 6
    slope_x = (
        height_ext[1 : columns + 1]
        - 8.0 * height_ext[2 : columns + 2]
        + 8.0 * height_ext[4 : columns + 4]
        - height_ext[5 : columns + 5]
    ) / (12.0 * STREAM_STEP)
    height = height_ext[3 : columns + 3]
    slope_z = (
        zshift(height, 2, planes)
        - 8.0 * zshift(height, 1, planes)
        + 8.0 * zshift(height, -1, planes)
        - zshift(height, -2, planes)
    ) / (12.0 * SPAN_STEP)
    return (slope_x, slope_z)


def shock_speed(top_row, slope_x, slope_z):
    specific_volume_inverse, vel_x, vel_y, vel_z, thermodynamic_stress, sound_speed = primitives(
        top_row
    )
    tilt_norm = jnp.sqrt(1.0 + slope_x * slope_x + slope_z * slope_z)
    normal = (vel_y - vel_x * slope_x - vel_z * slope_z) / tilt_norm
    sine_sq = slope_x * slope_x / (tilt_norm * tilt_norm)
    jump_pressure = FREE_PRESSURE * (
        1.0 + 2.0 * HEAT_RATIO / (HEAT_RATIO + 1.0) * (FREE_MACH * FREE_MACH * sine_sq - 1.0)
    )
    return tilt_norm * (
        normal + (jump_pressure - thermodynamic_stress) / (specific_volume_inverse * sound_speed)
    )


def wall_ghosts(first_rows, blowing, planes):
    mirror = jnp.concatenate(
        [
            first_rows[..., 2 * planes : 3 * planes],
            first_rows[..., planes : 2 * planes],
            first_rows[..., 0:planes],
        ],
        axis=-1,
    )
    blown_y = 2.0 * jnp.tile(blowing, (1, 3)) - mirror[2]
    stagnation_enthalpy_sum = (
        mirror[4] + 0.5 * (blown_y * blown_y - mirror[2] * mirror[2]) / mirror[0]
    )
    return jnp.stack([mirror[0], mirror[1], blown_y, mirror[3], stagnation_enthalpy_sum, mirror[5]])


def wall_flux(wall_segment, segment_level, blow_table):
    seg_hit = wall_segment[:, None] == jnp.arange(segment_level.shape[0], dtype=jnp.int32)[None, :]
    levels = jnp.sum(jnp.where(seg_hit, segment_level[None, :], 0), axis=1)
    level_hit = levels[:, None] == jnp.arange(blow_table.shape[0], dtype=jnp.int32)[None, :]
    return jnp.sum(jnp.where(level_hit[:, :, None], blow_table[None, :, :], 0.0), axis=1)


def replicate_lanes(small, planes):
    pick = (
        jnp.arange(LANES, dtype=jnp.int32)[None, :] % planes
        == jnp.arange(planes, dtype=jnp.int32)[:, None]
    ).astype(jnp.float32)
    return jnp.dot(small, pick, precision=lax.Precision.HIGHEST, preferred_element_type=jnp.float32)


def shards(state, shock_height, wall_segment, segment_level, blow_table):
    planes = blow_table.shape[1]
    columns = state.shape[1]
    length = state.shape[2]
    row_count = length // planes
    col_devs = lax.axis_size("gx")
    row_devs = lax.axis_size("gy")
    col_dev = lax.axis_index("gx")
    row_dev = lax.axis_index("gy")
    total_rows = row_count * row_devs
    band = HALO * planes

    def pack(cols, heights):
        extra = jnp.zeros((1, HALO, length), jnp.float32)
        extra = lax.dynamic_update_slice(extra, heights[None], (0, 0, 0))
        return jnp.concatenate([cols, extra], axis=0)

    from_low = shifted(pack(state[:, columns - HALO :], shock_height[columns - HALO :]), "gx", True)
    from_high = shifted(pack(state[:, :HALO], shock_height[:HALO]), "gx", False)
    plane_lane = jnp.arange(PAD, dtype=jnp.int32)[None, None, :]
    top_block = state[..., length - PAD :]
    below = shifted(top_block, "gy", True, cyclic=True)
    above = shifted(jnp.where(plane_lane < band, state[..., :PAD], top_block), "gy", False)
    low_height = jnp.where(
        col_dev == 0, jnp.broadcast_to(shock_height[:1], (HALO, planes)), from_low[6, :, :planes]
    )
    high_height = jnp.where(
        col_dev == col_devs - 1,
        jnp.broadcast_to(shock_height[columns - 1 :], (HALO, planes)),
        from_high[6, :, :planes],
    )
    height_ext = jnp.concatenate([low_height, shock_height, high_height], axis=0)
    slope_x, slope_z = slopes(height_ext, planes)

    top_seed = jnp.where(row_dev == row_devs - 1, top_block, jnp.where(row_dev == 0, below, above))
    top_seed, below, above = lax.optimization_barrier((top_seed, below, above))
    seeded = sorted({row_devs - 1, 0, max(row_devs - 2, 0)}, reverse=True)
    top_before, top_last, last_targets = broadcast(top_seed, "gy", seeded, (2, 1, 1, 1, 1))

    blowing = wall_flux(wall_segment, segment_level, blow_table)

    height = shock_height
    height_x = jnp.concatenate(
        [
            jnp.broadcast_to(height_ext[:1], (XPAD - HALO, planes)),
            height_ext,
            jnp.broadcast_to(height_ext[-1:], (XPAD - HALO, planes)),
        ],
        axis=0,
    )
    small = jnp.concatenate([height_x, slope_x, slope_z, height, blowing], axis=0)
    geo = replicate_lanes(small, planes)
    state_new, shock_new = update(
        state,
        from_low,
        from_high,
        below,
        above,
        geo,
        top_before,
        top_last,
        shock_height,
        tuple(last_targets),
        planes,
        total_rows,
        COURANT / total_rows,
    )
    return (state_new, shock_new)


def solution(mesh):
    in_specs = (P(None, "gx", "gy"), P("gx", None), P("gx"), P(), P())
    out_specs = (P(None, "gx", "gy"), P("gx", None))
    return jax.shard_map(shards, mesh=mesh, in_specs=in_specs, out_specs=out_specs, check_vma=False)
```

```python
import math

import jax
import jax.numpy as jnp
from jax import lax
from jax.experimental import pallas as pl
from jax.experimental.pallas import tpu as pltpu
from jax.sharding import PartitionSpec as P

HEAT_RATIO = 1.4
STREAM_STEP = 0.05
SPAN_STEP = 0.05
STRETCH_RATE = 2.0
CHARACTER_KELVIN = 3.0
WHITE_LAW_FACTOR = 1.0
LANDAU_TELLER = 0.002
FREE_PRESSURE = 0.1
FREE_MACH = 6.0
COURANT = 0.05

FLUX_WEIGHTS = (45.0, -9.0, 1.0)
SPEED_WEIGHTS = (20.0, -15.0, 6.0, -1.0)
CHUNK = 512
PAD = 128
HALO = 3
XPAD = 8
LANES = 128


def kernel_primitives(q):
    inverse = 1.0 / q[0]
    vel_x = q[1] * inverse
    vel_y = q[2] * inverse
    vel_z = q[3] * inverse
    stress = (HEAT_RATIO - 1.0) * (q[4] - 0.5 * (q[1] * vel_x + q[2] * vel_y + q[3] * vel_z) - q[5])
    sound = jnp.sqrt(HEAT_RATIO * stress * inverse)
    return inverse, vel_x, vel_y, vel_z, stress, sound


def pair_terms(flux, damped, t):
    odd = FLUX_WEIGHTS[t - 1]
    even = SPEED_WEIGHTS[t]
    odd_part = flux if odd == 1.0 else odd * flux
    if even == -1.0:
        return odd_part - damped, -(odd_part + damped)
    even_part = even * damped
    return even_part + odd_part, even_part - odd_part


def lane_tile(values, width):
    return jnp.concatenate([values] * (width // values.shape[-1]), axis=-1)


def stretch_factors(rows, total_rows):
    growth = jnp.exp(STRETCH_RATE * (rows + 0.5) / total_rows)
    denominator = math.exp(STRETCH_RATE) - 1.0
    return (growth - 1.0) / denominator, STRETCH_RATE * growth / (total_rows * denominator)


def make_kernel(columns, length, planes, total_rows, dt, targets):
    width = CHUNK + 2 * PAD
    face_area = STREAM_STEP * SPAN_STEP
    xrows = columns + 2 * XPAD

    def kernel(state_ref, xlo_ref, xhi_ref, below_ref, above_ref, geo_ref, before_ref, last_ref,
               height_ref, out_ref, shock_ref, qx_ref, qy_ref, pair_ref):
        col_dev = lax.axis_index("gx")
        first_row = lax.axis_index("gy") * (length // planes)
        for c in range(6):
            qx_ref[c, 0:XPAD, :] = state_ref[c, 0:XPAD, :]
            qx_ref[c, XPAD:XPAD + columns, :] = state_ref[c]
            qx_ref[c, XPAD + columns:, :] = state_ref[c, columns - XPAD:, :]
            qx_ref[c, XPAD - HALO:XPAD, :] = xlo_ref[c]
            qx_ref[c, XPAD + columns:XPAD + columns + HALO, :] = xhi_ref[c]
            qy_ref[c, :, 0:PAD] = below_ref[c]
            qy_ref[c, :, PAD:PAD + length] = state_ref[c]
            qy_ref[c, :, PAD + length:] = above_ref[c]

        @pl.when(col_dev == 0)
        def _():
            for c in range(6):
                qx_ref[c, XPAD - HALO:XPAD, :] = jnp.broadcast_to(state_ref[c, 0:1, :], (HALO, length))

        @pl.when(col_dev == lax.axis_size("gx") - 1)
        def _():
            for c in range(6):
                qx_ref[c, XPAD + columns:XPAD + columns + HALO, :] = jnp.broadcast_to(
                    state_ref[c, columns - 1:columns, :], (HALO, length))

        height_x = lane_tile(geo_ref[0:xrows, :], CHUNK)
        slope_x_row = geo_ref[xrows:xrows + columns, :]
        slope_z_row = geo_ref[xrows + columns:xrows + 2 * columns, :]
        height_row = geo_ref[xrows + 2 * columns:xrows + 3 * columns, :]
        group = lax.broadcasted_iota(jnp.int32, (columns, LANES), 1) // planes

        @pl.when(lax.axis_index("gy") == 0)
        def _():
            mirror = []
            for c in range(6):
                rows = state_ref[c, :, 0:LANES]
                mirror.append(jnp.where(group == 2, pltpu.roll(rows, planes, 1),
                                        pltpu.roll(rows, 3 * planes, 1)))
            blown_y = 2.0 * geo_ref[xrows + 3 * columns:xrows + 4 * columns, :] - mirror[2]
            energy = mirror[4] + 0.5 * (blown_y * blown_y - mirror[2] * mirror[2]) / mirror[0]
            ghosts = [mirror[0], mirror[1], blown_y, mirror[3], energy, mirror[5]]
            for c in range(6):
                qy_ref[c, :, 0:PAD] = ghosts[c]

        @pl.when(lax.axis_index("gy") == lax.axis_size("gy") - 1)
        def _():
            for c in range(6):
                rows = state_ref[c, :, length - LANES:]
                qy_ref[c, :, PAD + length:] = jnp.where(
                    group == 0, pltpu.roll(rows, planes, 1),
                    jnp.where(group == 1, pltpu.roll(rows, 2 * planes, 1),
                              jnp.where(group == 2, pltpu.roll(rows, 3 * planes, 1), rows)))
        top = []
        row_dev = lax.axis_index("gy")
        hit = jnp.zeros((columns, LANES), jnp.bool_)
        for target in targets:
            hit = hit | (row_dev == target)
        for c in range(6):
            held = jnp.where(hit, last_ref[c], before_ref[c])
            spread = jnp.where(group == 0, pltpu.roll(held, planes, 1),
                               jnp.where(group == 1, pltpu.roll(held, 2 * planes, 1),
                                         jnp.where(group == 2, pltpu.roll(held, 3 * planes, 1), held)))
            top.append(spread)
        rate_row = shock_speed(top, slope_x_row, slope_z_row)
        shock_ref[...] = height_ref[...] + dt * rate_row[:, 0:planes]
        slope_x = lane_tile(slope_x_row, width)
        slope_z = lane_tile(slope_z_row, width)
        rate = lane_tile(rate_row, width)
        ratio = lane_tile(rate_row / height_row, CHUNK)
        height = lane_tile(height_row, CHUNK)
        lane = lax.broadcasted_iota(jnp.int32, (columns, CHUNK), 1) % planes
        lane_in = lax.broadcasted_iota(jnp.int32, (1, CHUNK), 1)
        lane_out = lax.broadcasted_iota(jnp.int32, (1, width), 1)

        def body(k, carry):
            o = pl.multiple_of(k * CHUNK, CHUNK)
            rows_in = (first_row + (o + lane_in) // planes).astype(jnp.float32)
            spacing = stretch_factors(rows_in, total_rows)[1]
            rows_out = (first_row - PAD // planes + (o + lane_out) // planes).astype(jnp.float32)
            eta = stretch_factors(rows_out, total_rows)[0]
            xa = [qx_ref[c, :, pl.ds(o, CHUNK)] for c in range(6)]
            inverse, vel_x, vel_y, vel_z, stress, sound = kernel_primitives(xa)
            metric = STREAM_STEP * height_x * spacing
            fluxes = [xa[1], xa[1] * vel_x + stress, xa[2] * vel_x, xa[3] * vel_x,
                      (xa[4] + stress) * vel_x, xa[5] * vel_x]
            speed = (jnp.abs(vel_x) + sound) * metric
            div = []
            for c in range(6):
                flux = fluxes[c] * metric
                damped = speed * xa[c]
                for t in range(1, 4):
                    up, down = pair_terms(flux, damped, t)
                    pair_ref[c, 2 * t - 2] = up
                    pair_ref[c, 2 * t - 1] = down
                acc = SPEED_WEIGHTS[0] * damped[XPAD:XPAD + columns]
                for t in range(1, 4):
                    acc = acc + pair_ref[c, 2 * t - 2, pl.ds(XPAD + t, columns), :]
                    acc = acc + pair_ref[c, 2 * t - 1, pl.ds(XPAD - t, columns), :]
                div.append(acc)
            ya = [qy_ref[c, :, pl.ds(o, width)] for c in range(6)]
            inverse, vel_x, vel_y, vel_z, stress, sound = kernel_primitives(ya)
            scaled = -face_area * eta
            metric_x = scaled * slope_x
            metric_z = scaled * slope_z
            metric_t = scaled * rate
            contra = metric_t + metric_x * vel_x + face_area * vel_y + metric_z * vel_z
            fluxes = [ya[0] * contra, ya[1] * contra + metric_x * stress,
                      ya[2] * contra + face_area * stress, ya[3] * contra + metric_z * stress,
                      (ya[4] + stress) * contra - metric_t * stress, ya[5] * contra]
            speed = jnp.abs(contra) + sound * jnp.sqrt(
                metric_x * metric_x + face_area * face_area + metric_z * metric_z)
            for c in range(6):
                damped = speed * ya[c]
                acc = SPEED_WEIGHTS[0] * damped
                for t in range(1, 4):
                    up, down = pair_terms(fluxes[c], damped, t)
                    acc = acc + pltpu.roll(up, (-planes * t) % width, 1) + pltpu.roll(down, planes * t, 1)
                div[c] = div[c] + acc[:, PAD:PAD + CHUNK]
            q = [v[:, PAD:PAD + CHUNK] for v in ya]
            inverse = inverse[:, PAD:PAD + CHUNK]
            vel_z = vel_z[:, PAD:PAD + CHUNK]
            stress = stress[:, PAD:PAD + CHUNK]
            sound = sound[:, PAD:PAD + CHUNK]
            metric = STREAM_STEP * height * spacing
            fluxes = [q[3], q[1] * vel_z, q[2] * vel_z, q[3] * vel_z + stress,
                      (q[4] + stress) * vel_z, q[5] * vel_z]
            speed = (jnp.abs(vel_z) + sound) * metric
            for c in range(6):
                damped = speed * q[c]
                acc = SPEED_WEIGHTS[0] * damped
                for t in range(1, 4):
                    up, down = pair_terms(fluxes[c] * metric, damped, t)
                    up = jnp.where(lane < planes - t, pltpu.roll(up, CHUNK - t, 1),
                                   pltpu.roll(up, planes - t, 1))
                    down = jnp.where(lane >= t, pltpu.roll(down, t, 1),
                                     pltpu.roll(down, CHUNK - planes + t, 1))
                    acc = acc + up + down
                div[c] = div[c] + acc
            kelvin = stress * inverse
            balanced = CHARACTER_KELVIN / (jnp.exp(CHARACTER_KELVIN / kelvin) - 1.0)
            teller = stress / (LANDAU_TELLER * jnp.exp(
                WHITE_LAW_FACTOR * jnp.exp(-jnp.log(kelvin) / 3.0)))
            source = q[0] * (balanced - q[5] * inverse) * teller
            scale = 1.0 / (60.0 * (face_area * height * spacing))
            for c in range(6):
                change = -(div[c] * scale) - q[c] * ratio
                if c == 5:
                    change = change + source
                out_ref[c, :, pl.ds(o, CHUNK)] = q[c] + dt * change
            return carry

        lax.fori_loop(0, length // CHUNK, body, 0)

    return kernel


def update(state, xlo, xhi, below, above, geo, top_before, top_last, height, targets, planes, total_rows,
           dt):
    columns = state.shape[1]
    length = state.shape[2]
    kern = make_kernel(columns, length, planes, total_rows, dt, targets)
    vmem = pl.BlockSpec(memory_space=pltpu.VMEM)
    return pl.pallas_call(
        kern,
        out_shape=(
            jax.ShapeDtypeStruct((6, columns, length), jnp.float32),
            jax.ShapeDtypeStruct((columns, planes), jnp.float32),
        ),
        in_specs=[vmem] * 9,
        out_specs=(vmem, vmem),
        scratch_shapes=[
            pltpu.VMEM((6, columns + 2 * XPAD, length), jnp.float32),
            pltpu.VMEM((6, columns, length + 2 * PAD), jnp.float32),
            pltpu.VMEM((6, 6, columns + 2 * XPAD, CHUNK), jnp.float32),
        ],
    )(state, xlo, xhi, below, above, geo, top_before, top_last, height)


def shifted(block, axis, forward, cyclic=False):
    count = lax.axis_size(axis)
    pairs = [(i, i + 1) for i in range(count - 1)]
    if cyclic and count > 1:
        pairs.append((count - 1, 0))
    if not forward:
        pairs = [(target, source) for source, target in pairs]
    return lax.ppermute(block, axis, pairs)


def broadcast(array, axis, holders, fanouts):
    count = lax.axis_size(axis)
    index = lax.axis_index(axis)
    last = (array, array, [])
    for fanout in fanouts:
        if len(holders) >= count:
            break
        waiting = [i for i in range(count) if i not in holders]
        targets = jnp.zeros((), jnp.bool_)
        arrived = array
        reached = []
        for _ in range(fanout):
            pairs = list(zip(holders, waiting))
            waiting = waiting[len(pairs) :]
            if not pairs:
                break
            received = lax.ppermute(array, axis, pairs)
            last = (arrived, received, [target for _, target in pairs])
            hit = jnp.zeros((), jnp.bool_)
            for _, target in pairs:
                hit = hit | (index == target)
            arrived = jnp.where(hit, received, arrived)
            reached = reached + [target for _, target in pairs]
        array = arrived
        holders = holders + reached
    return last


def zshift(values, offset, planes):
    length = values.shape[-1]
    plane_at = jnp.arange(length, dtype=jnp.int32) % planes
    if offset > 0:
        return jnp.where(
            plane_at >= offset,
            jnp.roll(values, offset, axis=-1),
            jnp.roll(values, offset - planes, axis=-1),
        )
    return jnp.where(
        plane_at < planes + offset,
        jnp.roll(values, offset, axis=-1),
        jnp.roll(values, offset + planes, axis=-1),
    )


def primitives(conserved):
    specific_volume_inverse = conserved[0]
    vel_x = conserved[1] / specific_volume_inverse
    vel_y = conserved[2] / specific_volume_inverse
    vel_z = conserved[3] / specific_volume_inverse
    thermodynamic_stress = (HEAT_RATIO - 1.0) * (
        conserved[4]
        - 0.5 * (conserved[1] * vel_x + conserved[2] * vel_y + conserved[3] * vel_z)
        - conserved[5]
    )
    sound_speed = jnp.sqrt(HEAT_RATIO * thermodynamic_stress / specific_volume_inverse)
    return (specific_volume_inverse, vel_x, vel_y, vel_z, thermodynamic_stress, sound_speed)


def slopes(height_ext, planes):
    columns = height_ext.shape[0] - 6
    slope_x = (
        height_ext[1 : columns + 1]
        - 8.0 * height_ext[2 : columns + 2]
        + 8.0 * height_ext[4 : columns + 4]
        - height_ext[5 : columns + 5]
    ) / (12.0 * STREAM_STEP)
    height = height_ext[3 : columns + 3]
    slope_z = (
        zshift(height, 2, planes)
        - 8.0 * zshift(height, 1, planes)
        + 8.0 * zshift(height, -1, planes)
        - zshift(height, -2, planes)
    ) / (12.0 * SPAN_STEP)
    return (slope_x, slope_z)


def shock_speed(top_row, slope_x, slope_z):
    specific_volume_inverse, vel_x, vel_y, vel_z, thermodynamic_stress, sound_speed = primitives(
        top_row
    )
    tilt_norm = jnp.sqrt(1.0 + slope_x * slope_x + slope_z * slope_z)
    normal = (vel_y - vel_x * slope_x - vel_z * slope_z) / tilt_norm
    sine_sq = slope_x * slope_x / (tilt_norm * tilt_norm)
    jump_pressure = FREE_PRESSURE * (
        1.0 + 2.0 * HEAT_RATIO / (HEAT_RATIO + 1.0) * (FREE_MACH * FREE_MACH * sine_sq - 1.0)
    )
    return tilt_norm * (
        normal + (jump_pressure - thermodynamic_stress) / (specific_volume_inverse * sound_speed)
    )


def wall_ghosts(first_rows, blowing, planes):
    mirror = jnp.concatenate(
        [
            first_rows[..., 2 * planes : 3 * planes],
            first_rows[..., planes : 2 * planes],
            first_rows[..., 0:planes],
        ],
        axis=-1,
    )
    blown_y = 2.0 * jnp.tile(blowing, (1, 3)) - mirror[2]
    stagnation_enthalpy_sum = (
        mirror[4] + 0.5 * (blown_y * blown_y - mirror[2] * mirror[2]) / mirror[0]
    )
    return jnp.stack([mirror[0], mirror[1], blown_y, mirror[3], stagnation_enthalpy_sum, mirror[5]])


def wall_flux(wall_segment, segment_level, blow_table):
    seg_hit = wall_segment[:, None] == jnp.arange(segment_level.shape[0], dtype=jnp.int32)[None, :]
    levels = jnp.sum(jnp.where(seg_hit, segment_level[None, :], 0), axis=1)
    level_hit = levels[:, None] == jnp.arange(blow_table.shape[0], dtype=jnp.int32)[None, :]
    return jnp.sum(jnp.where(level_hit[:, :, None], blow_table[None, :, :], 0.0), axis=1)


def replicate_lanes(small, planes):
    pick = (
        jnp.arange(LANES, dtype=jnp.int32)[None, :] % planes
        == jnp.arange(planes, dtype=jnp.int32)[:, None]
    ).astype(jnp.float32)
    return jnp.dot(small, pick, precision=lax.Precision.HIGHEST, preferred_element_type=jnp.float32)


def shards(state, shock_height, wall_segment, segment_level, blow_table):
    planes = blow_table.shape[1]
    columns = state.shape[1]
    length = state.shape[2]
    row_count = length // planes
    col_devs = lax.axis_size("gx")
    row_devs = lax.axis_size("gy")
    col_dev = lax.axis_index("gx")
    row_dev = lax.axis_index("gy")
    total_rows = row_count * row_devs
    band = HALO * planes

    def pack(cols, heights):
        extra = jnp.zeros((1, HALO, length), jnp.float32)
        extra = lax.dynamic_update_slice(extra, heights[None], (0, 0, 0))
        return jnp.concatenate([cols, extra], axis=0)

    from_low = shifted(pack(state[:, columns - HALO :], shock_height[columns - HALO :]), "gx", True)
    from_high = shifted(pack(state[:, :HALO], shock_height[:HALO]), "gx", False)
    plane_lane = jnp.arange(PAD, dtype=jnp.int32)[None, None, :]
    top_block = state[..., length - PAD :]
    below = shifted(top_block, "gy", True, cyclic=True)
    above = shifted(jnp.where(plane_lane < band, state[..., :PAD], top_block), "gy", False)
    low_height = jnp.where(
        col_dev == 0, jnp.broadcast_to(shock_height[:1], (HALO, planes)), from_low[6, :, :planes]
    )
    high_height = jnp.where(
        col_dev == col_devs - 1,
        jnp.broadcast_to(shock_height[columns - 1 :], (HALO, planes)),
        from_high[6, :, :planes],
    )
    height_ext = jnp.concatenate([low_height, shock_height, high_height], axis=0)
    slope_x, slope_z = slopes(height_ext, planes)

    top_seed = jnp.where(row_dev == row_devs - 1, top_block, jnp.where(row_dev == 0, below, above))
    top_seed, below, above = lax.optimization_barrier((top_seed, below, above))
    seeded = sorted({row_devs - 1, 0, max(row_devs - 2, 0)}, reverse=True)
    top_before, top_last, last_targets = broadcast(top_seed, "gy", seeded, (1, 2, 1, 1, 1))

    blowing = wall_flux(wall_segment, segment_level, blow_table)

    height = shock_height
    height_x = jnp.concatenate(
        [
            jnp.broadcast_to(height_ext[:1], (XPAD - HALO, planes)),
            height_ext,
            jnp.broadcast_to(height_ext[-1:], (XPAD - HALO, planes)),
        ],
        axis=0,
    )
    small = jnp.concatenate([height_x, slope_x, slope_z, height, blowing], axis=0)
    geo = replicate_lanes(small, planes)
    state_new, shock_new = update(
        state,
        from_low,
        from_high,
        below,
        above,
        geo,
        top_before,
        top_last,
        shock_height,
        tuple(last_targets),
        planes,
        total_rows,
        COURANT / total_rows,
    )
    return (state_new, shock_new)


def solution(mesh):
    in_specs = (P(None, "gx", "gy"), P("gx", None), P("gx"), P(), P())
    out_specs = (P(None, "gx", "gy"), P("gx", None))
    return jax.shard_map(shards, mesh=mesh, in_specs=in_specs, out_specs=out_specs, check_vma=False)
```

```python
import math

import jax
import jax.numpy as jnp
from jax import lax
from jax.experimental import pallas as pl
from jax.experimental.pallas import tpu as pltpu
from jax.sharding import PartitionSpec as P

HEAT_RATIO = 1.4
STREAM_STEP = 0.05
SPAN_STEP = 0.05
STRETCH_RATE = 2.0
CHARACTER_KELVIN = 3.0
WHITE_LAW_FACTOR = 1.0
LANDAU_TELLER = 0.002
FREE_PRESSURE = 0.1
FREE_MACH = 6.0
COURANT = 0.05

FLUX_WEIGHTS = (45.0, -9.0, 1.0)
SPEED_WEIGHTS = (20.0, -15.0, 6.0, -1.0)
CHUNK = 512
PAD = 128
HALO = 3
XPAD = 8
LANES = 128


def kernel_primitives(q):
    inverse = 1.0 / q[0]
    vel_x = q[1] * inverse
    vel_y = q[2] * inverse
    vel_z = q[3] * inverse
    stress = (HEAT_RATIO - 1.0) * (q[4] - 0.5 * (q[1] * vel_x + q[2] * vel_y + q[3] * vel_z) - q[5])
    sound = jnp.sqrt(HEAT_RATIO * stress * inverse)
    return inverse, vel_x, vel_y, vel_z, stress, sound


def pair_terms(flux, damped, t):
    odd = FLUX_WEIGHTS[t - 1]
    even = SPEED_WEIGHTS[t]
    odd_part = flux if odd == 1.0 else odd * flux
    if even == -1.0:
        return odd_part - damped, -(odd_part + damped)
    even_part = even * damped
    return even_part + odd_part, even_part - odd_part


def lane_tile(values, width):
    return jnp.concatenate([values] * (width // values.shape[-1]), axis=-1)


def stretch_factors(rows, total_rows):
    growth = jnp.exp(STRETCH_RATE * (rows + 0.5) / total_rows)
    denominator = math.exp(STRETCH_RATE) - 1.0
    return (growth - 1.0) / denominator, STRETCH_RATE * growth / (total_rows * denominator)


def make_kernel(columns, length, planes, total_rows, dt, targets):
    width = CHUNK + 2 * PAD
    face_area = STREAM_STEP * SPAN_STEP
    xrows = columns + 2 * XPAD

    def kernel(state_ref, xlo_ref, xhi_ref, below_ref, above_ref, geo_ref, before_ref, last_ref,
               height_ref, out_ref, shock_ref, qx_ref, qy_ref, pair_ref):
        col_dev = lax.axis_index("gx")
        first_row = lax.axis_index("gy") * (length // planes)
        for c in range(6):
            qx_ref[c, 0:XPAD, :] = state_ref[c, 0:XPAD, :]
            qx_ref[c, XPAD:XPAD + columns, :] = state_ref[c]
            qx_ref[c, XPAD + columns:, :] = state_ref[c, columns - XPAD:, :]
            qx_ref[c, XPAD - HALO:XPAD, :] = xlo_ref[c, :, 0:length]
            qx_ref[c, XPAD + columns:XPAD + columns + HALO, :] = xhi_ref[c, :, 0:length]
            qy_ref[c, :, 0:PAD] = below_ref[c]
            qy_ref[c, :, PAD:PAD + length] = state_ref[c]
            qy_ref[c, :, PAD + length:] = above_ref[c]

        @pl.when(col_dev == 0)
        def _():
            for c in range(6):
                qx_ref[c, XPAD - HALO:XPAD, :] = jnp.broadcast_to(state_ref[c, 0:1, :], (HALO, length))

        @pl.when(col_dev == lax.axis_size("gx") - 1)
        def _():
            for c in range(6):
                qx_ref[c, XPAD + columns:XPAD + columns + HALO, :] = jnp.broadcast_to(
                    state_ref[c, columns - 1:columns, :], (HALO, length))

        height_x = lane_tile(geo_ref[0:xrows, :], CHUNK)
        slope_x_row = geo_ref[xrows:xrows + columns, :]
        slope_z_row = geo_ref[xrows + columns:xrows + 2 * columns, :]
        height_row = geo_ref[xrows + 2 * columns:xrows + 3 * columns, :]
        group = lax.broadcasted_iota(jnp.int32, (columns, LANES), 1) // planes

        @pl.when(lax.axis_index("gy") == 0)
        def _():
            mirror = []
            for c in range(6):
                rows = state_ref[c, :, 0:LANES]
                mirror.append(jnp.where(group == 2, pltpu.roll(rows, planes, 1),
                                        pltpu.roll(rows, 3 * planes, 1)))
            blown_y = 2.0 * geo_ref[xrows + 3 * columns:xrows + 4 * columns, :] - mirror[2]
            energy = mirror[4] + 0.5 * (blown_y * blown_y - mirror[2] * mirror[2]) / mirror[0]
            ghosts = [mirror[0], mirror[1], blown_y, mirror[3], energy, mirror[5]]
            for c in range(6):
                qy_ref[c, :, 0:PAD] = ghosts[c]

        @pl.when(lax.axis_index("gy") == lax.axis_size("gy") - 1)
        def _():
            for c in range(6):
                rows = state_ref[c, :, length - LANES:]
                qy_ref[c, :, PAD + length:] = jnp.where(
                    group == 0, pltpu.roll(rows, planes, 1),
                    jnp.where(group == 1, pltpu.roll(rows, 2 * planes, 1),
                              jnp.where(group == 2, pltpu.roll(rows, 3 * planes, 1), rows)))
        top = []
        row_dev = lax.axis_index("gy")
        hit = jnp.zeros((columns, LANES), jnp.bool_)
        for target in targets:
            hit = hit | (row_dev == target)
        for c in range(6):
            held = jnp.where(hit, last_ref[c], before_ref[c])
            spread = jnp.where(group == 0, pltpu.roll(held, planes, 1),
                               jnp.where(group == 1, pltpu.roll(held, 2 * planes, 1),
                                         jnp.where(group == 2, pltpu.roll(held, 3 * planes, 1), held)))
            top.append(spread)
        rate_row = shock_speed(top, slope_x_row, slope_z_row)
        shock_ref[...] = height_ref[...] + dt * rate_row[:, 0:planes]
        slope_x = lane_tile(slope_x_row, width)
        slope_z = lane_tile(slope_z_row, width)
        rate = lane_tile(rate_row, width)
        ratio = lane_tile(rate_row / height_row, CHUNK)
        height = lane_tile(height_row, CHUNK)
        lane = lax.broadcasted_iota(jnp.int32, (columns, CHUNK), 1) % planes
        lane_in = lax.broadcasted_iota(jnp.int32, (1, CHUNK), 1)
        lane_out = lax.broadcasted_iota(jnp.int32, (1, width), 1)

        def body(k, carry):
            o = pl.multiple_of(k * CHUNK, CHUNK)
            rows_in = (first_row + (o + lane_in) // planes).astype(jnp.float32)
            spacing = stretch_factors(rows_in, total_rows)[1]
            rows_out = (first_row - PAD // planes + (o + lane_out) // planes).astype(jnp.float32)
            eta = stretch_factors(rows_out, total_rows)[0]
            xa = [qx_ref[c, :, pl.ds(o, CHUNK)] for c in range(6)]
            inverse, vel_x, vel_y, vel_z, stress, sound = kernel_primitives(xa)
            metric = STREAM_STEP * height_x * spacing
            fluxes = [xa[1], xa[1] * vel_x + stress, xa[2] * vel_x, xa[3] * vel_x,
                      (xa[4] + stress) * vel_x, xa[5] * vel_x]
            speed = (jnp.abs(vel_x) + sound) * metric
            div = []
            for c in range(6):
                flux = fluxes[c] * metric
                damped = speed * xa[c]
                for t in range(1, 4):
                    up, down = pair_terms(flux, damped, t)
                    pair_ref[c, 2 * t - 2] = up
                    pair_ref[c, 2 * t - 1] = down
                acc = SPEED_WEIGHTS[0] * damped[XPAD:XPAD + columns]
                for t in range(1, 4):
                    acc = acc + pair_ref[c, 2 * t - 2, pl.ds(XPAD + t, columns), :]
                    acc = acc + pair_ref[c, 2 * t - 1, pl.ds(XPAD - t, columns), :]
                div.append(acc)
            ya = [qy_ref[c, :, pl.ds(o, width)] for c in range(6)]
            inverse, vel_x, vel_y, vel_z, stress, sound = kernel_primitives(ya)
            scaled = -face_area * eta
            metric_x = scaled * slope_x
            metric_z = scaled * slope_z
            metric_t = scaled * rate
            contra = metric_t + metric_x * vel_x + face_area * vel_y + metric_z * vel_z
            fluxes = [ya[0] * contra, ya[1] * contra + metric_x * stress,
                      ya[2] * contra + face_area * stress, ya[3] * contra + metric_z * stress,
                      (ya[4] + stress) * contra - metric_t * stress, ya[5] * contra]
            speed = jnp.abs(contra) + sound * jnp.sqrt(
                metric_x * metric_x + face_area * face_area + metric_z * metric_z)
            for c in range(6):
                damped = speed * ya[c]
                acc = SPEED_WEIGHTS[0] * damped
                for t in range(1, 4):
                    up, down = pair_terms(fluxes[c], damped, t)
                    acc = acc + pltpu.roll(up, (-planes * t) % width, 1) + pltpu.roll(down, planes * t, 1)
                div[c] = div[c] + acc[:, PAD:PAD + CHUNK]
            q = [v[:, PAD:PAD + CHUNK] for v in ya]
            inverse = inverse[:, PAD:PAD + CHUNK]
            vel_z = vel_z[:, PAD:PAD + CHUNK]
            stress = stress[:, PAD:PAD + CHUNK]
            sound = sound[:, PAD:PAD + CHUNK]
            metric = STREAM_STEP * height * spacing
            fluxes = [q[3], q[1] * vel_z, q[2] * vel_z, q[3] * vel_z + stress,
                      (q[4] + stress) * vel_z, q[5] * vel_z]
            speed = (jnp.abs(vel_z) + sound) * metric
            for c in range(6):
                damped = speed * q[c]
                acc = SPEED_WEIGHTS[0] * damped
                for t in range(1, 4):
                    up, down = pair_terms(fluxes[c] * metric, damped, t)
                    up = jnp.where(lane < planes - t, pltpu.roll(up, CHUNK - t, 1),
                                   pltpu.roll(up, planes - t, 1))
                    down = jnp.where(lane >= t, pltpu.roll(down, t, 1),
                                     pltpu.roll(down, CHUNK - planes + t, 1))
                    acc = acc + up + down
                div[c] = div[c] + acc
            kelvin = stress * inverse
            balanced = CHARACTER_KELVIN / (jnp.exp(CHARACTER_KELVIN / kelvin) - 1.0)
            teller = stress / (LANDAU_TELLER * jnp.exp(
                WHITE_LAW_FACTOR * jnp.exp(-jnp.log(kelvin) / 3.0)))
            source = q[0] * (balanced - q[5] * inverse) * teller
            scale = 1.0 / (60.0 * (face_area * height * spacing))
            for c in range(6):
                change = -(div[c] * scale) - q[c] * ratio
                if c == 5:
                    change = change + source
                out_ref[c, :, pl.ds(o, CHUNK)] = q[c] + dt * change
            return carry

        lax.fori_loop(0, length // CHUNK, body, 0)

    return kernel


def update(state, xlo, xhi, below, above, geo, top_before, top_last, height, targets, planes, total_rows,
           dt):
    columns = state.shape[1]
    length = state.shape[2]
    kern = make_kernel(columns, length, planes, total_rows, dt, targets)
    vmem = pl.BlockSpec(memory_space=pltpu.VMEM)
    return pl.pallas_call(
        kern,
        out_shape=(
            jax.ShapeDtypeStruct((6, columns, length), jnp.float32),
            jax.ShapeDtypeStruct((columns, planes), jnp.float32),
        ),
        in_specs=[vmem] * 9,
        out_specs=(vmem, vmem),
        scratch_shapes=[
            pltpu.VMEM((6, columns + 2 * XPAD, length), jnp.float32),
            pltpu.VMEM((6, columns, length + 2 * PAD), jnp.float32),
            pltpu.VMEM((6, 6, columns + 2 * XPAD, CHUNK), jnp.float32),
        ],
    )(state, xlo, xhi, below, above, geo, top_before, top_last, height)


def shifted(block, axis, forward, cyclic=False):
    count = lax.axis_size(axis)
    pairs = [(i, i + 1) for i in range(count - 1)]
    if cyclic and count > 1:
        pairs.append((count - 1, 0))
    if not forward:
        pairs = [(target, source) for source, target in pairs]
    return lax.ppermute(block, axis, pairs)


def broadcast(array, axis, holders, fanouts):
    count = lax.axis_size(axis)
    index = lax.axis_index(axis)
    last = (array, array, [])
    for fanout in fanouts:
        if len(holders) >= count:
            break
        waiting = [i for i in range(count) if i not in holders]
        targets = jnp.zeros((), jnp.bool_)
        arrived = array
        reached = []
        for _ in range(fanout):
            pairs = list(zip(holders, waiting))
            waiting = waiting[len(pairs) :]
            if not pairs:
                break
            received = lax.ppermute(array, axis, pairs)
            last = (arrived, received, [target for _, target in pairs])
            hit = jnp.zeros((), jnp.bool_)
            for _, target in pairs:
                hit = hit | (index == target)
            arrived = jnp.where(hit, received, arrived)
            reached = reached + [target for _, target in pairs]
        array = arrived
        holders = holders + reached
    return last


def zshift(values, offset, planes):
    length = values.shape[-1]
    plane_at = jnp.arange(length, dtype=jnp.int32) % planes
    if offset > 0:
        return jnp.where(
            plane_at >= offset,
            jnp.roll(values, offset, axis=-1),
            jnp.roll(values, offset - planes, axis=-1),
        )
    return jnp.where(
        plane_at < planes + offset,
        jnp.roll(values, offset, axis=-1),
        jnp.roll(values, offset + planes, axis=-1),
    )


def primitives(conserved):
    specific_volume_inverse = conserved[0]
    vel_x = conserved[1] / specific_volume_inverse
    vel_y = conserved[2] / specific_volume_inverse
    vel_z = conserved[3] / specific_volume_inverse
    thermodynamic_stress = (HEAT_RATIO - 1.0) * (
        conserved[4]
        - 0.5 * (conserved[1] * vel_x + conserved[2] * vel_y + conserved[3] * vel_z)
        - conserved[5]
    )
    sound_speed = jnp.sqrt(HEAT_RATIO * thermodynamic_stress / specific_volume_inverse)
    return (specific_volume_inverse, vel_x, vel_y, vel_z, thermodynamic_stress, sound_speed)


def slopes(height_ext, planes):
    columns = height_ext.shape[0] - 6
    slope_x = (
        height_ext[1 : columns + 1]
        - 8.0 * height_ext[2 : columns + 2]
        + 8.0 * height_ext[4 : columns + 4]
        - height_ext[5 : columns + 5]
    ) / (12.0 * STREAM_STEP)
    height = height_ext[3 : columns + 3]
    slope_z = (
        zshift(height, 2, planes)
        - 8.0 * zshift(height, 1, planes)
        + 8.0 * zshift(height, -1, planes)
        - zshift(height, -2, planes)
    ) / (12.0 * SPAN_STEP)
    return (slope_x, slope_z)


def shock_speed(top_row, slope_x, slope_z):
    specific_volume_inverse, vel_x, vel_y, vel_z, thermodynamic_stress, sound_speed = primitives(
        top_row
    )
    tilt_norm = jnp.sqrt(1.0 + slope_x * slope_x + slope_z * slope_z)
    normal = (vel_y - vel_x * slope_x - vel_z * slope_z) / tilt_norm
    sine_sq = slope_x * slope_x / (tilt_norm * tilt_norm)
    jump_pressure = FREE_PRESSURE * (
        1.0 + 2.0 * HEAT_RATIO / (HEAT_RATIO + 1.0) * (FREE_MACH * FREE_MACH * sine_sq - 1.0)
    )
    return tilt_norm * (
        normal + (jump_pressure - thermodynamic_stress) / (specific_volume_inverse * sound_speed)
    )


def wall_ghosts(first_rows, blowing, planes):
    mirror = jnp.concatenate(
        [
            first_rows[..., 2 * planes : 3 * planes],
            first_rows[..., planes : 2 * planes],
            first_rows[..., 0:planes],
        ],
        axis=-1,
    )
    blown_y = 2.0 * jnp.tile(blowing, (1, 3)) - mirror[2]
    stagnation_enthalpy_sum = (
        mirror[4] + 0.5 * (blown_y * blown_y - mirror[2] * mirror[2]) / mirror[0]
    )
    return jnp.stack([mirror[0], mirror[1], blown_y, mirror[3], stagnation_enthalpy_sum, mirror[5]])


def wall_flux(wall_segment, segment_level, blow_table):
    seg_hit = wall_segment[:, None] == jnp.arange(segment_level.shape[0], dtype=jnp.int32)[None, :]
    levels = jnp.sum(jnp.where(seg_hit, segment_level[None, :], 0), axis=1)
    level_hit = levels[:, None] == jnp.arange(blow_table.shape[0], dtype=jnp.int32)[None, :]
    return jnp.sum(jnp.where(level_hit[:, :, None], blow_table[None, :, :], 0.0), axis=1)


def replicate_lanes(small, planes):
    pick = (
        jnp.arange(LANES, dtype=jnp.int32)[None, :] % planes
        == jnp.arange(planes, dtype=jnp.int32)[:, None]
    ).astype(jnp.float32)
    return jnp.dot(small, pick, precision=lax.Precision.HIGHEST, preferred_element_type=jnp.float32)


def shards(state, shock_height, wall_segment, segment_level, blow_table):
    planes = blow_table.shape[1]
    columns = state.shape[1]
    length = state.shape[2]
    row_count = length // planes
    col_devs = lax.axis_size("gx")
    row_devs = lax.axis_size("gy")
    col_dev = lax.axis_index("gx")
    row_dev = lax.axis_index("gy")
    total_rows = row_count * row_devs
    band = HALO * planes

    def pack(cols, heights):
        extra = jnp.zeros((6, HALO, LANES), jnp.float32)
        extra = lax.dynamic_update_slice(extra, heights[None], (0, 0, 0))
        return jnp.concatenate([cols, extra], axis=2)

    from_low = shifted(pack(state[:, columns - HALO :], shock_height[columns - HALO :]), "gx", True)
    from_high = shifted(pack(state[:, :HALO], shock_height[:HALO]), "gx", False)
    plane_lane = jnp.arange(PAD, dtype=jnp.int32)[None, None, :]
    top_block = state[..., length - PAD :]
    below = shifted(top_block, "gy", True, cyclic=True)
    above = shifted(jnp.where(plane_lane < band, state[..., :PAD], top_block), "gy", False)
    low_height = jnp.where(
        col_dev == 0, jnp.broadcast_to(shock_height[:1], (HALO, planes)), from_low[0, :, length : length + planes]
    )
    high_height = jnp.where(
        col_dev == col_devs - 1,
        jnp.broadcast_to(shock_height[columns - 1 :], (HALO, planes)),
        from_high[0, :, length : length + planes],
    )
    height_ext = jnp.concatenate([low_height, shock_height, high_height], axis=0)
    slope_x, slope_z = slopes(height_ext, planes)

    top_seed = jnp.where(row_dev == row_devs - 1, top_block, jnp.where(row_dev == 0, below, above))
    top_seed, below, above = lax.optimization_barrier((top_seed, below, above))
    seeded = sorted({row_devs - 1, 0, max(row_devs - 2, 0)}, reverse=True)
    top_before, top_last, last_targets = broadcast(top_seed, "gy", seeded, (1, 2, 1, 1, 1))

    blowing = wall_flux(wall_segment, segment_level, blow_table)

    height = shock_height
    height_x = jnp.concatenate(
        [
            jnp.broadcast_to(height_ext[:1], (XPAD - HALO, planes)),
            height_ext,
            jnp.broadcast_to(height_ext[-1:], (XPAD - HALO, planes)),
        ],
        axis=0,
    )
    small = jnp.concatenate([height_x, slope_x, slope_z, height, blowing], axis=0)
    geo = replicate_lanes(small, planes)
    state_new, shock_new = update(
        state,
        from_low,
        from_high,
        below,
        above,
        geo,
        top_before,
        top_last,
        shock_height,
        tuple(last_targets),
        planes,
        total_rows,
        COURANT / total_rows,
    )
    return (state_new, shock_new)


def solution(mesh):
    in_specs = (P(None, "gx", "gy"), P("gx", None), P("gx"), P(), P())
    out_specs = (P(None, "gx", "gy"), P("gx", None))
    return jax.shard_map(shards, mesh=mesh, in_specs=in_specs, out_specs=out_specs, check_vma=False)
```

```python
import math

import jax
import jax.numpy as jnp
from jax import lax
from jax.experimental import pallas as pl
from jax.experimental.pallas import tpu as pltpu
from jax.sharding import PartitionSpec as P

HEAT_RATIO = 1.4
STREAM_STEP = 0.05
SPAN_STEP = 0.05
STRETCH_RATE = 2.0
CHARACTER_KELVIN = 3.0
WHITE_LAW_FACTOR = 1.0
LANDAU_TELLER = 0.002
FREE_PRESSURE = 0.1
FREE_MACH = 6.0
COURANT = 0.05

FLUX_WEIGHTS = (45.0, -9.0, 1.0)
SPEED_WEIGHTS = (20.0, -15.0, 6.0, -1.0)
CHUNK = 512
PAD = 128
HALO = 3
XPAD = 8
LANES = 128


def kernel_primitives(q):
    inverse = 1.0 / q[0]
    vel_x = q[1] * inverse
    vel_y = q[2] * inverse
    vel_z = q[3] * inverse
    stress = (HEAT_RATIO - 1.0) * (q[4] - 0.5 * (q[1] * vel_x + q[2] * vel_y + q[3] * vel_z) - q[5])
    sound = jnp.sqrt(HEAT_RATIO * stress * inverse)
    return inverse, vel_x, vel_y, vel_z, stress, sound


def pair_terms(flux, damped, t):
    odd = FLUX_WEIGHTS[t - 1]
    even = SPEED_WEIGHTS[t]
    odd_part = flux if odd == 1.0 else odd * flux
    if even == -1.0:
        return odd_part - damped, -(odd_part + damped)
    even_part = even * damped
    return even_part + odd_part, even_part - odd_part


def lane_tile(values, width):
    return jnp.concatenate([values] * (width // values.shape[-1]), axis=-1)


def stretch_factors(rows, total_rows):
    growth = jnp.exp(STRETCH_RATE * (rows + 0.5) / total_rows)
    denominator = math.exp(STRETCH_RATE) - 1.0
    return (growth - 1.0) / denominator, STRETCH_RATE * growth / (total_rows * denominator)


def make_kernel(columns, length, planes, total_rows, dt, targets):
    width = CHUNK + 2 * PAD
    face_area = STREAM_STEP * SPAN_STEP
    xrows = columns + 2 * XPAD

    def kernel(state_ref, xlo_ref, xhi_ref, below_ref, above_ref, geo_ref, before_ref, last_ref,
               height_ref, out_ref, shock_ref, qx_ref, qy_ref, pair_ref):
        col_dev = lax.axis_index("gx")
        first_row = lax.axis_index("gy") * (length // planes)
        for c in range(6):
            qx_ref[c, 0:XPAD, :] = state_ref[c, 0:XPAD, :]
            qx_ref[c, XPAD:XPAD + columns, :] = state_ref[c]
            qx_ref[c, XPAD + columns:, :] = state_ref[c, columns - XPAD:, :]
            qx_ref[c, XPAD - HALO:XPAD, :] = xlo_ref[c]
            qx_ref[c, XPAD + columns:XPAD + columns + HALO, :] = xhi_ref[c]
            qy_ref[c, :, 0:PAD] = below_ref[c]
            qy_ref[c, :, PAD:PAD + length] = state_ref[c]
            qy_ref[c, :, PAD + length:] = above_ref[c]

        @pl.when(col_dev == 0)
        def _():
            for c in range(6):
                qx_ref[c, XPAD - HALO:XPAD, :] = jnp.broadcast_to(state_ref[c, 0:1, :], (HALO, length))

        @pl.when(col_dev == lax.axis_size("gx") - 1)
        def _():
            for c in range(6):
                qx_ref[c, XPAD + columns:XPAD + columns + HALO, :] = jnp.broadcast_to(
                    state_ref[c, columns - 1:columns, :], (HALO, length))

        height_x = lane_tile(geo_ref[0:xrows, :], CHUNK)
        slope_x_row = geo_ref[xrows:xrows + columns, :]
        slope_z_row = geo_ref[xrows + columns:xrows + 2 * columns, :]
        height_row = geo_ref[xrows + 2 * columns:xrows + 3 * columns, :]
        group = lax.broadcasted_iota(jnp.int32, (columns, LANES), 1) // planes

        @pl.when(lax.axis_index("gy") == 0)
        def _():
            mirror = []
            for c in range(6):
                rows = state_ref[c, :, 0:LANES]
                mirror.append(jnp.where(group == 2, pltpu.roll(rows, planes, 1),
                                        pltpu.roll(rows, 3 * planes, 1)))
            blown_y = 2.0 * geo_ref[xrows + 3 * columns:xrows + 4 * columns, :] - mirror[2]
            energy = mirror[4] + 0.5 * (blown_y * blown_y - mirror[2] * mirror[2]) / mirror[0]
            ghosts = [mirror[0], mirror[1], blown_y, mirror[3], energy, mirror[5]]
            for c in range(6):
                qy_ref[c, :, 0:PAD] = ghosts[c]

        @pl.when(lax.axis_index("gy") == lax.axis_size("gy") - 1)
        def _():
            for c in range(6):
                rows = state_ref[c, :, length - LANES:]
                qy_ref[c, :, PAD + length:] = jnp.where(
                    group == 0, pltpu.roll(rows, planes, 1),
                    jnp.where(group == 1, pltpu.roll(rows, 2 * planes, 1),
                              jnp.where(group == 2, pltpu.roll(rows, 3 * planes, 1), rows)))
        top = []
        row_dev = lax.axis_index("gy")
        hit = jnp.zeros((columns, LANES), jnp.bool_)
        for target in targets:
            hit = hit | (row_dev == target)
        for c in range(6):
            held = jnp.where(hit, last_ref[c], before_ref[c])
            spread = jnp.where(group == 0, pltpu.roll(held, planes, 1),
                               jnp.where(group == 1, pltpu.roll(held, 2 * planes, 1),
                                         jnp.where(group == 2, pltpu.roll(held, 3 * planes, 1), held)))
            top.append(spread)
        rate_row = shock_speed(top, slope_x_row, slope_z_row)
        shock_ref[...] = height_ref[...] + dt * rate_row[:, 0:planes]
        slope_x = lane_tile(slope_x_row, width)
        slope_z = lane_tile(slope_z_row, width)
        rate = lane_tile(rate_row, width)
        ratio = lane_tile(rate_row / height_row, CHUNK)
        height = lane_tile(height_row, CHUNK)
        lane = lax.broadcasted_iota(jnp.int32, (columns, CHUNK), 1) % planes
        lane_in = lax.broadcasted_iota(jnp.int32, (1, CHUNK), 1)
        lane_out = lax.broadcasted_iota(jnp.int32, (1, width), 1)

        def body(k, carry):
            o = pl.multiple_of(k * CHUNK, CHUNK)
            rows_in = (first_row + (o + lane_in) // planes).astype(jnp.float32)
            spacing = stretch_factors(rows_in, total_rows)[1]
            rows_out = (first_row - PAD // planes + (o + lane_out) // planes).astype(jnp.float32)
            eta = stretch_factors(rows_out, total_rows)[0]
            xa = [qx_ref[c, :, pl.ds(o, CHUNK)] for c in range(6)]
            inverse, vel_x, vel_y, vel_z, stress, sound = kernel_primitives(xa)
            metric = STREAM_STEP * height_x * spacing
            fluxes = [xa[1], xa[1] * vel_x + stress, xa[2] * vel_x, xa[3] * vel_x,
                      (xa[4] + stress) * vel_x, xa[5] * vel_x]
            speed = (jnp.abs(vel_x) + sound) * metric
            div = []
            for c in range(6):
                flux = fluxes[c] * metric
                damped = speed * xa[c]
                for t in range(1, 4):
                    up, down = pair_terms(flux, damped, t)
                    pair_ref[c, 2 * t - 2] = up
                    pair_ref[c, 2 * t - 1] = down
                acc = SPEED_WEIGHTS[0] * damped[XPAD:XPAD + columns]
                for t in range(1, 4):
                    acc = acc + pair_ref[c, 2 * t - 2, pl.ds(XPAD + t, columns), :]
                    acc = acc + pair_ref[c, 2 * t - 1, pl.ds(XPAD - t, columns), :]
                div.append(acc)
            ya = [qy_ref[c, :, pl.ds(o, width)] for c in range(6)]
            inverse, vel_x, vel_y, vel_z, stress, sound = kernel_primitives(ya)
            scaled = -face_area * eta
            metric_x = scaled * slope_x
            metric_z = scaled * slope_z
            metric_t = scaled * rate
            contra = metric_t + metric_x * vel_x + face_area * vel_y + metric_z * vel_z
            fluxes = [ya[0] * contra, ya[1] * contra + metric_x * stress,
                      ya[2] * contra + face_area * stress, ya[3] * contra + metric_z * stress,
                      (ya[4] + stress) * contra - metric_t * stress, ya[5] * contra]
            speed = jnp.abs(contra) + sound * jnp.sqrt(
                metric_x * metric_x + face_area * face_area + metric_z * metric_z)
            for c in range(6):
                damped = speed * ya[c]
                acc = SPEED_WEIGHTS[0] * damped
                for t in range(1, 4):
                    up, down = pair_terms(fluxes[c], damped, t)
                    acc = acc + pltpu.roll(up, (-planes * t) % width, 1) + pltpu.roll(down, planes * t, 1)
                div[c] = div[c] + acc[:, PAD:PAD + CHUNK]
            q = [v[:, PAD:PAD + CHUNK] for v in ya]
            inverse = inverse[:, PAD:PAD + CHUNK]
            vel_z = vel_z[:, PAD:PAD + CHUNK]
            stress = stress[:, PAD:PAD + CHUNK]
            sound = sound[:, PAD:PAD + CHUNK]
            metric = STREAM_STEP * height * spacing
            fluxes = [q[3], q[1] * vel_z, q[2] * vel_z, q[3] * vel_z + stress,
                      (q[4] + stress) * vel_z, q[5] * vel_z]
            speed = (jnp.abs(vel_z) + sound) * metric
            for c in range(6):
                damped = speed * q[c]
                acc = SPEED_WEIGHTS[0] * damped
                for t in range(1, 4):
                    up, down = pair_terms(fluxes[c] * metric, damped, t)
                    up = jnp.where(lane < planes - t, pltpu.roll(up, CHUNK - t, 1),
                                   pltpu.roll(up, planes - t, 1))
                    down = jnp.where(lane >= t, pltpu.roll(down, t, 1),
                                     pltpu.roll(down, CHUNK - planes + t, 1))
                    acc = acc + up + down
                div[c] = div[c] + acc
            kelvin = stress * inverse
            balanced = CHARACTER_KELVIN / (jnp.exp(CHARACTER_KELVIN / kelvin) - 1.0)
            teller = stress / (LANDAU_TELLER * jnp.exp(
                WHITE_LAW_FACTOR * jnp.exp(-jnp.log(kelvin) / 3.0)))
            source = q[0] * (balanced - q[5] * inverse) * teller
            scale = 1.0 / (60.0 * (face_area * height * spacing))
            for c in range(6):
                change = -(div[c] * scale) - q[c] * ratio
                if c == 5:
                    change = change + source
                out_ref[c, :, pl.ds(o, CHUNK)] = q[c] + dt * change
            return carry

        lax.fori_loop(0, length // CHUNK, body, 0, unroll=True)

    return kernel


def update(state, xlo, xhi, below, above, geo, top_before, top_last, height, targets, planes, total_rows,
           dt):
    columns = state.shape[1]
    length = state.shape[2]
    kern = make_kernel(columns, length, planes, total_rows, dt, targets)
    vmem = pl.BlockSpec(memory_space=pltpu.VMEM)
    return pl.pallas_call(
        kern,
        out_shape=(
            jax.ShapeDtypeStruct((6, columns, length), jnp.float32),
            jax.ShapeDtypeStruct((columns, planes), jnp.float32),
        ),
        in_specs=[vmem] * 9,
        out_specs=(vmem, vmem),
        scratch_shapes=[
            pltpu.VMEM((6, columns + 2 * XPAD, length), jnp.float32),
            pltpu.VMEM((6, columns, length + 2 * PAD), jnp.float32),
            pltpu.VMEM((6, 6, columns + 2 * XPAD, CHUNK), jnp.float32),
        ],
    )(state, xlo, xhi, below, above, geo, top_before, top_last, height)


def shifted(block, axis, forward, cyclic=False):
    count = lax.axis_size(axis)
    pairs = [(i, i + 1) for i in range(count - 1)]
    if cyclic and count > 1:
        pairs.append((count - 1, 0))
    if not forward:
        pairs = [(target, source) for source, target in pairs]
    return lax.ppermute(block, axis, pairs)


def broadcast(array, axis, holders, fanouts):
    count = lax.axis_size(axis)
    index = lax.axis_index(axis)
    last = (array, array, [])
    for fanout in fanouts:
        if len(holders) >= count:
            break
        waiting = [i for i in range(count) if i not in holders]
        targets = jnp.zeros((), jnp.bool_)
        arrived = array
        reached = []
        for _ in range(fanout):
            pairs = list(zip(holders, waiting))
            waiting = waiting[len(pairs) :]
            if not pairs:
                break
            received = lax.ppermute(array, axis, pairs)
            last = (arrived, received, [target for _, target in pairs])
            hit = jnp.zeros((), jnp.bool_)
            for _, target in pairs:
                hit = hit | (index == target)
            arrived = jnp.where(hit, received, arrived)
            reached = reached + [target for _, target in pairs]
        array = arrived
        holders = holders + reached
    return last


def zshift(values, offset, planes):
    length = values.shape[-1]
    plane_at = jnp.arange(length, dtype=jnp.int32) % planes
    if offset > 0:
        return jnp.where(
            plane_at >= offset,
            jnp.roll(values, offset, axis=-1),
            jnp.roll(values, offset - planes, axis=-1),
        )
    return jnp.where(
        plane_at < planes + offset,
        jnp.roll(values, offset, axis=-1),
        jnp.roll(values, offset + planes, axis=-1),
    )


def primitives(conserved):
    specific_volume_inverse = conserved[0]
    vel_x = conserved[1] / specific_volume_inverse
    vel_y = conserved[2] / specific_volume_inverse
    vel_z = conserved[3] / specific_volume_inverse
    thermodynamic_stress = (HEAT_RATIO - 1.0) * (
        conserved[4]
        - 0.5 * (conserved[1] * vel_x + conserved[2] * vel_y + conserved[3] * vel_z)
        - conserved[5]
    )
    sound_speed = jnp.sqrt(HEAT_RATIO * thermodynamic_stress / specific_volume_inverse)
    return (specific_volume_inverse, vel_x, vel_y, vel_z, thermodynamic_stress, sound_speed)


def slopes(height_ext, planes):
    columns = height_ext.shape[0] - 6
    slope_x = (
        height_ext[1 : columns + 1]
        - 8.0 * height_ext[2 : columns + 2]
        + 8.0 * height_ext[4 : columns + 4]
        - height_ext[5 : columns + 5]
    ) / (12.0 * STREAM_STEP)
    height = height_ext[3 : columns + 3]
    slope_z = (
        zshift(height, 2, planes)
        - 8.0 * zshift(height, 1, planes)
        + 8.0 * zshift(height, -1, planes)
        - zshift(height, -2, planes)
    ) / (12.0 * SPAN_STEP)
    return (slope_x, slope_z)


def shock_speed(top_row, slope_x, slope_z):
    specific_volume_inverse, vel_x, vel_y, vel_z, thermodynamic_stress, sound_speed = primitives(
        top_row
    )
    tilt_norm = jnp.sqrt(1.0 + slope_x * slope_x + slope_z * slope_z)
    normal = (vel_y - vel_x * slope_x - vel_z * slope_z) / tilt_norm
    sine_sq = slope_x * slope_x / (tilt_norm * tilt_norm)
    jump_pressure = FREE_PRESSURE * (
        1.0 + 2.0 * HEAT_RATIO / (HEAT_RATIO + 1.0) * (FREE_MACH * FREE_MACH * sine_sq - 1.0)
    )
    return tilt_norm * (
        normal + (jump_pressure - thermodynamic_stress) / (specific_volume_inverse * sound_speed)
    )


def wall_ghosts(first_rows, blowing, planes):
    mirror = jnp.concatenate(
        [
            first_rows[..., 2 * planes : 3 * planes],
            first_rows[..., planes : 2 * planes],
            first_rows[..., 0:planes],
        ],
        axis=-1,
    )
    blown_y = 2.0 * jnp.tile(blowing, (1, 3)) - mirror[2]
    stagnation_enthalpy_sum = (
        mirror[4] + 0.5 * (blown_y * blown_y - mirror[2] * mirror[2]) / mirror[0]
    )
    return jnp.stack([mirror[0], mirror[1], blown_y, mirror[3], stagnation_enthalpy_sum, mirror[5]])


def wall_flux(wall_segment, segment_level, blow_table):
    seg_hit = wall_segment[:, None] == jnp.arange(segment_level.shape[0], dtype=jnp.int32)[None, :]
    levels = jnp.sum(jnp.where(seg_hit, segment_level[None, :], 0), axis=1)
    level_hit = levels[:, None] == jnp.arange(blow_table.shape[0], dtype=jnp.int32)[None, :]
    return jnp.sum(jnp.where(level_hit[:, :, None], blow_table[None, :, :], 0.0), axis=1)


def replicate_lanes(small, planes):
    pick = (
        jnp.arange(LANES, dtype=jnp.int32)[None, :] % planes
        == jnp.arange(planes, dtype=jnp.int32)[:, None]
    ).astype(jnp.float32)
    return jnp.dot(small, pick, precision=lax.Precision.HIGHEST, preferred_element_type=jnp.float32)


def shards(state, shock_height, wall_segment, segment_level, blow_table):
    planes = blow_table.shape[1]
    columns = state.shape[1]
    length = state.shape[2]
    row_count = length // planes
    col_devs = lax.axis_size("gx")
    row_devs = lax.axis_size("gy")
    col_dev = lax.axis_index("gx")
    row_dev = lax.axis_index("gy")
    total_rows = row_count * row_devs
    band = HALO * planes

    def pack(cols, heights):
        extra = jnp.zeros((1, HALO, length), jnp.float32)
        extra = lax.dynamic_update_slice(extra, heights[None], (0, 0, 0))
        return jnp.concatenate([cols, extra], axis=0)

    from_low = shifted(pack(state[:, columns - HALO :], shock_height[columns - HALO :]), "gx", True)
    from_high = shifted(pack(state[:, :HALO], shock_height[:HALO]), "gx", False)
    plane_lane = jnp.arange(PAD, dtype=jnp.int32)[None, None, :]
    top_block = state[..., length - PAD :]
    below = shifted(top_block, "gy", True, cyclic=True)
    above = shifted(jnp.where(plane_lane < band, state[..., :PAD], top_block), "gy", False)
    low_height = jnp.where(
        col_dev == 0, jnp.broadcast_to(shock_height[:1], (HALO, planes)), from_low[6, :, :planes]
    )
    high_height = jnp.where(
        col_dev == col_devs - 1,
        jnp.broadcast_to(shock_height[columns - 1 :], (HALO, planes)),
        from_high[6, :, :planes],
    )
    height_ext = jnp.concatenate([low_height, shock_height, high_height], axis=0)
    slope_x, slope_z = slopes(height_ext, planes)

    top_seed = jnp.where(row_dev == row_devs - 1, top_block, jnp.where(row_dev == 0, below, above))
    top_seed, below, above = lax.optimization_barrier((top_seed, below, above))
    seeded = sorted({row_devs - 1, 0, max(row_devs - 2, 0)}, reverse=True)
    top_before, top_last, last_targets = broadcast(top_seed, "gy", seeded, (1, 2, 1, 1, 1))

    blowing = wall_flux(wall_segment, segment_level, blow_table)

    height = shock_height
    height_x = jnp.concatenate(
        [
            jnp.broadcast_to(height_ext[:1], (XPAD - HALO, planes)),
            height_ext,
            jnp.broadcast_to(height_ext[-1:], (XPAD - HALO, planes)),
        ],
        axis=0,
    )
    small = jnp.concatenate([height_x, slope_x, slope_z, height, blowing], axis=0)
    geo = replicate_lanes(small, planes)
    state_new, shock_new = update(
        state,
        from_low,
        from_high,
        below,
        above,
        geo,
        top_before,
        top_last,
        shock_height,
        tuple(last_targets),
        planes,
        total_rows,
        COURANT / total_rows,
    )
    return (state_new, shock_new)


def solution(mesh):
    in_specs = (P(None, "gx", "gy"), P("gx", None), P("gx"), P(), P())
    out_specs = (P(None, "gx", "gy"), P("gx", None))
    return jax.shard_map(shards, mesh=mesh, in_specs=in_specs, out_specs=out_specs, check_vma=False)
```

```python
import math

import jax
import jax.numpy as jnp
from jax import lax
from jax.experimental import pallas as pl
from jax.experimental.pallas import tpu as pltpu
from jax.sharding import PartitionSpec as P

HEAT_RATIO = 1.4
STREAM_STEP = 0.05
SPAN_STEP = 0.05
STRETCH_RATE = 2.0
CHARACTER_KELVIN = 3.0
WHITE_LAW_FACTOR = 1.0
LANDAU_TELLER = 0.002
FREE_PRESSURE = 0.1
FREE_MACH = 6.0
COURANT = 0.05

FLUX_WEIGHTS = (45.0, -9.0, 1.0)
SPEED_WEIGHTS = (20.0, -15.0, 6.0, -1.0)
CHUNK = 384
PAD = 128
HALO = 3
XPAD = 8
LANES = 128


def kernel_primitives(q):
    inverse = 1.0 / q[0]
    vel_x = q[1] * inverse
    vel_y = q[2] * inverse
    vel_z = q[3] * inverse
    stress = (HEAT_RATIO - 1.0) * (q[4] - 0.5 * (q[1] * vel_x + q[2] * vel_y + q[3] * vel_z) - q[5])
    sound = jnp.sqrt(HEAT_RATIO * stress * inverse)
    return inverse, vel_x, vel_y, vel_z, stress, sound


def pair_terms(flux, damped, t):
    odd = FLUX_WEIGHTS[t - 1]
    even = SPEED_WEIGHTS[t]
    odd_part = flux if odd == 1.0 else odd * flux
    if even == -1.0:
        return odd_part - damped, -(odd_part + damped)
    even_part = even * damped
    return even_part + odd_part, even_part - odd_part


def lane_tile(values, width):
    return jnp.concatenate([values] * (width // values.shape[-1]), axis=-1)


def stretch_factors(rows, total_rows):
    growth = jnp.exp(STRETCH_RATE * (rows + 0.5) / total_rows)
    denominator = math.exp(STRETCH_RATE) - 1.0
    return (growth - 1.0) / denominator, STRETCH_RATE * growth / (total_rows * denominator)


def make_kernel(columns, length, planes, total_rows, dt, targets):
    width = CHUNK + 2 * PAD
    face_area = STREAM_STEP * SPAN_STEP
    xrows = columns + 2 * XPAD

    def kernel(state_ref, xlo_ref, xhi_ref, below_ref, above_ref, geo_ref, before_ref, last_ref,
               height_ref, out_ref, shock_ref, qx_ref, qy_ref, pair_ref):
        col_dev = lax.axis_index("gx")
        first_row = lax.axis_index("gy") * (length // planes)
        for c in range(6):
            qx_ref[c, 0:XPAD, :] = state_ref[c, 0:XPAD, :]
            qx_ref[c, XPAD:XPAD + columns, :] = state_ref[c]
            qx_ref[c, XPAD + columns:, :] = state_ref[c, columns - XPAD:, :]
            qx_ref[c, XPAD - HALO:XPAD, :] = xlo_ref[c]
            qx_ref[c, XPAD + columns:XPAD + columns + HALO, :] = xhi_ref[c]
            qy_ref[c, :, 0:PAD] = below_ref[c]
            qy_ref[c, :, PAD:PAD + length] = state_ref[c]
            qy_ref[c, :, PAD + length:] = above_ref[c]

        @pl.when(col_dev == 0)
        def _():
            for c in range(6):
                qx_ref[c, XPAD - HALO:XPAD, :] = jnp.broadcast_to(state_ref[c, 0:1, :], (HALO, length))

        @pl.when(col_dev == lax.axis_size("gx") - 1)
        def _():
            for c in range(6):
                qx_ref[c, XPAD + columns:XPAD + columns + HALO, :] = jnp.broadcast_to(
                    state_ref[c, columns - 1:columns, :], (HALO, length))

        height_x = lane_tile(geo_ref[0:xrows, :], CHUNK)
        slope_x_row = geo_ref[xrows:xrows + columns, :]
        slope_z_row = geo_ref[xrows + columns:xrows + 2 * columns, :]
        height_row = geo_ref[xrows + 2 * columns:xrows + 3 * columns, :]
        group = lax.broadcasted_iota(jnp.int32, (columns, LANES), 1) // planes

        @pl.when(lax.axis_index("gy") == 0)
        def _():
            mirror = []
            for c in range(6):
                rows = state_ref[c, :, 0:LANES]
                mirror.append(jnp.where(group == 2, pltpu.roll(rows, planes, 1),
                                        pltpu.roll(rows, 3 * planes, 1)))
            blown_y = 2.0 * geo_ref[xrows + 3 * columns:xrows + 4 * columns, :] - mirror[2]
            energy = mirror[4] + 0.5 * (blown_y * blown_y - mirror[2] * mirror[2]) / mirror[0]
            ghosts = [mirror[0], mirror[1], blown_y, mirror[3], energy, mirror[5]]
            for c in range(6):
                qy_ref[c, :, 0:PAD] = ghosts[c]

        @pl.when(lax.axis_index("gy") == lax.axis_size("gy") - 1)
        def _():
            for c in range(6):
                rows = state_ref[c, :, length - LANES:]
                qy_ref[c, :, PAD + length:] = jnp.where(
                    group == 0, pltpu.roll(rows, planes, 1),
                    jnp.where(group == 1, pltpu.roll(rows, 2 * planes, 1),
                              jnp.where(group == 2, pltpu.roll(rows, 3 * planes, 1), rows)))
        top = []
        row_dev = lax.axis_index("gy")
        hit = jnp.zeros((columns, LANES), jnp.bool_)
        for target in targets:
            hit = hit | (row_dev == target)
        for c in range(6):
            held = jnp.where(hit, last_ref[c], before_ref[c])
            spread = jnp.where(group == 0, pltpu.roll(held, planes, 1),
                               jnp.where(group == 1, pltpu.roll(held, 2 * planes, 1),
                                         jnp.where(group == 2, pltpu.roll(held, 3 * planes, 1), held)))
            top.append(spread)
        rate_row = shock_speed(top, slope_x_row, slope_z_row)
        shock_ref[...] = height_ref[...] + dt * rate_row[:, 0:planes]
        slope_x = lane_tile(slope_x_row, width)
        slope_z = lane_tile(slope_z_row, width)
        rate = lane_tile(rate_row, width)
        ratio = lane_tile(rate_row / height_row, CHUNK)
        height = lane_tile(height_row, CHUNK)
        lane = lax.broadcasted_iota(jnp.int32, (columns, CHUNK), 1) % planes
        lane_in = lax.broadcasted_iota(jnp.int32, (1, CHUNK), 1)
        lane_out = lax.broadcasted_iota(jnp.int32, (1, width), 1)

        def body(k, carry):
            o = pl.multiple_of(k * CHUNK, CHUNK)
            rows_in = (first_row + (o + lane_in) // planes).astype(jnp.float32)
            spacing = stretch_factors(rows_in, total_rows)[1]
            rows_out = (first_row - PAD // planes + (o + lane_out) // planes).astype(jnp.float32)
            eta = stretch_factors(rows_out, total_rows)[0]
            xa = [qx_ref[c, :, pl.ds(o, CHUNK)] for c in range(6)]
            inverse, vel_x, vel_y, vel_z, stress, sound = kernel_primitives(xa)
            metric = STREAM_STEP * height_x * spacing
            fluxes = [xa[1], xa[1] * vel_x + stress, xa[2] * vel_x, xa[3] * vel_x,
                      (xa[4] + stress) * vel_x, xa[5] * vel_x]
            speed = (jnp.abs(vel_x) + sound) * metric
            div = []
            for c in range(6):
                flux = fluxes[c] * metric
                damped = speed * xa[c]
                for t in range(1, 4):
                    up, down = pair_terms(flux, damped, t)
                    pair_ref[c, 2 * t - 2] = up
                    pair_ref[c, 2 * t - 1] = down
                acc = SPEED_WEIGHTS[0] * damped[XPAD:XPAD + columns]
                for t in range(1, 4):
                    acc = acc + pair_ref[c, 2 * t - 2, pl.ds(XPAD + t, columns), :]
                    acc = acc + pair_ref[c, 2 * t - 1, pl.ds(XPAD - t, columns), :]
                div.append(acc)
            ya = [qy_ref[c, :, pl.ds(o, width)] for c in range(6)]
            inverse, vel_x, vel_y, vel_z, stress, sound = kernel_primitives(ya)
            scaled = -face_area * eta
            metric_x = scaled * slope_x
            metric_z = scaled * slope_z
            metric_t = scaled * rate
            contra = metric_t + metric_x * vel_x + face_area * vel_y + metric_z * vel_z
            fluxes = [ya[0] * contra, ya[1] * contra + metric_x * stress,
                      ya[2] * contra + face_area * stress, ya[3] * contra + metric_z * stress,
                      (ya[4] + stress) * contra - metric_t * stress, ya[5] * contra]
            speed = jnp.abs(contra) + sound * jnp.sqrt(
                metric_x * metric_x + face_area * face_area + metric_z * metric_z)
            for c in range(6):
                damped = speed * ya[c]
                acc = SPEED_WEIGHTS[0] * damped
                for t in range(1, 4):
                    up, down = pair_terms(fluxes[c], damped, t)
                    acc = acc + pltpu.roll(up, (-planes * t) % width, 1) + pltpu.roll(down, planes * t, 1)
                div[c] = div[c] + acc[:, PAD:PAD + CHUNK]
            q = [v[:, PAD:PAD + CHUNK] for v in ya]
            inverse = inverse[:, PAD:PAD + CHUNK]
            vel_z = vel_z[:, PAD:PAD + CHUNK]
            stress = stress[:, PAD:PAD + CHUNK]
            sound = sound[:, PAD:PAD + CHUNK]
            metric = STREAM_STEP * height * spacing
            fluxes = [q[3], q[1] * vel_z, q[2] * vel_z, q[3] * vel_z + stress,
                      (q[4] + stress) * vel_z, q[5] * vel_z]
            speed = (jnp.abs(vel_z) + sound) * metric
            for c in range(6):
                damped = speed * q[c]
                acc = SPEED_WEIGHTS[0] * damped
                for t in range(1, 4):
                    up, down = pair_terms(fluxes[c] * metric, damped, t)
                    up = jnp.where(lane < planes - t, pltpu.roll(up, CHUNK - t, 1),
                                   pltpu.roll(up, planes - t, 1))
                    down = jnp.where(lane >= t, pltpu.roll(down, t, 1),
                                     pltpu.roll(down, CHUNK - planes + t, 1))
                    acc = acc + up + down
                div[c] = div[c] + acc
            kelvin = stress * inverse
            balanced = CHARACTER_KELVIN / (jnp.exp(CHARACTER_KELVIN / kelvin) - 1.0)
            teller = stress / (LANDAU_TELLER * jnp.exp(
                WHITE_LAW_FACTOR * jnp.exp(-jnp.log(kelvin) / 3.0)))
            source = q[0] * (balanced - q[5] * inverse) * teller
            scale = 1.0 / (60.0 * (face_area * height * spacing))
            for c in range(6):
                change = -(div[c] * scale) - q[c] * ratio
                if c == 5:
                    change = change + source
                out_ref[c, :, pl.ds(o, CHUNK)] = q[c] + dt * change
            return carry

        lax.fori_loop(0, length // CHUNK, body, 0, unroll=True)

    return kernel


def update(state, xlo, xhi, below, above, geo, top_before, top_last, height, targets, planes, total_rows,
           dt):
    columns = state.shape[1]
    length = state.shape[2]
    kern = make_kernel(columns, length, planes, total_rows, dt, targets)
    vmem = pl.BlockSpec(memory_space=pltpu.VMEM)
    return pl.pallas_call(
        kern,
        out_shape=(
            jax.ShapeDtypeStruct((6, columns, length), jnp.float32),
            jax.ShapeDtypeStruct((columns, planes), jnp.float32),
        ),
        in_specs=[vmem] * 9,
        out_specs=(vmem, vmem),
        scratch_shapes=[
            pltpu.VMEM((6, columns + 2 * XPAD, length), jnp.float32),
            pltpu.VMEM((6, columns, length + 2 * PAD), jnp.float32),
            pltpu.VMEM((6, 6, columns + 2 * XPAD, CHUNK), jnp.float32),
        ],
    )(state, xlo, xhi, below, above, geo, top_before, top_last, height)


def shifted(block, axis, forward, cyclic=False):
    count = lax.axis_size(axis)
    pairs = [(i, i + 1) for i in range(count - 1)]
    if cyclic and count > 1:
        pairs.append((count - 1, 0))
    if not forward:
        pairs = [(target, source) for source, target in pairs]
    return lax.ppermute(block, axis, pairs)


def broadcast(array, axis, holders, fanouts):
    count = lax.axis_size(axis)
    index = lax.axis_index(axis)
    last = (array, array, [])
    for fanout in fanouts:
        if len(holders) >= count:
            break
        waiting = [i for i in range(count) if i not in holders]
        targets = jnp.zeros((), jnp.bool_)
        arrived = array
        reached = []
        for _ in range(fanout):
            pairs = list(zip(holders, waiting))
            waiting = waiting[len(pairs) :]
            if not pairs:
                break
            received = lax.ppermute(array, axis, pairs)
            last = (arrived, received, [target for _, target in pairs])
            hit = jnp.zeros((), jnp.bool_)
            for _, target in pairs:
                hit = hit | (index == target)
            arrived = jnp.where(hit, received, arrived)
            reached = reached + [target for _, target in pairs]
        array = arrived
        holders = holders + reached
    return last


def zshift(values, offset, planes):
    length = values.shape[-1]
    plane_at = jnp.arange(length, dtype=jnp.int32) % planes
    if offset > 0:
        return jnp.where(
            plane_at >= offset,
            jnp.roll(values, offset, axis=-1),
            jnp.roll(values, offset - planes, axis=-1),
        )
    return jnp.where(
        plane_at < planes + offset,
        jnp.roll(values, offset, axis=-1),
        jnp.roll(values, offset + planes, axis=-1),
    )


def primitives(conserved):
    specific_volume_inverse = conserved[0]
    vel_x = conserved[1] / specific_volume_inverse
    vel_y = conserved[2] / specific_volume_inverse
    vel_z = conserved[3] / specific_volume_inverse
    thermodynamic_stress = (HEAT_RATIO - 1.0) * (
        conserved[4]
        - 0.5 * (conserved[1] * vel_x + conserved[2] * vel_y + conserved[3] * vel_z)
        - conserved[5]
    )
    sound_speed = jnp.sqrt(HEAT_RATIO * thermodynamic_stress / specific_volume_inverse)
    return (specific_volume_inverse, vel_x, vel_y, vel_z, thermodynamic_stress, sound_speed)


def slopes(height_ext, planes):
    columns = height_ext.shape[0] - 6
    slope_x = (
        height_ext[1 : columns + 1]
        - 8.0 * height_ext[2 : columns + 2]
        + 8.0 * height_ext[4 : columns + 4]
        - height_ext[5 : columns + 5]
    ) / (12.0 * STREAM_STEP)
    height = height_ext[3 : columns + 3]
    slope_z = (
        zshift(height, 2, planes)
        - 8.0 * zshift(height, 1, planes)
        + 8.0 * zshift(height, -1, planes)
        - zshift(height, -2, planes)
    ) / (12.0 * SPAN_STEP)
    return (slope_x, slope_z)


def shock_speed(top_row, slope_x, slope_z):
    specific_volume_inverse, vel_x, vel_y, vel_z, thermodynamic_stress, sound_speed = primitives(
        top_row
    )
    tilt_norm = jnp.sqrt(1.0 + slope_x * slope_x + slope_z * slope_z)
    normal = (vel_y - vel_x * slope_x - vel_z * slope_z) / tilt_norm
    sine_sq = slope_x * slope_x / (tilt_norm * tilt_norm)
    jump_pressure = FREE_PRESSURE * (
        1.0 + 2.0 * HEAT_RATIO / (HEAT_RATIO + 1.0) * (FREE_MACH * FREE_MACH * sine_sq - 1.0)
    )
    return tilt_norm * (
        normal + (jump_pressure - thermodynamic_stress) / (specific_volume_inverse * sound_speed)
    )


def wall_ghosts(first_rows, blowing, planes):
    mirror = jnp.concatenate(
        [
            first_rows[..., 2 * planes : 3 * planes],
            first_rows[..., planes : 2 * planes],
            first_rows[..., 0:planes],
        ],
        axis=-1,
    )
    blown_y = 2.0 * jnp.tile(blowing, (1, 3)) - mirror[2]
    stagnation_enthalpy_sum = (
        mirror[4] + 0.5 * (blown_y * blown_y - mirror[2] * mirror[2]) / mirror[0]
    )
    return jnp.stack([mirror[0], mirror[1], blown_y, mirror[3], stagnation_enthalpy_sum, mirror[5]])


def wall_flux(wall_segment, segment_level, blow_table):
    seg_hit = wall_segment[:, None] == jnp.arange(segment_level.shape[0], dtype=jnp.int32)[None, :]
    levels = jnp.sum(jnp.where(seg_hit, segment_level[None, :], 0), axis=1)
    level_hit = levels[:, None] == jnp.arange(blow_table.shape[0], dtype=jnp.int32)[None, :]
    return jnp.sum(jnp.where(level_hit[:, :, None], blow_table[None, :, :], 0.0), axis=1)


def replicate_lanes(small, planes):
    pick = (
        jnp.arange(LANES, dtype=jnp.int32)[None, :] % planes
        == jnp.arange(planes, dtype=jnp.int32)[:, None]
    ).astype(jnp.float32)
    return jnp.dot(small, pick, precision=lax.Precision.HIGHEST, preferred_element_type=jnp.float32)


def shards(state, shock_height, wall_segment, segment_level, blow_table):
    planes = blow_table.shape[1]
    columns = state.shape[1]
    length = state.shape[2]
    row_count = length // planes
    col_devs = lax.axis_size("gx")
    row_devs = lax.axis_size("gy")
    col_dev = lax.axis_index("gx")
    row_dev = lax.axis_index("gy")
    total_rows = row_count * row_devs
    band = HALO * planes

    def pack(cols, heights):
        extra = jnp.zeros((1, HALO, length), jnp.float32)
        extra = lax.dynamic_update_slice(extra, heights[None], (0, 0, 0))
        return jnp.concatenate([cols, extra], axis=0)

    from_low = shifted(pack(state[:, columns - HALO :], shock_height[columns - HALO :]), "gx", True)
    from_high = shifted(pack(state[:, :HALO], shock_height[:HALO]), "gx", False)
    plane_lane = jnp.arange(PAD, dtype=jnp.int32)[None, None, :]
    top_block = state[..., length - PAD :]
    below = shifted(top_block, "gy", True, cyclic=True)
    above = shifted(jnp.where(plane_lane < band, state[..., :PAD], top_block), "gy", False)
    low_height = jnp.where(
        col_dev == 0, jnp.broadcast_to(shock_height[:1], (HALO, planes)), from_low[6, :, :planes]
    )
    high_height = jnp.where(
        col_dev == col_devs - 1,
        jnp.broadcast_to(shock_height[columns - 1 :], (HALO, planes)),
        from_high[6, :, :planes],
    )
    height_ext = jnp.concatenate([low_height, shock_height, high_height], axis=0)
    slope_x, slope_z = slopes(height_ext, planes)

    top_seed = jnp.where(row_dev == row_devs - 1, top_block, jnp.where(row_dev == 0, below, above))
    top_seed, below, above = lax.optimization_barrier((top_seed, below, above))
    seeded = sorted({row_devs - 1, 0, max(row_devs - 2, 0)}, reverse=True)
    top_before, top_last, last_targets = broadcast(top_seed, "gy", seeded, (1, 2, 1, 1, 1))

    blowing = wall_flux(wall_segment, segment_level, blow_table)

    height = shock_height
    height_x = jnp.concatenate(
        [
            jnp.broadcast_to(height_ext[:1], (XPAD - HALO, planes)),
            height_ext,
            jnp.broadcast_to(height_ext[-1:], (XPAD - HALO, planes)),
        ],
        axis=0,
    )
    small = jnp.concatenate([height_x, slope_x, slope_z, height, blowing], axis=0)
    geo = replicate_lanes(small, planes)
    state_new, shock_new = update(
        state,
        from_low,
        from_high,
        below,
        above,
        geo,
        top_before,
        top_last,
        shock_height,
        tuple(last_targets),
        planes,
        total_rows,
        COURANT / total_rows,
    )
    return (state_new, shock_new)


def solution(mesh):
    in_specs = (P(None, "gx", "gy"), P("gx", None), P("gx"), P(), P())
    out_specs = (P(None, "gx", "gy"), P("gx", None))
    return jax.shard_map(shards, mesh=mesh, in_specs=in_specs, out_specs=out_specs, check_vma=False)
```
